32 devices in a mesh: rep: 4 (over z), fsdp: 4 (over x, core), ctx: 2 (over y).
Axes of the slice: x: 2, y: 2, z: 4, core: 2. Of those that a mesh axis runs over, the one named last changes fastest.
Arguments:
- tokens: bfloat16 [16, 1024, 1024], P(('rep', 'fsdp'), 'ctx'), may hold values from -6 to 6
- initial_layer_values: bfloat16 [16, 1024, 1024], P(('rep', 'fsdp'), 'ctx'), may hold values from -6 to 6
- cotangent: bfloat16 [16, 1024, 1024], P(('rep', 'fsdp'), 'ctx'), may hold values from -6 to 6
- lengths: int32 [16], P(('rep', 'fsdp')), may hold values from 256 to 1024, as said below
- w_query: bfloat16 [1024, 1024], P(('fsdp', 'ctx')), may hold values from -0.1875 to 0.1875
- w_key: bfloat16 [1024, 1024], P(('fsdp', 'ctx')), may hold values from -0.1875 to 0.1875
- w_value: bfloat16 [1024, 1024], P(('fsdp', 'ctx')), may hold values from -0.1875 to 0.1875
- w_out: bfloat16 [1024, 1024], P(('fsdp', 'ctx')), may hold values from -1.5 to 1.5
- w_gate: bfloat16 [1024, 2816], P(('fsdp', 'ctx')), may hold values from -0.1875 to 0.1875
- w_up: bfloat16 [1024, 2816], P(('fsdp', 'ctx')), may hold values from -0.1875 to 0.1875
- w_down: bfloat16 [2816, 1024], P(('fsdp', 'ctx')), may hold values from -0.109375 to 0.109375
- gain_attn: bfloat16 [1024], P(('fsdp', 'ctx')), may hold values from 0.099609375 to 1.8984375
- gain_mlp: bfloat16 [1024], P(('fsdp', 'ctx')), may hold values from 0.099609375 to 1.8984375
Outputs:
- output: bfloat16 [16, 1024, 1024], P(('rep', 'fsdp'), 'ctx')
- d_tokens: float32 [16, 1024, 1024], P(('rep', 'fsdp'), 'ctx')
- d_first: float32 [16, 1024, 1024], P(('rep', 'fsdp'), 'ctx')
- grad_query: float32 [1024, 1024], P(('fsdp', 'ctx'))
- grad_key: float32 [1024, 1024], P(('fsdp', 'ctx'))
- grad_value: float32 [1024, 1024], P(('fsdp', 'ctx'))
- grad_out: float32 [1024, 1024], P(('fsdp', 'ctx'))
- grad_gate: float32 [1024, 2816], P(('fsdp', 'ctx'))
- grad_up: float32 [1024, 2816], P(('fsdp', 'ctx'))
- grad_down: float32 [2816, 1024], P(('fsdp', 'ctx'))
- grad_gain_attn: float32 [1024], P(('fsdp', 'ctx'))
- grad_gain_mlp: float32 [1024], P(('fsdp', 'ctx'))
The draws below stay inside these ranges and needn't reach their ends.
Inputs may be any that keep to these rules, and one draw needn't show every extreme that they name: Slot s holds one sequence at positions below lengths[s]; the rest of the slot is padding. Some slot is full and some slot holds a quarter of 1024.
All inputs are finite; a program needn't handle non-finite values.
Results may differ from the reference program's by a relative error of at most 0.019.
Values may be sent and summed in bfloat16 or wider, within the bound.
No kernel may reach another device: no remote copies, remote signals or barrier semaphores. Data moves between devices by JAX's collectives and lax.ppermute only.
A program may use at most 320 MiB of HBM per device.

```python
import math
import jax
import jax.numpy as jnp
from jax import lax

MODEL_DIM = 1024
HEADS = 16
HEAD_DIM = 64
FF = 2816
SLOT_POSITIONS = 1024
SLOT_TOTAL = 16


def draw_lengths(key, part):
    key_lengths, key_selection = jax.random.split(key)
    sampled_lengths = jax.random.randint(key_lengths, (SLOT_TOTAL,), SLOT_POSITIONS // 4, SLOT_POSITIONS + 1)
    picked_slots = jax.random.randint(key_selection, (), 0, SLOT_TOTAL)
    slot_index = jnp.arange(SLOT_TOTAL)
    sampled_lengths = jnp.where(slot_index == picked_slots, SLOT_POSITIONS, sampled_lengths)
    sampled_lengths = jnp.where(slot_index == (picked_slots + 1) % SLOT_TOTAL, SLOT_POSITIONS // 4, sampled_lengths)
    return sampled_lengths.astype(jnp.int32)


def shard_levels(own_key, dims, cuts, least, largest):
    def one(dim, shards_of):
        steps = jax.random.uniform(jax.random.fold_in(jax.random.fold_in(own_key, 6), dim), (shards_of,), jnp.float32, least / len(cuts), largest / len(cuts))
        return jnp.repeat(jnp.exp(steps), dims[dim] // shards_of).reshape((-1,) + (1,) * (len(dims) - dim - 1))

    level = one(*cuts[0])
    for cut in cuts[1:]:
        level = level * one(*cut)
    return level


def scatter_about(key, extent, spread, most, cuts=(), kind=jnp.bfloat16):
    level = shard_levels(key, extent, cuts, -0.22, 0.18) if cuts else 1.0
    values = jax.random.normal(key, extent, jnp.float32) * spread * level
    return jnp.minimum(jnp.maximum(values, -most), most).astype(kind)


def setup_inputs(seed: int = 0) -> dict:
    streams_of = jax.random.split(jax.random.key(seed), 14)
    tokens = scatter_about(streams_of[0], (SLOT_TOTAL, SLOT_POSITIONS, MODEL_DIM), 1.0, 6.0, ((0, 16), (1, 2)))
    initial_layer_values = scatter_about(streams_of[1], (SLOT_TOTAL, SLOT_POSITIONS, MODEL_DIM), 1.0, 6.0, ((0, 16), (1, 2)))
    cotangent = scatter_about(streams_of[2], (SLOT_TOTAL, SLOT_POSITIONS, MODEL_DIM), 1.0, 6.0, ((0, 16), (1, 2)))
    lengths = draw_lengths(jax.random.fold_in(streams_of[13], 71), 0)
    w_query = scatter_about(streams_of[4], (MODEL_DIM, MODEL_DIM), MODEL_DIM ** -0.5, 0.1875, ((0, 8),))
    w_key = scatter_about(streams_of[5], (MODEL_DIM, MODEL_DIM), MODEL_DIM ** -0.5, 0.1875, ((0, 8),))
    w_value = scatter_about(streams_of[6], (MODEL_DIM, MODEL_DIM), MODEL_DIM ** -0.5, 0.1875, ((0, 8),))
    w_out = scatter_about(streams_of[7], (MODEL_DIM, MODEL_DIM), (MODEL_DIM // 64) ** -0.5, 1.5, ((0, 8),))
    w_gate = scatter_about(streams_of[8], (MODEL_DIM, FF), MODEL_DIM ** -0.5, 0.1875, ((0, 8),))
    w_up = scatter_about(streams_of[9], (MODEL_DIM, FF), MODEL_DIM ** -0.5, 0.1875, ((0, 8),))
    w_down = scatter_about(streams_of[10], (FF, MODEL_DIM), FF ** -0.5, 0.109375, ((0, 8),))
    gain_attn = jnp.clip(1.0 + 0.18 * jax.random.normal(streams_of[11], (MODEL_DIM,), jnp.float32), 0.099609375, 1.8984375).astype(jnp.bfloat16)
    gain_mlp = jnp.clip(1.0 + 0.18 * jax.random.normal(streams_of[12], (MODEL_DIM,), jnp.float32), 0.099609375, 1.8984375).astype(jnp.bfloat16)
    return {"tokens": tokens, "initial_layer_values": initial_layer_values, "cotangent": cotangent, "lengths": lengths, "w_query": w_query, "w_key": w_key, "w_value": w_value, "w_out": w_out, "w_gate": w_gate, "w_up": w_up, "w_down": w_down, "gain_attn": gain_attn, "gain_mlp": gain_mlp}


EPS = 1e-06
NEG = -1e+30
THETA = 10000.0

@jax.custom_vjp
def low(v):
    return lax.optimization_barrier(v.astype(jnp.bfloat16)).astype(jnp.float32)

@jax.custom_vjp
def low_back(v):
    return v

def low_keep(v):
    return (low(v), None)

def low_pass(kept, grad):
    return (grad,)

def back_keep(v):
    return (v, None)

def back_low(kept, grad):
    return (low(grad),)
low.defvjp(low_keep, low_pass)
low_back.defvjp(back_keep, back_low)

def rotate(field, positions, direction):
    head_width = field.shape[-1]
    half_width = head_width // 2
    frequency = THETA ** (-(jnp.arange(half_width, dtype=jnp.float32) * 2.0) / head_width)
    angles = positions.astype(jnp.float32)[:, None] * frequency[None, :]
    cosine = jnp.cos(angles)[:, None, :]
    sine_part = direction * jnp.sin(angles)[:, None, :]
    former = field[..., :half_width]
    latter = field[..., half_width:]
    return jnp.concatenate([former * cosine - latter * sine_part, latter * cosine + former * sine_part], axis=-1)

def rms_norm(values, gain):
    return values * lax.rsqrt(lax.optimization_barrier(jnp.mean(values * values, axis=-1, keepdims=True)) + EPS) * gain

def matmul(left, right):
    return jnp.einsum('bld,de->ble', left, right, precision=lax.Precision.HIGHEST)

def attention(queries, keys, values, lengths):
    n_slots, length, n_heads, head_width = queries.shape
    q_block = min(length, 512)
    n_blocks = length // q_block
    k_pos = jnp.arange(length)
    q_blocks = jnp.moveaxis(queries.reshape(n_slots, n_blocks, q_block, n_heads, head_width), 1, 0)
    starts = jnp.arange(n_blocks) * q_block

    @jax.checkpoint
    def rows_of(packed):
        q_rows, start = packed
        q_pos = start + jnp.arange(q_block)
        scores = jnp.einsum('sqhe,skhe->shqk', q_rows, keys, precision=lax.Precision.HIGHEST) * head_width ** (-0.5)
        causal = k_pos[None, None, None, :] <= q_pos[None, None, :, None]
        filled = k_pos[None, None, None, :] < lengths[:, None, None, None]
        scores = low_back(jnp.where(causal & filled, scores, NEG))
        probabilities = low(jax.nn.softmax(scores, axis=-1))
        return jnp.einsum('shqk,skhe->sqhe', probabilities, values, precision=lax.Precision.HIGHEST)
    mixture = lax.map(rows_of, (q_blocks, starts))
    return jnp.moveaxis(mixture, 0, 1).reshape(n_slots, length, n_heads, head_width)

def layer(params, inputs, first_values, lengths):
    w_query, w_key, w_value, w_out, w_gate, w_up, w_down, gain_attn, gain_mlp = params
    n_slots = inputs.shape[0]
    positions = jnp.arange(SLOT_POSITIONS)
    live_rows = positions[None, :] < lengths[:, None]
    head_shape = (n_slots, SLOT_POSITIONS, HEADS, HEAD_DIM)
    normed = low(rms_norm(inputs, gain_attn))
    queries = low(rotate(low_back(matmul(normed, w_query)).reshape(head_shape), positions, 1.0))
    keys = low(rotate(low_back(matmul(normed, w_key)).reshape(head_shape), positions, 1.0))
    values = low(low_back(0.5 * matmul(normed, w_value) + 0.5 * first_values)).reshape(head_shape)
    attended = low(low_back(attention(queries, keys, values, lengths))).reshape(n_slots, SLOT_POSITIONS, MODEL_DIM)
    residual = inputs + low_back(matmul(attended, w_out))
    normed_mlp = low(rms_norm(residual, gain_mlp))
    gate_proj = low_back(matmul(normed_mlp, w_gate))
    up_proj = low_back(matmul(normed_mlp, w_up))
    hidden = low(jax.nn.silu(gate_proj) * up_proj)
    final = residual + matmul(hidden, w_down)
    return jnp.where(live_rows[..., None], final, 0.0)

def reference(tokens, initial_layer_values, cotangent, lengths, w_query, w_key, w_value, w_out, w_gate, w_up, w_down, gain_attn, gain_mlp):
    params = tuple((weight.astype(jnp.float32) for weight in (w_query, w_key, w_value, w_out, w_gate, w_up, w_down, gain_attn, gain_mlp)))
    step_body = math.gcd(SLOT_TOTAL, max(1, 4096 // SLOT_POSITIONS))
    step_count = SLOT_TOTAL // step_body

    def split_slots(array):
        return array.reshape((step_count, step_body) + array.shape[1:])

    def one_step(totals, packed):
        slot_tokens, slot_first, slot_cot, slot_lengths = packed

        def forward(weights, inputs, first_values):
            return layer(weights, inputs, first_values, slot_lengths)
        result, pull = jax.vjp(forward, params, slot_tokens.astype(jnp.float32), slot_first.astype(jnp.float32))
        grad_params, grad_inputs, grad_first = pull(slot_cot.astype(jnp.float32))
        totals = jax.tree.map(lambda acc, term: acc + term, totals, grad_params)
        return (totals, (result.astype(jnp.bfloat16), grad_inputs, grad_first))
    start_grads = tuple((jnp.zeros_like(weight) for weight in params))
    grads, (layer_outputs, token_gradients, first_value_gradients) = lax.scan(one_step, start_grads, (split_slots(tokens), split_slots(initial_layer_values), split_slots(cotangent), split_slots(lengths)))
    query_gradient, key_gradient, value_gradient, output_gradient, gate_gradient, up_gradient, down_gradient, attention_gain_gradient, perceptron_gain_gradient = grads
    return (layer_outputs.reshape(SLOT_TOTAL, SLOT_POSITIONS, MODEL_DIM), token_gradients.reshape(SLOT_TOTAL, SLOT_POSITIONS, MODEL_DIM), first_value_gradients.reshape(SLOT_TOTAL, SLOT_POSITIONS, MODEL_DIM), query_gradient, key_gradient, value_gradient, output_gradient, gate_gradient, up_gradient, down_gradient, attention_gain_gradient, perceptron_gain_gradient)
```

```python
import jax
import jax.numpy as jnp
from jax import lax
from jax.sharding import PartitionSpec as P

HEADS = 16
HEAD_DIM = 64


EPS = 1e-06
NEG = -1e30
THETA = 10000.0
SCORE_CAP = 4194304


def rotate(field, positions, direction):
    head_width = field.shape[-1]
    half_width = head_width // 2
    frequency = THETA ** (-(jnp.arange(half_width, dtype=jnp.float32) * 2.0) / head_width)
    angles = positions.astype(jnp.float32)[:, None] * frequency[None, :]
    cosine = jnp.cos(angles)[:, None, :]
    sine_part = direction * jnp.sin(angles)[:, None, :]
    former = field[..., :half_width]
    latter = field[..., half_width:]
    return jnp.concatenate(
        [former * cosine - latter * sine_part, latter * cosine + former * sine_part], axis=-1
    )


def normalize(values, gain):
    inverse = lax.rsqrt(jnp.mean(values * values, axis=-1, keepdims=True) + EPS)
    return (values * inverse * gain, inverse)


def normalize_back(values, inverse, gain, upstream):
    unit_rows = values * inverse
    scaled = upstream * gain
    grad_gain = jnp.sum(upstream * unit_rows, axis=(0, 1))
    grad_values = inverse * (
        scaled - unit_rows * jnp.mean(scaled * unit_rows, axis=-1, keepdims=True)
    )
    return (grad_values, grad_gain)


def head_groups(n_slots, q_len, n_heads, k_len):
    q_block = min(q_len, 512)
    per_group = max(1, min(n_heads, SCORE_CAP // (n_slots * q_block * k_len)))
    while n_heads % per_group:
        per_group = per_group - 1
    return (q_block, per_group)


def split_heads(packed, n_groups):
    n_slots, length, n_heads, head_width = packed.shape
    return jnp.moveaxis(
        packed.reshape(n_slots, length, n_groups, n_heads // n_groups, head_width), 2, 0
    )


def join_heads(grouped):
    n_groups, n_slots, length, per_group, head_width = grouped.shape
    return jnp.moveaxis(grouped, 0, 2).reshape(n_slots, length, n_groups * per_group, head_width)


def score_block(q_rows, k_rows, q_pos, k_pos, lengths):
    products = jnp.einsum(
        "sqhe,skhe->shqk", q_rows, k_rows, preferred_element_type=jnp.float32
    ) * q_rows.shape[-1] ** (-0.5)
    causal = (k_pos[None, None, None, :] <= q_pos[None, None, :, None]) & (
        k_pos[None, None, None, :] >= 0
    )
    filled = k_pos[None, None, None, :] < lengths[:, None, None, None]
    return jnp.where(causal & filled, products, NEG)


def attend_forward(queries, keys, values, q_pos, k_pos, lengths):
    n_slots, q_len, n_heads, head_width = queries.shape
    q_block, per_group = head_groups(n_slots, q_len, n_heads, keys.shape[1])
    n_groups = n_heads // per_group
    n_blocks = q_len // q_block
    pos_blocks = q_pos.reshape(n_blocks, q_block)

    def one_group(packed):
        q_group, k_group, v_group = packed
        q_blocks = jnp.moveaxis(
            q_group.reshape(n_slots, n_blocks, q_block, per_group, head_width), 1, 0
        )

        def one_block(streams):
            q_rows, pos_rows = streams
            scores = score_block(q_rows, k_group, pos_rows, k_pos, lengths)
            highest = jnp.max(scores, axis=-1, keepdims=True)
            exponent = jnp.exp(scores - highest)
            totals = jnp.sum(exponent, axis=-1, keepdims=True)
            probabilities = (exponent / totals).astype(jnp.bfloat16)
            mixture = jnp.einsum(
                "shqk,skhe->sqhe", probabilities, v_group, preferred_element_type=jnp.float32
            )
            return (mixture, (highest + jnp.log(totals))[..., 0])

        mixture, log_sums = lax.map(one_block, (q_blocks, pos_blocks))
        return (
            jnp.moveaxis(mixture, 0, 1).reshape(n_slots, q_len, per_group, head_width),
            log_sums,
        )

    grouped = (
        split_heads(queries, n_groups),
        split_heads(keys, n_groups),
        split_heads(values, n_groups),
    )
    mixture, log_sums = lax.map(one_group, grouped)
    return (join_heads(mixture), log_sums)


def attend_backward(queries, keys, values, upstream, row_dots, log_sums, q_pos, k_pos, lengths):
    n_slots, q_len, n_heads, head_width = queries.shape
    q_block, per_group = head_groups(n_slots, q_len, n_heads, keys.shape[1])
    n_groups = n_heads // per_group
    n_blocks = q_len // q_block
    score_scale = head_width ** (-0.5)
    pos_blocks = q_pos.reshape(n_blocks, q_block)
    dot_groups = jnp.moveaxis(row_dots.reshape(n_slots, q_len, n_groups, per_group), 2, 0)

    def blocks_of(grouped):
        return jnp.moveaxis(grouped.reshape((n_slots, n_blocks, q_block) + grouped.shape[2:]), 1, 0)

    def one_group(packed):
        q_group, k_group, v_group, g_group, d_group, l_group = packed

        def one_block(running, streams):
            k_grad, v_grad = running
            q_rows, g_rows, d_rows, l_rows, pos_rows = streams
            scores = score_block(q_rows, k_group, pos_rows, k_pos, lengths)
            probabilities = jnp.exp(scores - l_rows[..., None])
            v_grad = v_grad + jnp.einsum(
                "shqk,sqhe->skhe",
                probabilities.astype(jnp.bfloat16),
                g_rows,
                preferred_element_type=jnp.float32,
            )
            p_grad = jnp.einsum(
                "sqhe,skhe->shqk", g_rows, v_group, preferred_element_type=jnp.float32
            )
            s_grad = (probabilities * (p_grad - jnp.moveaxis(d_rows, 2, 1)[..., None])).astype(
                jnp.bfloat16
            )
            q_grad = (
                jnp.einsum("shqk,skhe->sqhe", s_grad, k_group, preferred_element_type=jnp.float32)
                * score_scale
            )
            k_grad = (
                k_grad
                + jnp.einsum("shqk,sqhe->skhe", s_grad, q_rows, preferred_element_type=jnp.float32)
                * score_scale
            )
            return ((k_grad, v_grad), q_grad)

        empty_grads = jnp.zeros(k_group.shape, jnp.float32)
        streams = (blocks_of(q_group), blocks_of(g_group), blocks_of(d_group), l_group, pos_blocks)
        (k_grad, v_grad), q_grads = lax.scan(one_block, (empty_grads, empty_grads), streams)
        return (
            jnp.moveaxis(q_grads, 0, 1).reshape(n_slots, q_len, per_group, head_width),
            k_grad,
            v_grad,
        )

    grouped = (
        split_heads(queries, n_groups),
        split_heads(keys, n_groups),
        split_heads(values, n_groups),
        split_heads(upstream, n_groups),
        dot_groups,
        log_sums,
    )
    q_grads, k_grads, v_grads = lax.map(one_group, grouped)
    return (join_heads(q_grads), join_heads(k_grads), join_heads(v_grads))


GROUP = ("fsdp", "ctx")


def as_rows(block, width):
    return block.reshape(-1, width)


def gather_rows(pieces, width):
    flat = [as_rows(p, width) for p in pieces]
    gathered = lax.all_gather(jnp.concatenate(flat, axis=0), GROUP, axis=0, tiled=False)
    n_group = gathered.shape[0]
    fulls, offset = [], 0
    for piece, rows in zip(pieces, flat):
        part = gathered[:, offset : offset + rows.shape[0], :]
        fulls.append(part.reshape((n_group * piece.shape[0],) + piece.shape[1:]))
        offset += rows.shape[0]
    return fulls


def scatter_rows(fulls, width, n_group):
    flat = [f.reshape(n_group, -1, width) for f in fulls]
    packed = jnp.concatenate(flat, axis=1).astype(jnp.bfloat16)
    summed = lax.psum_scatter(packed, GROUP, scatter_dimension=0, tiled=True)
    summed = lax.psum(summed, "rep")[0].astype(jnp.float32)
    parts, offset = [], 0
    for full, rows in zip(fulls, flat):
        part = summed[offset : offset + rows.shape[1], :]
        parts.append(part.reshape((full.shape[0] // n_group,) + full.shape[1:]))
        offset += rows.shape[1]
    return parts


def gain_block(full, n_group, width):
    own = full.reshape(n_group, 1, -1)
    padded = jnp.pad(own, ((0, 0), (0, 7), (0, width - own.shape[-1])))
    return padded.reshape(n_group * 8, width)


def gain_rows(first, second, width):
    row = jnp.zeros((8, width), first.dtype)
    row = row.at[0, : first.shape[-1]].set(first)
    return row.at[0, first.shape[-1] : first.shape[-1] + second.shape[-1]].set(second)


def shards(
    tokens,
    initial_layer_values,
    cotangent,
    lengths,
    w_query,
    w_key,
    w_value,
    w_out,
    w_gate,
    w_up,
    w_down,
    gain_attn,
    gain_mlp,
):
    n_slots, slot_rows, model_width = tokens.shape
    n_ctx = lax.axis_size("ctx")
    n_group = lax.axis_size("fsdp") * n_ctx
    own_rows = gain_attn.shape[0]
    full_query, full_key, full_value, gains = gather_rows(
        [w_query, w_key, w_value, gain_rows(gain_attn, gain_mlp, model_width)], model_width
    )
    gains = gains.reshape(n_group, 8, model_width)[:, 0, :]
    full_gain_attn = gains[:, :own_rows].reshape(-1)
    full_gain_mlp = gains[:, own_rows : 2 * own_rows].reshape(-1)
    full_out, full_gate, full_up, full_down = gather_rows(
        [w_out, w_gate, w_up, w_down], model_width
    )
    ctx_index = lax.axis_index("ctx")
    q_pos = ctx_index * slot_rows + jnp.arange(slot_rows)
    live_rows = q_pos[None, :] < lengths[:, None]
    head_shape = (n_slots, slot_rows, HEADS, HEAD_DIM)
    inputs = tokens.astype(jnp.float32)
    attn_scale = full_gain_attn.astype(jnp.float32)
    mlp_scale = full_gain_mlp.astype(jnp.float32)
    normed, inv_attn = normalize(inputs, attn_scale)
    normed_low = normed.astype(jnp.bfloat16)
    q_pre = jnp.einsum("srd,de->sre", normed_low, full_query, preferred_element_type=jnp.float32)
    k_pre = jnp.einsum("srd,de->sre", normed_low, full_key, preferred_element_type=jnp.float32)
    v_pre = jnp.einsum("srd,de->sre", normed_low, full_value, preferred_element_type=jnp.float32)
    queries = rotate(q_pre.reshape(head_shape), q_pos, 1.0).astype(jnp.bfloat16)
    keys = rotate(k_pre.reshape(head_shape), q_pos, 1.0).astype(jnp.bfloat16)
    values = (
        (0.5 * v_pre + 0.5 * initial_layer_values.astype(jnp.float32))
        .astype(jnp.bfloat16)
        .reshape(head_shape)
    )
    if n_ctx == 2:
        shift_up = [(0, 1)]
        earlier = lax.ppermute(jnp.stack([keys, values]), "ctx", shift_up)
        slot_k = jnp.concatenate([earlier[0], keys], axis=1)
        slot_v = jnp.concatenate([earlier[1], values], axis=1)
        k_pos = jnp.concatenate([q_pos - slot_rows, q_pos])
    else:
        slot_k, slot_v = (
            lax.all_gather(keys, "ctx", axis=1, tiled=True),
            lax.all_gather(values, "ctx", axis=1, tiled=True),
        )
        k_pos = jnp.arange(n_ctx * slot_rows)
    attn_raw, attn_lse = attend_forward(queries, slot_k, slot_v, q_pos, k_pos, lengths)
    attended = attn_raw.astype(jnp.bfloat16)
    att_flat = attended.reshape(n_slots, slot_rows, model_width)
    branch = jnp.einsum("sre,ed->srd", att_flat, full_out, preferred_element_type=jnp.float32)
    residual = inputs + branch
    normed_mlp, inv_mlp = normalize(residual, mlp_scale)
    mlp_low = normed_mlp.astype(jnp.bfloat16)
    gate_proj = jnp.einsum("srd,df->srf", mlp_low, full_gate, preferred_element_type=jnp.float32)
    up_proj = jnp.einsum("srd,df->srf", mlp_low, full_up, preferred_element_type=jnp.float32)
    sigmoid_gate = jax.nn.sigmoid(gate_proj)
    hidden = (gate_proj * sigmoid_gate * up_proj).astype(jnp.bfloat16)
    final = residual + jnp.einsum(
        "srf,fd->srd", hidden, full_down, preferred_element_type=jnp.float32
    )
    output = jnp.where(live_rows[..., None], final, 0.0).astype(jnp.bfloat16)
    output_gradient = jnp.where(live_rows[..., None], cotangent.astype(jnp.float32), 0.0)
    g_low = output_gradient.astype(jnp.bfloat16)
    grad_down = jnp.einsum("srf,srd->fd", hidden, g_low, preferred_element_type=jnp.float32)
    g_hidden = jnp.einsum("srd,fd->srf", g_low, full_down, preferred_element_type=jnp.float32)
    gate_gradient = (
        g_hidden * up_proj * sigmoid_gate * (1.0 + gate_proj * (1.0 - sigmoid_gate))
    ).astype(jnp.bfloat16)
    up_gradient = (g_hidden * gate_proj * sigmoid_gate).astype(jnp.bfloat16)
    grad_gate = jnp.einsum(
        "srd,srf->df", mlp_low, gate_gradient, preferred_element_type=jnp.float32
    )
    grad_up = jnp.einsum("srd,srf->df", mlp_low, up_gradient, preferred_element_type=jnp.float32)
    g_normed_mlp = jnp.einsum(
        "srf,df->srd", gate_gradient, full_gate, preferred_element_type=jnp.float32
    ) + jnp.einsum("srf,df->srd", up_gradient, full_up, preferred_element_type=jnp.float32)
    g_mlp_in, grad_gain_mlp = normalize_back(residual, inv_mlp, mlp_scale, g_normed_mlp)
    g_residual = output_gradient + g_mlp_in
    g_branch = g_residual.astype(jnp.bfloat16)
    grad_out = jnp.einsum("sre,srd->ed", att_flat, g_branch, preferred_element_type=jnp.float32)
    part_down, part_gate, part_up, part_out, part_gain_mlp = scatter_rows(
        [grad_down, grad_gate, grad_up, grad_out, gain_block(grad_gain_mlp, n_group, model_width)],
        model_width,
        n_group,
    )
    g_attended = (
        jnp.einsum("srd,ed->sre", g_branch, full_out, preferred_element_type=jnp.float32)
        .astype(jnp.bfloat16)
        .reshape(head_shape)
    )
    row_dots = jnp.sum(g_attended.astype(jnp.float32) * attended.astype(jnp.float32), axis=-1)
    g_queries, slot_dk, slot_dv = attend_backward(
        queries, slot_k, slot_v, g_attended, row_dots, attn_lse, q_pos, k_pos, lengths
    )
    if n_ctx == 2:
        shift_down = [(1, 0)]
        later = lax.ppermute(
            jnp.stack([slot_dk[:, :slot_rows], slot_dv[:, :slot_rows]]).astype(jnp.bfloat16),
            "ctx",
            shift_down,
        ).astype(jnp.float32)
        g_keys = slot_dk[:, slot_rows:] + later[0]
        g_values = slot_dv[:, slot_rows:] + later[1]
    else:
        g_keys, g_values = (
            lax.psum_scatter(
                slot_dk.astype(jnp.bfloat16), "ctx", scatter_dimension=1, tiled=True
            ).astype(jnp.float32),
            lax.psum_scatter(
                slot_dv.astype(jnp.bfloat16), "ctx", scatter_dimension=1, tiled=True
            ).astype(jnp.float32),
        )
    flat_shape = (n_slots, slot_rows, model_width)
    gq_low = rotate(g_queries, q_pos, -1.0).reshape(flat_shape).astype(jnp.bfloat16)
    gk_low = rotate(g_keys, q_pos, -1.0).reshape(flat_shape).astype(jnp.bfloat16)
    gv_rounded = g_values.reshape(flat_shape).astype(jnp.bfloat16).astype(jnp.float32)
    d_first = 0.5 * gv_rounded
    gv_half = d_first.astype(jnp.bfloat16)
    grad_query = jnp.einsum("srd,sre->de", normed_low, gq_low, preferred_element_type=jnp.float32)
    grad_key = jnp.einsum("srd,sre->de", normed_low, gk_low, preferred_element_type=jnp.float32)
    grad_value = jnp.einsum("srd,sre->de", normed_low, gv_half, preferred_element_type=jnp.float32)
    g_normed = jnp.einsum("sre,de->srd", gq_low, full_query, preferred_element_type=jnp.float32)
    g_normed = g_normed + jnp.einsum(
        "sre,de->srd", gk_low, full_key, preferred_element_type=jnp.float32
    )
    g_normed = g_normed + jnp.einsum(
        "sre,de->srd", gv_half, full_value, preferred_element_type=jnp.float32
    )
    g_attn_in, grad_gain_attn = normalize_back(inputs, inv_attn, attn_scale, g_normed)
    d_tokens = g_residual + g_attn_in
    part_query, part_key, part_value, part_gain_attn = scatter_rows(
        [grad_query, grad_key, grad_value, gain_block(grad_gain_attn, n_group, model_width)],
        model_width,
        n_group,
    )
    return (
        output,
        d_tokens,
        d_first,
        part_query,
        part_key,
        part_value,
        part_out,
        part_gate,
        part_up,
        part_down,
        part_gain_attn[0, :own_rows],
        part_gain_mlp[0, :own_rows],
    )


def solution(mesh):
    in_specs = (
        P(("rep", "fsdp"), "ctx", None),
        P(("rep", "fsdp"), "ctx", None),
        P(("rep", "fsdp"), "ctx", None),
        P(("rep", "fsdp")),
        P(("fsdp", "ctx"), None),
        P(("fsdp", "ctx"), None),
        P(("fsdp", "ctx"), None),
        P(("fsdp", "ctx"), None),
        P(("fsdp", "ctx"), None),
        P(("fsdp", "ctx"), None),
        P(("fsdp", "ctx"), None),
        P(("fsdp", "ctx")),
        P(("fsdp", "ctx")),
    )
    out_specs = (
        P(("rep", "fsdp"), "ctx", None),
        P(("rep", "fsdp"), "ctx", None),
        P(("rep", "fsdp"), "ctx", None),
        P(("fsdp", "ctx"), None),
        P(("fsdp", "ctx"), None),
        P(("fsdp", "ctx"), None),
        P(("fsdp", "ctx"), None),
        P(("fsdp", "ctx"), None),
        P(("fsdp", "ctx"), None),
        P(("fsdp", "ctx"), None),
        P(("fsdp", "ctx")),
        P(("fsdp", "ctx")),
    )
    return jax.shard_map(shards, mesh=mesh, in_specs=in_specs, out_specs=out_specs, check_vma=False)
```

```python
import jax
import jax.numpy as jnp
from jax import lax
from jax.sharding import PartitionSpec as P


HEADS = 16
HEAD_DIM = 64


EPS = 1e-06
NEG = -1e30
THETA = 10000.0
SCORE_CAP = 4194304


def rotate(field, positions, direction):
    head_width = field.shape[-1]
    half_width = head_width // 2
    frequency = THETA ** (-(jnp.arange(half_width, dtype=jnp.float32) * 2.0) / head_width)
    angles = positions.astype(jnp.float32)[:, None] * frequency[None, :]
    cosine = jnp.cos(angles)[:, None, :]
    sine_part = direction * jnp.sin(angles)[:, None, :]
    former = field[..., :half_width]
    latter = field[..., half_width:]
    return jnp.concatenate(
        [former * cosine - latter * sine_part, latter * cosine + former * sine_part], axis=-1
    )


def normalize(values, gain):
    inverse = lax.rsqrt(jnp.mean(values * values, axis=-1, keepdims=True) + EPS)
    return (values * inverse * gain, inverse)


def normalize_back(values, inverse, gain, upstream):
    unit_rows = values * inverse
    scaled = upstream * gain
    grad_gain = jnp.sum(upstream * unit_rows, axis=(0, 1))
    grad_values = inverse * (
        scaled - unit_rows * jnp.mean(scaled * unit_rows, axis=-1, keepdims=True)
    )
    return (grad_values, grad_gain)


def head_groups(n_slots, q_len, n_heads, k_len):
    q_block = min(q_len, 512)
    per_group = max(1, min(n_heads, SCORE_CAP // (n_slots * q_block * k_len)))
    while n_heads % per_group:
        per_group = per_group - 1
    return (q_block, per_group)


def split_heads(packed, n_groups):
    n_slots, length, n_heads, head_width = packed.shape
    return jnp.moveaxis(
        packed.reshape(n_slots, length, n_groups, n_heads // n_groups, head_width), 2, 0
    )


def join_heads(grouped):
    n_groups, n_slots, length, per_group, head_width = grouped.shape
    return jnp.moveaxis(grouped, 0, 2).reshape(n_slots, length, n_groups * per_group, head_width)


def score_block(q_rows, k_rows, q_pos, k_pos, lengths):
    products = jnp.einsum(
        "sqhe,skhe->shqk", q_rows, k_rows, preferred_element_type=jnp.float32
    ) * q_rows.shape[-1] ** (-0.5)
    causal = (k_pos[None, None, None, :] <= q_pos[None, None, :, None]) & (
        k_pos[None, None, None, :] >= 0
    )
    filled = k_pos[None, None, None, :] < lengths[:, None, None, None]
    return jnp.where(causal & filled, products, NEG)


def attend_forward(queries, keys, values, q_pos, k_pos, lengths):
    n_slots, q_len, n_heads, head_width = queries.shape
    q_block, per_group = head_groups(n_slots, q_len, n_heads, keys.shape[1])
    n_groups = n_heads // per_group
    n_blocks = q_len // q_block
    pos_blocks = q_pos.reshape(n_blocks, q_block)

    def one_group(packed):
        q_group, k_group, v_group = packed
        q_blocks = jnp.moveaxis(
            q_group.reshape(n_slots, n_blocks, q_block, per_group, head_width), 1, 0
        )

        def one_block(streams):
            q_rows, pos_rows = streams
            scores = score_block(q_rows, k_group, pos_rows, k_pos, lengths)
            highest = jnp.max(scores, axis=-1, keepdims=True)
            exponent = jnp.exp(scores - highest)
            totals = jnp.sum(exponent, axis=-1, keepdims=True)
            probabilities = (exponent / totals).astype(jnp.bfloat16)
            mixture = jnp.einsum(
                "shqk,skhe->sqhe", probabilities, v_group, preferred_element_type=jnp.float32
            )
            return (mixture, (highest + jnp.log(totals))[..., 0])

        mixture, log_sums = lax.map(one_block, (q_blocks, pos_blocks))
        return (
            jnp.moveaxis(mixture, 0, 1).reshape(n_slots, q_len, per_group, head_width),
            log_sums,
        )

    grouped = (
        split_heads(queries, n_groups),
        split_heads(keys, n_groups),
        split_heads(values, n_groups),
    )
    mixture, log_sums = lax.map(one_group, grouped)
    return (join_heads(mixture), log_sums)


def attend_backward(queries, keys, values, upstream, row_dots, log_sums, q_pos, k_pos, lengths):
    n_slots, q_len, n_heads, head_width = queries.shape
    q_block, per_group = head_groups(n_slots, q_len, n_heads, keys.shape[1])
    n_groups = n_heads // per_group
    n_blocks = q_len // q_block
    score_scale = head_width ** (-0.5)
    pos_blocks = q_pos.reshape(n_blocks, q_block)
    dot_groups = jnp.moveaxis(row_dots.reshape(n_slots, q_len, n_groups, per_group), 2, 0)

    def blocks_of(grouped):
        return jnp.moveaxis(grouped.reshape((n_slots, n_blocks, q_block) + grouped.shape[2:]), 1, 0)

    def one_group(packed):
        q_group, k_group, v_group, g_group, d_group, l_group = packed

        def one_block(running, streams):
            k_grad, v_grad = running
            q_rows, g_rows, d_rows, l_rows, pos_rows = streams
            scores = score_block(q_rows, k_group, pos_rows, k_pos, lengths)
            probabilities = jnp.exp(scores - l_rows[..., None])
            v_grad = v_grad + jnp.einsum(
                "shqk,sqhe->skhe",
                probabilities.astype(jnp.bfloat16),
                g_rows,
                preferred_element_type=jnp.float32,
            )
            p_grad = jnp.einsum(
                "sqhe,skhe->shqk", g_rows, v_group, preferred_element_type=jnp.float32
            )
            s_grad = (probabilities * (p_grad - jnp.moveaxis(d_rows, 2, 1)[..., None])).astype(
                jnp.bfloat16
            )
            q_grad = (
                jnp.einsum("shqk,skhe->sqhe", s_grad, k_group, preferred_element_type=jnp.float32)
                * score_scale
            )
            k_grad = (
                k_grad
                + jnp.einsum("shqk,sqhe->skhe", s_grad, q_rows, preferred_element_type=jnp.float32)
                * score_scale
            )
            return ((k_grad, v_grad), q_grad)

        empty_grads = jnp.zeros(k_group.shape, jnp.float32)
        streams = (blocks_of(q_group), blocks_of(g_group), blocks_of(d_group), l_group, pos_blocks)
        (k_grad, v_grad), q_grads = lax.scan(one_block, (empty_grads, empty_grads), streams)
        return (
            jnp.moveaxis(q_grads, 0, 1).reshape(n_slots, q_len, per_group, head_width),
            k_grad,
            v_grad,
        )

    grouped = (
        split_heads(queries, n_groups),
        split_heads(keys, n_groups),
        split_heads(values, n_groups),
        split_heads(upstream, n_groups),
        dot_groups,
        log_sums,
    )
    q_grads, k_grads, v_grads = lax.map(one_group, grouped)
    return (join_heads(q_grads), join_heads(k_grads), join_heads(v_grads))


GROUP = ("fsdp", "ctx")


def gather_blocks(pieces):
    packed = jnp.concatenate(pieces, axis=0)
    gathered = lax.all_gather(packed, GROUP, axis=0, tiled=False)
    fulls, offset = [], 0
    for piece in pieces:
        fulls.append(gathered[:, offset : offset + piece.shape[0], :])
        offset += piece.shape[0]
    return fulls


def rep_sum(x):
    n_rep = lax.axis_size("rep")
    if n_rep != 4:
        return lax.psum(x, "rep")
    me = lax.axis_index("rep")
    folded = (x.astype(jnp.float32) + lax.ppermute(x, "rep", [(0, 1), (3, 2)]).astype(jnp.float32)).astype(x.dtype)
    total = (
        folded.astype(jnp.float32) + lax.ppermute(folded, "rep", [(1, 2), (2, 1)]).astype(jnp.float32)
    ).astype(x.dtype)
    sent_out = lax.ppermute(total, "rep", [(1, 0), (2, 3)])
    return jnp.where((me == 0) | (me == 3), sent_out, total)


def scatter_blocks(blocks, by_permutes):
    packed = jnp.concatenate(blocks, axis=1).astype(jnp.bfloat16)
    summed = lax.psum_scatter(packed, GROUP, scatter_dimension=0, tiled=True)
    summed = (rep_sum(summed) if by_permutes else lax.psum(summed, "rep"))[0].astype(jnp.float32)
    parts, offset = [], 0
    for block in blocks:
        parts.append(summed[offset : offset + block.shape[1], :])
        offset += block.shape[1]
    return parts


def gain_block(first, second, width):
    lead = first.shape[:-1]
    row = jnp.concatenate([first, second], axis=-1)
    row = jnp.pad(row, [(0, 0)] * len(lead) + [(0, width - row.shape[-1])])
    return jnp.pad(row[..., None, :], [(0, 0)] * len(lead) + [(0, 7), (0, 0)])


def shards(
    tokens,
    initial_layer_values,
    cotangent,
    lengths,
    w_query,
    w_key,
    w_value,
    w_out,
    w_gate,
    w_up,
    w_down,
    gain_attn,
    gain_mlp,
):
    n_slots, slot_rows, model_width = tokens.shape
    n_ctx = lax.axis_size("ctx")
    n_group = lax.axis_size("fsdp") * n_ctx
    own_rows = gain_attn.shape[0]
    ff_width = w_gate.shape[1]
    attn_width = w_query.shape[1]
    qkv_width = 3 * attn_width
    (qkv_blocks, gain_rows) = gather_blocks(
        [
            jnp.concatenate([w_query, w_key, w_value], axis=1),
            gain_block(gain_attn, gain_mlp, qkv_width),
        ]
    )
    full_qkv = qkv_blocks.reshape(n_group * own_rows, qkv_width)
    full_gain_attn = gain_rows[:, 0, :own_rows].reshape(-1)
    full_gain_mlp = gain_rows[:, 0, own_rows : 2 * own_rows].reshape(-1)
    out_blocks, down_blocks = gather_blocks([w_out, w_down])
    full_out = out_blocks.reshape(-1, model_width)
    full_down = down_blocks.reshape(-1, model_width)
    (gu_blocks,) = gather_blocks([jnp.concatenate([w_gate, w_up], axis=1)])
    full_gu = gu_blocks.reshape(n_group * own_rows, 2 * ff_width)
    ctx_index = lax.axis_index("ctx")
    q_pos = ctx_index * slot_rows + jnp.arange(slot_rows)
    live_rows = q_pos[None, :] < lengths[:, None]
    head_shape = (n_slots, slot_rows, HEADS, HEAD_DIM)
    inputs = tokens.astype(jnp.float32)
    attn_scale = full_gain_attn.astype(jnp.float32)
    mlp_scale = full_gain_mlp.astype(jnp.float32)
    normed, inv_attn = normalize(inputs, attn_scale)
    normed_low = normed.astype(jnp.bfloat16)
    qkv_pre = jnp.einsum("srd,de->sre", normed_low, full_qkv, preferred_element_type=jnp.float32)
    q_pre = qkv_pre[..., :attn_width]
    k_pre = qkv_pre[..., attn_width : 2 * attn_width]
    v_pre = qkv_pre[..., 2 * attn_width :]
    queries = rotate(q_pre.reshape(head_shape), q_pos, 1.0).astype(jnp.bfloat16)
    keys = rotate(k_pre.reshape(head_shape), q_pos, 1.0).astype(jnp.bfloat16)
    values = (
        (0.5 * v_pre + 0.5 * initial_layer_values.astype(jnp.float32))
        .astype(jnp.bfloat16)
        .reshape(head_shape)
    )
    if n_ctx == 2:
        earlier = lax.ppermute(jnp.stack([keys, values]), "ctx", [(0, 1)])
        slot_k = jnp.concatenate([earlier[0], keys], axis=1)
        slot_v = jnp.concatenate([earlier[1], values], axis=1)
        k_pos = jnp.concatenate([q_pos - slot_rows, q_pos])
    else:
        slot_k, slot_v = (
            lax.all_gather(keys, "ctx", axis=1, tiled=True),
            lax.all_gather(values, "ctx", axis=1, tiled=True),
        )
        k_pos = jnp.arange(n_ctx * slot_rows)
    attn_raw, attn_lse = attend_forward(queries, slot_k, slot_v, q_pos, k_pos, lengths)
    attended = attn_raw.astype(jnp.bfloat16)
    att_flat = attended.reshape(n_slots, slot_rows, model_width)
    branch = jnp.einsum("sre,ed->srd", att_flat, full_out, preferred_element_type=jnp.float32)
    residual = inputs + branch
    normed_mlp, inv_mlp = normalize(residual, mlp_scale)
    mlp_low = normed_mlp.astype(jnp.bfloat16)
    gu_proj = jnp.einsum("srd,df->srf", mlp_low, full_gu, preferred_element_type=jnp.float32)
    gate_proj = gu_proj[..., :ff_width]
    up_proj = gu_proj[..., ff_width:]
    sigmoid_gate = jax.nn.sigmoid(gate_proj)
    hidden = (gate_proj * sigmoid_gate * up_proj).astype(jnp.bfloat16)
    final = residual + jnp.einsum(
        "srf,fd->srd", hidden, full_down, preferred_element_type=jnp.float32
    )
    output = jnp.where(live_rows[..., None], final, 0.0).astype(jnp.bfloat16)
    output_gradient = jnp.where(live_rows[..., None], cotangent.astype(jnp.float32), 0.0)
    g_low = output_gradient.astype(jnp.bfloat16)
    grad_down = jnp.einsum("srf,srd->fd", hidden, g_low, preferred_element_type=jnp.float32)
    g_hidden = jnp.einsum("srd,fd->srf", g_low, full_down, preferred_element_type=jnp.float32)
    gate_gradient = (
        g_hidden * up_proj * sigmoid_gate * (1.0 + gate_proj * (1.0 - sigmoid_gate))
    ).astype(jnp.bfloat16)
    up_gradient = (g_hidden * gate_proj * sigmoid_gate).astype(jnp.bfloat16)
    gu_gradient = jnp.concatenate([gate_gradient, up_gradient], axis=-1)
    grad_gu = jnp.einsum("srd,srf->df", mlp_low, gu_gradient, preferred_element_type=jnp.float32)
    g_normed_mlp = jnp.einsum(
        "srf,df->srd", gu_gradient, full_gu, preferred_element_type=jnp.float32
    )
    g_mlp_in, grad_gain_mlp = normalize_back(residual, inv_mlp, mlp_scale, g_normed_mlp)
    g_residual = output_gradient + g_mlp_in
    g_branch = g_residual.astype(jnp.bfloat16)
    grad_out = jnp.einsum("sre,srd->ed", att_flat, g_branch, preferred_element_type=jnp.float32)
    gu_block = grad_gu.reshape(n_group, own_rows, 2 * ff_width).astype(jnp.bfloat16)
    od_blocks = [
        grad_out.reshape(n_group, -1, model_width).astype(jnp.bfloat16),
        grad_down.reshape(n_group, -1, model_width).astype(jnp.bfloat16),
    ]
    g_attended = (
        jnp.einsum("srd,ed->sre", g_branch, full_out, preferred_element_type=jnp.float32)
        .astype(jnp.bfloat16)
        .reshape(head_shape)
    )
    gu_block, od_blocks, g_attended = lax.optimization_barrier((gu_block, od_blocks, g_attended))
    (part_gu,) = scatter_blocks([gu_block], True)
    part_out, part_down = scatter_blocks(od_blocks, True)
    row_dots = jnp.sum(g_attended.astype(jnp.float32) * attended.astype(jnp.float32), axis=-1)
    g_queries, slot_dk, slot_dv = attend_backward(
        queries, slot_k, slot_v, g_attended, row_dots, attn_lse, q_pos, k_pos, lengths
    )
    if n_ctx == 2:
        later = lax.ppermute(
            jnp.stack([slot_dk[:, :slot_rows], slot_dv[:, :slot_rows]]).astype(jnp.bfloat16),
            "ctx",
            [(1, 0)],
        ).astype(jnp.float32)
        g_keys = slot_dk[:, slot_rows:] + later[0]
        g_values = slot_dv[:, slot_rows:] + later[1]
    else:
        g_keys, g_values = (
            lax.psum_scatter(
                slot_dk.astype(jnp.bfloat16), "ctx", scatter_dimension=1, tiled=True
            ).astype(jnp.float32),
            lax.psum_scatter(
                slot_dv.astype(jnp.bfloat16), "ctx", scatter_dimension=1, tiled=True
            ).astype(jnp.float32),
        )
    flat_shape = (n_slots, slot_rows, model_width)
    gq_low = rotate(g_queries, q_pos, -1.0).reshape(flat_shape).astype(jnp.bfloat16)
    gk_low = rotate(g_keys, q_pos, -1.0).reshape(flat_shape).astype(jnp.bfloat16)
    gv_rounded = g_values.reshape(flat_shape).astype(jnp.bfloat16).astype(jnp.float32)
    d_first = 0.5 * gv_rounded
    gv_half = d_first.astype(jnp.bfloat16)
    g_qkv = jnp.concatenate([gq_low, gk_low, gv_half], axis=-1)
    grad_qkv = jnp.einsum("srd,sre->de", normed_low, g_qkv, preferred_element_type=jnp.float32)
    g_normed = jnp.einsum("sre,de->srd", g_qkv, full_qkv, preferred_element_type=jnp.float32)
    g_attn_in, grad_gain_attn = normalize_back(inputs, inv_attn, attn_scale, g_normed)
    d_tokens = g_residual + g_attn_in
    part_qkv, part_gains = scatter_blocks(
        [
            grad_qkv.reshape(n_group, own_rows, qkv_width),
            gain_block(
                grad_gain_attn.reshape(n_group, own_rows),
                grad_gain_mlp.reshape(n_group, own_rows),
                qkv_width,
            ),
        ],
        False,
    )
    return (
        output,
        d_tokens,
        d_first,
        part_qkv[:, :attn_width],
        part_qkv[:, attn_width : 2 * attn_width],
        part_qkv[:, 2 * attn_width :],
        part_out,
        part_gu[:, :ff_width],
        part_gu[:, ff_width:],
        part_down,
        part_gains[0, :own_rows],
        part_gains[0, own_rows : 2 * own_rows],
    )


def solution(mesh):
    in_specs = (
        P(("rep", "fsdp"), "ctx", None),
        P(("rep", "fsdp"), "ctx", None),
        P(("rep", "fsdp"), "ctx", None),
        P(("rep", "fsdp")),
        P(("fsdp", "ctx"), None),
        P(("fsdp", "ctx"), None),
        P(("fsdp", "ctx"), None),
        P(("fsdp", "ctx"), None),
        P(("fsdp", "ctx"), None),
        P(("fsdp", "ctx"), None),
        P(("fsdp", "ctx"), None),
        P(("fsdp", "ctx")),
        P(("fsdp", "ctx")),
    )
    out_specs = (
        P(("rep", "fsdp"), "ctx", None),
        P(("rep", "fsdp"), "ctx", None),
        P(("rep", "fsdp"), "ctx", None),
        P(("fsdp", "ctx"), None),
        P(("fsdp", "ctx"), None),
        P(("fsdp", "ctx"), None),
        P(("fsdp", "ctx"), None),
        P(("fsdp", "ctx"), None),
        P(("fsdp", "ctx"), None),
        P(("fsdp", "ctx"), None),
        P(("fsdp", "ctx")),
        P(("fsdp", "ctx")),
    )

    return jax.shard_map(shards, mesh=mesh, in_specs=in_specs, out_specs=out_specs, check_vma=False)
```

```python
import jax
import jax.numpy as jnp
from jax import lax
from jax.sharding import PartitionSpec as P


HEADS = 16
HEAD_DIM = 64


EPS = 1e-06
NEG = -1e30
THETA = 10000.0
SCORE_CAP = 4194304


def rotate(field, positions, direction):
    head_width = field.shape[-1]
    half_width = head_width // 2
    frequency = THETA ** (-(jnp.arange(half_width, dtype=jnp.float32) * 2.0) / head_width)
    angles = positions.astype(jnp.float32)[:, None] * frequency[None, :]
    cosine = jnp.cos(angles)[:, None, :]
    sine_part = direction * jnp.sin(angles)[:, None, :]
    former = field[..., :half_width]
    latter = field[..., half_width:]
    return jnp.concatenate(
        [former * cosine - latter * sine_part, latter * cosine + former * sine_part], axis=-1
    )


def normalize(values, gain):
    inverse = lax.rsqrt(jnp.mean(values * values, axis=-1, keepdims=True) + EPS)
    return (values * inverse * gain, inverse)


def normalize_back(values, inverse, gain, upstream):
    unit_rows = values * inverse
    scaled = upstream * gain
    grad_gain = jnp.sum(upstream * unit_rows, axis=(0, 1))
    grad_values = inverse * (
        scaled - unit_rows * jnp.mean(scaled * unit_rows, axis=-1, keepdims=True)
    )
    return (grad_values, grad_gain)


def head_groups(n_slots, q_len, n_heads, k_len):
    q_block = min(q_len, 512)
    per_group = max(1, min(n_heads, SCORE_CAP // (n_slots * q_block * k_len)))
    while n_heads % per_group:
        per_group = per_group - 1
    return (q_block, per_group)


def split_heads(packed, n_groups):
    n_slots, length, n_heads, head_width = packed.shape
    return jnp.moveaxis(
        packed.reshape(n_slots, length, n_groups, n_heads // n_groups, head_width), 2, 0
    )


def join_heads(grouped):
    n_groups, n_slots, length, per_group, head_width = grouped.shape
    return jnp.moveaxis(grouped, 0, 2).reshape(n_slots, length, n_groups * per_group, head_width)


def score_block(q_rows, k_rows, q_pos, k_pos, lengths):
    products = jnp.einsum(
        "sqhe,skhe->shqk", q_rows, k_rows, preferred_element_type=jnp.float32
    ) * q_rows.shape[-1] ** (-0.5)
    causal = (k_pos[None, None, None, :] <= q_pos[None, None, :, None]) & (
        k_pos[None, None, None, :] >= 0
    )
    filled = k_pos[None, None, None, :] < lengths[:, None, None, None]
    return jnp.where(causal & filled, products, NEG)


def attend_forward(queries, keys, values, q_pos, k_pos, lengths):
    n_slots, q_len, n_heads, head_width = queries.shape
    q_block, per_group = head_groups(n_slots, q_len, n_heads, keys.shape[1])
    n_groups = n_heads // per_group
    n_blocks = q_len // q_block
    pos_blocks = q_pos.reshape(n_blocks, q_block)

    def one_group(packed):
        q_group, k_group, v_group = packed
        q_blocks = jnp.moveaxis(
            q_group.reshape(n_slots, n_blocks, q_block, per_group, head_width), 1, 0
        )

        def one_block(streams):
            q_rows, pos_rows = streams
            scores = score_block(q_rows, k_group, pos_rows, k_pos, lengths)
            highest = jnp.max(scores, axis=-1, keepdims=True)
            exponent = jnp.exp(scores - highest)
            totals = jnp.sum(exponent, axis=-1, keepdims=True)
            probabilities = (exponent / totals).astype(jnp.bfloat16)
            mixture = jnp.einsum(
                "shqk,skhe->sqhe", probabilities, v_group, preferred_element_type=jnp.float32
            )
            return (mixture, (highest + jnp.log(totals))[..., 0])

        mixture, log_sums = lax.map(one_block, (q_blocks, pos_blocks))
        return (
            jnp.moveaxis(mixture, 0, 1).reshape(n_slots, q_len, per_group, head_width),
            log_sums,
        )

    grouped = (
        split_heads(queries, n_groups),
        split_heads(keys, n_groups),
        split_heads(values, n_groups),
    )
    mixture, log_sums = lax.map(one_group, grouped)
    return (join_heads(mixture), log_sums)


def attend_backward(queries, keys, values, upstream, row_dots, log_sums, q_pos, k_pos, lengths):
    n_slots, q_len, n_heads, head_width = queries.shape
    q_block, per_group = head_groups(n_slots, q_len, n_heads, keys.shape[1])
    n_groups = n_heads // per_group
    n_blocks = q_len // q_block
    score_scale = head_width ** (-0.5)
    pos_blocks = q_pos.reshape(n_blocks, q_block)
    dot_groups = jnp.moveaxis(row_dots.reshape(n_slots, q_len, n_groups, per_group), 2, 0)

    def blocks_of(grouped):
        return jnp.moveaxis(grouped.reshape((n_slots, n_blocks, q_block) + grouped.shape[2:]), 1, 0)

    def one_group(packed):
        q_group, k_group, v_group, g_group, d_group, l_group = packed

        def one_block(running, streams):
            k_grad, v_grad = running
            q_rows, g_rows, d_rows, l_rows, pos_rows = streams
            scores = score_block(q_rows, k_group, pos_rows, k_pos, lengths)
            probabilities = jnp.exp(scores - l_rows[..., None])
            v_grad = v_grad + jnp.einsum(
                "shqk,sqhe->skhe",
                probabilities.astype(jnp.bfloat16),
                g_rows,
                preferred_element_type=jnp.float32,
            )
            p_grad = jnp.einsum(
                "sqhe,skhe->shqk", g_rows, v_group, preferred_element_type=jnp.float32
            )
            s_grad = (probabilities * (p_grad - jnp.moveaxis(d_rows, 2, 1)[..., None])).astype(
                jnp.bfloat16
            )
            q_grad = (
                jnp.einsum("shqk,skhe->sqhe", s_grad, k_group, preferred_element_type=jnp.float32)
                * score_scale
            )
            k_grad = (
                k_grad
                + jnp.einsum("shqk,sqhe->skhe", s_grad, q_rows, preferred_element_type=jnp.float32)
                * score_scale
            )
            return ((k_grad, v_grad), q_grad)

        empty_grads = jnp.zeros(k_group.shape, jnp.float32)
        streams = (blocks_of(q_group), blocks_of(g_group), blocks_of(d_group), l_group, pos_blocks)
        (k_grad, v_grad), q_grads = lax.scan(one_block, (empty_grads, empty_grads), streams)
        return (
            jnp.moveaxis(q_grads, 0, 1).reshape(n_slots, q_len, per_group, head_width),
            k_grad,
            v_grad,
        )

    grouped = (
        split_heads(queries, n_groups),
        split_heads(keys, n_groups),
        split_heads(values, n_groups),
        split_heads(upstream, n_groups),
        dot_groups,
        log_sums,
    )
    q_grads, k_grads, v_grads = lax.map(one_group, grouped)
    return (join_heads(q_grads), join_heads(k_grads), join_heads(v_grads))


GROUP = ("fsdp", "ctx")


def gather_blocks(pieces):
    packed = jnp.concatenate(pieces, axis=0)
    gathered = lax.all_gather(packed, GROUP, axis=0, tiled=False)
    fulls, offset = [], 0
    for piece in pieces:
        fulls.append(gathered[:, offset : offset + piece.shape[0], :])
        offset += piece.shape[0]
    return fulls


def rep_sum(x):
    n_rep = lax.axis_size("rep")
    if n_rep != 4:
        return lax.psum(x, "rep")
    me = lax.axis_index("rep")
    folded = (x.astype(jnp.float32) + lax.ppermute(x, "rep", [(0, 1), (3, 2)]).astype(jnp.float32)).astype(x.dtype)
    total = (
        folded.astype(jnp.float32) + lax.ppermute(folded, "rep", [(1, 2), (2, 1)]).astype(jnp.float32)
    ).astype(x.dtype)
    sent_out = lax.ppermute(total, "rep", [(1, 0), (2, 3)])
    return jnp.where((me == 0) | (me == 3), sent_out, total)


def scatter_blocks(blocks, by_permutes):
    packed = jnp.concatenate(blocks, axis=1).astype(jnp.bfloat16)
    summed = lax.psum_scatter(packed, GROUP, scatter_dimension=0, tiled=True)
    summed = (rep_sum(summed) if by_permutes else lax.psum(summed, "rep"))[0].astype(jnp.float32)
    parts, offset = [], 0
    for block in blocks:
        parts.append(summed[offset : offset + block.shape[1], :])
        offset += block.shape[1]
    return parts


def gain_block(first, second, width):
    lead = first.shape[:-1]
    row = jnp.concatenate([first, second], axis=-1)
    row = jnp.pad(row, [(0, 0)] * len(lead) + [(0, width - row.shape[-1])])
    return jnp.pad(row[..., None, :], [(0, 0)] * len(lead) + [(0, 7), (0, 0)])


def shards(
    tokens,
    initial_layer_values,
    cotangent,
    lengths,
    w_query,
    w_key,
    w_value,
    w_out,
    w_gate,
    w_up,
    w_down,
    gain_attn,
    gain_mlp,
):
    n_slots, slot_rows, model_width = tokens.shape
    n_ctx = lax.axis_size("ctx")
    n_group = lax.axis_size("fsdp") * n_ctx
    own_rows = gain_attn.shape[0]
    ff_width = w_gate.shape[1]
    attn_width = w_query.shape[1]
    qkv_width = 3 * attn_width
    (qkv_blocks, gain_rows) = gather_blocks(
        [
            jnp.concatenate([w_query, w_key, w_value], axis=1),
            gain_block(gain_attn, gain_mlp, qkv_width),
        ]
    )
    full_qkv = qkv_blocks.reshape(n_group * own_rows, qkv_width)
    full_gain_attn = gain_rows[:, 0, :own_rows].reshape(-1)
    full_gain_mlp = gain_rows[:, 0, own_rows : 2 * own_rows].reshape(-1)
    (ogu_blocks,) = gather_blocks([jnp.concatenate([w_out, w_gate, w_up], axis=1)])
    full_ogu = ogu_blocks.reshape(n_group * own_rows, model_width + 2 * ff_width)
    full_out = full_ogu[:, :model_width]
    full_gu = full_ogu[:, model_width:]
    (down_blocks,) = gather_blocks([w_down])
    full_down = down_blocks.reshape(-1, model_width)
    ctx_index = lax.axis_index("ctx")
    q_pos = ctx_index * slot_rows + jnp.arange(slot_rows)
    live_rows = q_pos[None, :] < lengths[:, None]
    head_shape = (n_slots, slot_rows, HEADS, HEAD_DIM)
    inputs = tokens.astype(jnp.float32)
    attn_scale = full_gain_attn.astype(jnp.float32)
    mlp_scale = full_gain_mlp.astype(jnp.float32)
    normed, inv_attn = normalize(inputs, attn_scale)
    normed_low = normed.astype(jnp.bfloat16)
    qkv_pre = jnp.einsum("srd,de->sre", normed_low, full_qkv, preferred_element_type=jnp.float32)
    q_pre = qkv_pre[..., :attn_width]
    k_pre = qkv_pre[..., attn_width : 2 * attn_width]
    v_pre = qkv_pre[..., 2 * attn_width :]
    queries = rotate(q_pre.reshape(head_shape), q_pos, 1.0).astype(jnp.bfloat16)
    keys = rotate(k_pre.reshape(head_shape), q_pos, 1.0).astype(jnp.bfloat16)
    values = (
        (0.5 * v_pre + 0.5 * initial_layer_values.astype(jnp.float32))
        .astype(jnp.bfloat16)
        .reshape(head_shape)
    )
    if n_ctx == 2:
        earlier = lax.ppermute(jnp.stack([keys, values]), "ctx", [(0, 1)])
        slot_k = jnp.concatenate([earlier[0], keys], axis=1)
        slot_v = jnp.concatenate([earlier[1], values], axis=1)
        k_pos = jnp.concatenate([q_pos - slot_rows, q_pos])
    else:
        slot_k, slot_v = (
            lax.all_gather(keys, "ctx", axis=1, tiled=True),
            lax.all_gather(values, "ctx", axis=1, tiled=True),
        )
        k_pos = jnp.arange(n_ctx * slot_rows)
    attn_raw, attn_lse = attend_forward(queries, slot_k, slot_v, q_pos, k_pos, lengths)
    attended = attn_raw.astype(jnp.bfloat16)
    att_flat = attended.reshape(n_slots, slot_rows, model_width)
    branch = jnp.einsum("sre,ed->srd", att_flat, full_out, preferred_element_type=jnp.float32)
    residual = inputs + branch
    normed_mlp, inv_mlp = normalize(residual, mlp_scale)
    mlp_low = normed_mlp.astype(jnp.bfloat16)
    gu_proj = jnp.einsum("srd,df->srf", mlp_low, full_gu, preferred_element_type=jnp.float32)
    gate_proj = gu_proj[..., :ff_width]
    up_proj = gu_proj[..., ff_width:]
    sigmoid_gate = jax.nn.sigmoid(gate_proj)
    hidden = (gate_proj * sigmoid_gate * up_proj).astype(jnp.bfloat16)
    final = residual + jnp.einsum(
        "srf,fd->srd", hidden, full_down, preferred_element_type=jnp.float32
    )
    output = jnp.where(live_rows[..., None], final, 0.0).astype(jnp.bfloat16)
    output_gradient = jnp.where(live_rows[..., None], cotangent.astype(jnp.float32), 0.0)
    g_low = output_gradient.astype(jnp.bfloat16)
    grad_down = jnp.einsum("srf,srd->fd", hidden, g_low, preferred_element_type=jnp.float32)
    (part_down,) = scatter_blocks(
        [grad_down.reshape(n_group, -1, model_width).astype(jnp.bfloat16)], True
    )
    g_hidden = jnp.einsum("srd,fd->srf", g_low, full_down, preferred_element_type=jnp.float32)
    gate_gradient = (
        g_hidden * up_proj * sigmoid_gate * (1.0 + gate_proj * (1.0 - sigmoid_gate))
    ).astype(jnp.bfloat16)
    up_gradient = (g_hidden * gate_proj * sigmoid_gate).astype(jnp.bfloat16)
    gu_gradient = jnp.concatenate([gate_gradient, up_gradient], axis=-1)
    grad_gu = jnp.einsum("srd,srf->df", mlp_low, gu_gradient, preferred_element_type=jnp.float32)
    g_normed_mlp = jnp.einsum(
        "srf,df->srd", gu_gradient, full_gu, preferred_element_type=jnp.float32
    )
    g_mlp_in, grad_gain_mlp = normalize_back(residual, inv_mlp, mlp_scale, g_normed_mlp)
    g_residual = output_gradient + g_mlp_in
    g_branch = g_residual.astype(jnp.bfloat16)
    grad_out = jnp.einsum(
        "sre,srd->ed", att_flat, g_branch, preferred_element_type=jnp.float32
    )
    ogu_block = (
        jnp.concatenate([grad_out, grad_gu], axis=1)
        .reshape(n_group, own_rows, model_width + 2 * ff_width)
        .astype(jnp.bfloat16)
    )
    g_attended = (
        jnp.einsum("srd,ed->sre", g_branch, full_out, preferred_element_type=jnp.float32)
        .astype(jnp.bfloat16)
        .reshape(head_shape)
    )
    (part_ogu,) = scatter_blocks([ogu_block], True)
    row_dots = jnp.sum(g_attended.astype(jnp.float32) * attended.astype(jnp.float32), axis=-1)
    g_queries, slot_dk, slot_dv = attend_backward(
        queries, slot_k, slot_v, g_attended, row_dots, attn_lse, q_pos, k_pos, lengths
    )
    flat_shape = (n_slots, slot_rows, model_width)
    if n_ctx == 2:
        later = lax.ppermute(
            jnp.stack([slot_dk[:, :slot_rows], slot_dv[:, :slot_rows]]).astype(jnp.bfloat16),
            "ctx",
            [(1, 0)],
        )
    gq_low = rotate(g_queries, q_pos, -1.0).reshape(flat_shape).astype(jnp.bfloat16)
    grad_q = jnp.einsum("srd,sre->de", normed_low, gq_low, preferred_element_type=jnp.float32)
    g_normed_q = jnp.einsum(
        "sre,de->srd", gq_low, full_qkv[:, :attn_width], preferred_element_type=jnp.float32
    )
    (part_q,) = scatter_blocks(
        [grad_q.reshape(n_group, own_rows, attn_width).astype(jnp.bfloat16)], True
    )
    if n_ctx == 2:
        later = later.astype(jnp.float32)
        g_keys = slot_dk[:, slot_rows:] + later[0]
        g_values = slot_dv[:, slot_rows:] + later[1]
    else:
        g_keys, g_values = (
            lax.psum_scatter(
                slot_dk.astype(jnp.bfloat16), "ctx", scatter_dimension=1, tiled=True
            ).astype(jnp.float32),
            lax.psum_scatter(
                slot_dv.astype(jnp.bfloat16), "ctx", scatter_dimension=1, tiled=True
            ).astype(jnp.float32),
        )
    gk_low = rotate(g_keys, q_pos, -1.0).reshape(flat_shape).astype(jnp.bfloat16)
    gv_rounded = g_values.reshape(flat_shape).astype(jnp.bfloat16).astype(jnp.float32)
    d_first = 0.5 * gv_rounded
    gv_half = d_first.astype(jnp.bfloat16)
    g_kv = jnp.concatenate([gk_low, gv_half], axis=-1)
    grad_kv = jnp.einsum("srd,sre->de", normed_low, g_kv, preferred_element_type=jnp.float32)
    g_normed = g_normed_q + jnp.einsum(
        "sre,de->srd", g_kv, full_qkv[:, attn_width:], preferred_element_type=jnp.float32
    )
    g_attn_in, grad_gain_attn = normalize_back(inputs, inv_attn, attn_scale, g_normed)
    d_tokens = g_residual + g_attn_in
    part_kv, part_gains = scatter_blocks(
        [
            grad_kv.reshape(n_group, own_rows, 2 * attn_width).astype(jnp.bfloat16),
            gain_block(
                grad_gain_attn.reshape(n_group, own_rows),
                grad_gain_mlp.reshape(n_group, own_rows),
                2 * attn_width,
            ).astype(jnp.bfloat16),
        ],
        False,
    )
    return (
        output,
        d_tokens,
        d_first,
        part_q,
        part_kv[:, :attn_width],
        part_kv[:, attn_width:],
        part_ogu[:, :model_width],
        part_ogu[:, model_width : model_width + ff_width],
        part_ogu[:, model_width + ff_width :],
        part_down,
        part_gains[0, :own_rows],
        part_gains[0, own_rows : 2 * own_rows],
    )


def solution(mesh):
    in_specs = (
        P(("rep", "fsdp"), "ctx", None),
        P(("rep", "fsdp"), "ctx", None),
        P(("rep", "fsdp"), "ctx", None),
        P(("rep", "fsdp")),
        P(("fsdp", "ctx"), None),
        P(("fsdp", "ctx"), None),
        P(("fsdp", "ctx"), None),
        P(("fsdp", "ctx"), None),
        P(("fsdp", "ctx"), None),
        P(("fsdp", "ctx"), None),
        P(("fsdp", "ctx"), None),
        P(("fsdp", "ctx")),
        P(("fsdp", "ctx")),
    )
    out_specs = (
        P(("rep", "fsdp"), "ctx", None),
        P(("rep", "fsdp"), "ctx", None),
        P(("rep", "fsdp"), "ctx", None),
        P(("fsdp", "ctx"), None),
        P(("fsdp", "ctx"), None),
        P(("fsdp", "ctx"), None),
        P(("fsdp", "ctx"), None),
        P(("fsdp", "ctx"), None),
        P(("fsdp", "ctx"), None),
        P(("fsdp", "ctx"), None),
        P(("fsdp", "ctx")),
        P(("fsdp", "ctx")),
    )

    return jax.shard_map(shards, mesh=mesh, in_specs=in_specs, out_specs=out_specs, check_vma=False)
```

```python
import jax
import jax.numpy as jnp
from jax import lax
from jax.sharding import PartitionSpec as P


HEADS = 16
HEAD_DIM = 64


EPS = 1e-06
NEG = -1e30
THETA = 10000.0
SCORE_CAP = 4194304


def rotate(field, positions, direction):
    head_width = field.shape[-1]
    half_width = head_width // 2
    frequency = THETA ** (-(jnp.arange(half_width, dtype=jnp.float32) * 2.0) / head_width)
    angles = positions.astype(jnp.float32)[:, None] * frequency[None, :]
    cosine = jnp.cos(angles)[:, None, :]
    sine_part = direction * jnp.sin(angles)[:, None, :]
    former = field[..., :half_width]
    latter = field[..., half_width:]
    return jnp.concatenate(
        [former * cosine - latter * sine_part, latter * cosine + former * sine_part], axis=-1
    )


def normalize(values, gain):
    inverse = lax.rsqrt(jnp.mean(values * values, axis=-1, keepdims=True) + EPS)
    return (values * inverse * gain, inverse)


def normalize_back(values, inverse, gain, upstream):
    unit_rows = values * inverse
    scaled = upstream * gain
    grad_gain = jnp.sum(upstream * unit_rows, axis=(0, 1))
    grad_values = inverse * (
        scaled - unit_rows * jnp.mean(scaled * unit_rows, axis=-1, keepdims=True)
    )
    return (grad_values, grad_gain)


def head_groups(n_slots, q_len, n_heads, k_len):
    q_block = min(q_len, 512)
    per_group = max(1, min(n_heads, SCORE_CAP // (n_slots * q_block * k_len)))
    while n_heads % per_group:
        per_group = per_group - 1
    return (q_block, per_group)


def split_heads(packed, n_groups):
    n_slots, length, n_heads, head_width = packed.shape
    return jnp.moveaxis(
        packed.reshape(n_slots, length, n_groups, n_heads // n_groups, head_width), 2, 0
    )


def join_heads(grouped):
    n_groups, n_slots, length, per_group, head_width = grouped.shape
    return jnp.moveaxis(grouped, 0, 2).reshape(n_slots, length, n_groups * per_group, head_width)


def score_block(q_rows, k_rows, q_pos, k_pos, lengths):
    products = jnp.einsum(
        "sqhe,skhe->shqk", q_rows, k_rows, preferred_element_type=jnp.float32
    ) * q_rows.shape[-1] ** (-0.5)
    causal = (k_pos[None, None, None, :] <= q_pos[None, None, :, None]) & (
        k_pos[None, None, None, :] >= 0
    )
    filled = k_pos[None, None, None, :] < lengths[:, None, None, None]
    return jnp.where(causal & filled, products, NEG)


def attend_forward(queries, keys, values, q_pos, k_pos, lengths):
    n_slots, q_len, n_heads, head_width = queries.shape
    q_block, per_group = head_groups(n_slots, q_len, n_heads, keys.shape[1])
    n_groups = n_heads // per_group
    n_blocks = q_len // q_block
    pos_blocks = q_pos.reshape(n_blocks, q_block)

    def one_group(packed):
        q_group, k_group, v_group = packed
        q_blocks = jnp.moveaxis(
            q_group.reshape(n_slots, n_blocks, q_block, per_group, head_width), 1, 0
        )

        def one_block(streams):
            q_rows, pos_rows = streams
            scores = score_block(q_rows, k_group, pos_rows, k_pos, lengths)
            highest = jnp.max(scores, axis=-1, keepdims=True)
            exponent = jnp.exp(scores - highest)
            totals = jnp.sum(exponent, axis=-1, keepdims=True)
            probabilities = (exponent / totals).astype(jnp.bfloat16)
            mixture = jnp.einsum(
                "shqk,skhe->sqhe", probabilities, v_group, preferred_element_type=jnp.float32
            )
            return (mixture, (highest + jnp.log(totals))[..., 0])

        mixture, log_sums = lax.map(one_block, (q_blocks, pos_blocks))
        return (
            jnp.moveaxis(mixture, 0, 1).reshape(n_slots, q_len, per_group, head_width),
            log_sums,
        )

    grouped = (
        split_heads(queries, n_groups),
        split_heads(keys, n_groups),
        split_heads(values, n_groups),
    )
    mixture, log_sums = lax.map(one_group, grouped)
    return (join_heads(mixture), log_sums)


def attend_backward(queries, keys, values, upstream, row_dots, log_sums, q_pos, k_pos, lengths):
    n_slots, q_len, n_heads, head_width = queries.shape
    q_block, per_group = head_groups(n_slots, q_len, n_heads, keys.shape[1])
    n_groups = n_heads // per_group
    n_blocks = q_len // q_block
    score_scale = head_width ** (-0.5)
    pos_blocks = q_pos.reshape(n_blocks, q_block)
    dot_groups = jnp.moveaxis(row_dots.reshape(n_slots, q_len, n_groups, per_group), 2, 0)

    def blocks_of(grouped):
        return jnp.moveaxis(grouped.reshape((n_slots, n_blocks, q_block) + grouped.shape[2:]), 1, 0)

    def one_group(packed):
        q_group, k_group, v_group, g_group, d_group, l_group = packed

        def one_block(running, streams):
            k_grad, v_grad = running
            q_rows, g_rows, d_rows, l_rows, pos_rows = streams
            scores = score_block(q_rows, k_group, pos_rows, k_pos, lengths)
            probabilities = jnp.exp(scores - l_rows[..., None])
            v_grad = v_grad + jnp.einsum(
                "shqk,sqhe->skhe",
                probabilities.astype(jnp.bfloat16),
                g_rows,
                preferred_element_type=jnp.float32,
            )
            p_grad = jnp.einsum(
                "sqhe,skhe->shqk", g_rows, v_group, preferred_element_type=jnp.float32
            )
            s_grad = (probabilities * (p_grad - jnp.moveaxis(d_rows, 2, 1)[..., None])).astype(
                jnp.bfloat16
            )
            q_grad = (
                jnp.einsum("shqk,skhe->sqhe", s_grad, k_group, preferred_element_type=jnp.float32)
                * score_scale
            )
            k_grad = (
                k_grad
                + jnp.einsum("shqk,sqhe->skhe", s_grad, q_rows, preferred_element_type=jnp.float32)
                * score_scale
            )
            return ((k_grad, v_grad), q_grad)

        empty_grads = jnp.zeros(k_group.shape, jnp.float32)
        streams = (blocks_of(q_group), blocks_of(g_group), blocks_of(d_group), l_group, pos_blocks)
        (k_grad, v_grad), q_grads = lax.scan(one_block, (empty_grads, empty_grads), streams)
        return (
            jnp.moveaxis(q_grads, 0, 1).reshape(n_slots, q_len, per_group, head_width),
            k_grad,
            v_grad,
        )

    grouped = (
        split_heads(queries, n_groups),
        split_heads(keys, n_groups),
        split_heads(values, n_groups),
        split_heads(upstream, n_groups),
        dot_groups,
        log_sums,
    )
    q_grads, k_grads, v_grads = lax.map(one_group, grouped)
    return (join_heads(q_grads), join_heads(k_grads), join_heads(v_grads))


def sums_to_rows(log_sums):
    n_groups, n_blocks, n_slots, per_group, q_block = log_sums.shape
    return jnp.transpose(log_sums, (2, 0, 3, 1, 4)).reshape(
        n_slots, n_groups * per_group, n_blocks * q_block
    )


def rows_to_sums(rows, k_len):
    n_slots, n_heads, q_len = rows.shape
    q_block, per_group = head_groups(n_slots, q_len, n_heads, k_len)
    grouped = rows.reshape(n_slots, n_heads // per_group, per_group, q_len // q_block, q_block)
    return jnp.transpose(grouped, (1, 3, 0, 2, 4))


GROUP = ("fsdp", "ctx")


def gather_blocks(pieces):
    packed = jnp.concatenate(pieces, axis=0)
    gathered = lax.all_gather(packed, GROUP, axis=0, tiled=False)
    fulls, offset = [], 0
    for piece in pieces:
        fulls.append(gathered[:, offset : offset + piece.shape[0], :])
        offset += piece.shape[0]
    return fulls


def rep_sum(x):
    n_rep = lax.axis_size("rep")
    if n_rep != 4:
        return lax.psum(x, "rep")
    me = lax.axis_index("rep")
    folded = (x.astype(jnp.float32) + lax.ppermute(x, "rep", [(0, 1), (3, 2)]).astype(jnp.float32)).astype(x.dtype)
    total = (
        folded.astype(jnp.float32) + lax.ppermute(folded, "rep", [(1, 2), (2, 1)]).astype(jnp.float32)
    ).astype(x.dtype)
    sent_out = lax.ppermute(total, "rep", [(1, 0), (2, 3)])
    return jnp.where((me == 0) | (me == 3), sent_out, total)


def scatter_blocks(blocks, by_permutes):
    packed = jnp.concatenate(blocks, axis=1).astype(jnp.bfloat16)
    summed = lax.psum_scatter(packed, GROUP, scatter_dimension=0, tiled=True)
    summed = (rep_sum(summed) if by_permutes else lax.psum(summed, "rep"))[0].astype(jnp.float32)
    parts, offset = [], 0
    for block in blocks:
        parts.append(summed[offset : offset + block.shape[1], :])
        offset += block.shape[1]
    return parts


def gain_block(first, second, width):
    lead = first.shape[:-1]
    row = jnp.concatenate([first, second], axis=-1)
    row = jnp.pad(row, [(0, 0)] * len(lead) + [(0, width - row.shape[-1])])
    return jnp.pad(row[..., None, :], [(0, 0)] * len(lead) + [(0, 7), (0, 0)])


def shards(
    tokens,
    initial_layer_values,
    cotangent,
    lengths,
    w_query,
    w_key,
    w_value,
    w_out,
    w_gate,
    w_up,
    w_down,
    gain_attn,
    gain_mlp,
):
    n_slots, slot_rows, model_width = tokens.shape
    n_ctx = lax.axis_size("ctx")
    n_group = lax.axis_size("fsdp") * n_ctx
    own_rows = gain_attn.shape[0]
    ff_width = w_gate.shape[1]
    attn_width = w_query.shape[1]
    qkv_width = 3 * attn_width
    (qkv_blocks, gain_rows) = gather_blocks(
        [
            jnp.concatenate([w_query, w_key, w_value], axis=1),
            gain_block(gain_attn, gain_mlp, qkv_width),
        ]
    )
    full_qkv = qkv_blocks.reshape(n_group * own_rows, qkv_width)
    full_gain_attn = gain_rows[:, 0, :own_rows].reshape(-1)
    full_gain_mlp = gain_rows[:, 0, own_rows : 2 * own_rows].reshape(-1)
    out_blocks, down_blocks = gather_blocks([w_out, w_down])
    full_out = out_blocks.reshape(-1, model_width)
    full_down = down_blocks.reshape(-1, model_width)
    (gu_blocks,) = gather_blocks([jnp.concatenate([w_gate, w_up], axis=1)])
    full_gu = gu_blocks.reshape(n_group * own_rows, 2 * ff_width)
    ctx_index = lax.axis_index("ctx")
    q_pos = ctx_index * slot_rows + jnp.arange(slot_rows)
    live_rows = q_pos[None, :] < lengths[:, None]
    head_shape = (n_slots, slot_rows, HEADS, HEAD_DIM)
    paired = n_ctx == 2
    if paired:
        other_tokens = lax.ppermute(tokens, "ctx", [(0, 1), (1, 0)])
        other_first = lax.ppermute(initial_layer_values, "ctx", [(0, 1)])
        other_pos = (1 - ctx_index) * slot_rows + jnp.arange(slot_rows)
    inputs = tokens.astype(jnp.float32)
    attn_scale = full_gain_attn.astype(jnp.float32)
    mlp_scale = full_gain_mlp.astype(jnp.float32)

    def project(chunk_tokens, chunk_first, chunk_pos):
        chunk_normed, chunk_inv = normalize(chunk_tokens.astype(jnp.float32), attn_scale)
        chunk_low = chunk_normed.astype(jnp.bfloat16)
        qkv_pre = jnp.einsum(
            "srd,de->sre", chunk_low, full_qkv, preferred_element_type=jnp.float32
        )
        q_pre = qkv_pre[..., :attn_width]
        k_pre = qkv_pre[..., attn_width : 2 * attn_width]
        v_pre = qkv_pre[..., 2 * attn_width :]
        chunk_q = rotate(q_pre.reshape(head_shape), chunk_pos, 1.0).astype(jnp.bfloat16)
        chunk_k = rotate(k_pre.reshape(head_shape), chunk_pos, 1.0).astype(jnp.bfloat16)
        chunk_v = (
            (0.5 * v_pre + 0.5 * chunk_first.astype(jnp.float32))
            .astype(jnp.bfloat16)
            .reshape(head_shape)
        )
        return chunk_low, chunk_inv, chunk_q, chunk_k, chunk_v

    normed_low, inv_attn, queries, keys, values = project(tokens, initial_layer_values, q_pos)
    if paired:
        _, _, other_q, other_k, other_v = project(other_tokens, other_first, other_pos)
        slot_k = jnp.concatenate([other_k, keys], axis=1)
        slot_v = jnp.concatenate([other_v, values], axis=1)
        k_pos = jnp.concatenate([other_pos, q_pos])
    else:
        slot_k, slot_v = (
            lax.all_gather(keys, "ctx", axis=1, tiled=True),
            lax.all_gather(values, "ctx", axis=1, tiled=True),
        )
        k_pos = jnp.arange(n_ctx * slot_rows)
    attn_raw, attn_lse = attend_forward(queries, slot_k, slot_v, q_pos, k_pos, lengths)
    attended = attn_raw.astype(jnp.bfloat16)
    att_flat = attended.reshape(n_slots, slot_rows, model_width)
    branch = jnp.einsum("sre,ed->srd", att_flat, full_out, preferred_element_type=jnp.float32)
    residual = inputs + branch
    normed_mlp, inv_mlp = normalize(residual, mlp_scale)
    mlp_low = normed_mlp.astype(jnp.bfloat16)
    gu_proj = jnp.einsum("srd,df->srf", mlp_low, full_gu, preferred_element_type=jnp.float32)
    gate_proj = gu_proj[..., :ff_width]
    up_proj = gu_proj[..., ff_width:]
    sigmoid_gate = jax.nn.sigmoid(gate_proj)
    hidden = (gate_proj * sigmoid_gate * up_proj).astype(jnp.bfloat16)
    final = residual + jnp.einsum(
        "srf,fd->srd", hidden, full_down, preferred_element_type=jnp.float32
    )
    output = jnp.where(live_rows[..., None], final, 0.0).astype(jnp.bfloat16)
    output_gradient = jnp.where(live_rows[..., None], cotangent.astype(jnp.float32), 0.0)
    g_low = output_gradient.astype(jnp.bfloat16)
    grad_down = jnp.einsum("srf,srd->fd", hidden, g_low, preferred_element_type=jnp.float32)
    g_hidden = jnp.einsum("srd,fd->srf", g_low, full_down, preferred_element_type=jnp.float32)
    gate_gradient = (
        g_hidden * up_proj * sigmoid_gate * (1.0 + gate_proj * (1.0 - sigmoid_gate))
    ).astype(jnp.bfloat16)
    up_gradient = (g_hidden * gate_proj * sigmoid_gate).astype(jnp.bfloat16)
    gu_gradient = jnp.concatenate([gate_gradient, up_gradient], axis=-1)
    grad_gu = jnp.einsum("srd,srf->df", mlp_low, gu_gradient, preferred_element_type=jnp.float32)
    g_normed_mlp = jnp.einsum(
        "srf,df->srd", gu_gradient, full_gu, preferred_element_type=jnp.float32
    )
    g_mlp_in, grad_gain_mlp = normalize_back(residual, inv_mlp, mlp_scale, g_normed_mlp)
    g_residual = output_gradient + g_mlp_in
    g_branch = g_residual.astype(jnp.bfloat16)
    grad_out = jnp.einsum("sre,srd->ed", att_flat, g_branch, preferred_element_type=jnp.float32)
    gu_block = grad_gu.reshape(n_group, own_rows, 2 * ff_width).astype(jnp.bfloat16)
    od_blocks = [
        grad_out.reshape(n_group, -1, model_width).astype(jnp.bfloat16),
        grad_down.reshape(n_group, -1, model_width).astype(jnp.bfloat16),
    ]
    g_attended = (
        jnp.einsum("srd,ed->sre", g_branch, full_out, preferred_element_type=jnp.float32)
        .astype(jnp.bfloat16)
        .reshape(head_shape)
    )
    gu_block, od_blocks, g_attended = lax.optimization_barrier((gu_block, od_blocks, g_attended))
    (part_gu,) = scatter_blocks([gu_block], True)
    part_out, part_down = scatter_blocks(od_blocks, True)
    row_dots = jnp.sum(g_attended.astype(jnp.float32) * attended.astype(jnp.float32), axis=-1)
    if paired:
        lse_rows = sums_to_rows(attn_lse)
        later_g, later_dots, later_lse = lax.ppermute(
            (g_attended, row_dots, lse_rows), "ctx", [(1, 0)]
        )
        g_queries, g_keys, g_values = attend_backward(
            queries, keys, values, g_attended, row_dots,
            rows_to_sums(lse_rows, slot_rows), q_pos, q_pos, lengths,
        )
        later = ctx_index == 1
        pick = lambda mine, theirs: jnp.where(later, mine, theirs)
        cross_q, cross_dq_k, cross_dq_v = (
            pick(queries, other_q), pick(other_k, keys), pick(other_v, values)
        )
        cross_g = pick(g_attended, later_g)
        cross_dots = pick(row_dots, later_dots)
        cross_lse = pick(lse_rows, later_lse)
        cross_qpos = pick(q_pos, other_pos)
        cross_kpos = pick(other_pos, q_pos)
        x_dq, x_dk, x_dv = attend_backward(
            cross_q, cross_dq_k, cross_dq_v, cross_g, cross_dots,
            rows_to_sums(cross_lse, slot_rows), cross_qpos, cross_kpos, lengths,
        )
        g_queries = g_queries + jnp.where(later, x_dq, 0.0)
        g_keys = g_keys + jnp.where(later, 0.0, x_dk)
        g_values = g_values + jnp.where(later, 0.0, x_dv)
    else:
        g_queries, slot_dk, slot_dv = attend_backward(
            queries, slot_k, slot_v, g_attended, row_dots, attn_lse, q_pos, k_pos, lengths
        )
        g_keys, g_values = (
            lax.psum_scatter(
                slot_dk.astype(jnp.bfloat16), "ctx", scatter_dimension=1, tiled=True
            ).astype(jnp.float32),
            lax.psum_scatter(
                slot_dv.astype(jnp.bfloat16), "ctx", scatter_dimension=1, tiled=True
            ).astype(jnp.float32),
        )
    flat_shape = (n_slots, slot_rows, model_width)
    gq_low = rotate(g_queries, q_pos, -1.0).reshape(flat_shape).astype(jnp.bfloat16)
    gk_low = rotate(g_keys, q_pos, -1.0).reshape(flat_shape).astype(jnp.bfloat16)
    gv_rounded = g_values.reshape(flat_shape).astype(jnp.bfloat16).astype(jnp.float32)
    d_first = 0.5 * gv_rounded
    gv_half = d_first.astype(jnp.bfloat16)
    g_qkv = jnp.concatenate([gq_low, gk_low, gv_half], axis=-1)
    grad_qkv = jnp.einsum("srd,sre->de", normed_low, g_qkv, preferred_element_type=jnp.float32)
    g_normed = jnp.einsum("sre,de->srd", g_qkv, full_qkv, preferred_element_type=jnp.float32)
    g_attn_in, grad_gain_attn = normalize_back(inputs, inv_attn, attn_scale, g_normed)
    d_tokens = g_residual + g_attn_in
    part_qkv, part_gains = scatter_blocks(
        [
            grad_qkv.reshape(n_group, own_rows, qkv_width),
            gain_block(
                grad_gain_attn.reshape(n_group, own_rows),
                grad_gain_mlp.reshape(n_group, own_rows),
                qkv_width,
            ),
        ],
        False,
    )
    return (
        output,
        d_tokens,
        d_first,
        part_qkv[:, :attn_width],
        part_qkv[:, attn_width : 2 * attn_width],
        part_qkv[:, 2 * attn_width :],
        part_out,
        part_gu[:, :ff_width],
        part_gu[:, ff_width:],
        part_down,
        part_gains[0, :own_rows],
        part_gains[0, own_rows : 2 * own_rows],
    )


def solution(mesh):
    in_specs = (
        P(("rep", "fsdp"), "ctx", None),
        P(("rep", "fsdp"), "ctx", None),
        P(("rep", "fsdp"), "ctx", None),
        P(("rep", "fsdp")),
        P(("fsdp", "ctx"), None),
        P(("fsdp", "ctx"), None),
        P(("fsdp", "ctx"), None),
        P(("fsdp", "ctx"), None),
        P(("fsdp", "ctx"), None),
        P(("fsdp", "ctx"), None),
        P(("fsdp", "ctx"), None),
        P(("fsdp", "ctx")),
        P(("fsdp", "ctx")),
    )
    out_specs = (
        P(("rep", "fsdp"), "ctx", None),
        P(("rep", "fsdp"), "ctx", None),
        P(("rep", "fsdp"), "ctx", None),
        P(("fsdp", "ctx"), None),
        P(("fsdp", "ctx"), None),
        P(("fsdp", "ctx"), None),
        P(("fsdp", "ctx"), None),
        P(("fsdp", "ctx"), None),
        P(("fsdp", "ctx"), None),
        P(("fsdp", "ctx"), None),
        P(("fsdp", "ctx")),
        P(("fsdp", "ctx")),
    )

    return jax.shard_map(shards, mesh=mesh, in_specs=in_specs, out_specs=out_specs, check_vma=False)
```

```python
import jax
import jax.numpy as jnp
from jax import lax
from jax.sharding import PartitionSpec as P


HEADS = 16
HEAD_DIM = 64


EPS = 1e-06
NEG = -1e30
THETA = 10000.0
SCORE_CAP = 4194304


def rotate(field, positions, direction):
    head_width = field.shape[-1]
    half_width = head_width // 2
    frequency = THETA ** (-(jnp.arange(half_width, dtype=jnp.float32) * 2.0) / head_width)
    angles = positions.astype(jnp.float32)[:, None] * frequency[None, :]
    cosine = jnp.cos(angles)[:, None, :]
    sine_part = direction * jnp.sin(angles)[:, None, :]
    former = field[..., :half_width]
    latter = field[..., half_width:]
    return jnp.concatenate(
        [former * cosine - latter * sine_part, latter * cosine + former * sine_part], axis=-1
    )


def normalize(values, gain):
    inverse = lax.rsqrt(jnp.mean(values * values, axis=-1, keepdims=True) + EPS)
    return (values * inverse * gain, inverse)


def normalize_back(values, inverse, gain, upstream):
    unit_rows = values * inverse
    scaled = upstream * gain
    grad_gain = jnp.sum(upstream * unit_rows, axis=(0, 1))
    grad_values = inverse * (
        scaled - unit_rows * jnp.mean(scaled * unit_rows, axis=-1, keepdims=True)
    )
    return (grad_values, grad_gain)


def head_groups(n_slots, q_len, n_heads, k_len):
    q_block = min(q_len, 512)
    per_group = max(1, min(n_heads, SCORE_CAP // (n_slots * q_block * k_len)))
    while n_heads % per_group:
        per_group = per_group - 1
    return (q_block, per_group)


def split_heads(packed, n_groups):
    n_slots, length, n_heads, head_width = packed.shape
    return jnp.moveaxis(
        packed.reshape(n_slots, length, n_groups, n_heads // n_groups, head_width), 2, 0
    )


def join_heads(grouped):
    n_groups, n_slots, length, per_group, head_width = grouped.shape
    return jnp.moveaxis(grouped, 0, 2).reshape(n_slots, length, n_groups * per_group, head_width)


def score_block(q_rows, k_rows, q_pos, k_pos, lengths):
    products = jnp.einsum(
        "sqhe,skhe->shqk", q_rows, k_rows, preferred_element_type=jnp.float32
    ) * q_rows.shape[-1] ** (-0.5)
    causal = (k_pos[None, None, None, :] <= q_pos[None, None, :, None]) & (
        k_pos[None, None, None, :] >= 0
    )
    filled = k_pos[None, None, None, :] < lengths[:, None, None, None]
    return jnp.where(causal & filled, products, NEG)


def attend_forward(queries, keys, values, q_pos, k_pos, lengths):
    n_slots, q_len, n_heads, head_width = queries.shape
    q_block, per_group = head_groups(n_slots, q_len, n_heads, keys.shape[1])
    n_groups = n_heads // per_group
    n_blocks = q_len // q_block
    pos_blocks = q_pos.reshape(n_blocks, q_block)

    def one_group(packed):
        q_group, k_group, v_group = packed
        q_blocks = jnp.moveaxis(
            q_group.reshape(n_slots, n_blocks, q_block, per_group, head_width), 1, 0
        )

        def one_block(streams):
            q_rows, pos_rows = streams
            scores = score_block(q_rows, k_group, pos_rows, k_pos, lengths)
            highest = jnp.max(scores, axis=-1, keepdims=True)
            exponent = jnp.exp(scores - highest)
            totals = jnp.sum(exponent, axis=-1, keepdims=True)
            probabilities = (exponent / totals).astype(jnp.bfloat16)
            mixture = jnp.einsum(
                "shqk,skhe->sqhe", probabilities, v_group, preferred_element_type=jnp.float32
            )
            return (mixture, (highest + jnp.log(totals))[..., 0])

        mixture, log_sums = lax.map(one_block, (q_blocks, pos_blocks))
        return (
            jnp.moveaxis(mixture, 0, 1).reshape(n_slots, q_len, per_group, head_width),
            log_sums,
        )

    grouped = (
        split_heads(queries, n_groups),
        split_heads(keys, n_groups),
        split_heads(values, n_groups),
    )
    mixture, log_sums = lax.map(one_group, grouped)
    return (join_heads(mixture), log_sums)


def attend_backward(queries, keys, values, upstream, row_dots, log_sums, q_pos, k_pos, lengths):
    n_slots, q_len, n_heads, head_width = queries.shape
    q_block, per_group = head_groups(n_slots, q_len, n_heads, keys.shape[1])
    n_groups = n_heads // per_group
    n_blocks = q_len // q_block
    score_scale = head_width ** (-0.5)
    pos_blocks = q_pos.reshape(n_blocks, q_block)
    dot_groups = jnp.moveaxis(row_dots.reshape(n_slots, q_len, n_groups, per_group), 2, 0)

    def blocks_of(grouped):
        return jnp.moveaxis(grouped.reshape((n_slots, n_blocks, q_block) + grouped.shape[2:]), 1, 0)

    def one_group(packed):
        q_group, k_group, v_group, g_group, d_group, l_group = packed

        def one_block(running, streams):
            k_grad, v_grad = running
            q_rows, g_rows, d_rows, l_rows, pos_rows = streams
            scores = score_block(q_rows, k_group, pos_rows, k_pos, lengths)
            probabilities = jnp.exp(scores - l_rows[..., None])
            v_grad = v_grad + jnp.einsum(
                "shqk,sqhe->skhe",
                probabilities.astype(jnp.bfloat16),
                g_rows,
                preferred_element_type=jnp.float32,
            )
            p_grad = jnp.einsum(
                "sqhe,skhe->shqk", g_rows, v_group, preferred_element_type=jnp.float32
            )
            s_grad = (probabilities * (p_grad - jnp.moveaxis(d_rows, 2, 1)[..., None])).astype(
                jnp.bfloat16
            )
            q_grad = (
                jnp.einsum("shqk,skhe->sqhe", s_grad, k_group, preferred_element_type=jnp.float32)
                * score_scale
            )
            k_grad = (
                k_grad
                + jnp.einsum("shqk,sqhe->skhe", s_grad, q_rows, preferred_element_type=jnp.float32)
                * score_scale
            )
            return ((k_grad, v_grad), q_grad)

        empty_grads = jnp.zeros(k_group.shape, jnp.float32)
        streams = (blocks_of(q_group), blocks_of(g_group), blocks_of(d_group), l_group, pos_blocks)
        (k_grad, v_grad), q_grads = lax.scan(one_block, (empty_grads, empty_grads), streams)
        return (
            jnp.moveaxis(q_grads, 0, 1).reshape(n_slots, q_len, per_group, head_width),
            k_grad,
            v_grad,
        )

    grouped = (
        split_heads(queries, n_groups),
        split_heads(keys, n_groups),
        split_heads(values, n_groups),
        split_heads(upstream, n_groups),
        dot_groups,
        log_sums,
    )
    q_grads, k_grads, v_grads = lax.map(one_group, grouped)
    return (join_heads(q_grads), join_heads(k_grads), join_heads(v_grads))


def sums_to_rows(log_sums):
    n_groups, n_blocks, n_slots, per_group, q_block = log_sums.shape
    return jnp.transpose(log_sums, (2, 0, 3, 1, 4)).reshape(
        n_slots, n_groups * per_group, n_blocks * q_block
    )


def rows_to_sums(rows, k_len):
    n_slots, n_heads, q_len = rows.shape
    q_block, per_group = head_groups(n_slots, q_len, n_heads, k_len)
    grouped = rows.reshape(n_slots, n_heads // per_group, per_group, q_len // q_block, q_block)
    return jnp.transpose(grouped, (1, 3, 0, 2, 4))


GROUP = ("fsdp", "ctx")


def gather_blocks(pieces):
    packed = jnp.concatenate(pieces, axis=0)
    gathered = lax.all_gather(packed, GROUP, axis=0, tiled=False)
    fulls, offset = [], 0
    for piece in pieces:
        fulls.append(gathered[:, offset : offset + piece.shape[0], :])
        offset += piece.shape[0]
    return fulls


def rep_sum(x):
    n_rep = lax.axis_size("rep")
    if n_rep != 4:
        return lax.psum(x, "rep")
    me = lax.axis_index("rep")
    folded = (x.astype(jnp.float32) + lax.ppermute(x, "rep", [(0, 1), (3, 2)]).astype(jnp.float32)).astype(x.dtype)
    total = (
        folded.astype(jnp.float32) + lax.ppermute(folded, "rep", [(1, 2), (2, 1)]).astype(jnp.float32)
    ).astype(x.dtype)
    sent_out = lax.ppermute(total, "rep", [(1, 0), (2, 3)])
    return jnp.where((me == 0) | (me == 3), sent_out, total)


def scatter_blocks(blocks, by_permutes):
    packed = jnp.concatenate(blocks, axis=1).astype(jnp.bfloat16)
    summed = lax.psum_scatter(packed, GROUP, scatter_dimension=0, tiled=True)
    summed = (rep_sum(summed) if by_permutes else lax.psum(summed, "rep"))[0].astype(jnp.float32)
    parts, offset = [], 0
    for block in blocks:
        parts.append(summed[offset : offset + block.shape[1], :])
        offset += block.shape[1]
    return parts


def gain_block(first, second, width):
    lead = first.shape[:-1]
    row = jnp.concatenate([first, second], axis=-1)
    row = jnp.pad(row, [(0, 0)] * len(lead) + [(0, width - row.shape[-1])])
    return jnp.pad(row[..., None, :], [(0, 0)] * len(lead) + [(0, 7), (0, 0)])


def shards(
    tokens,
    initial_layer_values,
    cotangent,
    lengths,
    w_query,
    w_key,
    w_value,
    w_out,
    w_gate,
    w_up,
    w_down,
    gain_attn,
    gain_mlp,
):
    n_slots, slot_rows, model_width = tokens.shape
    n_ctx = lax.axis_size("ctx")
    n_group = lax.axis_size("fsdp") * n_ctx
    own_rows = gain_attn.shape[0]
    ff_width = w_gate.shape[1]
    attn_width = w_query.shape[1]
    qkv_width = 3 * attn_width
    (qkv_blocks, gain_rows) = gather_blocks(
        [
            jnp.concatenate([w_query, w_key, w_value], axis=1),
            gain_block(gain_attn, gain_mlp, qkv_width),
        ]
    )
    full_qkv = qkv_blocks.reshape(n_group * own_rows, qkv_width)
    full_gain_attn = gain_rows[:, 0, :own_rows].reshape(-1)
    full_gain_mlp = gain_rows[:, 0, own_rows : 2 * own_rows].reshape(-1)
    out_blocks, down_blocks = gather_blocks([w_out, w_down])
    full_out = out_blocks.reshape(-1, model_width)
    full_down = down_blocks.reshape(-1, model_width)
    (gu_blocks,) = gather_blocks([jnp.concatenate([w_gate, w_up], axis=1)])
    full_gu = gu_blocks.reshape(n_group * own_rows, 2 * ff_width)
    ctx_index = lax.axis_index("ctx")
    q_pos = ctx_index * slot_rows + jnp.arange(slot_rows)
    live_rows = q_pos[None, :] < lengths[:, None]
    head_shape = (n_slots, slot_rows, HEADS, HEAD_DIM)
    paired = n_ctx == 2
    if paired:
        other_tokens = lax.ppermute(tokens, "ctx", [(0, 1), (1, 0)])
        other_first = lax.ppermute(initial_layer_values, "ctx", [(0, 1)])
        other_pos = (1 - ctx_index) * slot_rows + jnp.arange(slot_rows)
    inputs = tokens.astype(jnp.float32)
    attn_scale = full_gain_attn.astype(jnp.float32)
    mlp_scale = full_gain_mlp.astype(jnp.float32)

    def project(chunk_tokens, chunk_first, chunk_pos):
        chunk_normed, chunk_inv = normalize(chunk_tokens.astype(jnp.float32), attn_scale)
        chunk_low = chunk_normed.astype(jnp.bfloat16)
        qkv_pre = jnp.einsum(
            "srd,de->sre", chunk_low, full_qkv, preferred_element_type=jnp.float32
        )
        q_pre = qkv_pre[..., :attn_width]
        k_pre = qkv_pre[..., attn_width : 2 * attn_width]
        v_pre = qkv_pre[..., 2 * attn_width :]
        chunk_q = rotate(q_pre.reshape(head_shape), chunk_pos, 1.0).astype(jnp.bfloat16)
        chunk_k = rotate(k_pre.reshape(head_shape), chunk_pos, 1.0).astype(jnp.bfloat16)
        chunk_v = (
            (0.5 * v_pre + 0.5 * chunk_first.astype(jnp.float32))
            .astype(jnp.bfloat16)
            .reshape(head_shape)
        )
        return chunk_low, chunk_inv, chunk_q, chunk_k, chunk_v

    normed_low, inv_attn, queries, keys, values = project(tokens, initial_layer_values, q_pos)
    if paired:
        _, _, other_q, other_k, other_v = project(other_tokens, other_first, other_pos)
        slot_k = jnp.concatenate([other_k, keys], axis=1)
        slot_v = jnp.concatenate([other_v, values], axis=1)
        k_pos = jnp.concatenate([other_pos, q_pos])
    else:
        slot_k, slot_v = (
            lax.all_gather(keys, "ctx", axis=1, tiled=True),
            lax.all_gather(values, "ctx", axis=1, tiled=True),
        )
        k_pos = jnp.arange(n_ctx * slot_rows)
    attn_raw, attn_lse = attend_forward(queries, slot_k, slot_v, q_pos, k_pos, lengths)
    attended = attn_raw.astype(jnp.bfloat16)
    att_flat = attended.reshape(n_slots, slot_rows, model_width)
    branch = jnp.einsum("sre,ed->srd", att_flat, full_out, preferred_element_type=jnp.float32)
    residual = inputs + branch
    normed_mlp, inv_mlp = normalize(residual, mlp_scale)
    mlp_low = normed_mlp.astype(jnp.bfloat16)
    gu_proj = jnp.einsum("srd,df->srf", mlp_low, full_gu, preferred_element_type=jnp.float32)
    gate_proj = gu_proj[..., :ff_width]
    up_proj = gu_proj[..., ff_width:]
    sigmoid_gate = jax.nn.sigmoid(gate_proj)
    hidden = (gate_proj * sigmoid_gate * up_proj).astype(jnp.bfloat16)
    final = residual + jnp.einsum(
        "srf,fd->srd", hidden, full_down, preferred_element_type=jnp.float32
    )
    output = jnp.where(live_rows[..., None], final, 0.0).astype(jnp.bfloat16)
    output_gradient = jnp.where(live_rows[..., None], cotangent.astype(jnp.float32), 0.0)
    g_low = output_gradient.astype(jnp.bfloat16)
    grad_down = jnp.einsum("srf,srd->fd", hidden, g_low, preferred_element_type=jnp.float32)
    (part_down,) = scatter_blocks(
        [grad_down.reshape(n_group, -1, model_width).astype(jnp.bfloat16)], True
    )
    g_hidden = jnp.einsum("srd,fd->srf", g_low, full_down, preferred_element_type=jnp.float32)
    gate_gradient = (
        g_hidden * up_proj * sigmoid_gate * (1.0 + gate_proj * (1.0 - sigmoid_gate))
    ).astype(jnp.bfloat16)
    up_gradient = (g_hidden * gate_proj * sigmoid_gate).astype(jnp.bfloat16)
    gu_gradient = jnp.concatenate([gate_gradient, up_gradient], axis=-1)
    grad_gu = jnp.einsum("srd,srf->df", mlp_low, gu_gradient, preferred_element_type=jnp.float32)
    g_normed_mlp = jnp.einsum(
        "srf,df->srd", gu_gradient, full_gu, preferred_element_type=jnp.float32
    )
    g_mlp_in, grad_gain_mlp = normalize_back(residual, inv_mlp, mlp_scale, g_normed_mlp)
    g_residual = output_gradient + g_mlp_in
    g_branch = g_residual.astype(jnp.bfloat16)
    grad_out = jnp.einsum(
        "sre,srd->ed", att_flat, g_branch, preferred_element_type=jnp.float32
    )
    ogu_block = (
        jnp.concatenate([grad_out, grad_gu], axis=1)
        .reshape(n_group, own_rows, model_width + 2 * ff_width)
        .astype(jnp.bfloat16)
    )
    g_attended = (
        jnp.einsum("srd,ed->sre", g_branch, full_out, preferred_element_type=jnp.float32)
        .astype(jnp.bfloat16)
        .reshape(head_shape)
    )
    (part_ogu,) = scatter_blocks([ogu_block], True)
    row_dots = jnp.sum(g_attended.astype(jnp.float32) * attended.astype(jnp.float32), axis=-1)
    if paired:
        lse_rows = sums_to_rows(attn_lse)
        later_g, later_dots, later_lse = lax.ppermute(
            (g_attended, row_dots, lse_rows), "ctx", [(1, 0)]
        )
        g_queries, g_keys, g_values = attend_backward(
            queries, keys, values, g_attended, row_dots,
            rows_to_sums(lse_rows, slot_rows), q_pos, q_pos, lengths,
        )
        later = ctx_index == 1
        pick = lambda mine, theirs: jnp.where(later, mine, theirs)
        cross_q, cross_dq_k, cross_dq_v = (
            pick(queries, other_q), pick(other_k, keys), pick(other_v, values)
        )
        cross_g = pick(g_attended, later_g)
        cross_dots = pick(row_dots, later_dots)
        cross_lse = pick(lse_rows, later_lse)
        cross_qpos = pick(q_pos, other_pos)
        cross_kpos = pick(other_pos, q_pos)
        x_dq, x_dk, x_dv = attend_backward(
            cross_q, cross_dq_k, cross_dq_v, cross_g, cross_dots,
            rows_to_sums(cross_lse, slot_rows), cross_qpos, cross_kpos, lengths,
        )
        g_queries = g_queries + jnp.where(later, x_dq, 0.0)
        g_keys = g_keys + jnp.where(later, 0.0, x_dk)
        g_values = g_values + jnp.where(later, 0.0, x_dv)
    else:
        g_queries, slot_dk, slot_dv = attend_backward(
            queries, slot_k, slot_v, g_attended, row_dots, attn_lse, q_pos, k_pos, lengths
        )
        g_keys, g_values = (
            lax.psum_scatter(
                slot_dk.astype(jnp.bfloat16), "ctx", scatter_dimension=1, tiled=True
            ).astype(jnp.float32),
            lax.psum_scatter(
                slot_dv.astype(jnp.bfloat16), "ctx", scatter_dimension=1, tiled=True
            ).astype(jnp.float32),
        )
    flat_shape = (n_slots, slot_rows, model_width)
    gq_low = rotate(g_queries, q_pos, -1.0).reshape(flat_shape).astype(jnp.bfloat16)
    gk_low = rotate(g_keys, q_pos, -1.0).reshape(flat_shape).astype(jnp.bfloat16)
    gv_rounded = g_values.reshape(flat_shape).astype(jnp.bfloat16).astype(jnp.float32)
    d_first = 0.5 * gv_rounded
    gv_half = d_first.astype(jnp.bfloat16)
    g_qkv = jnp.concatenate([gq_low, gk_low, gv_half], axis=-1)
    grad_qkv = jnp.einsum("srd,sre->de", normed_low, g_qkv, preferred_element_type=jnp.float32)
    g_normed = jnp.einsum("sre,de->srd", g_qkv, full_qkv, preferred_element_type=jnp.float32)
    g_attn_in, grad_gain_attn = normalize_back(inputs, inv_attn, attn_scale, g_normed)
    d_tokens = g_residual + g_attn_in
    part_qkv, part_gains = scatter_blocks(
        [
            grad_qkv.reshape(n_group, own_rows, qkv_width),
            gain_block(
                grad_gain_attn.reshape(n_group, own_rows),
                grad_gain_mlp.reshape(n_group, own_rows),
                qkv_width,
            ),
        ],
        False,
    )
    return (
        output,
        d_tokens,
        d_first,
        part_qkv[:, :attn_width],
        part_qkv[:, attn_width : 2 * attn_width],
        part_qkv[:, 2 * attn_width :],
        part_ogu[:, :model_width],
        part_ogu[:, model_width : model_width + ff_width],
        part_ogu[:, model_width + ff_width :],
        part_down,
        part_gains[0, :own_rows],
        part_gains[0, own_rows : 2 * own_rows],
    )


def solution(mesh):
    in_specs = (
        P(("rep", "fsdp"), "ctx", None),
        P(("rep", "fsdp"), "ctx", None),
        P(("rep", "fsdp"), "ctx", None),
        P(("rep", "fsdp")),
        P(("fsdp", "ctx"), None),
        P(("fsdp", "ctx"), None),
        P(("fsdp", "ctx"), None),
        P(("fsdp", "ctx"), None),
        P(("fsdp", "ctx"), None),
        P(("fsdp", "ctx"), None),
        P(("fsdp", "ctx"), None),
        P(("fsdp", "ctx")),
        P(("fsdp", "ctx")),
    )
    out_specs = (
        P(("rep", "fsdp"), "ctx", None),
        P(("rep", "fsdp"), "ctx", None),
        P(("rep", "fsdp"), "ctx", None),
        P(("fsdp", "ctx"), None),
        P(("fsdp", "ctx"), None),
        P(("fsdp", "ctx"), None),
        P(("fsdp", "ctx"), None),
        P(("fsdp", "ctx"), None),
        P(("fsdp", "ctx"), None),
        P(("fsdp", "ctx"), None),
        P(("fsdp", "ctx")),
        P(("fsdp", "ctx")),
    )

    return jax.shard_map(shards, mesh=mesh, in_specs=in_specs, out_specs=out_specs, check_vma=False)
```

```python
import jax
import jax.numpy as jnp
from jax import lax
from jax.sharding import PartitionSpec as P


HEADS = 16
HEAD_DIM = 64


EPS = 1e-06
NEG = -1e30
THETA = 10000.0
SCORE_CAP = 4194304


def rotate(field, positions, direction):
    head_width = field.shape[-1]
    half_width = head_width // 2
    frequency = THETA ** (-(jnp.arange(half_width, dtype=jnp.float32) * 2.0) / head_width)
    angles = positions.astype(jnp.float32)[:, None] * frequency[None, :]
    cosine = jnp.cos(angles)[:, None, :]
    sine_part = direction * jnp.sin(angles)[:, None, :]
    former = field[..., :half_width]
    latter = field[..., half_width:]
    return jnp.concatenate(
        [former * cosine - latter * sine_part, latter * cosine + former * sine_part], axis=-1
    )


def normalize(values, gain):
    inverse = lax.rsqrt(jnp.mean(values * values, axis=-1, keepdims=True) + EPS)
    return (values * inverse * gain, inverse)


def normalize_back(values, inverse, gain, upstream):
    unit_rows = values * inverse
    scaled = upstream * gain
    grad_gain = jnp.sum(upstream * unit_rows, axis=(0, 1))
    grad_values = inverse * (
        scaled - unit_rows * jnp.mean(scaled * unit_rows, axis=-1, keepdims=True)
    )
    return (grad_values, grad_gain)


def head_groups(n_slots, q_len, n_heads, k_len):
    q_block = min(q_len, 512)
    per_group = max(1, min(n_heads, SCORE_CAP // (n_slots * q_block * k_len)))
    while n_heads % per_group:
        per_group = per_group - 1
    return (q_block, per_group)


def split_heads(packed, n_groups):
    n_slots, length, n_heads, head_width = packed.shape
    return jnp.moveaxis(
        packed.reshape(n_slots, length, n_groups, n_heads // n_groups, head_width), 2, 0
    )


def join_heads(grouped):
    n_groups, n_slots, length, per_group, head_width = grouped.shape
    return jnp.moveaxis(grouped, 0, 2).reshape(n_slots, length, n_groups * per_group, head_width)


def score_block(q_rows, k_rows, q_pos, k_pos, lengths):
    products = jnp.einsum(
        "sqhe,skhe->shqk", q_rows, k_rows, preferred_element_type=jnp.float32
    ) * q_rows.shape[-1] ** (-0.5)
    causal = (k_pos[None, None, None, :] <= q_pos[None, None, :, None]) & (
        k_pos[None, None, None, :] >= 0
    )
    filled = k_pos[None, None, None, :] < lengths[:, None, None, None]
    return jnp.where(causal & filled, products, NEG)


def attend_forward(queries, keys, values, q_pos, k_pos, lengths):
    n_slots, q_len, n_heads, head_width = queries.shape
    q_block, per_group = head_groups(n_slots, q_len, n_heads, keys.shape[1])
    n_groups = n_heads // per_group
    n_blocks = q_len // q_block
    pos_blocks = q_pos.reshape(n_blocks, q_block)

    def one_group(packed):
        q_group, k_group, v_group = packed
        q_blocks = jnp.moveaxis(
            q_group.reshape(n_slots, n_blocks, q_block, per_group, head_width), 1, 0
        )

        def one_block(streams):
            q_rows, pos_rows = streams
            scores = score_block(q_rows, k_group, pos_rows, k_pos, lengths)
            highest = jnp.max(scores, axis=-1, keepdims=True)
            exponent = jnp.exp(scores - highest)
            totals = jnp.sum(exponent, axis=-1, keepdims=True)
            probabilities = (exponent / totals).astype(jnp.bfloat16)
            mixture = jnp.einsum(
                "shqk,skhe->sqhe", probabilities, v_group, preferred_element_type=jnp.float32
            )
            return (mixture, (highest + jnp.log(totals))[..., 0])

        mixture, log_sums = lax.map(one_block, (q_blocks, pos_blocks))
        return (
            jnp.moveaxis(mixture, 0, 1).reshape(n_slots, q_len, per_group, head_width),
            log_sums,
        )

    grouped = (
        split_heads(queries, n_groups),
        split_heads(keys, n_groups),
        split_heads(values, n_groups),
    )
    mixture, log_sums = lax.map(one_group, grouped)
    return (join_heads(mixture), log_sums)


def attend_backward(queries, keys, values, upstream, row_dots, log_sums, q_pos, k_pos, lengths):
    n_slots, q_len, n_heads, head_width = queries.shape
    q_block, per_group = head_groups(n_slots, q_len, n_heads, keys.shape[1])
    n_groups = n_heads // per_group
    n_blocks = q_len // q_block
    score_scale = head_width ** (-0.5)
    pos_blocks = q_pos.reshape(n_blocks, q_block)
    dot_groups = jnp.moveaxis(row_dots.reshape(n_slots, q_len, n_groups, per_group), 2, 0)

    def blocks_of(grouped):
        return jnp.moveaxis(grouped.reshape((n_slots, n_blocks, q_block) + grouped.shape[2:]), 1, 0)

    def one_group(packed):
        q_group, k_group, v_group, g_group, d_group, l_group = packed

        def one_block(running, streams):
            k_grad, v_grad = running
            q_rows, g_rows, d_rows, l_rows, pos_rows = streams
            scores = score_block(q_rows, k_group, pos_rows, k_pos, lengths)
            probabilities = jnp.exp(scores - l_rows[..., None])
            v_grad = v_grad + jnp.einsum(
                "shqk,sqhe->skhe",
                probabilities.astype(jnp.bfloat16),
                g_rows,
                preferred_element_type=jnp.float32,
            )
            p_grad = jnp.einsum(
                "sqhe,skhe->shqk", g_rows, v_group, preferred_element_type=jnp.float32
            )
            s_grad = (probabilities * (p_grad - jnp.moveaxis(d_rows, 2, 1)[..., None])).astype(
                jnp.bfloat16
            )
            q_grad = (
                jnp.einsum("shqk,skhe->sqhe", s_grad, k_group, preferred_element_type=jnp.float32)
                * score_scale
            )
            k_grad = (
                k_grad
                + jnp.einsum("shqk,sqhe->skhe", s_grad, q_rows, preferred_element_type=jnp.float32)
                * score_scale
            )
            return ((k_grad, v_grad), q_grad)

        empty_grads = jnp.zeros(k_group.shape, jnp.float32)
        streams = (blocks_of(q_group), blocks_of(g_group), blocks_of(d_group), l_group, pos_blocks)
        (k_grad, v_grad), q_grads = lax.scan(one_block, (empty_grads, empty_grads), streams)
        return (
            jnp.moveaxis(q_grads, 0, 1).reshape(n_slots, q_len, per_group, head_width),
            k_grad,
            v_grad,
        )

    grouped = (
        split_heads(queries, n_groups),
        split_heads(keys, n_groups),
        split_heads(values, n_groups),
        split_heads(upstream, n_groups),
        dot_groups,
        log_sums,
    )
    q_grads, k_grads, v_grads = lax.map(one_group, grouped)
    return (join_heads(q_grads), join_heads(k_grads), join_heads(v_grads))


def sums_to_rows(log_sums):
    n_groups, n_blocks, n_slots, per_group, q_block = log_sums.shape
    return jnp.transpose(log_sums, (2, 0, 3, 1, 4)).reshape(
        n_slots, n_groups * per_group, n_blocks * q_block
    )


def rows_to_sums(rows, k_len):
    n_slots, n_heads, q_len = rows.shape
    q_block, per_group = head_groups(n_slots, q_len, n_heads, k_len)
    grouped = rows.reshape(n_slots, n_heads // per_group, per_group, q_len // q_block, q_block)
    return jnp.transpose(grouped, (1, 3, 0, 2, 4))


GROUP = ("fsdp", "ctx")


def gather_blocks(pieces):
    packed = jnp.concatenate(pieces, axis=0)
    gathered = lax.all_gather(packed, GROUP, axis=0, tiled=False)
    fulls, offset = [], 0
    for piece in pieces:
        fulls.append(gathered[:, offset : offset + piece.shape[0], :])
        offset += piece.shape[0]
    return fulls


def rep_sum(x):
    n_rep = lax.axis_size("rep")
    if n_rep != 4:
        return lax.psum(x, "rep")
    me = lax.axis_index("rep")
    arrived = lax.ppermute(x, "rep", [(0, 1), (3, 2)])
    folded = (x.astype(jnp.float32) + arrived.astype(jnp.float32)).astype(x.dtype)
    arrived = lax.ppermute(folded, "rep", [(1, 2), (2, 1)])
    total = (folded.astype(jnp.float32) + arrived.astype(jnp.float32)).astype(x.dtype)
    sent_out = lax.ppermute(total, "rep", [(1, 0), (2, 3)])
    return jnp.where((me == 0) | (me == 3), sent_out, total)


def scatter_blocks(blocks, by_permutes):
    packed = jnp.concatenate(blocks, axis=1).astype(jnp.bfloat16)
    summed = lax.psum_scatter(packed, GROUP, scatter_dimension=0, tiled=True)
    summed = (rep_sum(summed) if by_permutes else lax.psum(summed, "rep"))[0].astype(jnp.float32)
    parts, offset = [], 0
    for block in blocks:
        parts.append(summed[offset : offset + block.shape[1], :])
        offset += block.shape[1]
    return parts


def gain_block(first, second, width):
    lead = first.shape[:-1]
    row = jnp.concatenate([first, second], axis=-1)
    row = jnp.pad(row, [(0, 0)] * len(lead) + [(0, width - row.shape[-1])])
    return jnp.pad(row[..., None, :], [(0, 0)] * len(lead) + [(0, 7), (0, 0)])


def shards(
    tokens,
    initial_layer_values,
    cotangent,
    lengths,
    w_query,
    w_key,
    w_value,
    w_out,
    w_gate,
    w_up,
    w_down,
    gain_attn,
    gain_mlp,
):
    n_slots, slot_rows, model_width = tokens.shape
    n_ctx = lax.axis_size("ctx")
    n_group = lax.axis_size("fsdp") * n_ctx
    own_rows = gain_attn.shape[0]
    ff_width = w_gate.shape[1]
    attn_width = w_query.shape[1]
    qkv_width = 3 * attn_width
    (qkv_blocks, gain_rows) = gather_blocks(
        [
            jnp.concatenate([w_query, w_key, w_value], axis=1),
            gain_block(gain_attn, gain_mlp, qkv_width),
        ]
    )
    full_qkv = qkv_blocks.reshape(n_group * own_rows, qkv_width)
    full_gain_attn = gain_rows[:, 0, :own_rows].reshape(-1)
    full_gain_mlp = gain_rows[:, 0, own_rows : 2 * own_rows].reshape(-1)
    out_blocks, down_blocks = gather_blocks([w_out, w_down])
    full_out = out_blocks.reshape(-1, model_width)
    full_down = down_blocks.reshape(-1, model_width)
    (gu_blocks,) = gather_blocks([jnp.concatenate([w_gate, w_up], axis=1)])
    full_gu = gu_blocks.reshape(n_group * own_rows, 2 * ff_width)
    ctx_index = lax.axis_index("ctx")
    q_pos = ctx_index * slot_rows + jnp.arange(slot_rows)
    live_rows = q_pos[None, :] < lengths[:, None]
    head_shape = (n_slots, slot_rows, HEADS, HEAD_DIM)
    paired = n_ctx == 2
    if paired:
        other_tokens = lax.ppermute(tokens, "ctx", [(0, 1), (1, 0)])
        other_first = lax.ppermute(initial_layer_values, "ctx", [(0, 1)])
        other_pos = (1 - ctx_index) * slot_rows + jnp.arange(slot_rows)
    inputs = tokens.astype(jnp.float32)
    attn_scale = full_gain_attn.astype(jnp.float32)
    mlp_scale = full_gain_mlp.astype(jnp.float32)

    def project(chunk_tokens, chunk_first, chunk_pos):
        chunk_normed, chunk_inv = normalize(chunk_tokens.astype(jnp.float32), attn_scale)
        chunk_low = chunk_normed.astype(jnp.bfloat16)
        qkv_pre = jnp.einsum(
            "srd,de->sre", chunk_low, full_qkv, preferred_element_type=jnp.float32
        )
        q_pre = qkv_pre[..., :attn_width]
        k_pre = qkv_pre[..., attn_width : 2 * attn_width]
        v_pre = qkv_pre[..., 2 * attn_width :]
        chunk_q = rotate(q_pre.reshape(head_shape), chunk_pos, 1.0).astype(jnp.bfloat16)
        chunk_k = rotate(k_pre.reshape(head_shape), chunk_pos, 1.0).astype(jnp.bfloat16)
        chunk_v = (
            (0.5 * v_pre + 0.5 * chunk_first.astype(jnp.float32))
            .astype(jnp.bfloat16)
            .reshape(head_shape)
        )
        return chunk_low, chunk_inv, chunk_q, chunk_k, chunk_v

    normed_low, inv_attn, queries, keys, values = project(tokens, initial_layer_values, q_pos)
    if paired:
        _, _, other_q, other_k, other_v = project(other_tokens, other_first, other_pos)
        slot_k = jnp.concatenate([other_k, keys], axis=1)
        slot_v = jnp.concatenate([other_v, values], axis=1)
        k_pos = jnp.concatenate([other_pos, q_pos])
    else:
        slot_k, slot_v = (
            lax.all_gather(keys, "ctx", axis=1, tiled=True),
            lax.all_gather(values, "ctx", axis=1, tiled=True),
        )
        k_pos = jnp.arange(n_ctx * slot_rows)
    attn_raw, attn_lse = attend_forward(queries, slot_k, slot_v, q_pos, k_pos, lengths)
    attended = attn_raw.astype(jnp.bfloat16)
    att_flat = attended.reshape(n_slots, slot_rows, model_width)
    branch = jnp.einsum("sre,ed->srd", att_flat, full_out, preferred_element_type=jnp.float32)
    residual = inputs + branch
    normed_mlp, inv_mlp = normalize(residual, mlp_scale)
    mlp_low = normed_mlp.astype(jnp.bfloat16)
    gu_proj = jnp.einsum("srd,df->srf", mlp_low, full_gu, preferred_element_type=jnp.float32)
    gate_proj = gu_proj[..., :ff_width]
    up_proj = gu_proj[..., ff_width:]
    sigmoid_gate = jax.nn.sigmoid(gate_proj)
    hidden = (gate_proj * sigmoid_gate * up_proj).astype(jnp.bfloat16)
    final = residual + jnp.einsum(
        "srf,fd->srd", hidden, full_down, preferred_element_type=jnp.float32
    )
    output = jnp.where(live_rows[..., None], final, 0.0).astype(jnp.bfloat16)
    output_gradient = jnp.where(live_rows[..., None], cotangent.astype(jnp.float32), 0.0)
    g_low = output_gradient.astype(jnp.bfloat16)
    grad_down = jnp.einsum("srf,srd->fd", hidden, g_low, preferred_element_type=jnp.float32)
    (part_down,) = scatter_blocks(
        [grad_down.reshape(n_group, -1, model_width).astype(jnp.bfloat16)], True
    )
    g_hidden = jnp.einsum("srd,fd->srf", g_low, full_down, preferred_element_type=jnp.float32)
    gate_gradient = (
        g_hidden * up_proj * sigmoid_gate * (1.0 + gate_proj * (1.0 - sigmoid_gate))
    ).astype(jnp.bfloat16)
    up_gradient = (g_hidden * gate_proj * sigmoid_gate).astype(jnp.bfloat16)
    gu_gradient = jnp.concatenate([gate_gradient, up_gradient], axis=-1)
    grad_gu = jnp.einsum("srd,srf->df", mlp_low, gu_gradient, preferred_element_type=jnp.float32)
    g_normed_mlp = jnp.einsum(
        "srf,df->srd", gu_gradient, full_gu, preferred_element_type=jnp.float32
    )
    g_mlp_in, grad_gain_mlp = normalize_back(residual, inv_mlp, mlp_scale, g_normed_mlp)
    g_residual = output_gradient + g_mlp_in
    g_branch = g_residual.astype(jnp.bfloat16)
    grad_out = jnp.einsum(
        "sre,srd->ed", att_flat, g_branch, preferred_element_type=jnp.float32
    )
    ogu_block = (
        jnp.concatenate([grad_out, grad_gu], axis=1)
        .reshape(n_group, own_rows, model_width + 2 * ff_width)
        .astype(jnp.bfloat16)
    )
    g_attended = (
        jnp.einsum("srd,ed->sre", g_branch, full_out, preferred_element_type=jnp.float32)
        .astype(jnp.bfloat16)
        .reshape(head_shape)
    )
    (part_ogu,) = scatter_blocks([ogu_block], True)
    row_dots = jnp.sum(g_attended.astype(jnp.float32) * attended.astype(jnp.float32), axis=-1)
    if paired:
        lse_rows = sums_to_rows(attn_lse)
        later_g, later_dots, later_lse = lax.ppermute(
            (g_attended, row_dots, lse_rows), "ctx", [(1, 0)]
        )
        g_queries, g_keys, g_values = attend_backward(
            queries, keys, values, g_attended, row_dots,
            rows_to_sums(lse_rows, slot_rows), q_pos, q_pos, lengths,
        )
        later = ctx_index == 1
        pick = lambda mine, theirs: jnp.where(later, mine, theirs)
        cross_q, cross_dq_k, cross_dq_v = (
            pick(queries, other_q), pick(other_k, keys), pick(other_v, values)
        )
        cross_g = pick(g_attended, later_g)
        cross_dots = pick(row_dots, later_dots)
        cross_lse = pick(lse_rows, later_lse)
        cross_qpos = pick(q_pos, other_pos)
        cross_kpos = pick(other_pos, q_pos)
        x_dq, x_dk, x_dv = attend_backward(
            cross_q, cross_dq_k, cross_dq_v, cross_g, cross_dots,
            rows_to_sums(cross_lse, slot_rows), cross_qpos, cross_kpos, lengths,
        )
        g_queries = g_queries + jnp.where(later, x_dq, 0.0)
        g_keys = g_keys + jnp.where(later, 0.0, x_dk)
        g_values = g_values + jnp.where(later, 0.0, x_dv)
    else:
        g_queries, slot_dk, slot_dv = attend_backward(
            queries, slot_k, slot_v, g_attended, row_dots, attn_lse, q_pos, k_pos, lengths
        )
        g_keys, g_values = (
            lax.psum_scatter(
                slot_dk.astype(jnp.bfloat16), "ctx", scatter_dimension=1, tiled=True
            ).astype(jnp.float32),
            lax.psum_scatter(
                slot_dv.astype(jnp.bfloat16), "ctx", scatter_dimension=1, tiled=True
            ).astype(jnp.float32),
        )
    flat_shape = (n_slots, slot_rows, model_width)
    gq_low = rotate(g_queries, q_pos, -1.0).reshape(flat_shape).astype(jnp.bfloat16)
    gk_low = rotate(g_keys, q_pos, -1.0).reshape(flat_shape).astype(jnp.bfloat16)
    gv_rounded = g_values.reshape(flat_shape).astype(jnp.bfloat16).astype(jnp.float32)
    d_first = 0.5 * gv_rounded
    gv_half = d_first.astype(jnp.bfloat16)
    g_qkv = jnp.concatenate([gq_low, gk_low, gv_half], axis=-1)
    grad_qkv = jnp.einsum("srd,sre->de", normed_low, g_qkv, preferred_element_type=jnp.float32)
    g_normed = jnp.einsum("sre,de->srd", g_qkv, full_qkv, preferred_element_type=jnp.float32)
    g_attn_in, grad_gain_attn = normalize_back(inputs, inv_attn, attn_scale, g_normed)
    d_tokens = g_residual + g_attn_in
    part_qkv, part_gains = scatter_blocks(
        [
            grad_qkv.reshape(n_group, own_rows, qkv_width),
            gain_block(
                grad_gain_attn.reshape(n_group, own_rows),
                grad_gain_mlp.reshape(n_group, own_rows),
                qkv_width,
            ),
        ],
        False,
    )
    return (
        output,
        d_tokens,
        d_first,
        part_qkv[:, :attn_width],
        part_qkv[:, attn_width : 2 * attn_width],
        part_qkv[:, 2 * attn_width :],
        part_ogu[:, :model_width],
        part_ogu[:, model_width : model_width + ff_width],
        part_ogu[:, model_width + ff_width :],
        part_down,
        part_gains[0, :own_rows],
        part_gains[0, own_rows : 2 * own_rows],
    )


def solution(mesh):
    in_specs = (
        P(("rep", "fsdp"), "ctx", None),
        P(("rep", "fsdp"), "ctx", None),
        P(("rep", "fsdp"), "ctx", None),
        P(("rep", "fsdp")),
        P(("fsdp", "ctx"), None),
        P(("fsdp", "ctx"), None),
        P(("fsdp", "ctx"), None),
        P(("fsdp", "ctx"), None),
        P(("fsdp", "ctx"), None),
        P(("fsdp", "ctx"), None),
        P(("fsdp", "ctx"), None),
        P(("fsdp", "ctx")),
        P(("fsdp", "ctx")),
    )
    out_specs = (
        P(("rep", "fsdp"), "ctx", None),
        P(("rep", "fsdp"), "ctx", None),
        P(("rep", "fsdp"), "ctx", None),
        P(("fsdp", "ctx"), None),
        P(("fsdp", "ctx"), None),
        P(("fsdp", "ctx"), None),
        P(("fsdp", "ctx"), None),
        P(("fsdp", "ctx"), None),
        P(("fsdp", "ctx"), None),
        P(("fsdp", "ctx"), None),
        P(("fsdp", "ctx")),
        P(("fsdp", "ctx")),
    )

    return jax.shard_map(shards, mesh=mesh, in_specs=in_specs, out_specs=out_specs, check_vma=False)
```

```python
import functools

import jax
import jax.numpy as jnp
from jax import lax
from jax.experimental import pallas as pl
from jax.sharding import PartitionSpec as P


HEADS = 16
HEAD_DIM = 64


EPS = 1e-06
NEG = -1e30
THETA = 10000.0
SCORE_CAP = 4194304


def rotate(field, positions, direction):
    head_width = field.shape[-1]
    half_width = head_width // 2
    frequency = THETA ** (-(jnp.arange(half_width, dtype=jnp.float32) * 2.0) / head_width)
    angles = positions.astype(jnp.float32)[:, None] * frequency[None, :]
    cosine = jnp.cos(angles)[:, None, :]
    sine_part = direction * jnp.sin(angles)[:, None, :]
    former = field[..., :half_width]
    latter = field[..., half_width:]
    return jnp.concatenate(
        [former * cosine - latter * sine_part, latter * cosine + former * sine_part], axis=-1
    )


def normalize(values, gain):
    inverse = lax.rsqrt(jnp.mean(values * values, axis=-1, keepdims=True) + EPS)
    return (values * inverse * gain, inverse)


def normalize_back(values, inverse, gain, upstream):
    unit_rows = values * inverse
    scaled = upstream * gain
    grad_gain = jnp.sum(upstream * unit_rows, axis=(0, 1))
    grad_values = inverse * (
        scaled - unit_rows * jnp.mean(scaled * unit_rows, axis=-1, keepdims=True)
    )
    return (grad_values, grad_gain)


def head_groups(n_slots, q_len, n_heads, k_len):
    q_block = min(q_len, 512)
    per_group = max(1, min(n_heads, SCORE_CAP // (n_slots * q_block * k_len)))
    while n_heads % per_group:
        per_group = per_group - 1
    return (q_block, per_group)


def split_heads(packed, n_groups):
    n_slots, length, n_heads, head_width = packed.shape
    return jnp.moveaxis(
        packed.reshape(n_slots, length, n_groups, n_heads // n_groups, head_width), 2, 0
    )


def join_heads(grouped):
    n_groups, n_slots, length, per_group, head_width = grouped.shape
    return jnp.moveaxis(grouped, 0, 2).reshape(n_slots, length, n_groups * per_group, head_width)


def score_block(q_rows, k_rows, q_pos, k_pos, lengths):
    products = jnp.einsum(
        "sqhe,skhe->shqk", q_rows, k_rows, preferred_element_type=jnp.float32
    ) * q_rows.shape[-1] ** (-0.5)
    causal = (k_pos[None, None, None, :] <= q_pos[None, None, :, None]) & (
        k_pos[None, None, None, :] >= 0
    )
    filled = k_pos[None, None, None, :] < lengths[:, None, None, None]
    return jnp.where(causal & filled, products, NEG)


def attend_forward(queries, keys, values, q_pos, k_pos, lengths):
    n_slots, q_len, n_heads, head_width = queries.shape
    q_block, per_group = head_groups(n_slots, q_len, n_heads, keys.shape[1])
    n_groups = n_heads // per_group
    n_blocks = q_len // q_block
    pos_blocks = q_pos.reshape(n_blocks, q_block)

    def one_group(packed):
        q_group, k_group, v_group = packed
        q_blocks = jnp.moveaxis(
            q_group.reshape(n_slots, n_blocks, q_block, per_group, head_width), 1, 0
        )

        def one_block(streams):
            q_rows, pos_rows = streams
            scores = score_block(q_rows, k_group, pos_rows, k_pos, lengths)
            highest = jnp.max(scores, axis=-1, keepdims=True)
            exponent = jnp.exp(scores - highest)
            totals = jnp.sum(exponent, axis=-1, keepdims=True)
            probabilities = (exponent / totals).astype(jnp.bfloat16)
            mixture = jnp.einsum(
                "shqk,skhe->sqhe", probabilities, v_group, preferred_element_type=jnp.float32
            )
            return (mixture, (highest + jnp.log(totals))[..., 0])

        mixture, log_sums = lax.map(one_block, (q_blocks, pos_blocks))
        return (
            jnp.moveaxis(mixture, 0, 1).reshape(n_slots, q_len, per_group, head_width),
            log_sums,
        )

    grouped = (
        split_heads(queries, n_groups),
        split_heads(keys, n_groups),
        split_heads(values, n_groups),
    )
    mixture, log_sums = lax.map(one_group, grouped)
    return (join_heads(mixture), log_sums)


def attend_backward(queries, keys, values, upstream, row_dots, log_sums, q_pos, k_pos, lengths):
    n_slots, q_len, n_heads, head_width = queries.shape
    q_block, per_group = head_groups(n_slots, q_len, n_heads, keys.shape[1])
    n_groups = n_heads // per_group
    n_blocks = q_len // q_block
    score_scale = head_width ** (-0.5)
    pos_blocks = q_pos.reshape(n_blocks, q_block)
    dot_groups = jnp.moveaxis(row_dots.reshape(n_slots, q_len, n_groups, per_group), 2, 0)

    def blocks_of(grouped):
        return jnp.moveaxis(grouped.reshape((n_slots, n_blocks, q_block) + grouped.shape[2:]), 1, 0)

    def one_group(packed):
        q_group, k_group, v_group, g_group, d_group, l_group = packed

        def one_block(running, streams):
            k_grad, v_grad = running
            q_rows, g_rows, d_rows, l_rows, pos_rows = streams
            scores = score_block(q_rows, k_group, pos_rows, k_pos, lengths)
            probabilities = jnp.exp(scores - l_rows[..., None])
            v_grad = v_grad + jnp.einsum(
                "shqk,sqhe->skhe",
                probabilities.astype(jnp.bfloat16),
                g_rows,
                preferred_element_type=jnp.float32,
            )
            p_grad = jnp.einsum(
                "sqhe,skhe->shqk", g_rows, v_group, preferred_element_type=jnp.float32
            )
            s_grad = (probabilities * (p_grad - jnp.moveaxis(d_rows, 2, 1)[..., None])).astype(
                jnp.bfloat16
            )
            q_grad = (
                jnp.einsum("shqk,skhe->sqhe", s_grad, k_group, preferred_element_type=jnp.float32)
                * score_scale
            )
            k_grad = (
                k_grad
                + jnp.einsum("shqk,sqhe->skhe", s_grad, q_rows, preferred_element_type=jnp.float32)
                * score_scale
            )
            return ((k_grad, v_grad), q_grad)

        empty_grads = jnp.zeros(k_group.shape, jnp.float32)
        streams = (blocks_of(q_group), blocks_of(g_group), blocks_of(d_group), l_group, pos_blocks)
        (k_grad, v_grad), q_grads = lax.scan(one_block, (empty_grads, empty_grads), streams)
        return (
            jnp.moveaxis(q_grads, 0, 1).reshape(n_slots, q_len, per_group, head_width),
            k_grad,
            v_grad,
        )

    grouped = (
        split_heads(queries, n_groups),
        split_heads(keys, n_groups),
        split_heads(values, n_groups),
        split_heads(upstream, n_groups),
        dot_groups,
        log_sums,
    )
    q_grads, k_grads, v_grads = lax.map(one_group, grouped)
    return (join_heads(q_grads), join_heads(k_grads), join_heads(v_grads))


def sums_to_rows(log_sums):
    n_groups, n_blocks, n_slots, per_group, q_block = log_sums.shape
    return jnp.transpose(log_sums, (2, 0, 3, 1, 4)).reshape(
        n_slots, n_groups * per_group, n_blocks * q_block
    )


FAR = 1 << 30


def _block_backward_kernel(q_ref, k_ref, v_ref, g_ref, lse_ref, dots_ref, qpos_ref, kpos_ref,
                           dq_ref, dk_ref, dv_ref, *, head_width, scale):
    pair = pl.program_id(1)
    allowed = kpos_ref[0] <= qpos_ref[...]
    for j in range(2):
        cols = slice(j * head_width, (j + 1) * head_width)
        q = q_ref[0, :, cols]
        k = k_ref[0, :, cols]
        v = v_ref[0, :, cols]
        g = g_ref[0, :, cols]
        head = 2 * pair + j
        lse = lse_ref[0, pl.ds(head, 1), :]
        dots = dots_ref[0, pl.ds(head, 1), :]
        nt = (((1,), (1,)), ((), ()))
        scores = lax.dot_general(k, q, nt, preferred_element_type=jnp.float32) * scale
        scores = jnp.where(allowed, scores, -1e30)
        probs = jnp.exp(scores - lse)
        dv_ref[0, :, cols] = jnp.dot(probs.astype(jnp.bfloat16), g, preferred_element_type=jnp.float32)
        dprobs = lax.dot_general(v, g, nt, preferred_element_type=jnp.float32)
        dscores = (probs * (dprobs - dots)).astype(jnp.bfloat16)
        dk_ref[0, :, cols] = jnp.dot(dscores, q, preferred_element_type=jnp.float32) * scale
        tn = (((0,), (0,)), ((), ()))
        dq_ref[0, :, cols] = lax.dot_general(dscores, k, tn, preferred_element_type=jnp.float32) * scale


def block_backward(queries, keys, values, upstream, lse_rows, dot_rows, q_pos, k_pos, lengths):
    n_slots, q_len, n_heads, head_width = queries.shape
    k_len = keys.shape[1]
    width = n_heads * head_width
    pair_width = 2 * head_width
    flat = lambda a: a.reshape(a.shape[0], a.shape[1], width)
    kpos = jnp.where(
        (k_pos[None, :] < lengths[:, None]) & (k_pos[None, :] >= 0), k_pos[None, :], FAR
    ).astype(jnp.int32)[..., None]
    qpos = q_pos.astype(jnp.int32)[None, :]
    kernel = functools.partial(_block_backward_kernel, head_width=head_width, scale=head_width ** (-0.5))
    q_spec = pl.BlockSpec((1, q_len, pair_width), lambda s, p: (s, 0, p))
    k_spec = pl.BlockSpec((1, k_len, pair_width), lambda s, p: (s, 0, p))
    row_spec = pl.BlockSpec((1, n_heads, q_len), lambda s, p: (s, 0, 0))
    flops = n_slots * n_heads * 10 * q_len * k_len * head_width
    dq, dk, dv = pl.pallas_call(
        kernel,
        grid=(n_slots, n_heads // 2),
        in_specs=[
            q_spec, k_spec, k_spec, q_spec, row_spec, row_spec,
            pl.BlockSpec((1, q_len), lambda s, p: (0, 0)),
            pl.BlockSpec((1, k_len, 1), lambda s, p: (s, 0, 0)),
        ],
        out_specs=[q_spec, k_spec, k_spec],
        out_shape=[
            jax.ShapeDtypeStruct((n_slots, q_len, width), jnp.float32),
            jax.ShapeDtypeStruct((n_slots, k_len, width), jnp.float32),
            jax.ShapeDtypeStruct((n_slots, k_len, width), jnp.float32),
        ],
        cost_estimate=pl.CostEstimate(
            flops=flops,
            transcendentals=n_slots * n_heads * q_len * k_len,
            bytes_accessed=2 * (2 * q_len + 2 * k_len) * width * n_slots + 4 * (q_len + 2 * k_len) * width * n_slots,
        ),
    )(flat(queries), flat(keys), flat(values), flat(upstream), lse_rows, dot_rows, qpos, kpos)
    shape_q = (n_slots, q_len, n_heads, head_width)
    shape_k = (n_slots, k_len, n_heads, head_width)
    return dq.reshape(shape_q), dk.reshape(shape_k), dv.reshape(shape_k)


GROUP = ("fsdp", "ctx")


def gather_blocks(pieces):
    packed = jnp.concatenate(pieces, axis=0)
    gathered = lax.all_gather(packed, GROUP, axis=0, tiled=False)
    fulls, offset = [], 0
    for piece in pieces:
        fulls.append(gathered[:, offset : offset + piece.shape[0], :])
        offset += piece.shape[0]
    return fulls


def rep_sum(x):
    n_rep = lax.axis_size("rep")
    if n_rep != 4:
        return lax.psum(x, "rep")
    me = lax.axis_index("rep")
    arrived = lax.ppermute(x, "rep", [(0, 1), (3, 2)])
    folded = (x.astype(jnp.float32) + arrived.astype(jnp.float32)).astype(x.dtype)
    arrived = lax.ppermute(folded, "rep", [(1, 2), (2, 1)])
    total = (folded.astype(jnp.float32) + arrived.astype(jnp.float32)).astype(x.dtype)
    sent_out = lax.ppermute(total, "rep", [(1, 0), (2, 3)])
    return jnp.where((me == 0) | (me == 3), sent_out, total)


def scatter_blocks(blocks, by_permutes):
    packed = jnp.concatenate(blocks, axis=1).astype(jnp.bfloat16)
    summed = lax.psum_scatter(packed, GROUP, scatter_dimension=0, tiled=True)
    summed = (rep_sum(summed) if by_permutes else lax.psum(summed, "rep"))[0].astype(jnp.float32)
    parts, offset = [], 0
    for block in blocks:
        parts.append(summed[offset : offset + block.shape[1], :])
        offset += block.shape[1]
    return parts


def gain_block(first, second, width):
    lead = first.shape[:-1]
    row = jnp.concatenate([first, second], axis=-1)
    row = jnp.pad(row, [(0, 0)] * len(lead) + [(0, width - row.shape[-1])])
    return jnp.pad(row[..., None, :], [(0, 0)] * len(lead) + [(0, 7), (0, 0)])


def shards(
    tokens,
    initial_layer_values,
    cotangent,
    lengths,
    w_query,
    w_key,
    w_value,
    w_out,
    w_gate,
    w_up,
    w_down,
    gain_attn,
    gain_mlp,
):
    n_slots, slot_rows, model_width = tokens.shape
    n_ctx = lax.axis_size("ctx")
    n_group = lax.axis_size("fsdp") * n_ctx
    own_rows = gain_attn.shape[0]
    ff_width = w_gate.shape[1]
    attn_width = w_query.shape[1]
    qkv_width = 3 * attn_width
    (qkv_blocks, gain_rows) = gather_blocks(
        [
            jnp.concatenate([w_query, w_key, w_value], axis=1),
            gain_block(gain_attn, gain_mlp, qkv_width),
        ]
    )
    full_qkv = qkv_blocks.reshape(n_group * own_rows, qkv_width)
    full_gain_attn = gain_rows[:, 0, :own_rows].reshape(-1)
    full_gain_mlp = gain_rows[:, 0, own_rows : 2 * own_rows].reshape(-1)
    out_blocks, down_blocks = gather_blocks([w_out, w_down])
    full_out = out_blocks.reshape(-1, model_width)
    full_down = down_blocks.reshape(-1, model_width)
    (gu_blocks,) = gather_blocks([jnp.concatenate([w_gate, w_up], axis=1)])
    full_gu = gu_blocks.reshape(n_group * own_rows, 2 * ff_width)
    ctx_index = lax.axis_index("ctx")
    q_pos = ctx_index * slot_rows + jnp.arange(slot_rows)
    live_rows = q_pos[None, :] < lengths[:, None]
    head_shape = (n_slots, slot_rows, HEADS, HEAD_DIM)
    paired = n_ctx == 2
    if paired:
        other_tokens = lax.ppermute(tokens, "ctx", [(0, 1), (1, 0)])
        other_first = lax.ppermute(initial_layer_values, "ctx", [(0, 1)])
        other_pos = (1 - ctx_index) * slot_rows + jnp.arange(slot_rows)
    inputs = tokens.astype(jnp.float32)
    attn_scale = full_gain_attn.astype(jnp.float32)
    mlp_scale = full_gain_mlp.astype(jnp.float32)

    def project(chunk_tokens, chunk_first, chunk_pos):
        chunk_normed, chunk_inv = normalize(chunk_tokens.astype(jnp.float32), attn_scale)
        chunk_low = chunk_normed.astype(jnp.bfloat16)
        qkv_pre = jnp.einsum(
            "srd,de->sre", chunk_low, full_qkv, preferred_element_type=jnp.float32
        )
        q_pre = qkv_pre[..., :attn_width]
        k_pre = qkv_pre[..., attn_width : 2 * attn_width]
        v_pre = qkv_pre[..., 2 * attn_width :]
        chunk_q = rotate(q_pre.reshape(head_shape), chunk_pos, 1.0).astype(jnp.bfloat16)
        chunk_k = rotate(k_pre.reshape(head_shape), chunk_pos, 1.0).astype(jnp.bfloat16)
        chunk_v = (
            (0.5 * v_pre + 0.5 * chunk_first.astype(jnp.float32))
            .astype(jnp.bfloat16)
            .reshape(head_shape)
        )
        return chunk_low, chunk_inv, chunk_q, chunk_k, chunk_v

    normed_low, inv_attn, queries, keys, values = project(tokens, initial_layer_values, q_pos)
    if paired:
        _, _, other_q, other_k, other_v = project(other_tokens, other_first, other_pos)
        slot_k = jnp.concatenate([other_k, keys], axis=1)
        slot_v = jnp.concatenate([other_v, values], axis=1)
        k_pos = jnp.concatenate([other_pos, q_pos])
    else:
        slot_k, slot_v = (
            lax.all_gather(keys, "ctx", axis=1, tiled=True),
            lax.all_gather(values, "ctx", axis=1, tiled=True),
        )
        k_pos = jnp.arange(n_ctx * slot_rows)
    attn_raw, attn_lse = attend_forward(queries, slot_k, slot_v, q_pos, k_pos, lengths)
    attended = attn_raw.astype(jnp.bfloat16)
    att_flat = attended.reshape(n_slots, slot_rows, model_width)
    branch = jnp.einsum("sre,ed->srd", att_flat, full_out, preferred_element_type=jnp.float32)
    residual = inputs + branch
    normed_mlp, inv_mlp = normalize(residual, mlp_scale)
    mlp_low = normed_mlp.astype(jnp.bfloat16)
    gu_proj = jnp.einsum("srd,df->srf", mlp_low, full_gu, preferred_element_type=jnp.float32)
    gate_proj = gu_proj[..., :ff_width]
    up_proj = gu_proj[..., ff_width:]
    sigmoid_gate = jax.nn.sigmoid(gate_proj)
    hidden = (gate_proj * sigmoid_gate * up_proj).astype(jnp.bfloat16)
    final = residual + jnp.einsum(
        "srf,fd->srd", hidden, full_down, preferred_element_type=jnp.float32
    )
    output = jnp.where(live_rows[..., None], final, 0.0).astype(jnp.bfloat16)
    output_gradient = jnp.where(live_rows[..., None], cotangent.astype(jnp.float32), 0.0)
    g_low = output_gradient.astype(jnp.bfloat16)
    grad_down = jnp.einsum("srf,srd->fd", hidden, g_low, preferred_element_type=jnp.float32)
    (part_down,) = scatter_blocks(
        [grad_down.reshape(n_group, -1, model_width).astype(jnp.bfloat16)], True
    )
    g_hidden = jnp.einsum("srd,fd->srf", g_low, full_down, preferred_element_type=jnp.float32)
    gate_gradient = (
        g_hidden * up_proj * sigmoid_gate * (1.0 + gate_proj * (1.0 - sigmoid_gate))
    ).astype(jnp.bfloat16)
    up_gradient = (g_hidden * gate_proj * sigmoid_gate).astype(jnp.bfloat16)
    gu_gradient = jnp.concatenate([gate_gradient, up_gradient], axis=-1)
    grad_gu = jnp.einsum("srd,srf->df", mlp_low, gu_gradient, preferred_element_type=jnp.float32)
    g_normed_mlp = jnp.einsum(
        "srf,df->srd", gu_gradient, full_gu, preferred_element_type=jnp.float32
    )
    g_mlp_in, grad_gain_mlp = normalize_back(residual, inv_mlp, mlp_scale, g_normed_mlp)
    g_residual = output_gradient + g_mlp_in
    g_branch = g_residual.astype(jnp.bfloat16)
    grad_out = jnp.einsum(
        "sre,srd->ed", att_flat, g_branch, preferred_element_type=jnp.float32
    )
    ogu_block = (
        jnp.concatenate([grad_out, grad_gu], axis=1)
        .reshape(n_group, own_rows, model_width + 2 * ff_width)
        .astype(jnp.bfloat16)
    )
    g_attended = (
        jnp.einsum("srd,ed->sre", g_branch, full_out, preferred_element_type=jnp.float32)
        .astype(jnp.bfloat16)
        .reshape(head_shape)
    )
    (part_ogu,) = scatter_blocks([ogu_block], True)
    row_dots = jnp.sum(g_attended.astype(jnp.float32) * attended.astype(jnp.float32), axis=-1)
    if paired:
        lse_rows = sums_to_rows(attn_lse)
        dot_rows = jnp.transpose(row_dots, (0, 2, 1))
        later_g, later_dots, later_lse = lax.ppermute(
            (g_attended, dot_rows, lse_rows), "ctx", [(1, 0)]
        )
        g_queries, g_keys, g_values = block_backward(
            queries, keys, values, g_attended, lse_rows, dot_rows, q_pos, q_pos, lengths
        )
        later = ctx_index == 1
        pick = lambda mine, theirs: jnp.where(later, mine, theirs)
        x_dq, x_dk, x_dv = block_backward(
            pick(queries, other_q),
            pick(other_k, keys),
            pick(other_v, values),
            pick(g_attended, later_g),
            pick(lse_rows, later_lse),
            pick(dot_rows, later_dots),
            pick(q_pos, other_pos),
            pick(other_pos, q_pos),
            lengths,
        )
        g_queries = g_queries + jnp.where(later, x_dq, 0.0)
        g_keys = g_keys + jnp.where(later, 0.0, x_dk)
        g_values = g_values + jnp.where(later, 0.0, x_dv)
    else:
        g_queries, slot_dk, slot_dv = attend_backward(
            queries, slot_k, slot_v, g_attended, row_dots, attn_lse, q_pos, k_pos, lengths
        )
        g_keys, g_values = (
            lax.psum_scatter(
                slot_dk.astype(jnp.bfloat16), "ctx", scatter_dimension=1, tiled=True
            ).astype(jnp.float32),
            lax.psum_scatter(
                slot_dv.astype(jnp.bfloat16), "ctx", scatter_dimension=1, tiled=True
            ).astype(jnp.float32),
        )
    flat_shape = (n_slots, slot_rows, model_width)
    gq_low = rotate(g_queries, q_pos, -1.0).reshape(flat_shape).astype(jnp.bfloat16)
    gk_low = rotate(g_keys, q_pos, -1.0).reshape(flat_shape).astype(jnp.bfloat16)
    gv_rounded = g_values.reshape(flat_shape).astype(jnp.bfloat16).astype(jnp.float32)
    d_first = 0.5 * gv_rounded
    gv_half = d_first.astype(jnp.bfloat16)
    g_qkv = jnp.concatenate([gq_low, gk_low, gv_half], axis=-1)
    grad_qkv = jnp.einsum("srd,sre->de", normed_low, g_qkv, preferred_element_type=jnp.float32)
    g_normed = jnp.einsum("sre,de->srd", g_qkv, full_qkv, preferred_element_type=jnp.float32)
    g_attn_in, grad_gain_attn = normalize_back(inputs, inv_attn, attn_scale, g_normed)
    d_tokens = g_residual + g_attn_in
    part_qkv, part_gains = scatter_blocks(
        [
            grad_qkv.reshape(n_group, own_rows, qkv_width),
            gain_block(
                grad_gain_attn.reshape(n_group, own_rows),
                grad_gain_mlp.reshape(n_group, own_rows),
                qkv_width,
            ),
        ],
        False,
    )
    return (
        output,
        d_tokens,
        d_first,
        part_qkv[:, :attn_width],
        part_qkv[:, attn_width : 2 * attn_width],
        part_qkv[:, 2 * attn_width :],
        part_ogu[:, :model_width],
        part_ogu[:, model_width : model_width + ff_width],
        part_ogu[:, model_width + ff_width :],
        part_down,
        part_gains[0, :own_rows],
        part_gains[0, own_rows : 2 * own_rows],
    )


def solution(mesh):
    in_specs = (
        P(("rep", "fsdp"), "ctx", None),
        P(("rep", "fsdp"), "ctx", None),
        P(("rep", "fsdp"), "ctx", None),
        P(("rep", "fsdp")),
        P(("fsdp", "ctx"), None),
        P(("fsdp", "ctx"), None),
        P(("fsdp", "ctx"), None),
        P(("fsdp", "ctx"), None),
        P(("fsdp", "ctx"), None),
        P(("fsdp", "ctx"), None),
        P(("fsdp", "ctx"), None),
        P(("fsdp", "ctx")),
        P(("fsdp", "ctx")),
    )
    out_specs = (
        P(("rep", "fsdp"), "ctx", None),
        P(("rep", "fsdp"), "ctx", None),
        P(("rep", "fsdp"), "ctx", None),
        P(("fsdp", "ctx"), None),
        P(("fsdp", "ctx"), None),
        P(("fsdp", "ctx"), None),
        P(("fsdp", "ctx"), None),
        P(("fsdp", "ctx"), None),
        P(("fsdp", "ctx"), None),
        P(("fsdp", "ctx"), None),
        P(("fsdp", "ctx")),
        P(("fsdp", "ctx")),
    )

    return jax.shard_map(shards, mesh=mesh, in_specs=in_specs, out_specs=out_specs, check_vma=False)
```

```python
import functools

import jax
import jax.numpy as jnp
from jax import lax
from jax.experimental import pallas as pl
from jax.sharding import PartitionSpec as P


HEADS = 16
HEAD_DIM = 64


EPS = 1e-06
NEG = -1e30
THETA = 10000.0
SCORE_CAP = 4194304


def rotate(field, positions, direction):
    head_width = field.shape[-1]
    half_width = head_width // 2
    frequency = THETA ** (-(jnp.arange(half_width, dtype=jnp.float32) * 2.0) / head_width)
    angles = positions.astype(jnp.float32)[:, None] * frequency[None, :]
    cosine = jnp.cos(angles)[:, None, :]
    sine_part = direction * jnp.sin(angles)[:, None, :]
    former = field[..., :half_width]
    latter = field[..., half_width:]
    return jnp.concatenate(
        [former * cosine - latter * sine_part, latter * cosine + former * sine_part], axis=-1
    )


def normalize(values, gain):
    inverse = lax.rsqrt(jnp.mean(values * values, axis=-1, keepdims=True) + EPS)
    return (values * inverse * gain, inverse)


def normalize_back(values, inverse, gain, upstream):
    unit_rows = values * inverse
    scaled = upstream * gain
    grad_gain = jnp.sum(upstream * unit_rows, axis=(0, 1))
    grad_values = inverse * (
        scaled - unit_rows * jnp.mean(scaled * unit_rows, axis=-1, keepdims=True)
    )
    return (grad_values, grad_gain)


def head_groups(n_slots, q_len, n_heads, k_len):
    q_block = min(q_len, 512)
    per_group = max(1, min(n_heads, SCORE_CAP // (n_slots * q_block * k_len)))
    while n_heads % per_group:
        per_group = per_group - 1
    return (q_block, per_group)


def split_heads(packed, n_groups):
    n_slots, length, n_heads, head_width = packed.shape
    return jnp.moveaxis(
        packed.reshape(n_slots, length, n_groups, n_heads // n_groups, head_width), 2, 0
    )


def join_heads(grouped):
    n_groups, n_slots, length, per_group, head_width = grouped.shape
    return jnp.moveaxis(grouped, 0, 2).reshape(n_slots, length, n_groups * per_group, head_width)


def score_block(q_rows, k_rows, q_pos, k_pos, lengths):
    products = jnp.einsum(
        "sqhe,skhe->shqk", q_rows, k_rows, preferred_element_type=jnp.float32
    ) * q_rows.shape[-1] ** (-0.5)
    causal = (k_pos[None, None, None, :] <= q_pos[None, None, :, None]) & (
        k_pos[None, None, None, :] >= 0
    )
    filled = k_pos[None, None, None, :] < lengths[:, None, None, None]
    return jnp.where(causal & filled, products, NEG)


def attend_forward(queries, keys, values, q_pos, k_pos, lengths):
    n_slots, q_len, n_heads, head_width = queries.shape
    q_block, per_group = head_groups(n_slots, q_len, n_heads, keys.shape[1])
    n_groups = n_heads // per_group
    n_blocks = q_len // q_block
    pos_blocks = q_pos.reshape(n_blocks, q_block)

    def one_group(packed):
        q_group, k_group, v_group = packed
        q_blocks = jnp.moveaxis(
            q_group.reshape(n_slots, n_blocks, q_block, per_group, head_width), 1, 0
        )

        def one_block(streams):
            q_rows, pos_rows = streams
            scores = score_block(q_rows, k_group, pos_rows, k_pos, lengths)
            highest = jnp.max(scores, axis=-1, keepdims=True)
            exponent = jnp.exp(scores - highest)
            totals = jnp.sum(exponent, axis=-1, keepdims=True)
            probabilities = (exponent / totals).astype(jnp.bfloat16)
            mixture = jnp.einsum(
                "shqk,skhe->sqhe", probabilities, v_group, preferred_element_type=jnp.float32
            )
            return (mixture, (highest + jnp.log(totals))[..., 0])

        mixture, log_sums = lax.map(one_block, (q_blocks, pos_blocks))
        return (
            jnp.moveaxis(mixture, 0, 1).reshape(n_slots, q_len, per_group, head_width),
            log_sums,
        )

    grouped = (
        split_heads(queries, n_groups),
        split_heads(keys, n_groups),
        split_heads(values, n_groups),
    )
    mixture, log_sums = lax.map(one_group, grouped)
    return (join_heads(mixture), log_sums)


def attend_backward(queries, keys, values, upstream, row_dots, log_sums, q_pos, k_pos, lengths):
    n_slots, q_len, n_heads, head_width = queries.shape
    q_block, per_group = head_groups(n_slots, q_len, n_heads, keys.shape[1])
    n_groups = n_heads // per_group
    n_blocks = q_len // q_block
    score_scale = head_width ** (-0.5)
    pos_blocks = q_pos.reshape(n_blocks, q_block)
    dot_groups = jnp.moveaxis(row_dots.reshape(n_slots, q_len, n_groups, per_group), 2, 0)

    def blocks_of(grouped):
        return jnp.moveaxis(grouped.reshape((n_slots, n_blocks, q_block) + grouped.shape[2:]), 1, 0)

    def one_group(packed):
        q_group, k_group, v_group, g_group, d_group, l_group = packed

        def one_block(running, streams):
            k_grad, v_grad = running
            q_rows, g_rows, d_rows, l_rows, pos_rows = streams
            scores = score_block(q_rows, k_group, pos_rows, k_pos, lengths)
            probabilities = jnp.exp(scores - l_rows[..., None])
            v_grad = v_grad + jnp.einsum(
                "shqk,sqhe->skhe",
                probabilities.astype(jnp.bfloat16),
                g_rows,
                preferred_element_type=jnp.float32,
            )
            p_grad = jnp.einsum(
                "sqhe,skhe->shqk", g_rows, v_group, preferred_element_type=jnp.float32
            )
            s_grad = (probabilities * (p_grad - jnp.moveaxis(d_rows, 2, 1)[..., None])).astype(
                jnp.bfloat16
            )
            q_grad = (
                jnp.einsum("shqk,skhe->sqhe", s_grad, k_group, preferred_element_type=jnp.float32)
                * score_scale
            )
            k_grad = (
                k_grad
                + jnp.einsum("shqk,sqhe->skhe", s_grad, q_rows, preferred_element_type=jnp.float32)
                * score_scale
            )
            return ((k_grad, v_grad), q_grad)

        empty_grads = jnp.zeros(k_group.shape, jnp.float32)
        streams = (blocks_of(q_group), blocks_of(g_group), blocks_of(d_group), l_group, pos_blocks)
        (k_grad, v_grad), q_grads = lax.scan(one_block, (empty_grads, empty_grads), streams)
        return (
            jnp.moveaxis(q_grads, 0, 1).reshape(n_slots, q_len, per_group, head_width),
            k_grad,
            v_grad,
        )

    grouped = (
        split_heads(queries, n_groups),
        split_heads(keys, n_groups),
        split_heads(values, n_groups),
        split_heads(upstream, n_groups),
        dot_groups,
        log_sums,
    )
    q_grads, k_grads, v_grads = lax.map(one_group, grouped)
    return (join_heads(q_grads), join_heads(k_grads), join_heads(v_grads))


def sums_to_rows(log_sums):
    n_groups, n_blocks, n_slots, per_group, q_block = log_sums.shape
    return jnp.transpose(log_sums, (2, 0, 3, 1, 4)).reshape(
        n_slots, n_groups * per_group, n_blocks * q_block
    )


FAR = 1 << 30


def _block_backward_kernel(q_ref, k_ref, v_ref, g_ref, lse_ref, dots_ref, qpos_ref, kpos_ref,
                           dq_ref, dk_ref, dv_ref, *, head_width, scale):
    pair = pl.program_id(1)
    allowed = kpos_ref[0] <= qpos_ref[...]
    for j in range(2):
        cols = slice(j * head_width, (j + 1) * head_width)
        q = q_ref[0, :, cols]
        k = k_ref[0, :, cols]
        v = v_ref[0, :, cols]
        g = g_ref[0, :, cols]
        head = 2 * pair + j
        lse = lse_ref[0, pl.ds(head, 1), :]
        dots = dots_ref[0, pl.ds(head, 1), :]
        nt = (((1,), (1,)), ((), ()))
        scores = lax.dot_general(k, q, nt, preferred_element_type=jnp.float32) * scale
        scores = jnp.where(allowed, scores, -1e30)
        probs = jnp.exp(scores - lse)
        dv_ref[0, :, cols] = jnp.dot(probs.astype(jnp.bfloat16), g, preferred_element_type=jnp.float32)
        dprobs = lax.dot_general(v, g, nt, preferred_element_type=jnp.float32)
        dscores = (probs * (dprobs - dots)).astype(jnp.bfloat16)
        dk_ref[0, :, cols] = jnp.dot(dscores, q, preferred_element_type=jnp.float32) * scale
        tn = (((0,), (0,)), ((), ()))
        dq_ref[0, :, cols] = lax.dot_general(dscores, k, tn, preferred_element_type=jnp.float32) * scale


def block_backward(queries, keys, values, upstream, lse_rows, dot_rows, q_pos, k_pos, lengths):
    n_slots, q_len, n_heads, head_width = queries.shape
    k_len = keys.shape[1]
    width = n_heads * head_width
    pair_width = 2 * head_width
    flat = lambda a: a.reshape(a.shape[0], a.shape[1], width)
    kpos = jnp.where(
        (k_pos[None, :] < lengths[:, None]) & (k_pos[None, :] >= 0), k_pos[None, :], FAR
    ).astype(jnp.int32)[..., None]
    qpos = q_pos.astype(jnp.int32)[None, :]
    kernel = functools.partial(_block_backward_kernel, head_width=head_width, scale=head_width ** (-0.5))
    q_spec = pl.BlockSpec((1, q_len, pair_width), lambda s, p: (s, 0, p))
    k_spec = pl.BlockSpec((1, k_len, pair_width), lambda s, p: (s, 0, p))
    row_spec = pl.BlockSpec((1, n_heads, q_len), lambda s, p: (s, 0, 0))
    flops = n_slots * n_heads * 10 * q_len * k_len * head_width
    dq, dk, dv = pl.pallas_call(
        kernel,
        grid=(n_slots, n_heads // 2),
        in_specs=[
            q_spec, k_spec, k_spec, q_spec, row_spec, row_spec,
            pl.BlockSpec((1, q_len), lambda s, p: (0, 0)),
            pl.BlockSpec((1, k_len, 1), lambda s, p: (s, 0, 0)),
        ],
        out_specs=[q_spec, k_spec, k_spec],
        out_shape=[
            jax.ShapeDtypeStruct((n_slots, q_len, width), jnp.float32),
            jax.ShapeDtypeStruct((n_slots, k_len, width), jnp.float32),
            jax.ShapeDtypeStruct((n_slots, k_len, width), jnp.float32),
        ],
        cost_estimate=pl.CostEstimate(
            flops=flops,
            transcendentals=n_slots * n_heads * q_len * k_len,
            bytes_accessed=2 * (2 * q_len + 2 * k_len) * width * n_slots + 4 * (q_len + 2 * k_len) * width * n_slots,
        ),
    )(flat(queries), flat(keys), flat(values), flat(upstream), lse_rows, dot_rows, qpos, kpos)
    shape_q = (n_slots, q_len, n_heads, head_width)
    shape_k = (n_slots, k_len, n_heads, head_width)
    return dq.reshape(shape_q), dk.reshape(shape_k), dv.reshape(shape_k)


GROUP = ("fsdp", "ctx")


def gather_blocks(pieces):
    packed = jnp.concatenate(pieces, axis=0)
    gathered = lax.all_gather(packed, GROUP, axis=0, tiled=False)
    fulls, offset = [], 0
    for piece in pieces:
        fulls.append(gathered[:, offset : offset + piece.shape[0], :])
        offset += piece.shape[0]
    return fulls


def rep_sum(x):
    n_rep = lax.axis_size("rep")
    if n_rep != 4:
        return lax.psum(x, "rep")
    me = lax.axis_index("rep")
    arrived = lax.ppermute(x, "rep", [(0, 1), (3, 2)])
    folded = (x.astype(jnp.float32) + arrived.astype(jnp.float32)).astype(x.dtype)
    arrived = lax.ppermute(folded, "rep", [(1, 2), (2, 1)])
    total = (folded.astype(jnp.float32) + arrived.astype(jnp.float32)).astype(x.dtype)
    sent_out = lax.ppermute(total, "rep", [(1, 0), (2, 3)])
    return jnp.where((me == 0) | (me == 3), sent_out, total)


def scatter_blocks(blocks, by_permutes):
    packed = jnp.concatenate(blocks, axis=1).astype(jnp.bfloat16)
    summed = lax.psum_scatter(packed, GROUP, scatter_dimension=0, tiled=True)
    summed = (rep_sum(summed) if by_permutes else lax.psum(summed, "rep"))[0].astype(jnp.float32)
    parts, offset = [], 0
    for block in blocks:
        parts.append(summed[offset : offset + block.shape[1], :])
        offset += block.shape[1]
    return parts


def gain_block(first, second, width):
    lead = first.shape[:-1]
    row = jnp.concatenate([first, second], axis=-1)
    row = jnp.pad(row, [(0, 0)] * len(lead) + [(0, width - row.shape[-1])])
    return jnp.pad(row[..., None, :], [(0, 0)] * len(lead) + [(0, 7), (0, 0)])


def shards(
    tokens,
    initial_layer_values,
    cotangent,
    lengths,
    w_query,
    w_key,
    w_value,
    w_out,
    w_gate,
    w_up,
    w_down,
    gain_attn,
    gain_mlp,
):
    n_slots, slot_rows, model_width = tokens.shape
    n_ctx = lax.axis_size("ctx")
    n_group = lax.axis_size("fsdp") * n_ctx
    own_rows = gain_attn.shape[0]
    ff_width = w_gate.shape[1]
    attn_width = w_query.shape[1]
    qkv_width = 3 * attn_width
    qkvo_width = qkv_width + model_width
    (qkvo_blocks, gain_rows) = gather_blocks(
        [
            jnp.concatenate([w_query, w_key, w_value, w_out], axis=1),
            gain_block(gain_attn, gain_mlp, qkvo_width),
        ]
    )
    full_qkvo = qkvo_blocks.reshape(n_group * own_rows, qkvo_width)
    full_qkv = full_qkvo[:, :qkv_width]
    full_out = full_qkvo[:, qkv_width:]
    full_gain_attn = gain_rows[:, 0, :own_rows].reshape(-1)
    full_gain_mlp = gain_rows[:, 0, own_rows : 2 * own_rows].reshape(-1)
    (gu_blocks,) = gather_blocks([jnp.concatenate([w_gate, w_up], axis=1)])
    full_gu = gu_blocks.reshape(n_group * own_rows, 2 * ff_width)
    (down_blocks,) = gather_blocks([w_down])
    full_down = down_blocks.reshape(-1, model_width)
    ctx_index = lax.axis_index("ctx")
    q_pos = ctx_index * slot_rows + jnp.arange(slot_rows)
    live_rows = q_pos[None, :] < lengths[:, None]
    head_shape = (n_slots, slot_rows, HEADS, HEAD_DIM)
    paired = n_ctx == 2
    if paired:
        other_tokens = lax.ppermute(tokens, "ctx", [(0, 1), (1, 0)])
        other_first = lax.ppermute(initial_layer_values, "ctx", [(0, 1)])
        other_pos = (1 - ctx_index) * slot_rows + jnp.arange(slot_rows)
    inputs = tokens.astype(jnp.float32)
    attn_scale = full_gain_attn.astype(jnp.float32)
    mlp_scale = full_gain_mlp.astype(jnp.float32)

    def project(chunk_tokens, chunk_first, chunk_pos):
        chunk_normed, chunk_inv = normalize(chunk_tokens.astype(jnp.float32), attn_scale)
        chunk_low = chunk_normed.astype(jnp.bfloat16)
        qkv_pre = jnp.einsum(
            "srd,de->sre", chunk_low, full_qkv, preferred_element_type=jnp.float32
        )
        q_pre = qkv_pre[..., :attn_width]
        k_pre = qkv_pre[..., attn_width : 2 * attn_width]
        v_pre = qkv_pre[..., 2 * attn_width :]
        chunk_q = rotate(q_pre.reshape(head_shape), chunk_pos, 1.0).astype(jnp.bfloat16)
        chunk_k = rotate(k_pre.reshape(head_shape), chunk_pos, 1.0).astype(jnp.bfloat16)
        chunk_v = (
            (0.5 * v_pre + 0.5 * chunk_first.astype(jnp.float32))
            .astype(jnp.bfloat16)
            .reshape(head_shape)
        )
        return chunk_low, chunk_inv, chunk_q, chunk_k, chunk_v

    normed_low, inv_attn, queries, keys, values = project(tokens, initial_layer_values, q_pos)
    if paired:
        _, _, other_q, other_k, other_v = project(other_tokens, other_first, other_pos)
        slot_k = jnp.concatenate([other_k, keys], axis=1)
        slot_v = jnp.concatenate([other_v, values], axis=1)
        k_pos = jnp.concatenate([other_pos, q_pos])
    else:
        slot_k, slot_v = (
            lax.all_gather(keys, "ctx", axis=1, tiled=True),
            lax.all_gather(values, "ctx", axis=1, tiled=True),
        )
        k_pos = jnp.arange(n_ctx * slot_rows)
    attn_raw, attn_lse = attend_forward(queries, slot_k, slot_v, q_pos, k_pos, lengths)
    attended = attn_raw.astype(jnp.bfloat16)
    att_flat = attended.reshape(n_slots, slot_rows, model_width)
    branch = jnp.einsum("sre,ed->srd", att_flat, full_out, preferred_element_type=jnp.float32)
    residual = inputs + branch
    normed_mlp, inv_mlp = normalize(residual, mlp_scale)
    mlp_low = normed_mlp.astype(jnp.bfloat16)
    gu_proj = jnp.einsum("srd,df->srf", mlp_low, full_gu, preferred_element_type=jnp.float32)
    gate_proj = gu_proj[..., :ff_width]
    up_proj = gu_proj[..., ff_width:]
    sigmoid_gate = jax.nn.sigmoid(gate_proj)
    hidden = (gate_proj * sigmoid_gate * up_proj).astype(jnp.bfloat16)
    hidden, gate_proj, up_proj, sigmoid_gate = lax.optimization_barrier(
        (hidden, gate_proj, up_proj, sigmoid_gate)
    )
    final = residual + jnp.einsum(
        "srf,fd->srd", hidden, full_down, preferred_element_type=jnp.float32
    )
    output = jnp.where(live_rows[..., None], final, 0.0).astype(jnp.bfloat16)
    output_gradient = jnp.where(live_rows[..., None], cotangent.astype(jnp.float32), 0.0)
    g_low = output_gradient.astype(jnp.bfloat16)
    grad_down = jnp.einsum("srf,srd->fd", hidden, g_low, preferred_element_type=jnp.float32)
    (part_down,) = scatter_blocks(
        [grad_down.reshape(n_group, -1, model_width).astype(jnp.bfloat16)], True
    )
    g_hidden = jnp.einsum("srd,fd->srf", g_low, full_down, preferred_element_type=jnp.float32)
    gate_gradient = (
        g_hidden * up_proj * sigmoid_gate * (1.0 + gate_proj * (1.0 - sigmoid_gate))
    ).astype(jnp.bfloat16)
    up_gradient = (g_hidden * gate_proj * sigmoid_gate).astype(jnp.bfloat16)
    gu_gradient = jnp.concatenate([gate_gradient, up_gradient], axis=-1)
    grad_gu = jnp.einsum("srd,srf->df", mlp_low, gu_gradient, preferred_element_type=jnp.float32)
    g_normed_mlp = jnp.einsum(
        "srf,df->srd", gu_gradient, full_gu, preferred_element_type=jnp.float32
    )
    g_mlp_in, grad_gain_mlp = normalize_back(residual, inv_mlp, mlp_scale, g_normed_mlp)
    g_residual = output_gradient + g_mlp_in
    g_branch = g_residual.astype(jnp.bfloat16)
    grad_out = jnp.einsum(
        "sre,srd->ed", att_flat, g_branch, preferred_element_type=jnp.float32
    )
    ogu_block = (
        jnp.concatenate([grad_out, grad_gu], axis=1)
        .reshape(n_group, own_rows, model_width + 2 * ff_width)
        .astype(jnp.bfloat16)
    )
    g_attended = (
        jnp.einsum("srd,ed->sre", g_branch, full_out, preferred_element_type=jnp.float32)
        .astype(jnp.bfloat16)
        .reshape(head_shape)
    )
    (part_ogu,) = scatter_blocks([ogu_block], True)
    row_dots = jnp.sum(g_attended.astype(jnp.float32) * attended.astype(jnp.float32), axis=-1)
    if paired:
        lse_rows = sums_to_rows(attn_lse)
        dot_rows = jnp.transpose(row_dots, (0, 2, 1))
        later_g, later_dots, later_lse = lax.ppermute(
            (g_attended, dot_rows, lse_rows), "ctx", [(1, 0)]
        )
        g_queries, g_keys, g_values = block_backward(
            queries, keys, values, g_attended, lse_rows, dot_rows, q_pos, q_pos, lengths
        )
        later = ctx_index == 1
        pick = lambda mine, theirs: jnp.where(later, mine, theirs)
        x_dq, x_dk, x_dv = block_backward(
            pick(queries, other_q),
            pick(other_k, keys),
            pick(other_v, values),
            pick(g_attended, later_g),
            pick(lse_rows, later_lse),
            pick(dot_rows, later_dots),
            pick(q_pos, other_pos),
            pick(other_pos, q_pos),
            lengths,
        )
        g_queries = g_queries + jnp.where(later, x_dq, 0.0)
        g_keys = g_keys + jnp.where(later, 0.0, x_dk)
        g_values = g_values + jnp.where(later, 0.0, x_dv)
    else:
        g_queries, slot_dk, slot_dv = attend_backward(
            queries, slot_k, slot_v, g_attended, row_dots, attn_lse, q_pos, k_pos, lengths
        )
        g_keys, g_values = (
            lax.psum_scatter(
                slot_dk.astype(jnp.bfloat16), "ctx", scatter_dimension=1, tiled=True
            ).astype(jnp.float32),
            lax.psum_scatter(
                slot_dv.astype(jnp.bfloat16), "ctx", scatter_dimension=1, tiled=True
            ).astype(jnp.float32),
        )
    flat_shape = (n_slots, slot_rows, model_width)
    gq_low = rotate(g_queries, q_pos, -1.0).reshape(flat_shape).astype(jnp.bfloat16)
    gk_low = rotate(g_keys, q_pos, -1.0).reshape(flat_shape).astype(jnp.bfloat16)
    gv_rounded = g_values.reshape(flat_shape).astype(jnp.bfloat16).astype(jnp.float32)
    d_first = 0.5 * gv_rounded
    gv_half = d_first.astype(jnp.bfloat16)
    g_qkv = jnp.concatenate([gq_low, gk_low, gv_half], axis=-1)
    grad_qkv = jnp.einsum("srd,sre->de", normed_low, g_qkv, preferred_element_type=jnp.float32)
    g_normed = jnp.einsum("sre,de->srd", g_qkv, full_qkv, preferred_element_type=jnp.float32)
    g_attn_in, grad_gain_attn = normalize_back(inputs, inv_attn, attn_scale, g_normed)
    d_tokens = g_residual + g_attn_in
    part_qkv, part_gains = scatter_blocks(
        [
            grad_qkv.reshape(n_group, own_rows, qkv_width),
            gain_block(
                grad_gain_attn.reshape(n_group, own_rows),
                grad_gain_mlp.reshape(n_group, own_rows),
                qkv_width,
            ),
        ],
        False,
    )
    return (
        output,
        d_tokens,
        d_first,
        part_qkv[:, :attn_width],
        part_qkv[:, attn_width : 2 * attn_width],
        part_qkv[:, 2 * attn_width :],
        part_ogu[:, :model_width],
        part_ogu[:, model_width : model_width + ff_width],
        part_ogu[:, model_width + ff_width :],
        part_down,
        part_gains[0, :own_rows],
        part_gains[0, own_rows : 2 * own_rows],
    )


def solution(mesh):
    in_specs = (
        P(("rep", "fsdp"), "ctx", None),
        P(("rep", "fsdp"), "ctx", None),
        P(("rep", "fsdp"), "ctx", None),
        P(("rep", "fsdp")),
        P(("fsdp", "ctx"), None),
        P(("fsdp", "ctx"), None),
        P(("fsdp", "ctx"), None),
        P(("fsdp", "ctx"), None),
        P(("fsdp", "ctx"), None),
        P(("fsdp", "ctx"), None),
        P(("fsdp", "ctx"), None),
        P(("fsdp", "ctx")),
        P(("fsdp", "ctx")),
    )
    out_specs = (
        P(("rep", "fsdp"), "ctx", None),
        P(("rep", "fsdp"), "ctx", None),
        P(("rep", "fsdp"), "ctx", None),
        P(("fsdp", "ctx"), None),
        P(("fsdp", "ctx"), None),
        P(("fsdp", "ctx"), None),
        P(("fsdp", "ctx"), None),
        P(("fsdp", "ctx"), None),
        P(("fsdp", "ctx"), None),
        P(("fsdp", "ctx"), None),
        P(("fsdp", "ctx")),
        P(("fsdp", "ctx")),
    )

    return jax.shard_map(shards, mesh=mesh, in_specs=in_specs, out_specs=out_specs, check_vma=False)
```

```python
import functools

import jax
import jax.numpy as jnp
from jax import lax
from jax.experimental import pallas as pl
from jax.sharding import PartitionSpec as P


HEADS = 16
HEAD_DIM = 64


EPS = 1e-06
NEG = -1e30
THETA = 10000.0
SCORE_CAP = 4194304


def rotate(field, positions, direction):
    head_width = field.shape[-1]
    half_width = head_width // 2
    frequency = THETA ** (-(jnp.arange(half_width, dtype=jnp.float32) * 2.0) / head_width)
    angles = positions.astype(jnp.float32)[:, None] * frequency[None, :]
    cosine = jnp.cos(angles)[:, None, :]
    sine_part = direction * jnp.sin(angles)[:, None, :]
    former = field[..., :half_width]
    latter = field[..., half_width:]
    return jnp.concatenate(
        [former * cosine - latter * sine_part, latter * cosine + former * sine_part], axis=-1
    )


def normalize(values, gain):
    inverse = lax.rsqrt(jnp.mean(values * values, axis=-1, keepdims=True) + EPS)
    return (values * inverse * gain, inverse)


def normalize_back(values, inverse, gain, upstream):
    unit_rows = values * inverse
    scaled = upstream * gain
    grad_gain = jnp.sum(upstream * unit_rows, axis=(0, 1))
    grad_values = inverse * (
        scaled - unit_rows * jnp.mean(scaled * unit_rows, axis=-1, keepdims=True)
    )
    return (grad_values, grad_gain)


def head_groups(n_slots, q_len, n_heads, k_len):
    q_block = min(q_len, 512)
    per_group = max(1, min(n_heads, SCORE_CAP // (n_slots * q_block * k_len)))
    while n_heads % per_group:
        per_group = per_group - 1
    return (q_block, per_group)


def split_heads(packed, n_groups):
    n_slots, length, n_heads, head_width = packed.shape
    return jnp.moveaxis(
        packed.reshape(n_slots, length, n_groups, n_heads // n_groups, head_width), 2, 0
    )


def join_heads(grouped):
    n_groups, n_slots, length, per_group, head_width = grouped.shape
    return jnp.moveaxis(grouped, 0, 2).reshape(n_slots, length, n_groups * per_group, head_width)


def score_block(q_rows, k_rows, q_pos, k_pos, lengths):
    products = jnp.einsum(
        "sqhe,skhe->shqk", q_rows, k_rows, preferred_element_type=jnp.float32
    ) * q_rows.shape[-1] ** (-0.5)
    causal = (k_pos[None, None, None, :] <= q_pos[None, None, :, None]) & (
        k_pos[None, None, None, :] >= 0
    )
    filled = k_pos[None, None, None, :] < lengths[:, None, None, None]
    return jnp.where(causal & filled, products, NEG)


def attend_forward(queries, keys, values, q_pos, k_pos, lengths):
    n_slots, q_len, n_heads, head_width = queries.shape
    q_block, per_group = head_groups(n_slots, q_len, n_heads, keys.shape[1])
    n_groups = n_heads // per_group
    n_blocks = q_len // q_block
    pos_blocks = q_pos.reshape(n_blocks, q_block)

    def one_group(packed):
        q_group, k_group, v_group = packed
        q_blocks = jnp.moveaxis(
            q_group.reshape(n_slots, n_blocks, q_block, per_group, head_width), 1, 0
        )

        def one_block(streams):
            q_rows, pos_rows = streams
            scores = score_block(q_rows, k_group, pos_rows, k_pos, lengths)
            highest = jnp.max(scores, axis=-1, keepdims=True)
            exponent = jnp.exp(scores - highest)
            totals = jnp.sum(exponent, axis=-1, keepdims=True)
            probabilities = (exponent / totals).astype(jnp.bfloat16)
            mixture = jnp.einsum(
                "shqk,skhe->sqhe", probabilities, v_group, preferred_element_type=jnp.float32
            )
            return (mixture, (highest + jnp.log(totals))[..., 0])

        mixture, log_sums = lax.map(one_block, (q_blocks, pos_blocks))
        return (
            jnp.moveaxis(mixture, 0, 1).reshape(n_slots, q_len, per_group, head_width),
            log_sums,
        )

    grouped = (
        split_heads(queries, n_groups),
        split_heads(keys, n_groups),
        split_heads(values, n_groups),
    )
    mixture, log_sums = lax.map(one_group, grouped)
    return (join_heads(mixture), log_sums)


def attend_backward(queries, keys, values, upstream, row_dots, log_sums, q_pos, k_pos, lengths):
    n_slots, q_len, n_heads, head_width = queries.shape
    q_block, per_group = head_groups(n_slots, q_len, n_heads, keys.shape[1])
    n_groups = n_heads // per_group
    n_blocks = q_len // q_block
    score_scale = head_width ** (-0.5)
    pos_blocks = q_pos.reshape(n_blocks, q_block)
    dot_groups = jnp.moveaxis(row_dots.reshape(n_slots, q_len, n_groups, per_group), 2, 0)

    def blocks_of(grouped):
        return jnp.moveaxis(grouped.reshape((n_slots, n_blocks, q_block) + grouped.shape[2:]), 1, 0)

    def one_group(packed):
        q_group, k_group, v_group, g_group, d_group, l_group = packed

        def one_block(running, streams):
            k_grad, v_grad = running
            q_rows, g_rows, d_rows, l_rows, pos_rows = streams
            scores = score_block(q_rows, k_group, pos_rows, k_pos, lengths)
            probabilities = jnp.exp(scores - l_rows[..., None])
            v_grad = v_grad + jnp.einsum(
                "shqk,sqhe->skhe",
                probabilities.astype(jnp.bfloat16),
                g_rows,
                preferred_element_type=jnp.float32,
            )
            p_grad = jnp.einsum(
                "sqhe,skhe->shqk", g_rows, v_group, preferred_element_type=jnp.float32
            )
            s_grad = (probabilities * (p_grad - jnp.moveaxis(d_rows, 2, 1)[..., None])).astype(
                jnp.bfloat16
            )
            q_grad = (
                jnp.einsum("shqk,skhe->sqhe", s_grad, k_group, preferred_element_type=jnp.float32)
                * score_scale
            )
            k_grad = (
                k_grad
                + jnp.einsum("shqk,sqhe->skhe", s_grad, q_rows, preferred_element_type=jnp.float32)
                * score_scale
            )
            return ((k_grad, v_grad), q_grad)

        empty_grads = jnp.zeros(k_group.shape, jnp.float32)
        streams = (blocks_of(q_group), blocks_of(g_group), blocks_of(d_group), l_group, pos_blocks)
        (k_grad, v_grad), q_grads = lax.scan(one_block, (empty_grads, empty_grads), streams)
        return (
            jnp.moveaxis(q_grads, 0, 1).reshape(n_slots, q_len, per_group, head_width),
            k_grad,
            v_grad,
        )

    grouped = (
        split_heads(queries, n_groups),
        split_heads(keys, n_groups),
        split_heads(values, n_groups),
        split_heads(upstream, n_groups),
        dot_groups,
        log_sums,
    )
    q_grads, k_grads, v_grads = lax.map(one_group, grouped)
    return (join_heads(q_grads), join_heads(k_grads), join_heads(v_grads))


def sums_to_rows(log_sums):
    n_groups, n_blocks, n_slots, per_group, q_block = log_sums.shape
    return jnp.transpose(log_sums, (2, 0, 3, 1, 4)).reshape(
        n_slots, n_groups * per_group, n_blocks * q_block
    )


FAR = 1 << 30


def _block_backward_kernel(q_ref, k_ref, v_ref, g_ref, lse_ref, dots_ref, qpos_ref, kpos_ref,
                           dq_ref, dk_ref, dv_ref, *, head_width, scale):
    pair = pl.program_id(1)
    allowed = kpos_ref[0] <= qpos_ref[...]
    for j in range(2):
        cols = slice(j * head_width, (j + 1) * head_width)
        q = q_ref[0, :, cols]
        k = k_ref[0, :, cols]
        v = v_ref[0, :, cols]
        g = g_ref[0, :, cols]
        head = 2 * pair + j
        lse = lse_ref[0, pl.ds(head, 1), :]
        dots = dots_ref[0, pl.ds(head, 1), :]
        nt = (((1,), (1,)), ((), ()))
        scores = lax.dot_general(k, q, nt, preferred_element_type=jnp.float32) * scale
        scores = jnp.where(allowed, scores, -1e30)
        probs = jnp.exp(scores - lse)
        dv_ref[0, :, cols] = jnp.dot(probs.astype(jnp.bfloat16), g, preferred_element_type=jnp.float32)
        dprobs = lax.dot_general(v, g, nt, preferred_element_type=jnp.float32)
        dscores = (probs * (dprobs - dots)).astype(jnp.bfloat16)
        dk_ref[0, :, cols] = jnp.dot(dscores, q, preferred_element_type=jnp.float32) * scale
        tn = (((0,), (0,)), ((), ()))
        dq_ref[0, :, cols] = lax.dot_general(dscores, k, tn, preferred_element_type=jnp.float32) * scale


def block_backward(queries, keys, values, upstream, lse_rows, dot_rows, q_pos, k_pos, lengths):
    n_slots, q_len, n_heads, head_width = queries.shape
    k_len = keys.shape[1]
    width = n_heads * head_width
    pair_width = 2 * head_width
    flat = lambda a: a.reshape(a.shape[0], a.shape[1], width)
    kpos = jnp.where(
        (k_pos[None, :] < lengths[:, None]) & (k_pos[None, :] >= 0), k_pos[None, :], FAR
    ).astype(jnp.int32)[..., None]
    qpos = q_pos.astype(jnp.int32)[None, :]
    kernel = functools.partial(_block_backward_kernel, head_width=head_width, scale=head_width ** (-0.5))
    q_spec = pl.BlockSpec((1, q_len, pair_width), lambda s, p: (s, 0, p))
    k_spec = pl.BlockSpec((1, k_len, pair_width), lambda s, p: (s, 0, p))
    row_spec = pl.BlockSpec((1, n_heads, q_len), lambda s, p: (s, 0, 0))
    flops = n_slots * n_heads * 10 * q_len * k_len * head_width
    dq, dk, dv = pl.pallas_call(
        kernel,
        grid=(n_slots, n_heads // 2),
        in_specs=[
            q_spec, k_spec, k_spec, q_spec, row_spec, row_spec,
            pl.BlockSpec((1, q_len), lambda s, p: (0, 0)),
            pl.BlockSpec((1, k_len, 1), lambda s, p: (s, 0, 0)),
        ],
        out_specs=[q_spec, k_spec, k_spec],
        out_shape=[
            jax.ShapeDtypeStruct((n_slots, q_len, width), jnp.float32),
            jax.ShapeDtypeStruct((n_slots, k_len, width), jnp.float32),
            jax.ShapeDtypeStruct((n_slots, k_len, width), jnp.float32),
        ],
        cost_estimate=pl.CostEstimate(
            flops=flops,
            transcendentals=n_slots * n_heads * q_len * k_len,
            bytes_accessed=2 * (2 * q_len + 2 * k_len) * width * n_slots + 4 * (q_len + 2 * k_len) * width * n_slots,
        ),
    )(flat(queries), flat(keys), flat(values), flat(upstream), lse_rows, dot_rows, qpos, kpos)
    shape_q = (n_slots, q_len, n_heads, head_width)
    shape_k = (n_slots, k_len, n_heads, head_width)
    return dq.reshape(shape_q), dk.reshape(shape_k), dv.reshape(shape_k)


GROUP = ("fsdp", "ctx")


def gather_blocks(pieces):
    packed = jnp.concatenate(pieces, axis=0)
    gathered = lax.all_gather(packed, GROUP, axis=0, tiled=False)
    fulls, offset = [], 0
    for piece in pieces:
        fulls.append(gathered[:, offset : offset + piece.shape[0], :])
        offset += piece.shape[0]
    return fulls


def rep_sum(x):
    n_rep = lax.axis_size("rep")
    if n_rep != 4:
        return lax.psum(x, "rep")
    me = lax.axis_index("rep")
    arrived = lax.ppermute(x, "rep", [(0, 1), (3, 2)])
    folded = (x.astype(jnp.float32) + arrived.astype(jnp.float32)).astype(x.dtype)
    arrived = lax.ppermute(folded, "rep", [(1, 2), (2, 1)])
    total = (folded.astype(jnp.float32) + arrived.astype(jnp.float32)).astype(x.dtype)
    sent_out = lax.ppermute(total, "rep", [(1, 0), (2, 3)])
    return jnp.where((me == 0) | (me == 3), sent_out, total)


def scatter_blocks(blocks, by_permutes):
    packed = jnp.concatenate(blocks, axis=1).astype(jnp.bfloat16)
    summed = lax.psum_scatter(packed, GROUP, scatter_dimension=0, tiled=True)
    summed = (rep_sum(summed) if by_permutes else lax.psum(summed, "rep"))[0].astype(jnp.float32)
    parts, offset = [], 0
    for block in blocks:
        parts.append(summed[offset : offset + block.shape[1], :])
        offset += block.shape[1]
    return parts


def gain_block(first, second, width):
    lead = first.shape[:-1]
    row = jnp.concatenate([first, second], axis=-1)
    row = jnp.pad(row, [(0, 0)] * len(lead) + [(0, width - row.shape[-1])])
    return jnp.pad(row[..., None, :], [(0, 0)] * len(lead) + [(0, 7), (0, 0)])


def shards(
    tokens,
    initial_layer_values,
    cotangent,
    lengths,
    w_query,
    w_key,
    w_value,
    w_out,
    w_gate,
    w_up,
    w_down,
    gain_attn,
    gain_mlp,
):
    n_slots, slot_rows, model_width = tokens.shape
    n_ctx = lax.axis_size("ctx")
    n_group = lax.axis_size("fsdp") * n_ctx
    own_rows = gain_attn.shape[0]
    ff_width = w_gate.shape[1]
    attn_width = w_query.shape[1]
    qkv_width = 3 * attn_width
    (qkv_blocks, gain_rows) = gather_blocks(
        [
            jnp.concatenate([w_query, w_key, w_value], axis=1),
            gain_block(gain_attn, gain_mlp, qkv_width),
        ]
    )
    full_qkv = qkv_blocks.reshape(n_group * own_rows, qkv_width)
    full_gain_attn = gain_rows[:, 0, :own_rows].reshape(-1)
    full_gain_mlp = gain_rows[:, 0, own_rows : 2 * own_rows].reshape(-1)
    (out_blocks,) = gather_blocks([w_out])
    full_out = out_blocks.reshape(-1, model_width)
    (gu_blocks,) = gather_blocks([jnp.concatenate([w_gate, w_up], axis=1)])
    full_gu = gu_blocks.reshape(n_group * own_rows, 2 * ff_width)
    (down_blocks,) = gather_blocks([w_down])
    full_down = down_blocks.reshape(-1, model_width)
    ctx_index = lax.axis_index("ctx")
    q_pos = ctx_index * slot_rows + jnp.arange(slot_rows)
    live_rows = q_pos[None, :] < lengths[:, None]
    head_shape = (n_slots, slot_rows, HEADS, HEAD_DIM)
    paired = n_ctx == 2
    if paired:
        other_tokens = lax.ppermute(tokens, "ctx", [(0, 1), (1, 0)])
        other_first = lax.ppermute(initial_layer_values, "ctx", [(0, 1)])
        other_pos = (1 - ctx_index) * slot_rows + jnp.arange(slot_rows)
    inputs = tokens.astype(jnp.float32)
    attn_scale = full_gain_attn.astype(jnp.float32)
    mlp_scale = full_gain_mlp.astype(jnp.float32)

    def project(chunk_tokens, chunk_first, chunk_pos):
        chunk_normed, chunk_inv = normalize(chunk_tokens.astype(jnp.float32), attn_scale)
        chunk_low = chunk_normed.astype(jnp.bfloat16)
        qkv_pre = jnp.einsum(
            "srd,de->sre", chunk_low, full_qkv, preferred_element_type=jnp.float32
        )
        q_pre = qkv_pre[..., :attn_width]
        k_pre = qkv_pre[..., attn_width : 2 * attn_width]
        v_pre = qkv_pre[..., 2 * attn_width :]
        chunk_q = rotate(q_pre.reshape(head_shape), chunk_pos, 1.0).astype(jnp.bfloat16)
        chunk_k = rotate(k_pre.reshape(head_shape), chunk_pos, 1.0).astype(jnp.bfloat16)
        chunk_v = (
            (0.5 * v_pre + 0.5 * chunk_first.astype(jnp.float32))
            .astype(jnp.bfloat16)
            .reshape(head_shape)
        )
        return chunk_low, chunk_inv, chunk_q, chunk_k, chunk_v

    normed_low, inv_attn, queries, keys, values = project(tokens, initial_layer_values, q_pos)
    if paired:
        _, _, other_q, other_k, other_v = project(other_tokens, other_first, other_pos)
        slot_k = jnp.concatenate([other_k, keys], axis=1)
        slot_v = jnp.concatenate([other_v, values], axis=1)
        k_pos = jnp.concatenate([other_pos, q_pos])
    else:
        slot_k, slot_v = (
            lax.all_gather(keys, "ctx", axis=1, tiled=True),
            lax.all_gather(values, "ctx", axis=1, tiled=True),
        )
        k_pos = jnp.arange(n_ctx * slot_rows)
    attn_raw, attn_lse = attend_forward(queries, slot_k, slot_v, q_pos, k_pos, lengths)
    attended = attn_raw.astype(jnp.bfloat16)
    att_flat = attended.reshape(n_slots, slot_rows, model_width)
    branch = jnp.einsum("sre,ed->srd", att_flat, full_out, preferred_element_type=jnp.float32)
    residual = inputs + branch
    normed_mlp, inv_mlp = normalize(residual, mlp_scale)
    mlp_low = normed_mlp.astype(jnp.bfloat16)
    gu_proj = jnp.einsum("srd,df->srf", mlp_low, full_gu, preferred_element_type=jnp.float32)
    gate_proj = gu_proj[..., :ff_width]
    up_proj = gu_proj[..., ff_width:]
    sigmoid_gate = jax.nn.sigmoid(gate_proj)
    hidden = (gate_proj * sigmoid_gate * up_proj).astype(jnp.bfloat16)
    final = residual + jnp.einsum(
        "srf,fd->srd", hidden, full_down, preferred_element_type=jnp.float32
    )
    output = jnp.where(live_rows[..., None], final, 0.0).astype(jnp.bfloat16)
    output_gradient = jnp.where(live_rows[..., None], cotangent.astype(jnp.float32), 0.0)
    g_low = output_gradient.astype(jnp.bfloat16)
    gu_alone = lax.optimization_barrier(gu_proj)
    gate_alone = gu_alone[..., :ff_width]
    hidden_alone = (gate_alone * jax.nn.sigmoid(gate_alone) * gu_alone[..., ff_width:]).astype(
        jnp.bfloat16
    )
    grad_down = jnp.einsum("srf,srd->fd", hidden_alone, g_low, preferred_element_type=jnp.float32)
    (part_down,) = scatter_blocks(
        [grad_down.reshape(n_group, -1, model_width).astype(jnp.bfloat16)], True
    )
    g_hidden = jnp.einsum("srd,fd->srf", g_low, full_down, preferred_element_type=jnp.float32)
    gate_gradient = (
        g_hidden * up_proj * sigmoid_gate * (1.0 + gate_proj * (1.0 - sigmoid_gate))
    ).astype(jnp.bfloat16)
    up_gradient = (g_hidden * gate_proj * sigmoid_gate).astype(jnp.bfloat16)
    gu_gradient = jnp.concatenate([gate_gradient, up_gradient], axis=-1)
    grad_gu = jnp.einsum("srd,srf->df", mlp_low, gu_gradient, preferred_element_type=jnp.float32)
    g_normed_mlp = jnp.einsum(
        "srf,df->srd", gu_gradient, full_gu, preferred_element_type=jnp.float32
    )
    g_mlp_in, grad_gain_mlp = normalize_back(residual, inv_mlp, mlp_scale, g_normed_mlp)
    g_residual = output_gradient + g_mlp_in
    g_branch = g_residual.astype(jnp.bfloat16)
    grad_out = jnp.einsum(
        "sre,srd->ed", att_flat, g_branch, preferred_element_type=jnp.float32
    )
    ogu_block = (
        jnp.concatenate([grad_out, grad_gu], axis=1)
        .reshape(n_group, own_rows, model_width + 2 * ff_width)
        .astype(jnp.bfloat16)
    )
    g_attended = (
        jnp.einsum("srd,ed->sre", g_branch, full_out, preferred_element_type=jnp.float32)
        .astype(jnp.bfloat16)
        .reshape(head_shape)
    )
    (part_ogu,) = scatter_blocks([ogu_block], True)
    row_dots = jnp.sum(g_attended.astype(jnp.float32) * attended.astype(jnp.float32), axis=-1)
    if paired:
        lse_rows = sums_to_rows(attn_lse)
        dot_rows = jnp.transpose(row_dots, (0, 2, 1))
        later_g, later_dots, later_lse = lax.ppermute(
            (g_attended, dot_rows, lse_rows), "ctx", [(1, 0)]
        )
        g_queries, g_keys, g_values = block_backward(
            queries, keys, values, g_attended, lse_rows, dot_rows, q_pos, q_pos, lengths
        )
        later = ctx_index == 1
        pick = lambda mine, theirs: jnp.where(later, mine, theirs)
        x_dq, x_dk, x_dv = block_backward(
            pick(queries, other_q),
            pick(other_k, keys),
            pick(other_v, values),
            pick(g_attended, later_g),
            pick(lse_rows, later_lse),
            pick(dot_rows, later_dots),
            pick(q_pos, other_pos),
            pick(other_pos, q_pos),
            lengths,
        )
        g_queries = g_queries + jnp.where(later, x_dq, 0.0)
        g_keys = g_keys + jnp.where(later, 0.0, x_dk)
        g_values = g_values + jnp.where(later, 0.0, x_dv)
    else:
        g_queries, slot_dk, slot_dv = attend_backward(
            queries, slot_k, slot_v, g_attended, row_dots, attn_lse, q_pos, k_pos, lengths
        )
        g_keys, g_values = (
            lax.psum_scatter(
                slot_dk.astype(jnp.bfloat16), "ctx", scatter_dimension=1, tiled=True
            ).astype(jnp.float32),
            lax.psum_scatter(
                slot_dv.astype(jnp.bfloat16), "ctx", scatter_dimension=1, tiled=True
            ).astype(jnp.float32),
        )
    flat_shape = (n_slots, slot_rows, model_width)
    gq_low = rotate(g_queries, q_pos, -1.0).reshape(flat_shape).astype(jnp.bfloat16)
    gk_low = rotate(g_keys, q_pos, -1.0).reshape(flat_shape).astype(jnp.bfloat16)
    gv_rounded = g_values.reshape(flat_shape).astype(jnp.bfloat16).astype(jnp.float32)
    d_first = 0.5 * gv_rounded
    gv_half = d_first.astype(jnp.bfloat16)
    g_qkv = jnp.concatenate([gq_low, gk_low, gv_half], axis=-1)
    grad_qkv = jnp.einsum("srd,sre->de", normed_low, g_qkv, preferred_element_type=jnp.float32)
    g_normed = jnp.einsum("sre,de->srd", g_qkv, full_qkv, preferred_element_type=jnp.float32)
    g_attn_in, grad_gain_attn = normalize_back(inputs, inv_attn, attn_scale, g_normed)
    d_tokens = g_residual + g_attn_in
    part_qkv, part_gains = scatter_blocks(
        [
            grad_qkv.reshape(n_group, own_rows, qkv_width),
            gain_block(
                grad_gain_attn.reshape(n_group, own_rows),
                grad_gain_mlp.reshape(n_group, own_rows),
                qkv_width,
            ),
        ],
        False,
    )
    return (
        output,
        d_tokens,
        d_first,
        part_qkv[:, :attn_width],
        part_qkv[:, attn_width : 2 * attn_width],
        part_qkv[:, 2 * attn_width :],
        part_ogu[:, :model_width],
        part_ogu[:, model_width : model_width + ff_width],
        part_ogu[:, model_width + ff_width :],
        part_down,
        part_gains[0, :own_rows],
        part_gains[0, own_rows : 2 * own_rows],
    )


def solution(mesh):
    in_specs = (
        P(("rep", "fsdp"), "ctx", None),
        P(("rep", "fsdp"), "ctx", None),
        P(("rep", "fsdp"), "ctx", None),
        P(("rep", "fsdp")),
        P(("fsdp", "ctx"), None),
        P(("fsdp", "ctx"), None),
        P(("fsdp", "ctx"), None),
        P(("fsdp", "ctx"), None),
        P(("fsdp", "ctx"), None),
        P(("fsdp", "ctx"), None),
        P(("fsdp", "ctx"), None),
        P(("fsdp", "ctx")),
        P(("fsdp", "ctx")),
    )
    out_specs = (
        P(("rep", "fsdp"), "ctx", None),
        P(("rep", "fsdp"), "ctx", None),
        P(("rep", "fsdp"), "ctx", None),
        P(("fsdp", "ctx"), None),
        P(("fsdp", "ctx"), None),
        P(("fsdp", "ctx"), None),
        P(("fsdp", "ctx"), None),
        P(("fsdp", "ctx"), None),
        P(("fsdp", "ctx"), None),
        P(("fsdp", "ctx"), None),
        P(("fsdp", "ctx")),
        P(("fsdp", "ctx")),
    )

    return jax.shard_map(shards, mesh=mesh, in_specs=in_specs, out_specs=out_specs, check_vma=False)
```

```python
import functools

import jax
import jax.numpy as jnp
from jax import lax
from jax.experimental import pallas as pl
from jax.experimental.pallas import tpu as pltpu
from jax.sharding import PartitionSpec as P


HEADS = 16
HEAD_DIM = 64


EPS = 1e-06
NEG = -1e30
THETA = 10000.0
SCORE_CAP = 4194304


def rotate(field, positions, direction):
    head_width = field.shape[-1]
    half_width = head_width // 2
    frequency = THETA ** (-(jnp.arange(half_width, dtype=jnp.float32) * 2.0) / head_width)
    angles = positions.astype(jnp.float32)[:, None] * frequency[None, :]
    cosine = jnp.cos(angles)[:, None, :]
    sine_part = direction * jnp.sin(angles)[:, None, :]
    former = field[..., :half_width]
    latter = field[..., half_width:]
    return jnp.concatenate(
        [former * cosine - latter * sine_part, latter * cosine + former * sine_part], axis=-1
    )


def normalize(values, gain):
    inverse = lax.rsqrt(jnp.mean(values * values, axis=-1, keepdims=True) + EPS)
    return (values * inverse * gain, inverse)


def normalize_back(values, inverse, gain, upstream):
    unit_rows = values * inverse
    scaled = upstream * gain
    grad_gain = jnp.sum(upstream * unit_rows, axis=(0, 1))
    grad_values = inverse * (
        scaled - unit_rows * jnp.mean(scaled * unit_rows, axis=-1, keepdims=True)
    )
    return (grad_values, grad_gain)


def head_groups(n_slots, q_len, n_heads, k_len):
    q_block = min(q_len, 512)
    per_group = max(1, min(n_heads, SCORE_CAP // (n_slots * q_block * k_len)))
    while n_heads % per_group:
        per_group = per_group - 1
    return (q_block, per_group)


def split_heads(packed, n_groups):
    n_slots, length, n_heads, head_width = packed.shape
    return jnp.moveaxis(
        packed.reshape(n_slots, length, n_groups, n_heads // n_groups, head_width), 2, 0
    )


def join_heads(grouped):
    n_groups, n_slots, length, per_group, head_width = grouped.shape
    return jnp.moveaxis(grouped, 0, 2).reshape(n_slots, length, n_groups * per_group, head_width)


def score_block(q_rows, k_rows, q_pos, k_pos, lengths):
    products = jnp.einsum(
        "sqhe,skhe->shqk", q_rows, k_rows, preferred_element_type=jnp.float32
    ) * q_rows.shape[-1] ** (-0.5)
    causal = (k_pos[None, None, None, :] <= q_pos[None, None, :, None]) & (
        k_pos[None, None, None, :] >= 0
    )
    filled = k_pos[None, None, None, :] < lengths[:, None, None, None]
    return jnp.where(causal & filled, products, NEG)


def attend_forward(queries, keys, values, q_pos, k_pos, lengths):
    n_slots, q_len, n_heads, head_width = queries.shape
    q_block, per_group = head_groups(n_slots, q_len, n_heads, keys.shape[1])
    n_groups = n_heads // per_group
    n_blocks = q_len // q_block
    pos_blocks = q_pos.reshape(n_blocks, q_block)

    def one_group(packed):
        q_group, k_group, v_group = packed
        q_blocks = jnp.moveaxis(
            q_group.reshape(n_slots, n_blocks, q_block, per_group, head_width), 1, 0
        )

        def one_block(streams):
            q_rows, pos_rows = streams
            scores = score_block(q_rows, k_group, pos_rows, k_pos, lengths)
            highest = jnp.max(scores, axis=-1, keepdims=True)
            exponent = jnp.exp(scores - highest)
            totals = jnp.sum(exponent, axis=-1, keepdims=True)
            probabilities = (exponent / totals).astype(jnp.bfloat16)
            mixture = jnp.einsum(
                "shqk,skhe->sqhe", probabilities, v_group, preferred_element_type=jnp.float32
            )
            return (mixture, (highest + jnp.log(totals))[..., 0])

        mixture, log_sums = lax.map(one_block, (q_blocks, pos_blocks))
        return (
            jnp.moveaxis(mixture, 0, 1).reshape(n_slots, q_len, per_group, head_width),
            log_sums,
        )

    grouped = (
        split_heads(queries, n_groups),
        split_heads(keys, n_groups),
        split_heads(values, n_groups),
    )
    mixture, log_sums = lax.map(one_group, grouped)
    return (join_heads(mixture), log_sums)


def attend_backward(queries, keys, values, upstream, row_dots, log_sums, q_pos, k_pos, lengths):
    n_slots, q_len, n_heads, head_width = queries.shape
    q_block, per_group = head_groups(n_slots, q_len, n_heads, keys.shape[1])
    n_groups = n_heads // per_group
    n_blocks = q_len // q_block
    score_scale = head_width ** (-0.5)
    pos_blocks = q_pos.reshape(n_blocks, q_block)
    dot_groups = jnp.moveaxis(row_dots.reshape(n_slots, q_len, n_groups, per_group), 2, 0)

    def blocks_of(grouped):
        return jnp.moveaxis(grouped.reshape((n_slots, n_blocks, q_block) + grouped.shape[2:]), 1, 0)

    def one_group(packed):
        q_group, k_group, v_group, g_group, d_group, l_group = packed

        def one_block(running, streams):
            k_grad, v_grad = running
            q_rows, g_rows, d_rows, l_rows, pos_rows = streams
            scores = score_block(q_rows, k_group, pos_rows, k_pos, lengths)
            probabilities = jnp.exp(scores - l_rows[..., None])
            v_grad = v_grad + jnp.einsum(
                "shqk,sqhe->skhe",
                probabilities.astype(jnp.bfloat16),
                g_rows,
                preferred_element_type=jnp.float32,
            )
            p_grad = jnp.einsum(
                "sqhe,skhe->shqk", g_rows, v_group, preferred_element_type=jnp.float32
            )
            s_grad = (probabilities * (p_grad - jnp.moveaxis(d_rows, 2, 1)[..., None])).astype(
                jnp.bfloat16
            )
            q_grad = (
                jnp.einsum("shqk,skhe->sqhe", s_grad, k_group, preferred_element_type=jnp.float32)
                * score_scale
            )
            k_grad = (
                k_grad
                + jnp.einsum("shqk,sqhe->skhe", s_grad, q_rows, preferred_element_type=jnp.float32)
                * score_scale
            )
            return ((k_grad, v_grad), q_grad)

        empty_grads = jnp.zeros(k_group.shape, jnp.float32)
        streams = (blocks_of(q_group), blocks_of(g_group), blocks_of(d_group), l_group, pos_blocks)
        (k_grad, v_grad), q_grads = lax.scan(one_block, (empty_grads, empty_grads), streams)
        return (
            jnp.moveaxis(q_grads, 0, 1).reshape(n_slots, q_len, per_group, head_width),
            k_grad,
            v_grad,
        )

    grouped = (
        split_heads(queries, n_groups),
        split_heads(keys, n_groups),
        split_heads(values, n_groups),
        split_heads(upstream, n_groups),
        dot_groups,
        log_sums,
    )
    q_grads, k_grads, v_grads = lax.map(one_group, grouped)
    return (join_heads(q_grads), join_heads(k_grads), join_heads(v_grads))


FAR = 1 << 30


def _block_backward_kernel(q_ref, k_ref, v_ref, g_ref, lse_ref, dots_ref, qpos_ref, kpos_ref,
                           dq_ref, dk_ref, dv_ref, *, head_width, scale):
    pair = pl.program_id(1)
    allowed = kpos_ref[0] <= qpos_ref[...]
    for j in range(2):
        cols = slice(j * head_width, (j + 1) * head_width)
        q = q_ref[0, :, cols]
        k = k_ref[0, :, cols]
        v = v_ref[0, :, cols]
        g = g_ref[0, :, cols]
        head = 2 * pair + j
        lse = lse_ref[0, pl.ds(head, 1), :]
        dots = dots_ref[0, pl.ds(head, 1), :]
        nt = (((1,), (1,)), ((), ()))
        scores = lax.dot_general(k, q, nt, preferred_element_type=jnp.float32) * scale
        scores = jnp.where(allowed, scores, -1e30)
        probs = jnp.exp(scores - lse)
        dv_ref[0, :, cols] = jnp.dot(probs.astype(jnp.bfloat16), g, preferred_element_type=jnp.float32)
        dprobs = lax.dot_general(v, g, nt, preferred_element_type=jnp.float32)
        dscores = (probs * (dprobs - dots)).astype(jnp.bfloat16)
        dk_ref[0, :, cols] = jnp.dot(dscores, q, preferred_element_type=jnp.float32) * scale
        tn = (((0,), (0,)), ((), ()))
        dq_ref[0, :, cols] = lax.dot_general(dscores, k, tn, preferred_element_type=jnp.float32) * scale


def _block_forward_kernel(q_ref, k_ref, v_ref, qpos_ref, kpos_ref, out_ref, lse_ref, *, head_width, scale):
    pair = pl.program_id(1)
    allowed = kpos_ref[0] <= qpos_ref[...]
    nt = (((1,), (1,)), ((), ()))
    tn = (((0,), (0,)), ((), ()))
    for j in range(2):
        cols = slice(j * head_width, (j + 1) * head_width)
        q = q_ref[0, :, cols]
        k = k_ref[0, :, cols]
        v = v_ref[0, :, cols]
        scores = lax.dot_general(k, q, nt, preferred_element_type=jnp.float32) * scale
        scores = jnp.where(allowed, scores, -1e30)
        highest = jnp.max(scores, axis=0, keepdims=True)
        exponent = jnp.exp(scores - highest)
        totals = jnp.sum(exponent, axis=0, keepdims=True)
        probs = (exponent / totals).astype(jnp.bfloat16)
        mixture = lax.dot_general(probs, v, tn, preferred_element_type=jnp.float32)
        out_ref[0, :, cols] = mixture.astype(out_ref.dtype)
        lse_ref[0, pl.ds(2 * pair + j, 1), :] = highest + jnp.log(totals)


def block_forward(queries, keys, values, q_pos, k_pos, lengths):
    n_slots, q_len, n_heads, head_width = queries.shape
    k_len = keys.shape[1]
    width = n_heads * head_width
    pair_width = 2 * head_width
    flat = lambda a: a.reshape(a.shape[0], a.shape[1], width)
    kpos = jnp.where(
        (k_pos[None, :] < lengths[:, None]) & (k_pos[None, :] >= 0), k_pos[None, :], FAR
    ).astype(jnp.int32)[..., None]
    qpos = q_pos.astype(jnp.int32)[None, :]
    kernel = functools.partial(_block_forward_kernel, head_width=head_width, scale=head_width ** (-0.5))
    q_spec = pl.BlockSpec((1, q_len, pair_width), lambda s, p: (s, 0, p))
    k_spec = pl.BlockSpec((1, k_len, pair_width), lambda s, p: (s, 0, p))
    out, lse = pl.pallas_call(
        kernel,
        grid=(n_slots, n_heads // 2),
        in_specs=[
            q_spec, k_spec, k_spec,
            pl.BlockSpec((1, q_len), lambda s, p: (0, 0)),
            pl.BlockSpec((1, k_len, 1), lambda s, p: (s, 0, 0)),
        ],
        out_specs=[q_spec, pl.BlockSpec((1, n_heads, q_len), lambda s, p: (s, 0, 0))],
        out_shape=[
            jax.ShapeDtypeStruct((n_slots, q_len, width), jnp.bfloat16),
            jax.ShapeDtypeStruct((n_slots, n_heads, q_len), jnp.float32),
        ],
        compiler_params=pltpu.CompilerParams(dimension_semantics=("arbitrary", "arbitrary")),
        cost_estimate=pl.CostEstimate(
            flops=n_slots * n_heads * 4 * q_len * k_len * head_width,
            transcendentals=n_slots * n_heads * q_len * k_len,
            bytes_accessed=2 * (2 * q_len + 2 * k_len) * width * n_slots,
        ),
    )(flat(queries), flat(keys), flat(values), qpos, kpos)
    return out.reshape(n_slots, q_len, n_heads, head_width), lse


def block_backward(queries, keys, values, upstream, lse_rows, dot_rows, q_pos, k_pos, lengths):
    n_slots, q_len, n_heads, head_width = queries.shape
    k_len = keys.shape[1]
    width = n_heads * head_width
    pair_width = 2 * head_width
    flat = lambda a: a.reshape(a.shape[0], a.shape[1], width)
    kpos = jnp.where(
        (k_pos[None, :] < lengths[:, None]) & (k_pos[None, :] >= 0), k_pos[None, :], FAR
    ).astype(jnp.int32)[..., None]
    qpos = q_pos.astype(jnp.int32)[None, :]
    kernel = functools.partial(_block_backward_kernel, head_width=head_width, scale=head_width ** (-0.5))
    q_spec = pl.BlockSpec((1, q_len, pair_width), lambda s, p: (s, 0, p))
    k_spec = pl.BlockSpec((1, k_len, pair_width), lambda s, p: (s, 0, p))
    row_spec = pl.BlockSpec((1, n_heads, q_len), lambda s, p: (s, 0, 0))
    flops = n_slots * n_heads * 10 * q_len * k_len * head_width
    dq, dk, dv = pl.pallas_call(
        kernel,
        grid=(n_slots, n_heads // 2),
        in_specs=[
            q_spec, k_spec, k_spec, q_spec, row_spec, row_spec,
            pl.BlockSpec((1, q_len), lambda s, p: (0, 0)),
            pl.BlockSpec((1, k_len, 1), lambda s, p: (s, 0, 0)),
        ],
        out_specs=[q_spec, k_spec, k_spec],
        out_shape=[
            jax.ShapeDtypeStruct((n_slots, q_len, width), jnp.float32),
            jax.ShapeDtypeStruct((n_slots, k_len, width), jnp.float32),
            jax.ShapeDtypeStruct((n_slots, k_len, width), jnp.float32),
        ],
        cost_estimate=pl.CostEstimate(
            flops=flops,
            transcendentals=n_slots * n_heads * q_len * k_len,
            bytes_accessed=2 * (2 * q_len + 2 * k_len) * width * n_slots + 4 * (q_len + 2 * k_len) * width * n_slots,
        ),
    )(flat(queries), flat(keys), flat(values), flat(upstream), lse_rows, dot_rows, qpos, kpos)
    shape_q = (n_slots, q_len, n_heads, head_width)
    shape_k = (n_slots, k_len, n_heads, head_width)
    return dq.reshape(shape_q), dk.reshape(shape_k), dv.reshape(shape_k)


GROUP = ("fsdp", "ctx")


def gather_blocks(pieces):
    packed = jnp.concatenate(pieces, axis=0)
    gathered = lax.all_gather(packed, GROUP, axis=0, tiled=False)
    fulls, offset = [], 0
    for piece in pieces:
        fulls.append(gathered[:, offset : offset + piece.shape[0], :])
        offset += piece.shape[0]
    return fulls


def rep_sum(x):
    n_rep = lax.axis_size("rep")
    if n_rep != 4:
        return lax.psum(x, "rep")
    me = lax.axis_index("rep")
    arrived = lax.ppermute(x, "rep", [(0, 1), (3, 2)])
    folded = (x.astype(jnp.float32) + arrived.astype(jnp.float32)).astype(x.dtype)
    arrived = lax.ppermute(folded, "rep", [(1, 2), (2, 1)])
    total = (folded.astype(jnp.float32) + arrived.astype(jnp.float32)).astype(x.dtype)
    sent_out = lax.ppermute(total, "rep", [(1, 0), (2, 3)])
    return jnp.where((me == 0) | (me == 3), sent_out, total)


def scatter_blocks(blocks, by_permutes):
    packed = jnp.concatenate(blocks, axis=1).astype(jnp.bfloat16)
    summed = lax.psum_scatter(packed, GROUP, scatter_dimension=0, tiled=True)
    summed = (rep_sum(summed) if by_permutes else lax.psum(summed, "rep"))[0].astype(jnp.float32)
    parts, offset = [], 0
    for block in blocks:
        parts.append(summed[offset : offset + block.shape[1], :])
        offset += block.shape[1]
    return parts


def gain_block(first, second, width):
    lead = first.shape[:-1]
    row = jnp.concatenate([first, second], axis=-1)
    row = jnp.pad(row, [(0, 0)] * len(lead) + [(0, width - row.shape[-1])])
    return jnp.pad(row[..., None, :], [(0, 0)] * len(lead) + [(0, 7), (0, 0)])


def shards(
    tokens,
    initial_layer_values,
    cotangent,
    lengths,
    w_query,
    w_key,
    w_value,
    w_out,
    w_gate,
    w_up,
    w_down,
    gain_attn,
    gain_mlp,
):
    n_slots, slot_rows, model_width = tokens.shape
    n_ctx = lax.axis_size("ctx")
    n_group = lax.axis_size("fsdp") * n_ctx
    own_rows = gain_attn.shape[0]
    ff_width = w_gate.shape[1]
    attn_width = w_query.shape[1]
    qkv_width = 3 * attn_width
    (qkv_blocks, gain_rows) = gather_blocks(
        [
            jnp.concatenate([w_query, w_key, w_value], axis=1),
            gain_block(gain_attn, gain_mlp, qkv_width),
        ]
    )
    full_qkv = qkv_blocks.reshape(n_group * own_rows, qkv_width)
    full_gain_attn = gain_rows[:, 0, :own_rows].reshape(-1)
    full_gain_mlp = gain_rows[:, 0, own_rows : 2 * own_rows].reshape(-1)
    (out_blocks,) = gather_blocks([w_out])
    full_out = out_blocks.reshape(-1, model_width)
    (gu_blocks,) = gather_blocks([jnp.concatenate([w_gate, w_up], axis=1)])
    full_gu = gu_blocks.reshape(n_group * own_rows, 2 * ff_width)
    (down_blocks,) = gather_blocks([w_down])
    full_down = down_blocks.reshape(-1, model_width)
    ctx_index = lax.axis_index("ctx")
    q_pos = ctx_index * slot_rows + jnp.arange(slot_rows)
    live_rows = q_pos[None, :] < lengths[:, None]
    head_shape = (n_slots, slot_rows, HEADS, HEAD_DIM)
    paired = n_ctx == 2
    if paired:
        other_tokens = lax.ppermute(tokens, "ctx", [(0, 1), (1, 0)])
        other_first = lax.ppermute(initial_layer_values, "ctx", [(0, 1)])
        other_pos = (1 - ctx_index) * slot_rows + jnp.arange(slot_rows)
    inputs = tokens.astype(jnp.float32)
    attn_scale = full_gain_attn.astype(jnp.float32)
    mlp_scale = full_gain_mlp.astype(jnp.float32)

    def project(chunk_tokens, chunk_first, chunk_pos):
        chunk_normed, chunk_inv = normalize(chunk_tokens.astype(jnp.float32), attn_scale)
        chunk_low = chunk_normed.astype(jnp.bfloat16)
        qkv_pre = jnp.einsum(
            "srd,de->sre", chunk_low, full_qkv, preferred_element_type=jnp.float32
        )
        q_pre = qkv_pre[..., :attn_width]
        k_pre = qkv_pre[..., attn_width : 2 * attn_width]
        v_pre = qkv_pre[..., 2 * attn_width :]
        chunk_q = rotate(q_pre.reshape(head_shape), chunk_pos, 1.0).astype(jnp.bfloat16)
        chunk_k = rotate(k_pre.reshape(head_shape), chunk_pos, 1.0).astype(jnp.bfloat16)
        chunk_v = (
            (0.5 * v_pre + 0.5 * chunk_first.astype(jnp.float32))
            .astype(jnp.bfloat16)
            .reshape(head_shape)
        )
        return chunk_low, chunk_inv, chunk_q, chunk_k, chunk_v

    normed_low, inv_attn, queries, keys, values = project(tokens, initial_layer_values, q_pos)
    if paired:
        _, _, other_q, other_k, other_v = project(other_tokens, other_first, other_pos)
        slot_k = jnp.concatenate([other_k, keys], axis=1)
        slot_v = jnp.concatenate([other_v, values], axis=1)
        k_pos = jnp.concatenate([other_pos, q_pos])
    else:
        slot_k, slot_v = (
            lax.all_gather(keys, "ctx", axis=1, tiled=True),
            lax.all_gather(values, "ctx", axis=1, tiled=True),
        )
        k_pos = jnp.arange(n_ctx * slot_rows)
    if paired:
        attended, lse_rows = block_forward(queries, slot_k, slot_v, q_pos, k_pos, lengths)
    else:
        attn_raw, attn_lse = attend_forward(queries, slot_k, slot_v, q_pos, k_pos, lengths)
        attended = attn_raw.astype(jnp.bfloat16)
    att_flat = attended.reshape(n_slots, slot_rows, model_width)
    branch = jnp.einsum("sre,ed->srd", att_flat, full_out, preferred_element_type=jnp.float32)
    residual = inputs + branch
    normed_mlp, inv_mlp = normalize(residual, mlp_scale)
    mlp_low = normed_mlp.astype(jnp.bfloat16)
    gu_proj = jnp.einsum("srd,df->srf", mlp_low, full_gu, preferred_element_type=jnp.float32)
    gate_proj = gu_proj[..., :ff_width]
    up_proj = gu_proj[..., ff_width:]
    sigmoid_gate = jax.nn.sigmoid(gate_proj)
    hidden = (gate_proj * sigmoid_gate * up_proj).astype(jnp.bfloat16)
    final = residual + jnp.einsum(
        "srf,fd->srd", hidden, full_down, preferred_element_type=jnp.float32
    )
    output = jnp.where(live_rows[..., None], final, 0.0).astype(jnp.bfloat16)
    output_gradient = jnp.where(live_rows[..., None], cotangent.astype(jnp.float32), 0.0)
    g_low = output_gradient.astype(jnp.bfloat16)
    gu_alone = lax.optimization_barrier(gu_proj)
    gate_alone = gu_alone[..., :ff_width]
    hidden_alone = (gate_alone * jax.nn.sigmoid(gate_alone) * gu_alone[..., ff_width:]).astype(
        jnp.bfloat16
    )
    grad_down = jnp.einsum(
        "srf,srd->fd", hidden_alone, g_low, preferred_element_type=jnp.float32
    )
    (part_down,) = scatter_blocks(
        [grad_down.reshape(n_group, -1, model_width).astype(jnp.bfloat16)], True
    )
    g_hidden = jnp.einsum("srd,fd->srf", g_low, full_down, preferred_element_type=jnp.float32)
    gate_gradient = (g_hidden * up_proj * sigmoid_gate * (1.0 + gate_proj * (1.0 - sigmoid_gate))).astype(jnp.bfloat16)
    up_gradient = (g_hidden * gate_proj * sigmoid_gate).astype(jnp.bfloat16)
    gu_gradient = jnp.concatenate([gate_gradient, up_gradient], axis=-1)
    grad_gu = jnp.einsum(
        "srd,srf->df", mlp_low, gu_gradient, preferred_element_type=jnp.float32
    )
    g_normed_mlp = jnp.einsum(
        "srf,df->srd", gu_gradient, full_gu, preferred_element_type=jnp.float32
    )
    g_mlp_in, grad_gain_mlp = normalize_back(residual, inv_mlp, mlp_scale, g_normed_mlp)
    g_residual = output_gradient + g_mlp_in
    g_branch = g_residual.astype(jnp.bfloat16)
    grad_out = jnp.einsum(
        "sre,srd->ed", att_flat, g_branch, preferred_element_type=jnp.float32
    )
    ogu_block = (
        jnp.concatenate([grad_out, grad_gu], axis=1)
        .reshape(n_group, own_rows, model_width + 2 * ff_width)
        .astype(jnp.bfloat16)
    )
    g_attended = (
        jnp.einsum("srd,ed->sre", g_branch, full_out, preferred_element_type=jnp.float32)
        .astype(jnp.bfloat16)
        .reshape(head_shape)
    )
    (part_ogu,) = scatter_blocks([ogu_block], True)
    row_dots = jnp.sum(g_attended.astype(jnp.float32) * attended.astype(jnp.float32), axis=-1)
    if paired:
        dot_rows = jnp.transpose(row_dots, (0, 2, 1))
        later_g, later_dots, later_lse = lax.ppermute(
            (g_attended, dot_rows, lse_rows), "ctx", [(1, 0)]
        )
        g_queries, g_keys, g_values = block_backward(
            queries, keys, values, g_attended, lse_rows, dot_rows, q_pos, q_pos, lengths
        )
        later = ctx_index == 1
        pick = lambda mine, theirs: jnp.where(later, mine, theirs)
        x_dq, x_dk, x_dv = block_backward(
            pick(queries, other_q),
            pick(other_k, keys),
            pick(other_v, values),
            pick(g_attended, later_g),
            pick(lse_rows, later_lse),
            pick(dot_rows, later_dots),
            pick(q_pos, other_pos),
            pick(other_pos, q_pos),
            lengths,
        )
        g_queries = g_queries + jnp.where(later, x_dq, 0.0)
        g_keys = g_keys + jnp.where(later, 0.0, x_dk)
        g_values = g_values + jnp.where(later, 0.0, x_dv)
    else:
        g_queries, slot_dk, slot_dv = attend_backward(
            queries, slot_k, slot_v, g_attended, row_dots, attn_lse, q_pos, k_pos, lengths
        )
        g_keys, g_values = (
            lax.psum_scatter(
                slot_dk.astype(jnp.bfloat16), "ctx", scatter_dimension=1, tiled=True
            ).astype(jnp.float32),
            lax.psum_scatter(
                slot_dv.astype(jnp.bfloat16), "ctx", scatter_dimension=1, tiled=True
            ).astype(jnp.float32),
        )
    flat_shape = (n_slots, slot_rows, model_width)
    gq_low = rotate(g_queries, q_pos, -1.0).reshape(flat_shape).astype(jnp.bfloat16)
    gk_low = rotate(g_keys, q_pos, -1.0).reshape(flat_shape).astype(jnp.bfloat16)
    gv_rounded = g_values.reshape(flat_shape).astype(jnp.bfloat16).astype(jnp.float32)
    d_first = 0.5 * gv_rounded
    gv_half = d_first.astype(jnp.bfloat16)
    g_qkv = jnp.concatenate([gq_low, gk_low, gv_half], axis=-1)
    grad_qkv = jnp.einsum("srd,sre->de", normed_low, g_qkv, preferred_element_type=jnp.float32)
    g_normed = jnp.einsum("sre,de->srd", g_qkv, full_qkv, preferred_element_type=jnp.float32)
    g_attn_in, grad_gain_attn = normalize_back(inputs, inv_attn, attn_scale, g_normed)
    d_tokens = g_residual + g_attn_in
    part_qkv, part_gains = scatter_blocks(
        [
            grad_qkv.reshape(n_group, own_rows, qkv_width),
            gain_block(grad_gain_attn.reshape(n_group, own_rows), grad_gain_mlp.reshape(n_group, own_rows), qkv_width),
        ],
        False,
    )
    return (
        output,
        d_tokens,
        d_first,
        part_qkv[:, :attn_width],
        part_qkv[:, attn_width : 2 * attn_width],
        part_qkv[:, 2 * attn_width :],
        part_ogu[:, :model_width],
        part_ogu[:, model_width : model_width + ff_width],
        part_ogu[:, model_width + ff_width :],
        part_down,
        part_gains[0, :own_rows],
        part_gains[0, own_rows : 2 * own_rows],
    )


def solution(mesh):
    in_specs = (
        P(("rep", "fsdp"), "ctx", None),
        P(("rep", "fsdp"), "ctx", None),
        P(("rep", "fsdp"), "ctx", None),
        P(("rep", "fsdp")),
        P(("fsdp", "ctx"), None),
        P(("fsdp", "ctx"), None),
        P(("fsdp", "ctx"), None),
        P(("fsdp", "ctx"), None),
        P(("fsdp", "ctx"), None),
        P(("fsdp", "ctx"), None),
        P(("fsdp", "ctx"), None),
        P(("fsdp", "ctx")),
        P(("fsdp", "ctx")),
    )
    out_specs = (
        P(("rep", "fsdp"), "ctx", None),
        P(("rep", "fsdp"), "ctx", None),
        P(("rep", "fsdp"), "ctx", None),
        P(("fsdp", "ctx"), None),
        P(("fsdp", "ctx"), None),
        P(("fsdp", "ctx"), None),
        P(("fsdp", "ctx"), None),
        P(("fsdp", "ctx"), None),
        P(("fsdp", "ctx"), None),
        P(("fsdp", "ctx"), None),
        P(("fsdp", "ctx")),
        P(("fsdp", "ctx")),
    )

    return jax.shard_map(shards, mesh=mesh, in_specs=in_specs, out_specs=out_specs, check_vma=False)
```

```python
import functools

import jax
import jax.numpy as jnp
from jax import lax
from jax.experimental import pallas as pl
from jax.experimental.pallas import tpu as pltpu
from jax.sharding import PartitionSpec as P


HEADS = 16
HEAD_DIM = 64


EPS = 1e-06
NEG = -1e30
THETA = 10000.0
SCORE_CAP = 4194304


def rotate(field, positions, direction):
    head_width = field.shape[-1]
    half_width = head_width // 2
    frequency = THETA ** (-(jnp.arange(half_width, dtype=jnp.float32) * 2.0) / head_width)
    angles = positions.astype(jnp.float32)[:, None] * frequency[None, :]
    cosine = jnp.cos(angles)[:, None, :]
    sine_part = direction * jnp.sin(angles)[:, None, :]
    former = field[..., :half_width]
    latter = field[..., half_width:]
    return jnp.concatenate(
        [former * cosine - latter * sine_part, latter * cosine + former * sine_part], axis=-1
    )


def normalize(values, gain):
    inverse = lax.rsqrt(jnp.mean(values * values, axis=-1, keepdims=True) + EPS)
    return (values * inverse * gain, inverse)


def normalize_back(values, inverse, gain, upstream):
    unit_rows = values * inverse
    scaled = upstream * gain
    grad_gain = jnp.sum(upstream * unit_rows, axis=(0, 1))
    grad_values = inverse * (
        scaled - unit_rows * jnp.mean(scaled * unit_rows, axis=-1, keepdims=True)
    )
    return (grad_values, grad_gain)


def head_groups(n_slots, q_len, n_heads, k_len):
    q_block = min(q_len, 512)
    per_group = max(1, min(n_heads, SCORE_CAP // (n_slots * q_block * k_len)))
    while n_heads % per_group:
        per_group = per_group - 1
    return (q_block, per_group)


def split_heads(packed, n_groups):
    n_slots, length, n_heads, head_width = packed.shape
    return jnp.moveaxis(
        packed.reshape(n_slots, length, n_groups, n_heads // n_groups, head_width), 2, 0
    )


def join_heads(grouped):
    n_groups, n_slots, length, per_group, head_width = grouped.shape
    return jnp.moveaxis(grouped, 0, 2).reshape(n_slots, length, n_groups * per_group, head_width)


def score_block(q_rows, k_rows, q_pos, k_pos, lengths):
    products = jnp.einsum(
        "sqhe,skhe->shqk", q_rows, k_rows, preferred_element_type=jnp.float32
    ) * q_rows.shape[-1] ** (-0.5)
    causal = (k_pos[None, None, None, :] <= q_pos[None, None, :, None]) & (
        k_pos[None, None, None, :] >= 0
    )
    filled = k_pos[None, None, None, :] < lengths[:, None, None, None]
    return jnp.where(causal & filled, products, NEG)


def attend_forward(queries, keys, values, q_pos, k_pos, lengths):
    n_slots, q_len, n_heads, head_width = queries.shape
    q_block, per_group = head_groups(n_slots, q_len, n_heads, keys.shape[1])
    n_groups = n_heads // per_group
    n_blocks = q_len // q_block
    pos_blocks = q_pos.reshape(n_blocks, q_block)

    def one_group(packed):
        q_group, k_group, v_group = packed
        q_blocks = jnp.moveaxis(
            q_group.reshape(n_slots, n_blocks, q_block, per_group, head_width), 1, 0
        )

        def one_block(streams):
            q_rows, pos_rows = streams
            scores = score_block(q_rows, k_group, pos_rows, k_pos, lengths)
            highest = jnp.max(scores, axis=-1, keepdims=True)
            exponent = jnp.exp(scores - highest)
            totals = jnp.sum(exponent, axis=-1, keepdims=True)
            probabilities = (exponent / totals).astype(jnp.bfloat16)
            mixture = jnp.einsum(
                "shqk,skhe->sqhe", probabilities, v_group, preferred_element_type=jnp.float32
            )
            return (mixture, (highest + jnp.log(totals))[..., 0])

        mixture, log_sums = lax.map(one_block, (q_blocks, pos_blocks))
        return (
            jnp.moveaxis(mixture, 0, 1).reshape(n_slots, q_len, per_group, head_width),
            log_sums,
        )

    grouped = (
        split_heads(queries, n_groups),
        split_heads(keys, n_groups),
        split_heads(values, n_groups),
    )
    mixture, log_sums = lax.map(one_group, grouped)
    return (join_heads(mixture), log_sums)


def attend_backward(queries, keys, values, upstream, row_dots, log_sums, q_pos, k_pos, lengths):
    n_slots, q_len, n_heads, head_width = queries.shape
    q_block, per_group = head_groups(n_slots, q_len, n_heads, keys.shape[1])
    n_groups = n_heads // per_group
    n_blocks = q_len // q_block
    score_scale = head_width ** (-0.5)
    pos_blocks = q_pos.reshape(n_blocks, q_block)
    dot_groups = jnp.moveaxis(row_dots.reshape(n_slots, q_len, n_groups, per_group), 2, 0)

    def blocks_of(grouped):
        return jnp.moveaxis(grouped.reshape((n_slots, n_blocks, q_block) + grouped.shape[2:]), 1, 0)

    def one_group(packed):
        q_group, k_group, v_group, g_group, d_group, l_group = packed

        def one_block(running, streams):
            k_grad, v_grad = running
            q_rows, g_rows, d_rows, l_rows, pos_rows = streams
            scores = score_block(q_rows, k_group, pos_rows, k_pos, lengths)
            probabilities = jnp.exp(scores - l_rows[..., None])
            v_grad = v_grad + jnp.einsum(
                "shqk,sqhe->skhe",
                probabilities.astype(jnp.bfloat16),
                g_rows,
                preferred_element_type=jnp.float32,
            )
            p_grad = jnp.einsum(
                "sqhe,skhe->shqk", g_rows, v_group, preferred_element_type=jnp.float32
            )
            s_grad = (probabilities * (p_grad - jnp.moveaxis(d_rows, 2, 1)[..., None])).astype(
                jnp.bfloat16
            )
            q_grad = (
                jnp.einsum("shqk,skhe->sqhe", s_grad, k_group, preferred_element_type=jnp.float32)
                * score_scale
            )
            k_grad = (
                k_grad
                + jnp.einsum("shqk,sqhe->skhe", s_grad, q_rows, preferred_element_type=jnp.float32)
                * score_scale
            )
            return ((k_grad, v_grad), q_grad)

        empty_grads = jnp.zeros(k_group.shape, jnp.float32)
        streams = (blocks_of(q_group), blocks_of(g_group), blocks_of(d_group), l_group, pos_blocks)
        (k_grad, v_grad), q_grads = lax.scan(one_block, (empty_grads, empty_grads), streams)
        return (
            jnp.moveaxis(q_grads, 0, 1).reshape(n_slots, q_len, per_group, head_width),
            k_grad,
            v_grad,
        )

    grouped = (
        split_heads(queries, n_groups),
        split_heads(keys, n_groups),
        split_heads(values, n_groups),
        split_heads(upstream, n_groups),
        dot_groups,
        log_sums,
    )
    q_grads, k_grads, v_grads = lax.map(one_group, grouped)
    return (join_heads(q_grads), join_heads(k_grads), join_heads(v_grads))


FAR = 1 << 30


def _block_backward_kernel(q_ref, k_ref, v_ref, g_ref, lse_ref, dots_ref, qpos_ref, kpos_ref,
                           dq_ref, dk_ref, dv_ref, *, head_width, scale):
    pair = pl.program_id(1)
    allowed = kpos_ref[0] <= qpos_ref[...]
    for j in range(2):
        cols = slice(j * head_width, (j + 1) * head_width)
        q = q_ref[0, :, cols]
        k = k_ref[0, :, cols]
        v = v_ref[0, :, cols]
        g = g_ref[0, :, cols]
        head = 2 * pair + j
        lse = lse_ref[0, pl.ds(head, 1), :]
        dots = dots_ref[0, pl.ds(head, 1), :]
        nt = (((1,), (1,)), ((), ()))
        scores = lax.dot_general(k, q, nt, preferred_element_type=jnp.float32) * scale
        scores = jnp.where(allowed, scores, -1e30)
        probs = jnp.exp(scores - lse)
        dv_ref[0, :, cols] = jnp.dot(probs.astype(jnp.bfloat16), g, preferred_element_type=jnp.float32)
        dprobs = lax.dot_general(v, g, nt, preferred_element_type=jnp.float32)
        dscores = (probs * (dprobs - dots)).astype(jnp.bfloat16)
        dk_ref[0, :, cols] = jnp.dot(dscores, q, preferred_element_type=jnp.float32) * scale
        tn = (((0,), (0,)), ((), ()))
        dq_ref[0, :, cols] = lax.dot_general(dscores, k, tn, preferred_element_type=jnp.float32) * scale


def _block_forward_kernel(q_ref, k_ref, v_ref, qpos_ref, kpos_ref, out_ref, lse_ref, *, head_width, scale):
    pair = pl.program_id(1)
    allowed = kpos_ref[0] <= qpos_ref[...]
    nt = (((1,), (1,)), ((), ()))
    tn = (((0,), (0,)), ((), ()))
    for j in range(2):
        cols = slice(j * head_width, (j + 1) * head_width)
        q = q_ref[0, :, cols]
        k = k_ref[0, :, cols]
        v = v_ref[0, :, cols]
        scores = lax.dot_general(k, q, nt, preferred_element_type=jnp.float32) * scale
        scores = jnp.where(allowed, scores, -1e30)
        highest = jnp.max(scores, axis=0, keepdims=True)
        exponent = jnp.exp(scores - highest)
        totals = jnp.sum(exponent, axis=0, keepdims=True)
        probs = (exponent / totals).astype(jnp.bfloat16)
        mixture = lax.dot_general(probs, v, tn, preferred_element_type=jnp.float32)
        out_ref[0, :, cols] = mixture.astype(out_ref.dtype)
        lse_ref[0, pl.ds(2 * pair + j, 1), :] = highest + jnp.log(totals)


def block_forward(queries, keys, values, q_pos, k_pos, lengths):
    n_slots, q_len, n_heads, head_width = queries.shape
    k_len = keys.shape[1]
    width = n_heads * head_width
    pair_width = 2 * head_width
    flat = lambda a: a.reshape(a.shape[0], a.shape[1], width)
    kpos = jnp.where(
        (k_pos[None, :] < lengths[:, None]) & (k_pos[None, :] >= 0), k_pos[None, :], FAR
    ).astype(jnp.int32)[..., None]
    qpos = q_pos.astype(jnp.int32)[None, :]
    kernel = functools.partial(_block_forward_kernel, head_width=head_width, scale=head_width ** (-0.5))
    q_spec = pl.BlockSpec((1, q_len, pair_width), lambda s, p: (s, 0, p))
    k_spec = pl.BlockSpec((1, k_len, pair_width), lambda s, p: (s, 0, p))
    out, lse = pl.pallas_call(
        kernel,
        grid=(n_slots, n_heads // 2),
        in_specs=[
            q_spec, k_spec, k_spec,
            pl.BlockSpec((1, q_len), lambda s, p: (0, 0)),
            pl.BlockSpec((1, k_len, 1), lambda s, p: (s, 0, 0)),
        ],
        out_specs=[q_spec, pl.BlockSpec((1, n_heads, q_len), lambda s, p: (s, 0, 0))],
        out_shape=[
            jax.ShapeDtypeStruct((n_slots, q_len, width), jnp.bfloat16),
            jax.ShapeDtypeStruct((n_slots, n_heads, q_len), jnp.float32),
        ],
        compiler_params=pltpu.CompilerParams(dimension_semantics=("arbitrary", "arbitrary")),
        cost_estimate=pl.CostEstimate(
            flops=n_slots * n_heads * 4 * q_len * k_len * head_width,
            transcendentals=n_slots * n_heads * q_len * k_len,
            bytes_accessed=2 * (2 * q_len + 2 * k_len) * width * n_slots,
        ),
    )(flat(queries), flat(keys), flat(values), qpos, kpos)
    return out.reshape(n_slots, q_len, n_heads, head_width), lse


def block_backward(queries, keys, values, upstream, lse_rows, dot_rows, q_pos, k_pos, lengths):
    n_slots, q_len, n_heads, head_width = queries.shape
    k_len = keys.shape[1]
    width = n_heads * head_width
    pair_width = 2 * head_width
    flat = lambda a: a.reshape(a.shape[0], a.shape[1], width)
    kpos = jnp.where(
        (k_pos[None, :] < lengths[:, None]) & (k_pos[None, :] >= 0), k_pos[None, :], FAR
    ).astype(jnp.int32)[..., None]
    qpos = q_pos.astype(jnp.int32)[None, :]
    kernel = functools.partial(_block_backward_kernel, head_width=head_width, scale=head_width ** (-0.5))
    q_spec = pl.BlockSpec((1, q_len, pair_width), lambda s, p: (s, 0, p))
    k_spec = pl.BlockSpec((1, k_len, pair_width), lambda s, p: (s, 0, p))
    row_spec = pl.BlockSpec((1, n_heads, q_len), lambda s, p: (s, 0, 0))
    flops = n_slots * n_heads * 10 * q_len * k_len * head_width
    dq, dk, dv = pl.pallas_call(
        kernel,
        grid=(n_slots, n_heads // 2),
        in_specs=[
            q_spec, k_spec, k_spec, q_spec, row_spec, row_spec,
            pl.BlockSpec((1, q_len), lambda s, p: (0, 0)),
            pl.BlockSpec((1, k_len, 1), lambda s, p: (s, 0, 0)),
        ],
        out_specs=[q_spec, k_spec, k_spec],
        out_shape=[
            jax.ShapeDtypeStruct((n_slots, q_len, width), jnp.float32),
            jax.ShapeDtypeStruct((n_slots, k_len, width), jnp.float32),
            jax.ShapeDtypeStruct((n_slots, k_len, width), jnp.float32),
        ],
        cost_estimate=pl.CostEstimate(
            flops=flops,
            transcendentals=n_slots * n_heads * q_len * k_len,
            bytes_accessed=2 * (2 * q_len + 2 * k_len) * width * n_slots + 4 * (q_len + 2 * k_len) * width * n_slots,
        ),
    )(flat(queries), flat(keys), flat(values), flat(upstream), lse_rows, dot_rows, qpos, kpos)
    shape_q = (n_slots, q_len, n_heads, head_width)
    shape_k = (n_slots, k_len, n_heads, head_width)
    return dq.reshape(shape_q), dk.reshape(shape_k), dv.reshape(shape_k)


GROUP = ("fsdp", "ctx")


def gather_blocks(pieces):
    packed = jnp.concatenate(pieces, axis=0)
    gathered = lax.all_gather(packed, GROUP, axis=0, tiled=False)
    fulls, offset = [], 0
    for piece in pieces:
        fulls.append(gathered[:, offset : offset + piece.shape[0], :])
        offset += piece.shape[0]
    return fulls


def rep_sum(x):
    n_rep = lax.axis_size("rep")
    if n_rep != 4:
        return lax.psum(x, "rep")
    me = lax.axis_index("rep")
    arrived = lax.ppermute(x, "rep", [(0, 1), (3, 2)])
    folded = (x.astype(jnp.float32) + arrived.astype(jnp.float32)).astype(x.dtype)
    arrived = lax.ppermute(folded, "rep", [(1, 2), (2, 1)])
    total = (folded.astype(jnp.float32) + arrived.astype(jnp.float32)).astype(x.dtype)
    sent_out = lax.ppermute(total, "rep", [(1, 0), (2, 3)])
    return jnp.where((me == 0) | (me == 3), sent_out, total)


def scatter_blocks(blocks, by_permutes):
    packed = jnp.concatenate(blocks, axis=1).astype(jnp.bfloat16)
    summed = lax.psum_scatter(packed, GROUP, scatter_dimension=0, tiled=True)
    summed = (rep_sum(summed) if by_permutes else lax.psum(summed, "rep"))[0].astype(jnp.float32)
    parts, offset = [], 0
    for block in blocks:
        parts.append(summed[offset : offset + block.shape[1], :])
        offset += block.shape[1]
    return parts


def gain_block(first, second, width):
    lead = first.shape[:-1]
    row = jnp.concatenate([first, second], axis=-1)
    row = jnp.pad(row, [(0, 0)] * len(lead) + [(0, width - row.shape[-1])])
    return jnp.pad(row[..., None, :], [(0, 0)] * len(lead) + [(0, 7), (0, 0)])


def shards(
    tokens,
    initial_layer_values,
    cotangent,
    lengths,
    w_query,
    w_key,
    w_value,
    w_out,
    w_gate,
    w_up,
    w_down,
    gain_attn,
    gain_mlp,
):
    n_slots, slot_rows, model_width = tokens.shape
    n_ctx = lax.axis_size("ctx")
    n_group = lax.axis_size("fsdp") * n_ctx
    own_rows = gain_attn.shape[0]
    ff_width = w_gate.shape[1]
    attn_width = w_query.shape[1]
    qkv_width = 3 * attn_width
    (qkv_blocks, gain_rows) = gather_blocks(
        [
            jnp.concatenate([w_query, w_key, w_value], axis=1),
            gain_block(gain_attn, gain_mlp, qkv_width),
        ]
    )
    full_qkv = qkv_blocks.reshape(n_group * own_rows, qkv_width)
    full_gain_attn = gain_rows[:, 0, :own_rows].reshape(-1)
    full_gain_mlp = gain_rows[:, 0, own_rows : 2 * own_rows].reshape(-1)
    (out_blocks,) = gather_blocks([w_out])
    full_out = out_blocks.reshape(-1, model_width)
    (gu_blocks,) = gather_blocks([jnp.concatenate([w_gate, w_up], axis=1)])
    full_gu = gu_blocks.reshape(n_group * own_rows, 2 * ff_width)
    (down_blocks,) = gather_blocks([w_down])
    full_down = down_blocks.reshape(-1, model_width)
    ctx_index = lax.axis_index("ctx")
    q_pos = ctx_index * slot_rows + jnp.arange(slot_rows)
    live_rows = q_pos[None, :] < lengths[:, None]
    head_shape = (n_slots, slot_rows, HEADS, HEAD_DIM)
    paired = n_ctx == 2
    if paired:
        other_tokens = lax.ppermute(tokens, "ctx", [(0, 1), (1, 0)])
        other_first = lax.ppermute(initial_layer_values, "ctx", [(0, 1)])
        other_pos = (1 - ctx_index) * slot_rows + jnp.arange(slot_rows)
    inputs = tokens.astype(jnp.float32)
    attn_scale = full_gain_attn.astype(jnp.float32)
    mlp_scale = full_gain_mlp.astype(jnp.float32)

    def project(chunk_tokens, chunk_first, chunk_pos):
        chunk_normed, chunk_inv = normalize(chunk_tokens.astype(jnp.float32), attn_scale)
        chunk_low = chunk_normed.astype(jnp.bfloat16)
        qkv_pre = jnp.einsum(
            "srd,de->sre", chunk_low, full_qkv, preferred_element_type=jnp.float32
        )
        q_pre = qkv_pre[..., :attn_width]
        k_pre = qkv_pre[..., attn_width : 2 * attn_width]
        v_pre = qkv_pre[..., 2 * attn_width :]
        chunk_q = rotate(q_pre.reshape(head_shape), chunk_pos, 1.0).astype(jnp.bfloat16)
        chunk_k = rotate(k_pre.reshape(head_shape), chunk_pos, 1.0).astype(jnp.bfloat16)
        chunk_v = (
            (0.5 * v_pre + 0.5 * chunk_first.astype(jnp.float32))
            .astype(jnp.bfloat16)
            .reshape(head_shape)
        )
        return chunk_low, chunk_inv, chunk_q, chunk_k, chunk_v

    normed_low, inv_attn, queries, keys, values = project(tokens, initial_layer_values, q_pos)
    if paired:
        _, _, other_q, other_k, other_v = project(other_tokens, other_first, other_pos)
        slot_k = jnp.concatenate([other_k, keys], axis=1)
        slot_v = jnp.concatenate([other_v, values], axis=1)
        k_pos = jnp.concatenate([other_pos, q_pos])
    else:
        slot_k, slot_v = (
            lax.all_gather(keys, "ctx", axis=1, tiled=True),
            lax.all_gather(values, "ctx", axis=1, tiled=True),
        )
        k_pos = jnp.arange(n_ctx * slot_rows)
    if paired:
        attended, lse_rows = block_forward(queries, slot_k, slot_v, q_pos, k_pos, lengths)
    else:
        attn_raw, attn_lse = attend_forward(queries, slot_k, slot_v, q_pos, k_pos, lengths)
        attended = attn_raw.astype(jnp.bfloat16)
    att_flat = attended.reshape(n_slots, slot_rows, model_width)
    branch = jnp.einsum("sre,ed->srd", att_flat, full_out, preferred_element_type=jnp.float32)
    residual = inputs + branch
    normed_mlp, inv_mlp = normalize(residual, mlp_scale)
    mlp_low = normed_mlp.astype(jnp.bfloat16)
    gu_proj = jnp.einsum("srd,df->srf", mlp_low, full_gu, preferred_element_type=jnp.float32)
    gate_proj = gu_proj[..., :ff_width]
    up_proj = gu_proj[..., ff_width:]
    sigmoid_gate = jax.nn.sigmoid(gate_proj)
    hidden = (gate_proj * sigmoid_gate * up_proj).astype(jnp.bfloat16)
    final = residual + jnp.einsum(
        "srf,fd->srd", hidden, full_down, preferred_element_type=jnp.float32
    )
    output = jnp.where(live_rows[..., None], final, 0.0).astype(jnp.bfloat16)
    output_gradient = jnp.where(live_rows[..., None], cotangent.astype(jnp.float32), 0.0)
    g_low = output_gradient.astype(jnp.bfloat16)
    gu_alone = lax.optimization_barrier(gu_proj)
    gate_alone = gu_alone[..., :ff_width]
    hidden_alone = (gate_alone * jax.nn.sigmoid(gate_alone) * gu_alone[..., ff_width:]).astype(
        jnp.bfloat16
    )
    grad_down = jnp.einsum(
        "srf,srd->fd", hidden_alone, g_low, preferred_element_type=jnp.float32
    )
    (part_down,) = scatter_blocks(
        [grad_down.reshape(n_group, -1, model_width).astype(jnp.bfloat16)], True
    )
    g_hidden = jnp.einsum("srd,fd->srf", g_low, full_down, preferred_element_type=jnp.float32)
    gate_gradient = (g_hidden * up_proj * sigmoid_gate * (1.0 + gate_proj * (1.0 - sigmoid_gate))).astype(jnp.bfloat16)
    up_gradient = (g_hidden * gate_proj * sigmoid_gate).astype(jnp.bfloat16)
    gu_gradient = jnp.concatenate([gate_gradient, up_gradient], axis=-1)
    grad_gu = jnp.einsum(
        "srd,srf->df", mlp_low, gu_gradient, preferred_element_type=jnp.float32
    )
    g_normed_mlp = jnp.einsum(
        "srf,df->srd", gu_gradient, full_gu, preferred_element_type=jnp.float32
    )
    g_mlp_in, grad_gain_mlp = normalize_back(residual, inv_mlp, mlp_scale, g_normed_mlp)
    g_residual = output_gradient + g_mlp_in
    g_branch = g_residual.astype(jnp.bfloat16)
    grad_out = jnp.einsum(
        "sre,srd->ed", att_flat, g_branch, preferred_element_type=jnp.float32
    )
    gu_block = grad_gu.reshape(n_group, own_rows, 2 * ff_width).astype(jnp.bfloat16)
    g_attended = (
        jnp.einsum("srd,ed->sre", g_branch, full_out, preferred_element_type=jnp.float32)
        .astype(jnp.bfloat16)
        .reshape(head_shape)
    )
    (part_gu,) = scatter_blocks([gu_block], True)
    row_dots = jnp.sum(g_attended.astype(jnp.float32) * attended.astype(jnp.float32), axis=-1)
    if paired:
        dot_rows = jnp.transpose(row_dots, (0, 2, 1))
        later_g, later_dots, later_lse = lax.ppermute(
            (g_attended, dot_rows, lse_rows), "ctx", [(1, 0)]
        )
        g_queries, g_keys, g_values = block_backward(
            queries, keys, values, g_attended, lse_rows, dot_rows, q_pos, q_pos, lengths
        )
        later = ctx_index == 1
        pick = lambda mine, theirs: jnp.where(later, mine, theirs)
        x_dq, x_dk, x_dv = block_backward(
            pick(queries, other_q),
            pick(other_k, keys),
            pick(other_v, values),
            pick(g_attended, later_g),
            pick(lse_rows, later_lse),
            pick(dot_rows, later_dots),
            pick(q_pos, other_pos),
            pick(other_pos, q_pos),
            lengths,
        )
        g_queries = g_queries + jnp.where(later, x_dq, 0.0)
        g_keys = g_keys + jnp.where(later, 0.0, x_dk)
        g_values = g_values + jnp.where(later, 0.0, x_dv)
    else:
        g_queries, slot_dk, slot_dv = attend_backward(
            queries, slot_k, slot_v, g_attended, row_dots, attn_lse, q_pos, k_pos, lengths
        )
        g_keys, g_values = (
            lax.psum_scatter(
                slot_dk.astype(jnp.bfloat16), "ctx", scatter_dimension=1, tiled=True
            ).astype(jnp.float32),
            lax.psum_scatter(
                slot_dv.astype(jnp.bfloat16), "ctx", scatter_dimension=1, tiled=True
            ).astype(jnp.float32),
        )
    flat_shape = (n_slots, slot_rows, model_width)
    gq_low = rotate(g_queries, q_pos, -1.0).reshape(flat_shape).astype(jnp.bfloat16)
    gk_low = rotate(g_keys, q_pos, -1.0).reshape(flat_shape).astype(jnp.bfloat16)
    gv_rounded = g_values.reshape(flat_shape).astype(jnp.bfloat16).astype(jnp.float32)
    d_first = 0.5 * gv_rounded
    gv_half = d_first.astype(jnp.bfloat16)
    g_qkv = jnp.concatenate([gq_low, gk_low, gv_half], axis=-1)
    grad_qkv = jnp.einsum("srd,sre->de", normed_low, g_qkv, preferred_element_type=jnp.float32)
    g_normed = jnp.einsum("sre,de->srd", g_qkv, full_qkv, preferred_element_type=jnp.float32)
    g_attn_in, grad_gain_attn = normalize_back(inputs, inv_attn, attn_scale, g_normed)
    d_tokens = g_residual + g_attn_in
    part_qkvo, part_gains = scatter_blocks(
        [
            jnp.concatenate([grad_qkv, grad_out], axis=1).reshape(
                n_group, own_rows, qkv_width + model_width
            ),
            gain_block(
                grad_gain_attn.reshape(n_group, own_rows),
                grad_gain_mlp.reshape(n_group, own_rows),
                qkv_width + model_width,
            ),
        ],
        False,
    )
    part_qkv = part_qkvo[:, :qkv_width]
    return (
        output,
        d_tokens,
        d_first,
        part_qkv[:, :attn_width],
        part_qkv[:, attn_width : 2 * attn_width],
        part_qkv[:, 2 * attn_width :],
        part_qkvo[:, qkv_width:],
        part_gu[:, :ff_width],
        part_gu[:, ff_width:],
        part_down,
        part_gains[0, :own_rows],
        part_gains[0, own_rows : 2 * own_rows],
    )


def solution(mesh):
    in_specs = (
        P(("rep", "fsdp"), "ctx", None),
        P(("rep", "fsdp"), "ctx", None),
        P(("rep", "fsdp"), "ctx", None),
        P(("rep", "fsdp")),
        P(("fsdp", "ctx"), None),
        P(("fsdp", "ctx"), None),
        P(("fsdp", "ctx"), None),
        P(("fsdp", "ctx"), None),
        P(("fsdp", "ctx"), None),
        P(("fsdp", "ctx"), None),
        P(("fsdp", "ctx"), None),
        P(("fsdp", "ctx")),
        P(("fsdp", "ctx")),
    )
    out_specs = (
        P(("rep", "fsdp"), "ctx", None),
        P(("rep", "fsdp"), "ctx", None),
        P(("rep", "fsdp"), "ctx", None),
        P(("fsdp", "ctx"), None),
        P(("fsdp", "ctx"), None),
        P(("fsdp", "ctx"), None),
        P(("fsdp", "ctx"), None),
        P(("fsdp", "ctx"), None),
        P(("fsdp", "ctx"), None),
        P(("fsdp", "ctx"), None),
        P(("fsdp", "ctx")),
        P(("fsdp", "ctx")),
    )

    return jax.shard_map(shards, mesh=mesh, in_specs=in_specs, out_specs=out_specs, check_vma=False)
```

```python
import functools

import jax
import jax.numpy as jnp
from jax import lax
from jax.experimental import pallas as pl
from jax.experimental.pallas import tpu as pltpu
from jax.sharding import PartitionSpec as P


HEADS = 16
HEAD_DIM = 64


EPS = 1e-06
NEG = -1e30
THETA = 10000.0
SCORE_CAP = 4194304


def rotate(field, positions, direction):
    head_width = field.shape[-1]
    half_width = head_width // 2
    frequency = THETA ** (-(jnp.arange(half_width, dtype=jnp.float32) * 2.0) / head_width)
    angles = positions.astype(jnp.float32)[:, None] * frequency[None, :]
    cosine = jnp.cos(angles)[:, None, :]
    sine_part = direction * jnp.sin(angles)[:, None, :]
    former = field[..., :half_width]
    latter = field[..., half_width:]
    return jnp.concatenate(
        [former * cosine - latter * sine_part, latter * cosine + former * sine_part], axis=-1
    )


def normalize(values, gain):
    inverse = lax.rsqrt(jnp.mean(values * values, axis=-1, keepdims=True) + EPS)
    return (values * inverse * gain, inverse)


def normalize_back(values, inverse, gain, upstream):
    unit_rows = values * inverse
    scaled = upstream * gain
    grad_gain = jnp.sum(upstream * unit_rows, axis=(0, 1))
    grad_values = inverse * (
        scaled - unit_rows * jnp.mean(scaled * unit_rows, axis=-1, keepdims=True)
    )
    return (grad_values, grad_gain)


def head_groups(n_slots, q_len, n_heads, k_len):
    q_block = min(q_len, 512)
    per_group = max(1, min(n_heads, SCORE_CAP // (n_slots * q_block * k_len)))
    while n_heads % per_group:
        per_group = per_group - 1
    return (q_block, per_group)


def split_heads(packed, n_groups):
    n_slots, length, n_heads, head_width = packed.shape
    return jnp.moveaxis(
        packed.reshape(n_slots, length, n_groups, n_heads // n_groups, head_width), 2, 0
    )


def join_heads(grouped):
    n_groups, n_slots, length, per_group, head_width = grouped.shape
    return jnp.moveaxis(grouped, 0, 2).reshape(n_slots, length, n_groups * per_group, head_width)


def score_block(q_rows, k_rows, q_pos, k_pos, lengths):
    products = jnp.einsum(
        "sqhe,skhe->shqk", q_rows, k_rows, preferred_element_type=jnp.float32
    ) * q_rows.shape[-1] ** (-0.5)
    causal = (k_pos[None, None, None, :] <= q_pos[None, None, :, None]) & (
        k_pos[None, None, None, :] >= 0
    )
    filled = k_pos[None, None, None, :] < lengths[:, None, None, None]
    return jnp.where(causal & filled, products, NEG)


def attend_forward(queries, keys, values, q_pos, k_pos, lengths):
    n_slots, q_len, n_heads, head_width = queries.shape
    q_block, per_group = head_groups(n_slots, q_len, n_heads, keys.shape[1])
    n_groups = n_heads // per_group
    n_blocks = q_len // q_block
    pos_blocks = q_pos.reshape(n_blocks, q_block)

    def one_group(packed):
        q_group, k_group, v_group = packed
        q_blocks = jnp.moveaxis(
            q_group.reshape(n_slots, n_blocks, q_block, per_group, head_width), 1, 0
        )

        def one_block(streams):
            q_rows, pos_rows = streams
            scores = score_block(q_rows, k_group, pos_rows, k_pos, lengths)
            highest = jnp.max(scores, axis=-1, keepdims=True)
            exponent = jnp.exp(scores - highest)
            totals = jnp.sum(exponent, axis=-1, keepdims=True)
            probabilities = (exponent / totals).astype(jnp.bfloat16)
            mixture = jnp.einsum(
                "shqk,skhe->sqhe", probabilities, v_group, preferred_element_type=jnp.float32
            )
            return (mixture, (highest + jnp.log(totals))[..., 0])

        mixture, log_sums = lax.map(one_block, (q_blocks, pos_blocks))
        return (
            jnp.moveaxis(mixture, 0, 1).reshape(n_slots, q_len, per_group, head_width),
            log_sums,
        )

    grouped = (
        split_heads(queries, n_groups),
        split_heads(keys, n_groups),
        split_heads(values, n_groups),
    )
    mixture, log_sums = lax.map(one_group, grouped)
    return (join_heads(mixture), log_sums)


def attend_backward(queries, keys, values, upstream, row_dots, log_sums, q_pos, k_pos, lengths):
    n_slots, q_len, n_heads, head_width = queries.shape
    q_block, per_group = head_groups(n_slots, q_len, n_heads, keys.shape[1])
    n_groups = n_heads // per_group
    n_blocks = q_len // q_block
    score_scale = head_width ** (-0.5)
    pos_blocks = q_pos.reshape(n_blocks, q_block)
    dot_groups = jnp.moveaxis(row_dots.reshape(n_slots, q_len, n_groups, per_group), 2, 0)

    def blocks_of(grouped):
        return jnp.moveaxis(grouped.reshape((n_slots, n_blocks, q_block) + grouped.shape[2:]), 1, 0)

    def one_group(packed):
        q_group, k_group, v_group, g_group, d_group, l_group = packed

        def one_block(running, streams):
            k_grad, v_grad = running
            q_rows, g_rows, d_rows, l_rows, pos_rows = streams
            scores = score_block(q_rows, k_group, pos_rows, k_pos, lengths)
            probabilities = jnp.exp(scores - l_rows[..., None])
            v_grad = v_grad + jnp.einsum(
                "shqk,sqhe->skhe",
                probabilities.astype(jnp.bfloat16),
                g_rows,
                preferred_element_type=jnp.float32,
            )
            p_grad = jnp.einsum(
                "sqhe,skhe->shqk", g_rows, v_group, preferred_element_type=jnp.float32
            )
            s_grad = (probabilities * (p_grad - jnp.moveaxis(d_rows, 2, 1)[..., None])).astype(
                jnp.bfloat16
            )
            q_grad = (
                jnp.einsum("shqk,skhe->sqhe", s_grad, k_group, preferred_element_type=jnp.float32)
                * score_scale
            )
            k_grad = (
                k_grad
                + jnp.einsum("shqk,sqhe->skhe", s_grad, q_rows, preferred_element_type=jnp.float32)
                * score_scale
            )
            return ((k_grad, v_grad), q_grad)

        empty_grads = jnp.zeros(k_group.shape, jnp.float32)
        streams = (blocks_of(q_group), blocks_of(g_group), blocks_of(d_group), l_group, pos_blocks)
        (k_grad, v_grad), q_grads = lax.scan(one_block, (empty_grads, empty_grads), streams)
        return (
            jnp.moveaxis(q_grads, 0, 1).reshape(n_slots, q_len, per_group, head_width),
            k_grad,
            v_grad,
        )

    grouped = (
        split_heads(queries, n_groups),
        split_heads(keys, n_groups),
        split_heads(values, n_groups),
        split_heads(upstream, n_groups),
        dot_groups,
        log_sums,
    )
    q_grads, k_grads, v_grads = lax.map(one_group, grouped)
    return (join_heads(q_grads), join_heads(k_grads), join_heads(v_grads))


FAR = 1 << 30


def _block_backward_kernel(q_ref, k_ref, v_ref, g_ref, lse_ref, dots_ref, qpos_ref, kpos_ref,
                           dq_ref, dk_ref, dv_ref, *, head_width, scale):
    pair = pl.program_id(1)
    allowed = kpos_ref[0] <= qpos_ref[...]
    for j in range(2):
        cols = slice(j * head_width, (j + 1) * head_width)
        q = q_ref[0, :, cols]
        k = k_ref[0, :, cols]
        v = v_ref[0, :, cols]
        g = g_ref[0, :, cols]
        head = 2 * pair + j
        lse = lse_ref[0, pl.ds(head, 1), :]
        dots = dots_ref[0, pl.ds(head, 1), :]
        nt = (((1,), (1,)), ((), ()))
        scores = lax.dot_general(k, q, nt, preferred_element_type=jnp.float32) * scale
        scores = jnp.where(allowed, scores, -1e30)
        probs = jnp.exp(scores - lse)
        dv_ref[0, :, cols] = jnp.dot(probs.astype(jnp.bfloat16), g, preferred_element_type=jnp.float32)
        dprobs = lax.dot_general(v, g, nt, preferred_element_type=jnp.float32)
        dscores = (probs * (dprobs - dots)).astype(jnp.bfloat16)
        dk_ref[0, :, cols] = jnp.dot(dscores, q, preferred_element_type=jnp.float32) * scale
        tn = (((0,), (0,)), ((), ()))
        dq_ref[0, :, cols] = lax.dot_general(dscores, k, tn, preferred_element_type=jnp.float32) * scale


def _block_forward_kernel(q_ref, k_ref, v_ref, qpos_ref, kpos_ref, out_ref, lse_ref, *, head_width, scale):
    pair = pl.program_id(1)
    allowed = kpos_ref[0] <= qpos_ref[...]
    nt = (((1,), (1,)), ((), ()))
    tn = (((0,), (0,)), ((), ()))
    for j in range(2):
        cols = slice(j * head_width, (j + 1) * head_width)
        q = q_ref[0, :, cols]
        k = k_ref[0, :, cols]
        v = v_ref[0, :, cols]
        scores = lax.dot_general(k, q, nt, preferred_element_type=jnp.float32) * scale
        scores = jnp.where(allowed, scores, -1e30)
        highest = jnp.max(scores, axis=0, keepdims=True)
        exponent = jnp.exp(scores - highest)
        totals = jnp.sum(exponent, axis=0, keepdims=True)
        probs = (exponent / totals).astype(jnp.bfloat16)
        mixture = lax.dot_general(probs, v, tn, preferred_element_type=jnp.float32)
        out_ref[0, :, cols] = mixture.astype(out_ref.dtype)
        lse_ref[0, pl.ds(2 * pair + j, 1), :] = highest + jnp.log(totals)


def block_forward(queries, keys, values, q_pos, k_pos, lengths):
    n_slots, q_len, n_heads, head_width = queries.shape
    k_len = keys.shape[1]
    width = n_heads * head_width
    pair_width = 2 * head_width
    flat = lambda a: a.reshape(a.shape[0], a.shape[1], width)
    kpos = jnp.where(
        (k_pos[None, :] < lengths[:, None]) & (k_pos[None, :] >= 0), k_pos[None, :], FAR
    ).astype(jnp.int32)[..., None]
    qpos = q_pos.astype(jnp.int32)[None, :]
    kernel = functools.partial(_block_forward_kernel, head_width=head_width, scale=head_width ** (-0.5))
    q_spec = pl.BlockSpec((1, q_len, pair_width), lambda s, p: (s, 0, p))
    k_spec = pl.BlockSpec((1, k_len, pair_width), lambda s, p: (s, 0, p))
    out, lse = pl.pallas_call(
        kernel,
        grid=(n_slots, n_heads // 2),
        in_specs=[
            q_spec, k_spec, k_spec,
            pl.BlockSpec((1, q_len), lambda s, p: (0, 0)),
            pl.BlockSpec((1, k_len, 1), lambda s, p: (s, 0, 0)),
        ],
        out_specs=[q_spec, pl.BlockSpec((1, n_heads, q_len), lambda s, p: (s, 0, 0))],
        out_shape=[
            jax.ShapeDtypeStruct((n_slots, q_len, width), jnp.bfloat16),
            jax.ShapeDtypeStruct((n_slots, n_heads, q_len), jnp.float32),
        ],
        compiler_params=pltpu.CompilerParams(dimension_semantics=("arbitrary", "arbitrary")),
        cost_estimate=pl.CostEstimate(
            flops=n_slots * n_heads * 4 * q_len * k_len * head_width,
            transcendentals=n_slots * n_heads * q_len * k_len,
            bytes_accessed=2 * (2 * q_len + 2 * k_len) * width * n_slots,
        ),
    )(flat(queries), flat(keys), flat(values), qpos, kpos)
    return out.reshape(n_slots, q_len, n_heads, head_width), lse


def block_backward(queries, keys, values, upstream, lse_rows, dot_rows, q_pos, k_pos, lengths):
    n_slots, q_len, n_heads, head_width = queries.shape
    k_len = keys.shape[1]
    width = n_heads * head_width
    pair_width = 2 * head_width
    flat = lambda a: a.reshape(a.shape[0], a.shape[1], width)
    kpos = jnp.where(
        (k_pos[None, :] < lengths[:, None]) & (k_pos[None, :] >= 0), k_pos[None, :], FAR
    ).astype(jnp.int32)[..., None]
    qpos = q_pos.astype(jnp.int32)[None, :]
    kernel = functools.partial(_block_backward_kernel, head_width=head_width, scale=head_width ** (-0.5))
    q_spec = pl.BlockSpec((1, q_len, pair_width), lambda s, p: (s, 0, p))
    k_spec = pl.BlockSpec((1, k_len, pair_width), lambda s, p: (s, 0, p))
    row_spec = pl.BlockSpec((1, n_heads, q_len), lambda s, p: (s, 0, 0))
    flops = n_slots * n_heads * 10 * q_len * k_len * head_width
    dq, dk, dv = pl.pallas_call(
        kernel,
        grid=(n_slots, n_heads // 2),
        in_specs=[
            q_spec, k_spec, k_spec, q_spec, row_spec, row_spec,
            pl.BlockSpec((1, q_len), lambda s, p: (0, 0)),
            pl.BlockSpec((1, k_len, 1), lambda s, p: (s, 0, 0)),
        ],
        out_specs=[q_spec, k_spec, k_spec],
        out_shape=[
            jax.ShapeDtypeStruct((n_slots, q_len, width), jnp.float32),
            jax.ShapeDtypeStruct((n_slots, k_len, width), jnp.float32),
            jax.ShapeDtypeStruct((n_slots, k_len, width), jnp.float32),
        ],
        cost_estimate=pl.CostEstimate(
            flops=flops,
            transcendentals=n_slots * n_heads * q_len * k_len,
            bytes_accessed=2 * (2 * q_len + 2 * k_len) * width * n_slots + 4 * (q_len + 2 * k_len) * width * n_slots,
        ),
    )(flat(queries), flat(keys), flat(values), flat(upstream), lse_rows, dot_rows, qpos, kpos)
    shape_q = (n_slots, q_len, n_heads, head_width)
    shape_k = (n_slots, k_len, n_heads, head_width)
    return dq.reshape(shape_q), dk.reshape(shape_k), dv.reshape(shape_k)


GROUP = ("fsdp", "ctx")


def gather_blocks(pieces):
    packed = jnp.concatenate(pieces, axis=0)
    gathered = lax.all_gather(packed, GROUP, axis=0, tiled=False)
    fulls, offset = [], 0
    for piece in pieces:
        fulls.append(gathered[:, offset : offset + piece.shape[0], :])
        offset += piece.shape[0]
    return fulls


def rep_chain(x):
    me = lax.axis_index("rep")
    arrived = lax.ppermute(x, "rep", [(0, 1), (3, 2)])
    folded = (x.astype(jnp.float32) + arrived.astype(jnp.float32)).astype(x.dtype)
    arrived = lax.ppermute(folded, "rep", [(1, 2), (2, 1)])
    total = (folded.astype(jnp.float32) + arrived.astype(jnp.float32)).astype(x.dtype)
    sent_out = lax.ppermute(total, "rep", [(1, 0), (2, 3)])
    return jnp.where((me == 0) | (me == 3), sent_out, total)


def rep_sum(x, pieces=1):
    if lax.axis_size("rep") != 4:
        return lax.psum(x, "rep")
    rows = x.shape[1]
    if pieces == 1 or rows % (8 * pieces):
        return rep_chain(x)
    step = rows // pieces
    parts = []
    for i in range(pieces):
        parts.append(rep_chain(x[:, i * step : (i + 1) * step]))
    return jnp.concatenate(parts, axis=1)


def scatter_blocks(blocks, by_permutes, pieces=1):
    packed = jnp.concatenate(blocks, axis=1).astype(jnp.bfloat16)
    summed = lax.psum_scatter(packed, GROUP, scatter_dimension=0, tiled=True)
    summed = (rep_sum(summed, pieces) if by_permutes else lax.psum(summed, "rep"))[0].astype(
        jnp.float32
    )
    parts, offset = [], 0
    for block in blocks:
        parts.append(summed[offset : offset + block.shape[1], :])
        offset += block.shape[1]
    return parts


def gain_block(first, second, width):
    lead = first.shape[:-1]
    row = jnp.concatenate([first, second], axis=-1)
    row = jnp.pad(row, [(0, 0)] * len(lead) + [(0, width - row.shape[-1])])
    return jnp.pad(row[..., None, :], [(0, 0)] * len(lead) + [(0, 7), (0, 0)])


def shards(
    tokens,
    initial_layer_values,
    cotangent,
    lengths,
    w_query,
    w_key,
    w_value,
    w_out,
    w_gate,
    w_up,
    w_down,
    gain_attn,
    gain_mlp,
):
    n_slots, slot_rows, model_width = tokens.shape
    n_ctx = lax.axis_size("ctx")
    n_group = lax.axis_size("fsdp") * n_ctx
    own_rows = gain_attn.shape[0]
    ff_width = w_gate.shape[1]
    attn_width = w_query.shape[1]
    qkv_width = 3 * attn_width
    (qkv_blocks, gain_rows) = gather_blocks(
        [
            jnp.concatenate([w_query, w_key, w_value], axis=1),
            gain_block(gain_attn, gain_mlp, qkv_width),
        ]
    )
    full_qkv = qkv_blocks.reshape(n_group * own_rows, qkv_width)
    full_gain_attn = gain_rows[:, 0, :own_rows].reshape(-1)
    full_gain_mlp = gain_rows[:, 0, own_rows : 2 * own_rows].reshape(-1)
    (out_blocks,) = gather_blocks([w_out])
    full_out = out_blocks.reshape(-1, model_width)
    (gu_blocks,) = gather_blocks([jnp.concatenate([w_gate, w_up], axis=1)])
    full_gu = gu_blocks.reshape(n_group * own_rows, 2 * ff_width)
    (down_blocks,) = gather_blocks([w_down])
    full_down = down_blocks.reshape(-1, model_width)
    ctx_index = lax.axis_index("ctx")
    q_pos = ctx_index * slot_rows + jnp.arange(slot_rows)
    live_rows = q_pos[None, :] < lengths[:, None]
    head_shape = (n_slots, slot_rows, HEADS, HEAD_DIM)
    paired = n_ctx == 2
    if paired:
        other_tokens = lax.ppermute(tokens, "ctx", [(0, 1), (1, 0)])
        other_first = lax.ppermute(initial_layer_values, "ctx", [(0, 1)])
        other_pos = (1 - ctx_index) * slot_rows + jnp.arange(slot_rows)
    inputs = tokens.astype(jnp.float32)
    attn_scale = full_gain_attn.astype(jnp.float32)
    mlp_scale = full_gain_mlp.astype(jnp.float32)

    def project(chunk_tokens, chunk_first, chunk_pos):
        chunk_normed, chunk_inv = normalize(chunk_tokens.astype(jnp.float32), attn_scale)
        chunk_low = chunk_normed.astype(jnp.bfloat16)
        qkv_pre = jnp.einsum(
            "srd,de->sre", chunk_low, full_qkv, preferred_element_type=jnp.float32
        )
        q_pre = qkv_pre[..., :attn_width]
        k_pre = qkv_pre[..., attn_width : 2 * attn_width]
        v_pre = qkv_pre[..., 2 * attn_width :]
        chunk_q = rotate(q_pre.reshape(head_shape), chunk_pos, 1.0).astype(jnp.bfloat16)
        chunk_k = rotate(k_pre.reshape(head_shape), chunk_pos, 1.0).astype(jnp.bfloat16)
        chunk_v = (
            (0.5 * v_pre + 0.5 * chunk_first.astype(jnp.float32))
            .astype(jnp.bfloat16)
            .reshape(head_shape)
        )
        return chunk_low, chunk_inv, chunk_q, chunk_k, chunk_v

    normed_low, inv_attn, queries, keys, values = project(tokens, initial_layer_values, q_pos)
    if paired:
        _, _, other_q, other_k, other_v = project(other_tokens, other_first, other_pos)
        slot_k = jnp.concatenate([other_k, keys], axis=1)
        slot_v = jnp.concatenate([other_v, values], axis=1)
        k_pos = jnp.concatenate([other_pos, q_pos])
    else:
        slot_k, slot_v = (
            lax.all_gather(keys, "ctx", axis=1, tiled=True),
            lax.all_gather(values, "ctx", axis=1, tiled=True),
        )
        k_pos = jnp.arange(n_ctx * slot_rows)
    if paired:
        attended, lse_rows = block_forward(queries, slot_k, slot_v, q_pos, k_pos, lengths)
    else:
        attn_raw, attn_lse = attend_forward(queries, slot_k, slot_v, q_pos, k_pos, lengths)
        attended = attn_raw.astype(jnp.bfloat16)
    att_flat = attended.reshape(n_slots, slot_rows, model_width)
    branch = jnp.einsum("sre,ed->srd", att_flat, full_out, preferred_element_type=jnp.float32)
    residual = inputs + branch
    normed_mlp, inv_mlp = normalize(residual, mlp_scale)
    mlp_low = normed_mlp.astype(jnp.bfloat16)
    gu_proj = jnp.einsum("srd,df->srf", mlp_low, full_gu, preferred_element_type=jnp.float32)
    gate_proj = gu_proj[..., :ff_width]
    up_proj = gu_proj[..., ff_width:]
    sigmoid_gate = jax.nn.sigmoid(gate_proj)
    hidden = (gate_proj * sigmoid_gate * up_proj).astype(jnp.bfloat16)
    final = residual + jnp.einsum(
        "srf,fd->srd", hidden, full_down, preferred_element_type=jnp.float32
    )
    output = jnp.where(live_rows[..., None], final, 0.0).astype(jnp.bfloat16)
    output_gradient = jnp.where(live_rows[..., None], cotangent.astype(jnp.float32), 0.0)
    g_low = output_gradient.astype(jnp.bfloat16)
    gu_alone = lax.optimization_barrier(gu_proj)
    gate_alone = gu_alone[..., :ff_width]
    hidden_alone = (gate_alone * jax.nn.sigmoid(gate_alone) * gu_alone[..., ff_width:]).astype(
        jnp.bfloat16
    )
    grad_down = jnp.einsum(
        "srf,srd->fd", hidden_alone, g_low, preferred_element_type=jnp.float32
    )
    (part_down,) = scatter_blocks(
        [grad_down.reshape(n_group, -1, model_width).astype(jnp.bfloat16)], True
    )
    g_hidden = jnp.einsum("srd,fd->srf", g_low, full_down, preferred_element_type=jnp.float32)
    gate_gradient = (g_hidden * up_proj * sigmoid_gate * (1.0 + gate_proj * (1.0 - sigmoid_gate))).astype(jnp.bfloat16)
    up_gradient = (g_hidden * gate_proj * sigmoid_gate).astype(jnp.bfloat16)
    gu_gradient = jnp.concatenate([gate_gradient, up_gradient], axis=-1)
    grad_gu = jnp.einsum(
        "srd,srf->df", mlp_low, gu_gradient, preferred_element_type=jnp.float32
    )
    g_normed_mlp = jnp.einsum(
        "srf,df->srd", gu_gradient, full_gu, preferred_element_type=jnp.float32
    )
    g_mlp_in, grad_gain_mlp = normalize_back(residual, inv_mlp, mlp_scale, g_normed_mlp)
    g_residual = output_gradient + g_mlp_in
    g_branch = g_residual.astype(jnp.bfloat16)
    grad_out = jnp.einsum(
        "sre,srd->ed", att_flat, g_branch, preferred_element_type=jnp.float32
    )
    gu_block = (
        jnp.concatenate([grad_out, grad_gu], axis=1)
        .reshape(n_group, own_rows, model_width + 2 * ff_width)
        .astype(jnp.bfloat16)
    )
    g_attended = (
        jnp.einsum("srd,ed->sre", g_branch, full_out, preferred_element_type=jnp.float32)
        .astype(jnp.bfloat16)
        .reshape(head_shape)
    )
    (part_gu,) = scatter_blocks([gu_block], True, 2)
    row_dots = jnp.sum(g_attended.astype(jnp.float32) * attended.astype(jnp.float32), axis=-1)
    if paired:
        dot_rows = jnp.transpose(row_dots, (0, 2, 1))
        later_g, later_dots, later_lse = lax.ppermute(
            (g_attended, dot_rows, lse_rows), "ctx", [(1, 0)]
        )
        g_queries, g_keys, g_values = block_backward(
            queries, keys, values, g_attended, lse_rows, dot_rows, q_pos, q_pos, lengths
        )
        later = ctx_index == 1
        pick = lambda mine, theirs: jnp.where(later, mine, theirs)
        x_dq, x_dk, x_dv = block_backward(
            pick(queries, other_q),
            pick(other_k, keys),
            pick(other_v, values),
            pick(g_attended, later_g),
            pick(lse_rows, later_lse),
            pick(dot_rows, later_dots),
            pick(q_pos, other_pos),
            pick(other_pos, q_pos),
            lengths,
        )
        g_queries = g_queries + jnp.where(later, x_dq, 0.0)
        g_keys = g_keys + jnp.where(later, 0.0, x_dk)
        g_values = g_values + jnp.where(later, 0.0, x_dv)
    else:
        g_queries, slot_dk, slot_dv = attend_backward(
            queries, slot_k, slot_v, g_attended, row_dots, attn_lse, q_pos, k_pos, lengths
        )
        g_keys, g_values = (
            lax.psum_scatter(
                slot_dk.astype(jnp.bfloat16), "ctx", scatter_dimension=1, tiled=True
            ).astype(jnp.float32),
            lax.psum_scatter(
                slot_dv.astype(jnp.bfloat16), "ctx", scatter_dimension=1, tiled=True
            ).astype(jnp.float32),
        )
    flat_shape = (n_slots, slot_rows, model_width)
    gq_low = rotate(g_queries, q_pos, -1.0).reshape(flat_shape).astype(jnp.bfloat16)
    gk_low = rotate(g_keys, q_pos, -1.0).reshape(flat_shape).astype(jnp.bfloat16)
    gv_rounded = g_values.reshape(flat_shape).astype(jnp.bfloat16).astype(jnp.float32)
    d_first = 0.5 * gv_rounded
    gv_half = d_first.astype(jnp.bfloat16)
    g_qkv = jnp.concatenate([gq_low, gk_low, gv_half], axis=-1)
    grad_qkv = jnp.einsum("srd,sre->de", normed_low, g_qkv, preferred_element_type=jnp.float32)
    g_normed = jnp.einsum("sre,de->srd", g_qkv, full_qkv, preferred_element_type=jnp.float32)
    g_attn_in, grad_gain_attn = normalize_back(inputs, inv_attn, attn_scale, g_normed)
    d_tokens = g_residual + g_attn_in
    part_qkv, part_gains = scatter_blocks(
        [
            grad_qkv.reshape(n_group, own_rows, qkv_width),
            gain_block(grad_gain_attn.reshape(n_group, own_rows), grad_gain_mlp.reshape(n_group, own_rows), qkv_width),
        ],
        False,
    )
    return (
        output,
        d_tokens,
        d_first,
        part_qkv[:, :attn_width],
        part_qkv[:, attn_width : 2 * attn_width],
        part_qkv[:, 2 * attn_width :],
        part_gu[:, :model_width],
        part_gu[:, model_width : model_width + ff_width],
        part_gu[:, model_width + ff_width :],
        part_down,
        part_gains[0, :own_rows],
        part_gains[0, own_rows : 2 * own_rows],
    )


def solution(mesh):
    in_specs = (
        P(("rep", "fsdp"), "ctx", None),
        P(("rep", "fsdp"), "ctx", None),
        P(("rep", "fsdp"), "ctx", None),
        P(("rep", "fsdp")),
        P(("fsdp", "ctx"), None),
        P(("fsdp", "ctx"), None),
        P(("fsdp", "ctx"), None),
        P(("fsdp", "ctx"), None),
        P(("fsdp", "ctx"), None),
        P(("fsdp", "ctx"), None),
        P(("fsdp", "ctx"), None),
        P(("fsdp", "ctx")),
        P(("fsdp", "ctx")),
    )
    out_specs = (
        P(("rep", "fsdp"), "ctx", None),
        P(("rep", "fsdp"), "ctx", None),
        P(("rep", "fsdp"), "ctx", None),
        P(("fsdp", "ctx"), None),
        P(("fsdp", "ctx"), None),
        P(("fsdp", "ctx"), None),
        P(("fsdp", "ctx"), None),
        P(("fsdp", "ctx"), None),
        P(("fsdp", "ctx"), None),
        P(("fsdp", "ctx"), None),
        P(("fsdp", "ctx")),
        P(("fsdp", "ctx")),
    )

    return jax.shard_map(shards, mesh=mesh, in_specs=in_specs, out_specs=out_specs, check_vma=False)
```

```python
import functools

import jax
import jax.numpy as jnp
from jax import lax
from jax.experimental import pallas as pl
from jax.experimental.pallas import tpu as pltpu
from jax.sharding import PartitionSpec as P


HEADS = 16
HEAD_DIM = 64


EPS = 1e-06
NEG = -1e30
THETA = 10000.0
SCORE_CAP = 4194304


def rotate(field, positions, direction):
    head_width = field.shape[-1]
    half_width = head_width // 2
    frequency = THETA ** (-(jnp.arange(half_width, dtype=jnp.float32) * 2.0) / head_width)
    angles = positions.astype(jnp.float32)[:, None] * frequency[None, :]
    cosine = jnp.cos(angles)[:, None, :]
    sine_part = direction * jnp.sin(angles)[:, None, :]
    former = field[..., :half_width]
    latter = field[..., half_width:]
    return jnp.concatenate(
        [former * cosine - latter * sine_part, latter * cosine + former * sine_part], axis=-1
    )


def normalize(values, gain):
    inverse = lax.rsqrt(jnp.mean(values * values, axis=-1, keepdims=True) + EPS)
    return (values * inverse * gain, inverse)


def normalize_back(values, inverse, gain, upstream):
    unit_rows = values * inverse
    scaled = upstream * gain
    grad_gain = jnp.sum(upstream * unit_rows, axis=(0, 1))
    grad_values = inverse * (
        scaled - unit_rows * jnp.mean(scaled * unit_rows, axis=-1, keepdims=True)
    )
    return (grad_values, grad_gain)


def head_groups(n_slots, q_len, n_heads, k_len):
    q_block = min(q_len, 512)
    per_group = max(1, min(n_heads, SCORE_CAP // (n_slots * q_block * k_len)))
    while n_heads % per_group:
        per_group = per_group - 1
    return (q_block, per_group)


def split_heads(packed, n_groups):
    n_slots, length, n_heads, head_width = packed.shape
    return jnp.moveaxis(
        packed.reshape(n_slots, length, n_groups, n_heads // n_groups, head_width), 2, 0
    )


def join_heads(grouped):
    n_groups, n_slots, length, per_group, head_width = grouped.shape
    return jnp.moveaxis(grouped, 0, 2).reshape(n_slots, length, n_groups * per_group, head_width)


def score_block(q_rows, k_rows, q_pos, k_pos, lengths):
    products = jnp.einsum(
        "sqhe,skhe->shqk", q_rows, k_rows, preferred_element_type=jnp.float32
    ) * q_rows.shape[-1] ** (-0.5)
    causal = (k_pos[None, None, None, :] <= q_pos[None, None, :, None]) & (
        k_pos[None, None, None, :] >= 0
    )
    filled = k_pos[None, None, None, :] < lengths[:, None, None, None]
    return jnp.where(causal & filled, products, NEG)


def attend_forward(queries, keys, values, q_pos, k_pos, lengths):
    n_slots, q_len, n_heads, head_width = queries.shape
    q_block, per_group = head_groups(n_slots, q_len, n_heads, keys.shape[1])
    n_groups = n_heads // per_group
    n_blocks = q_len // q_block
    pos_blocks = q_pos.reshape(n_blocks, q_block)

    def one_group(packed):
        q_group, k_group, v_group = packed
        q_blocks = jnp.moveaxis(
            q_group.reshape(n_slots, n_blocks, q_block, per_group, head_width), 1, 0
        )

        def one_block(streams):
            q_rows, pos_rows = streams
            scores = score_block(q_rows, k_group, pos_rows, k_pos, lengths)
            highest = jnp.max(scores, axis=-1, keepdims=True)
            exponent = jnp.exp(scores - highest)
            totals = jnp.sum(exponent, axis=-1, keepdims=True)
            probabilities = (exponent / totals).astype(jnp.bfloat16)
            mixture = jnp.einsum(
                "shqk,skhe->sqhe", probabilities, v_group, preferred_element_type=jnp.float32
            )
            return (mixture, (highest + jnp.log(totals))[..., 0])

        mixture, log_sums = lax.map(one_block, (q_blocks, pos_blocks))
        return (
            jnp.moveaxis(mixture, 0, 1).reshape(n_slots, q_len, per_group, head_width),
            log_sums,
        )

    grouped = (
        split_heads(queries, n_groups),
        split_heads(keys, n_groups),
        split_heads(values, n_groups),
    )
    mixture, log_sums = lax.map(one_group, grouped)
    return (join_heads(mixture), log_sums)


def attend_backward(queries, keys, values, upstream, row_dots, log_sums, q_pos, k_pos, lengths):
    n_slots, q_len, n_heads, head_width = queries.shape
    q_block, per_group = head_groups(n_slots, q_len, n_heads, keys.shape[1])
    n_groups = n_heads // per_group
    n_blocks = q_len // q_block
    score_scale = head_width ** (-0.5)
    pos_blocks = q_pos.reshape(n_blocks, q_block)
    dot_groups = jnp.moveaxis(row_dots.reshape(n_slots, q_len, n_groups, per_group), 2, 0)

    def blocks_of(grouped):
        return jnp.moveaxis(grouped.reshape((n_slots, n_blocks, q_block) + grouped.shape[2:]), 1, 0)

    def one_group(packed):
        q_group, k_group, v_group, g_group, d_group, l_group = packed

        def one_block(running, streams):
            k_grad, v_grad = running
            q_rows, g_rows, d_rows, l_rows, pos_rows = streams
            scores = score_block(q_rows, k_group, pos_rows, k_pos, lengths)
            probabilities = jnp.exp(scores - l_rows[..., None])
            v_grad = v_grad + jnp.einsum(
                "shqk,sqhe->skhe",
                probabilities.astype(jnp.bfloat16),
                g_rows,
                preferred_element_type=jnp.float32,
            )
            p_grad = jnp.einsum(
                "sqhe,skhe->shqk", g_rows, v_group, preferred_element_type=jnp.float32
            )
            s_grad = (probabilities * (p_grad - jnp.moveaxis(d_rows, 2, 1)[..., None])).astype(
                jnp.bfloat16
            )
            q_grad = (
                jnp.einsum("shqk,skhe->sqhe", s_grad, k_group, preferred_element_type=jnp.float32)
                * score_scale
            )
            k_grad = (
                k_grad
                + jnp.einsum("shqk,sqhe->skhe", s_grad, q_rows, preferred_element_type=jnp.float32)
                * score_scale
            )
            return ((k_grad, v_grad), q_grad)

        empty_grads = jnp.zeros(k_group.shape, jnp.float32)
        streams = (blocks_of(q_group), blocks_of(g_group), blocks_of(d_group), l_group, pos_blocks)
        (k_grad, v_grad), q_grads = lax.scan(one_block, (empty_grads, empty_grads), streams)
        return (
            jnp.moveaxis(q_grads, 0, 1).reshape(n_slots, q_len, per_group, head_width),
            k_grad,
            v_grad,
        )

    grouped = (
        split_heads(queries, n_groups),
        split_heads(keys, n_groups),
        split_heads(values, n_groups),
        split_heads(upstream, n_groups),
        dot_groups,
        log_sums,
    )
    q_grads, k_grads, v_grads = lax.map(one_group, grouped)
    return (join_heads(q_grads), join_heads(k_grads), join_heads(v_grads))


FAR = 1 << 30


def _block_backward_kernel(q_ref, k_ref, v_ref, g_ref, lse_ref, dots_ref, qpos_ref, kpos_ref,
                           dq_ref, dk_ref, dv_ref, *, head_width, scale):
    pair = pl.program_id(1)
    allowed = kpos_ref[0] <= qpos_ref[...]
    for j in range(2):
        cols = slice(j * head_width, (j + 1) * head_width)
        q = q_ref[0, :, cols]
        k = k_ref[0, :, cols]
        v = v_ref[0, :, cols]
        g = g_ref[0, :, cols]
        head = 2 * pair + j
        lse = lse_ref[0, pl.ds(head, 1), :]
        dots = dots_ref[0, pl.ds(head, 1), :]
        nt = (((1,), (1,)), ((), ()))
        scores = lax.dot_general(k, q, nt, preferred_element_type=jnp.float32) * scale
        scores = jnp.where(allowed, scores, -1e30)
        probs = jnp.exp(scores - lse)
        dv_ref[0, :, cols] = jnp.dot(probs.astype(jnp.bfloat16), g, preferred_element_type=jnp.float32)
        dprobs = lax.dot_general(v, g, nt, preferred_element_type=jnp.float32)
        dscores = (probs * (dprobs - dots)).astype(jnp.bfloat16)
        dk_ref[0, :, cols] = jnp.dot(dscores, q, preferred_element_type=jnp.float32) * scale
        tn = (((0,), (0,)), ((), ()))
        dq_ref[0, :, cols] = lax.dot_general(dscores, k, tn, preferred_element_type=jnp.float32) * scale


def _block_forward_kernel(q_ref, k_ref, v_ref, qpos_ref, kpos_ref, out_ref, lse_ref, *, head_width, scale):
    pair = pl.program_id(1)
    allowed = kpos_ref[0] <= qpos_ref[...]
    nt = (((1,), (1,)), ((), ()))
    tn = (((0,), (0,)), ((), ()))
    for j in range(2):
        cols = slice(j * head_width, (j + 1) * head_width)
        q = q_ref[0, :, cols]
        k = k_ref[0, :, cols]
        v = v_ref[0, :, cols]
        scores = lax.dot_general(k, q, nt, preferred_element_type=jnp.float32) * scale
        scores = jnp.where(allowed, scores, -1e30)
        highest = jnp.max(scores, axis=0, keepdims=True)
        exponent = jnp.exp(scores - highest)
        totals = jnp.sum(exponent, axis=0, keepdims=True)
        probs = (exponent / totals).astype(jnp.bfloat16)
        mixture = lax.dot_general(probs, v, tn, preferred_element_type=jnp.float32)
        out_ref[0, :, cols] = mixture.astype(out_ref.dtype)
        lse_ref[0, pl.ds(2 * pair + j, 1), :] = highest + jnp.log(totals)


def block_forward(queries, keys, values, q_pos, k_pos, lengths):
    n_slots, q_len, n_heads, head_width = queries.shape
    k_len = keys.shape[1]
    width = n_heads * head_width
    pair_width = 2 * head_width
    flat = lambda a: a.reshape(a.shape[0], a.shape[1], width)
    kpos = jnp.where(
        (k_pos[None, :] < lengths[:, None]) & (k_pos[None, :] >= 0), k_pos[None, :], FAR
    ).astype(jnp.int32)[..., None]
    qpos = q_pos.astype(jnp.int32)[None, :]
    kernel = functools.partial(_block_forward_kernel, head_width=head_width, scale=head_width ** (-0.5))
    q_spec = pl.BlockSpec((1, q_len, pair_width), lambda s, p: (s, 0, p))
    k_spec = pl.BlockSpec((1, k_len, pair_width), lambda s, p: (s, 0, p))
    out, lse = pl.pallas_call(
        kernel,
        grid=(n_slots, n_heads // 2),
        in_specs=[
            q_spec, k_spec, k_spec,
            pl.BlockSpec((1, q_len), lambda s, p: (0, 0)),
            pl.BlockSpec((1, k_len, 1), lambda s, p: (s, 0, 0)),
        ],
        out_specs=[q_spec, pl.BlockSpec((1, n_heads, q_len), lambda s, p: (s, 0, 0))],
        out_shape=[
            jax.ShapeDtypeStruct((n_slots, q_len, width), jnp.bfloat16),
            jax.ShapeDtypeStruct((n_slots, n_heads, q_len), jnp.float32),
        ],
        compiler_params=pltpu.CompilerParams(dimension_semantics=("arbitrary", "arbitrary")),
        cost_estimate=pl.CostEstimate(
            flops=n_slots * n_heads * 4 * q_len * k_len * head_width,
            transcendentals=n_slots * n_heads * q_len * k_len,
            bytes_accessed=2 * (2 * q_len + 2 * k_len) * width * n_slots,
        ),
    )(flat(queries), flat(keys), flat(values), qpos, kpos)
    return out.reshape(n_slots, q_len, n_heads, head_width), lse


def block_backward(queries, keys, values, upstream, lse_rows, dot_rows, q_pos, k_pos, lengths):
    n_slots, q_len, n_heads, head_width = queries.shape
    k_len = keys.shape[1]
    width = n_heads * head_width
    pair_width = 2 * head_width
    flat = lambda a: a.reshape(a.shape[0], a.shape[1], width)
    kpos = jnp.where(
        (k_pos[None, :] < lengths[:, None]) & (k_pos[None, :] >= 0), k_pos[None, :], FAR
    ).astype(jnp.int32)[..., None]
    qpos = q_pos.astype(jnp.int32)[None, :]
    kernel = functools.partial(_block_backward_kernel, head_width=head_width, scale=head_width ** (-0.5))
    q_spec = pl.BlockSpec((1, q_len, pair_width), lambda s, p: (s, 0, p))
    k_spec = pl.BlockSpec((1, k_len, pair_width), lambda s, p: (s, 0, p))
    row_spec = pl.BlockSpec((1, n_heads, q_len), lambda s, p: (s, 0, 0))
    flops = n_slots * n_heads * 10 * q_len * k_len * head_width
    dq, dk, dv = pl.pallas_call(
        kernel,
        grid=(n_slots, n_heads // 2),
        in_specs=[
            q_spec, k_spec, k_spec, q_spec, row_spec, row_spec,
            pl.BlockSpec((1, q_len), lambda s, p: (0, 0)),
            pl.BlockSpec((1, k_len, 1), lambda s, p: (s, 0, 0)),
        ],
        out_specs=[q_spec, k_spec, k_spec],
        out_shape=[
            jax.ShapeDtypeStruct((n_slots, q_len, width), jnp.float32),
            jax.ShapeDtypeStruct((n_slots, k_len, width), jnp.float32),
            jax.ShapeDtypeStruct((n_slots, k_len, width), jnp.float32),
        ],
        cost_estimate=pl.CostEstimate(
            flops=flops,
            transcendentals=n_slots * n_heads * q_len * k_len,
            bytes_accessed=2 * (2 * q_len + 2 * k_len) * width * n_slots + 4 * (q_len + 2 * k_len) * width * n_slots,
        ),
    )(flat(queries), flat(keys), flat(values), flat(upstream), lse_rows, dot_rows, qpos, kpos)
    shape_q = (n_slots, q_len, n_heads, head_width)
    shape_k = (n_slots, k_len, n_heads, head_width)
    return dq.reshape(shape_q), dk.reshape(shape_k), dv.reshape(shape_k)


GROUP = ("fsdp", "ctx")


def gather_blocks(pieces):
    packed = jnp.concatenate(pieces, axis=0)
    gathered = lax.all_gather(packed, GROUP, axis=0, tiled=False)
    fulls, offset = [], 0
    for piece in pieces:
        fulls.append(gathered[:, offset : offset + piece.shape[0], :])
        offset += piece.shape[0]
    return fulls


def rep_chain(x):
    me = lax.axis_index("rep")
    arrived = lax.ppermute(x, "rep", [(0, 1), (3, 2)])
    folded = (x.astype(jnp.float32) + arrived.astype(jnp.float32)).astype(x.dtype)
    arrived = lax.ppermute(folded, "rep", [(1, 2), (2, 1)])
    total = (folded.astype(jnp.float32) + arrived.astype(jnp.float32)).astype(x.dtype)
    sent_out = lax.ppermute(total, "rep", [(1, 0), (2, 3)])
    return jnp.where((me == 0) | (me == 3), sent_out, total)


def rep_sum(x, pieces=1):
    if lax.axis_size("rep") != 4:
        return lax.psum(x, "rep")
    rows = x.shape[1]
    if pieces == 1 or rows % (8 * pieces):
        return rep_chain(x)
    step = rows // pieces
    parts = []
    for i in range(pieces):
        parts.append(rep_chain(x[:, i * step : (i + 1) * step]))
    return jnp.concatenate(parts, axis=1)


def scatter_blocks(blocks, by_permutes, pieces=1):
    packed = jnp.concatenate(blocks, axis=1).astype(jnp.bfloat16)
    summed = lax.psum_scatter(packed, GROUP, scatter_dimension=0, tiled=True)
    summed = (rep_sum(summed, pieces) if by_permutes else lax.psum(summed, "rep"))[0].astype(
        jnp.float32
    )
    parts, offset = [], 0
    for block in blocks:
        parts.append(summed[offset : offset + block.shape[1], :])
        offset += block.shape[1]
    return parts


def gain_block(first, second, width):
    lead = first.shape[:-1]
    row = jnp.concatenate([first, second], axis=-1)
    row = jnp.pad(row, [(0, 0)] * len(lead) + [(0, width - row.shape[-1])])
    return jnp.pad(row[..., None, :], [(0, 0)] * len(lead) + [(0, 7), (0, 0)])


def shards(
    tokens,
    initial_layer_values,
    cotangent,
    lengths,
    w_query,
    w_key,
    w_value,
    w_out,
    w_gate,
    w_up,
    w_down,
    gain_attn,
    gain_mlp,
):
    n_slots, slot_rows, model_width = tokens.shape
    n_ctx = lax.axis_size("ctx")
    n_group = lax.axis_size("fsdp") * n_ctx
    own_rows = gain_attn.shape[0]
    ff_width = w_gate.shape[1]
    attn_width = w_query.shape[1]
    qkv_width = 3 * attn_width
    (qkv_blocks, gain_rows) = gather_blocks(
        [
            jnp.concatenate([w_query, w_key, w_value], axis=1),
            gain_block(gain_attn, gain_mlp, qkv_width),
        ]
    )
    full_qkv = qkv_blocks.reshape(n_group * own_rows, qkv_width)
    full_gain_attn = gain_rows[:, 0, :own_rows].reshape(-1)
    full_gain_mlp = gain_rows[:, 0, own_rows : 2 * own_rows].reshape(-1)
    (out_blocks,) = gather_blocks([w_out])
    full_out = out_blocks.reshape(-1, model_width)
    (gu_blocks,) = gather_blocks([jnp.concatenate([w_gate, w_up], axis=1)])
    full_gu = gu_blocks.reshape(n_group * own_rows, 2 * ff_width)
    (down_blocks,) = gather_blocks([w_down])
    full_down = down_blocks.reshape(-1, model_width)
    ctx_index = lax.axis_index("ctx")
    q_pos = ctx_index * slot_rows + jnp.arange(slot_rows)
    live_rows = q_pos[None, :] < lengths[:, None]
    head_shape = (n_slots, slot_rows, HEADS, HEAD_DIM)
    paired = n_ctx == 2
    if paired:
        other_tokens = lax.ppermute(tokens, "ctx", [(0, 1), (1, 0)])
        other_first = lax.ppermute(initial_layer_values, "ctx", [(0, 1)])
        other_pos = (1 - ctx_index) * slot_rows + jnp.arange(slot_rows)
    inputs = tokens.astype(jnp.float32)
    attn_scale = full_gain_attn.astype(jnp.float32)
    mlp_scale = full_gain_mlp.astype(jnp.float32)

    def project(chunk_tokens, chunk_first, chunk_pos):
        chunk_normed, chunk_inv = normalize(chunk_tokens.astype(jnp.float32), attn_scale)
        chunk_low = chunk_normed.astype(jnp.bfloat16)
        qkv_pre = jnp.einsum(
            "srd,de->sre", chunk_low, full_qkv, preferred_element_type=jnp.float32
        )
        q_pre = qkv_pre[..., :attn_width]
        k_pre = qkv_pre[..., attn_width : 2 * attn_width]
        v_pre = qkv_pre[..., 2 * attn_width :]
        chunk_q = rotate(q_pre.reshape(head_shape), chunk_pos, 1.0).astype(jnp.bfloat16)
        chunk_k = rotate(k_pre.reshape(head_shape), chunk_pos, 1.0).astype(jnp.bfloat16)
        chunk_v = (
            (0.5 * v_pre + 0.5 * chunk_first.astype(jnp.float32))
            .astype(jnp.bfloat16)
            .reshape(head_shape)
        )
        return chunk_low, chunk_inv, chunk_q, chunk_k, chunk_v

    normed_low, inv_attn, queries, keys, values = project(tokens, initial_layer_values, q_pos)
    if paired:
        _, _, other_q, other_k, other_v = project(other_tokens, other_first, other_pos)
        slot_k = jnp.concatenate([other_k, keys], axis=1)
        slot_v = jnp.concatenate([other_v, values], axis=1)
        k_pos = jnp.concatenate([other_pos, q_pos])
    else:
        slot_k, slot_v = (
            lax.all_gather(keys, "ctx", axis=1, tiled=True),
            lax.all_gather(values, "ctx", axis=1, tiled=True),
        )
        k_pos = jnp.arange(n_ctx * slot_rows)
    if paired:
        attended, lse_rows = block_forward(queries, slot_k, slot_v, q_pos, k_pos, lengths)
    else:
        attn_raw, attn_lse = attend_forward(queries, slot_k, slot_v, q_pos, k_pos, lengths)
        attended = attn_raw.astype(jnp.bfloat16)
    att_flat = attended.reshape(n_slots, slot_rows, model_width)
    branch = jnp.einsum("sre,ed->srd", att_flat, full_out, preferred_element_type=jnp.float32)
    residual = inputs + branch
    normed_mlp, inv_mlp = normalize(residual, mlp_scale)
    mlp_low = normed_mlp.astype(jnp.bfloat16)
    gu_proj = jnp.einsum("srd,df->srf", mlp_low, full_gu, preferred_element_type=jnp.float32)
    gate_proj = gu_proj[..., :ff_width]
    up_proj = gu_proj[..., ff_width:]
    sigmoid_gate = jax.nn.sigmoid(gate_proj)
    hidden = (gate_proj * sigmoid_gate * up_proj).astype(jnp.bfloat16)
    final = residual + jnp.einsum(
        "srf,fd->srd", hidden, full_down, preferred_element_type=jnp.float32
    )
    output = jnp.where(live_rows[..., None], final, 0.0).astype(jnp.bfloat16)
    output_gradient = jnp.where(live_rows[..., None], cotangent.astype(jnp.float32), 0.0)
    g_low = output_gradient.astype(jnp.bfloat16)
    gu_alone = lax.optimization_barrier(gu_proj)
    gate_alone = gu_alone[..., :ff_width]
    hidden_alone = (gate_alone * jax.nn.sigmoid(gate_alone) * gu_alone[..., ff_width:]).astype(
        jnp.bfloat16
    )
    grad_down = jnp.einsum(
        "srf,srd->fd", hidden_alone, g_low, preferred_element_type=jnp.float32
    )
    (part_down,) = scatter_blocks(
        [grad_down.reshape(n_group, -1, model_width).astype(jnp.bfloat16)], True
    )
    g_hidden = jnp.einsum("srd,fd->srf", g_low, full_down, preferred_element_type=jnp.float32)
    gate_gradient = (g_hidden * up_proj * sigmoid_gate * (1.0 + gate_proj * (1.0 - sigmoid_gate))).astype(jnp.bfloat16)
    up_gradient = (g_hidden * gate_proj * sigmoid_gate).astype(jnp.bfloat16)
    gu_gradient = jnp.concatenate([gate_gradient, up_gradient], axis=-1)
    grad_gu = jnp.einsum(
        "srd,srf->df", mlp_low, gu_gradient, preferred_element_type=jnp.float32
    )
    g_normed_mlp = jnp.einsum(
        "srf,df->srd", gu_gradient, full_gu, preferred_element_type=jnp.float32
    )
    g_mlp_in, grad_gain_mlp = normalize_back(residual, inv_mlp, mlp_scale, g_normed_mlp)
    g_residual = output_gradient + g_mlp_in
    g_branch = g_residual.astype(jnp.bfloat16)
    grad_out = jnp.einsum(
        "sre,srd->ed", att_flat, g_branch, preferred_element_type=jnp.float32
    )
    gu_block = grad_gu.reshape(n_group, own_rows, 2 * ff_width).astype(jnp.bfloat16)
    g_attended = (
        jnp.einsum("srd,ed->sre", g_branch, full_out, preferred_element_type=jnp.float32)
        .astype(jnp.bfloat16)
        .reshape(head_shape)
    )
    (part_gu,) = scatter_blocks([gu_block], True, 2)
    row_dots = jnp.sum(g_attended.astype(jnp.float32) * attended.astype(jnp.float32), axis=-1)
    if paired:
        dot_rows = jnp.transpose(row_dots, (0, 2, 1))
        later_g, later_dots, later_lse = lax.ppermute(
            (g_attended, dot_rows, lse_rows), "ctx", [(1, 0)]
        )
        g_queries, g_keys, g_values = block_backward(
            queries, keys, values, g_attended, lse_rows, dot_rows, q_pos, q_pos, lengths
        )
        later = ctx_index == 1
        pick = lambda mine, theirs: jnp.where(later, mine, theirs)
        x_dq, x_dk, x_dv = block_backward(
            pick(queries, other_q),
            pick(other_k, keys),
            pick(other_v, values),
            pick(g_attended, later_g),
            pick(lse_rows, later_lse),
            pick(dot_rows, later_dots),
            pick(q_pos, other_pos),
            pick(other_pos, q_pos),
            lengths,
        )
        g_queries = g_queries + jnp.where(later, x_dq, 0.0)
        g_keys = g_keys + jnp.where(later, 0.0, x_dk)
        g_values = g_values + jnp.where(later, 0.0, x_dv)
    else:
        g_queries, slot_dk, slot_dv = attend_backward(
            queries, slot_k, slot_v, g_attended, row_dots, attn_lse, q_pos, k_pos, lengths
        )
        g_keys, g_values = (
            lax.psum_scatter(
                slot_dk.astype(jnp.bfloat16), "ctx", scatter_dimension=1, tiled=True
            ).astype(jnp.float32),
            lax.psum_scatter(
                slot_dv.astype(jnp.bfloat16), "ctx", scatter_dimension=1, tiled=True
            ).astype(jnp.float32),
        )
    flat_shape = (n_slots, slot_rows, model_width)
    gq_low = rotate(g_queries, q_pos, -1.0).reshape(flat_shape).astype(jnp.bfloat16)
    gk_low = rotate(g_keys, q_pos, -1.0).reshape(flat_shape).astype(jnp.bfloat16)
    gv_rounded = g_values.reshape(flat_shape).astype(jnp.bfloat16).astype(jnp.float32)
    d_first = 0.5 * gv_rounded
    gv_half = d_first.astype(jnp.bfloat16)
    g_qkv = jnp.concatenate([gq_low, gk_low, gv_half], axis=-1)
    grad_qkv = jnp.einsum("srd,sre->de", normed_low, g_qkv, preferred_element_type=jnp.float32)
    g_normed = jnp.einsum("sre,de->srd", g_qkv, full_qkv, preferred_element_type=jnp.float32)
    g_attn_in, grad_gain_attn = normalize_back(inputs, inv_attn, attn_scale, g_normed)
    d_tokens = g_residual + g_attn_in
    part_qkvo, part_gains = scatter_blocks(
        [
            jnp.concatenate([grad_qkv, grad_out], axis=1).reshape(
                n_group, own_rows, qkv_width + model_width
            ),
            gain_block(
                grad_gain_attn.reshape(n_group, own_rows),
                grad_gain_mlp.reshape(n_group, own_rows),
                qkv_width + model_width,
            ),
        ],
        False,
    )
    part_qkv = part_qkvo[:, :qkv_width]
    return (
        output,
        d_tokens,
        d_first,
        part_qkv[:, :attn_width],
        part_qkv[:, attn_width : 2 * attn_width],
        part_qkv[:, 2 * attn_width :],
        part_qkvo[:, qkv_width:],
        part_gu[:, :ff_width],
        part_gu[:, ff_width:],
        part_down,
        part_gains[0, :own_rows],
        part_gains[0, own_rows : 2 * own_rows],
    )


def solution(mesh):
    in_specs = (
        P(("rep", "fsdp"), "ctx", None),
        P(("rep", "fsdp"), "ctx", None),
        P(("rep", "fsdp"), "ctx", None),
        P(("rep", "fsdp")),
        P(("fsdp", "ctx"), None),
        P(("fsdp", "ctx"), None),
        P(("fsdp", "ctx"), None),
        P(("fsdp", "ctx"), None),
        P(("fsdp", "ctx"), None),
        P(("fsdp", "ctx"), None),
        P(("fsdp", "ctx"), None),
        P(("fsdp", "ctx")),
        P(("fsdp", "ctx")),
    )
    out_specs = (
        P(("rep", "fsdp"), "ctx", None),
        P(("rep", "fsdp"), "ctx", None),
        P(("rep", "fsdp"), "ctx", None),
        P(("fsdp", "ctx"), None),
        P(("fsdp", "ctx"), None),
        P(("fsdp", "ctx"), None),
        P(("fsdp", "ctx"), None),
        P(("fsdp", "ctx"), None),
        P(("fsdp", "ctx"), None),
        P(("fsdp", "ctx"), None),
        P(("fsdp", "ctx")),
        P(("fsdp", "ctx")),
    )

    return jax.shard_map(shards, mesh=mesh, in_specs=in_specs, out_specs=out_specs, check_vma=False)
```

```python
import functools

import jax
import jax.numpy as jnp
from jax import lax
from jax.experimental import pallas as pl
from jax.experimental.pallas import tpu as pltpu
from jax.sharding import PartitionSpec as P


HEADS = 16
HEAD_DIM = 64


EPS = 1e-06
NEG = -1e30
THETA = 10000.0
SCORE_CAP = 4194304


def rotate(field, positions, direction):
    head_width = field.shape[-1]
    half_width = head_width // 2
    frequency = THETA ** (-(jnp.arange(half_width, dtype=jnp.float32) * 2.0) / head_width)
    angles = positions.astype(jnp.float32)[:, None] * frequency[None, :]
    cosine = jnp.cos(angles)[:, None, :]
    sine_part = direction * jnp.sin(angles)[:, None, :]
    former = field[..., :half_width]
    latter = field[..., half_width:]
    return jnp.concatenate(
        [former * cosine - latter * sine_part, latter * cosine + former * sine_part], axis=-1
    )


def normalize(values, gain):
    inverse = lax.rsqrt(jnp.mean(values * values, axis=-1, keepdims=True) + EPS)
    return (values * inverse * gain, inverse)


def normalize_back(values, inverse, gain, upstream):
    unit_rows = values * inverse
    scaled = upstream * gain
    grad_gain = jnp.sum(upstream * unit_rows, axis=(0, 1))
    grad_values = inverse * (
        scaled - unit_rows * jnp.mean(scaled * unit_rows, axis=-1, keepdims=True)
    )
    return (grad_values, grad_gain)


def head_groups(n_slots, q_len, n_heads, k_len):
    q_block = min(q_len, 512)
    per_group = max(1, min(n_heads, SCORE_CAP // (n_slots * q_block * k_len)))
    while n_heads % per_group:
        per_group = per_group - 1
    return (q_block, per_group)


def split_heads(packed, n_groups):
    n_slots, length, n_heads, head_width = packed.shape
    return jnp.moveaxis(
        packed.reshape(n_slots, length, n_groups, n_heads // n_groups, head_width), 2, 0
    )


def join_heads(grouped):
    n_groups, n_slots, length, per_group, head_width = grouped.shape
    return jnp.moveaxis(grouped, 0, 2).reshape(n_slots, length, n_groups * per_group, head_width)


def score_block(q_rows, k_rows, q_pos, k_pos, lengths):
    products = jnp.einsum(
        "sqhe,skhe->shqk", q_rows, k_rows, preferred_element_type=jnp.float32
    ) * q_rows.shape[-1] ** (-0.5)
    causal = (k_pos[None, None, None, :] <= q_pos[None, None, :, None]) & (
        k_pos[None, None, None, :] >= 0
    )
    filled = k_pos[None, None, None, :] < lengths[:, None, None, None]
    return jnp.where(causal & filled, products, NEG)


def attend_forward(queries, keys, values, q_pos, k_pos, lengths):
    n_slots, q_len, n_heads, head_width = queries.shape
    q_block, per_group = head_groups(n_slots, q_len, n_heads, keys.shape[1])
    n_groups = n_heads // per_group
    n_blocks = q_len // q_block
    pos_blocks = q_pos.reshape(n_blocks, q_block)

    def one_group(packed):
        q_group, k_group, v_group = packed
        q_blocks = jnp.moveaxis(
            q_group.reshape(n_slots, n_blocks, q_block, per_group, head_width), 1, 0
        )

        def one_block(streams):
            q_rows, pos_rows = streams
            scores = score_block(q_rows, k_group, pos_rows, k_pos, lengths)
            highest = jnp.max(scores, axis=-1, keepdims=True)
            exponent = jnp.exp(scores - highest)
            totals = jnp.sum(exponent, axis=-1, keepdims=True)
            probabilities = (exponent / totals).astype(jnp.bfloat16)
            mixture = jnp.einsum(
                "shqk,skhe->sqhe", probabilities, v_group, preferred_element_type=jnp.float32
            )
            return (mixture, (highest + jnp.log(totals))[..., 0])

        mixture, log_sums = lax.map(one_block, (q_blocks, pos_blocks))
        return (
            jnp.moveaxis(mixture, 0, 1).reshape(n_slots, q_len, per_group, head_width),
            log_sums,
        )

    grouped = (
        split_heads(queries, n_groups),
        split_heads(keys, n_groups),
        split_heads(values, n_groups),
    )
    mixture, log_sums = lax.map(one_group, grouped)
    return (join_heads(mixture), log_sums)


def attend_backward(queries, keys, values, upstream, row_dots, log_sums, q_pos, k_pos, lengths):
    n_slots, q_len, n_heads, head_width = queries.shape
    q_block, per_group = head_groups(n_slots, q_len, n_heads, keys.shape[1])
    n_groups = n_heads // per_group
    n_blocks = q_len // q_block
    score_scale = head_width ** (-0.5)
    pos_blocks = q_pos.reshape(n_blocks, q_block)
    dot_groups = jnp.moveaxis(row_dots.reshape(n_slots, q_len, n_groups, per_group), 2, 0)

    def blocks_of(grouped):
        return jnp.moveaxis(grouped.reshape((n_slots, n_blocks, q_block) + grouped.shape[2:]), 1, 0)

    def one_group(packed):
        q_group, k_group, v_group, g_group, d_group, l_group = packed

        def one_block(running, streams):
            k_grad, v_grad = running
            q_rows, g_rows, d_rows, l_rows, pos_rows = streams
            scores = score_block(q_rows, k_group, pos_rows, k_pos, lengths)
            probabilities = jnp.exp(scores - l_rows[..., None])
            v_grad = v_grad + jnp.einsum(
                "shqk,sqhe->skhe",
                probabilities.astype(jnp.bfloat16),
                g_rows,
                preferred_element_type=jnp.float32,
            )
            p_grad = jnp.einsum(
                "sqhe,skhe->shqk", g_rows, v_group, preferred_element_type=jnp.float32
            )
            s_grad = (probabilities * (p_grad - jnp.moveaxis(d_rows, 2, 1)[..., None])).astype(
                jnp.bfloat16
            )
            q_grad = (
                jnp.einsum("shqk,skhe->sqhe", s_grad, k_group, preferred_element_type=jnp.float32)
                * score_scale
            )
            k_grad = (
                k_grad
                + jnp.einsum("shqk,sqhe->skhe", s_grad, q_rows, preferred_element_type=jnp.float32)
                * score_scale
            )
            return ((k_grad, v_grad), q_grad)

        empty_grads = jnp.zeros(k_group.shape, jnp.float32)
        streams = (blocks_of(q_group), blocks_of(g_group), blocks_of(d_group), l_group, pos_blocks)
        (k_grad, v_grad), q_grads = lax.scan(one_block, (empty_grads, empty_grads), streams)
        return (
            jnp.moveaxis(q_grads, 0, 1).reshape(n_slots, q_len, per_group, head_width),
            k_grad,
            v_grad,
        )

    grouped = (
        split_heads(queries, n_groups),
        split_heads(keys, n_groups),
        split_heads(values, n_groups),
        split_heads(upstream, n_groups),
        dot_groups,
        log_sums,
    )
    q_grads, k_grads, v_grads = lax.map(one_group, grouped)
    return (join_heads(q_grads), join_heads(k_grads), join_heads(v_grads))


FAR = 1 << 30


def _block_backward_kernel(q_ref, k_ref, v_ref, g_ref, lse_ref, dots_ref, qpos_ref, kpos_ref,
                           dq_ref, dk_ref, dv_ref, *, head_width, scale):
    pair = pl.program_id(1)
    allowed = kpos_ref[0] <= qpos_ref[...]
    for j in range(2):
        cols = slice(j * head_width, (j + 1) * head_width)
        q = q_ref[0, :, cols]
        k = k_ref[0, :, cols]
        v = v_ref[0, :, cols]
        g = g_ref[0, :, cols]
        head = 2 * pair + j
        lse = lse_ref[0, pl.ds(head, 1), :]
        dots = dots_ref[0, pl.ds(head, 1), :]
        nt = (((1,), (1,)), ((), ()))
        scores = lax.dot_general(k, q, nt, preferred_element_type=jnp.float32) * scale
        scores = jnp.where(allowed, scores, -1e30)
        probs = jnp.exp(scores - lse)
        dv_ref[0, :, cols] = jnp.dot(probs.astype(jnp.bfloat16), g, preferred_element_type=jnp.float32)
        dprobs = lax.dot_general(v, g, nt, preferred_element_type=jnp.float32)
        dscores = (probs * (dprobs - dots)).astype(jnp.bfloat16)
        dk_ref[0, :, cols] = jnp.dot(dscores, q, preferred_element_type=jnp.float32) * scale
        tn = (((0,), (0,)), ((), ()))
        dq_ref[0, :, cols] = lax.dot_general(dscores, k, tn, preferred_element_type=jnp.float32) * scale


def _block_forward_kernel(q_ref, k_ref, v_ref, qpos_ref, kpos_ref, out_ref, lse_ref, *, head_width, scale):
    pair = pl.program_id(1)
    allowed = kpos_ref[0] <= qpos_ref[...]
    nt = (((1,), (1,)), ((), ()))
    tn = (((0,), (0,)), ((), ()))
    for j in range(2):
        cols = slice(j * head_width, (j + 1) * head_width)
        q = q_ref[0, :, cols]
        k = k_ref[0, :, cols]
        v = v_ref[0, :, cols]
        scores = lax.dot_general(k, q, nt, preferred_element_type=jnp.float32) * scale
        scores = jnp.where(allowed, scores, -1e30)
        highest = jnp.max(scores, axis=0, keepdims=True)
        exponent = jnp.exp(scores - highest)
        totals = jnp.sum(exponent, axis=0, keepdims=True)
        probs = (exponent / totals).astype(jnp.bfloat16)
        mixture = lax.dot_general(probs, v, tn, preferred_element_type=jnp.float32)
        out_ref[0, :, cols] = mixture.astype(out_ref.dtype)
        lse_ref[0, pl.ds(2 * pair + j, 1), :] = highest + jnp.log(totals)


def block_forward(queries, keys, values, q_pos, k_pos, lengths):
    n_slots, q_len, n_heads, head_width = queries.shape
    k_len = keys.shape[1]
    width = n_heads * head_width
    pair_width = 2 * head_width
    flat = lambda a: a.reshape(a.shape[0], a.shape[1], width)
    kpos = jnp.where(
        (k_pos[None, :] < lengths[:, None]) & (k_pos[None, :] >= 0), k_pos[None, :], FAR
    ).astype(jnp.int32)[..., None]
    qpos = q_pos.astype(jnp.int32)[None, :]
    kernel = functools.partial(_block_forward_kernel, head_width=head_width, scale=head_width ** (-0.5))
    q_spec = pl.BlockSpec((1, q_len, pair_width), lambda s, p: (s, 0, p))
    k_spec = pl.BlockSpec((1, k_len, pair_width), lambda s, p: (s, 0, p))
    out, lse = pl.pallas_call(
        kernel,
        grid=(n_slots, n_heads // 2),
        in_specs=[
            q_spec, k_spec, k_spec,
            pl.BlockSpec((1, q_len), lambda s, p: (0, 0)),
            pl.BlockSpec((1, k_len, 1), lambda s, p: (s, 0, 0)),
        ],
        out_specs=[q_spec, pl.BlockSpec((1, n_heads, q_len), lambda s, p: (s, 0, 0))],
        out_shape=[
            jax.ShapeDtypeStruct((n_slots, q_len, width), jnp.bfloat16),
            jax.ShapeDtypeStruct((n_slots, n_heads, q_len), jnp.float32),
        ],
        compiler_params=pltpu.CompilerParams(dimension_semantics=("arbitrary", "arbitrary")),
        cost_estimate=pl.CostEstimate(
            flops=n_slots * n_heads * 4 * q_len * k_len * head_width,
            transcendentals=n_slots * n_heads * q_len * k_len,
            bytes_accessed=2 * (2 * q_len + 2 * k_len) * width * n_slots,
        ),
    )(flat(queries), flat(keys), flat(values), qpos, kpos)
    return out.reshape(n_slots, q_len, n_heads, head_width), lse


def block_backward(queries, keys, values, upstream, lse_rows, dot_rows, q_pos, k_pos, lengths):
    n_slots, q_len, n_heads, head_width = queries.shape
    k_len = keys.shape[1]
    width = n_heads * head_width
    pair_width = 2 * head_width
    flat = lambda a: a.reshape(a.shape[0], a.shape[1], width)
    kpos = jnp.where(
        (k_pos[None, :] < lengths[:, None]) & (k_pos[None, :] >= 0), k_pos[None, :], FAR
    ).astype(jnp.int32)[..., None]
    qpos = q_pos.astype(jnp.int32)[None, :]
    kernel = functools.partial(_block_backward_kernel, head_width=head_width, scale=head_width ** (-0.5))
    q_spec = pl.BlockSpec((1, q_len, pair_width), lambda s, p: (s, 0, p))
    k_spec = pl.BlockSpec((1, k_len, pair_width), lambda s, p: (s, 0, p))
    row_spec = pl.BlockSpec((1, n_heads, q_len), lambda s, p: (s, 0, 0))
    flops = n_slots * n_heads * 10 * q_len * k_len * head_width
    dq, dk, dv = pl.pallas_call(
        kernel,
        grid=(n_slots, n_heads // 2),
        in_specs=[
            q_spec, k_spec, k_spec, q_spec, row_spec, row_spec,
            pl.BlockSpec((1, q_len), lambda s, p: (0, 0)),
            pl.BlockSpec((1, k_len, 1), lambda s, p: (s, 0, 0)),
        ],
        out_specs=[q_spec, k_spec, k_spec],
        out_shape=[
            jax.ShapeDtypeStruct((n_slots, q_len, width), jnp.float32),
            jax.ShapeDtypeStruct((n_slots, k_len, width), jnp.float32),
            jax.ShapeDtypeStruct((n_slots, k_len, width), jnp.float32),
        ],
        cost_estimate=pl.CostEstimate(
            flops=flops,
            transcendentals=n_slots * n_heads * q_len * k_len,
            bytes_accessed=2 * (2 * q_len + 2 * k_len) * width * n_slots + 4 * (q_len + 2 * k_len) * width * n_slots,
        ),
    )(flat(queries), flat(keys), flat(values), flat(upstream), lse_rows, dot_rows, qpos, kpos)
    shape_q = (n_slots, q_len, n_heads, head_width)
    shape_k = (n_slots, k_len, n_heads, head_width)
    return dq.reshape(shape_q), dk.reshape(shape_k), dv.reshape(shape_k)


GROUP = ("fsdp", "ctx")


def gather_blocks(pieces):
    packed = jnp.concatenate(pieces, axis=0)
    gathered = lax.all_gather(packed, GROUP, axis=0, tiled=False)
    fulls, offset = [], 0
    for piece in pieces:
        fulls.append(gathered[:, offset : offset + piece.shape[0], :])
        offset += piece.shape[0]
    return fulls


def rep_chain(x):
    me = lax.axis_index("rep")
    arrived = lax.ppermute(x, "rep", [(0, 1), (3, 2)])
    folded = (x.astype(jnp.float32) + arrived.astype(jnp.float32)).astype(x.dtype)
    arrived = lax.ppermute(folded, "rep", [(1, 2), (2, 1)])
    total = (folded.astype(jnp.float32) + arrived.astype(jnp.float32)).astype(x.dtype)
    sent_out = lax.ppermute(total, "rep", [(1, 0), (2, 3)])
    return jnp.where((me == 0) | (me == 3), sent_out, total)


def rep_sum(x, pieces=1):
    if lax.axis_size("rep") != 4:
        return lax.psum(x, "rep")
    rows = x.shape[1]
    if pieces == 1 or rows % (8 * pieces):
        return rep_chain(x)
    step = rows // pieces
    parts = []
    for i in range(pieces):
        parts.append(rep_chain(x[:, i * step : (i + 1) * step]))
    return jnp.concatenate(parts, axis=1)


def scatter_blocks(blocks, by_permutes, pieces=1):
    packed = jnp.concatenate(blocks, axis=1).astype(jnp.bfloat16)
    summed = lax.psum_scatter(packed, GROUP, scatter_dimension=0, tiled=True)
    summed = (rep_sum(summed, pieces) if by_permutes else lax.psum(summed, "rep"))[0].astype(
        jnp.float32
    )
    parts, offset = [], 0
    for block in blocks:
        parts.append(summed[offset : offset + block.shape[1], :])
        offset += block.shape[1]
    return parts


def gain_block(first, second, width):
    lead = first.shape[:-1]
    row = jnp.concatenate([first, second], axis=-1)
    row = jnp.pad(row, [(0, 0)] * len(lead) + [(0, width - row.shape[-1])])
    return jnp.pad(row[..., None, :], [(0, 0)] * len(lead) + [(0, 7), (0, 0)])


def shards(
    tokens,
    initial_layer_values,
    cotangent,
    lengths,
    w_query,
    w_key,
    w_value,
    w_out,
    w_gate,
    w_up,
    w_down,
    gain_attn,
    gain_mlp,
):
    n_slots, slot_rows, model_width = tokens.shape
    n_ctx = lax.axis_size("ctx")
    n_group = lax.axis_size("fsdp") * n_ctx
    own_rows = gain_attn.shape[0]
    ff_width = w_gate.shape[1]
    attn_width = w_query.shape[1]
    qkv_width = 3 * attn_width
    qkvo_width = qkv_width + model_width
    (qkvo_blocks, gain_rows) = gather_blocks(
        [
            jnp.concatenate([w_query, w_key, w_value, w_out], axis=1),
            gain_block(gain_attn, gain_mlp, qkvo_width),
        ]
    )
    full_qkvo = qkvo_blocks.reshape(n_group * own_rows, qkvo_width)
    full_qkv = full_qkvo[:, :qkv_width]
    full_out = full_qkvo[:, qkv_width:]
    full_gain_attn = gain_rows[:, 0, :own_rows].reshape(-1)
    full_gain_mlp = gain_rows[:, 0, own_rows : 2 * own_rows].reshape(-1)
    (gu_blocks,) = gather_blocks([jnp.concatenate([w_gate, w_up], axis=1)])
    full_gu = gu_blocks.reshape(n_group * own_rows, 2 * ff_width)
    (down_blocks,) = gather_blocks([w_down])
    full_down = down_blocks.reshape(-1, model_width)
    ctx_index = lax.axis_index("ctx")
    q_pos = ctx_index * slot_rows + jnp.arange(slot_rows)
    live_rows = q_pos[None, :] < lengths[:, None]
    head_shape = (n_slots, slot_rows, HEADS, HEAD_DIM)
    paired = n_ctx == 2
    if paired:
        other_tokens = lax.ppermute(tokens, "ctx", [(0, 1), (1, 0)])
        other_first = lax.ppermute(initial_layer_values, "ctx", [(0, 1)])
        other_pos = (1 - ctx_index) * slot_rows + jnp.arange(slot_rows)
    inputs = tokens.astype(jnp.float32)
    attn_scale = full_gain_attn.astype(jnp.float32)
    mlp_scale = full_gain_mlp.astype(jnp.float32)

    def project(chunk_tokens, chunk_first, chunk_pos):
        chunk_normed, chunk_inv = normalize(chunk_tokens.astype(jnp.float32), attn_scale)
        chunk_low = chunk_normed.astype(jnp.bfloat16)
        qkv_pre = jnp.einsum(
            "srd,de->sre", chunk_low, full_qkv, preferred_element_type=jnp.float32
        )
        q_pre = qkv_pre[..., :attn_width]
        k_pre = qkv_pre[..., attn_width : 2 * attn_width]
        v_pre = qkv_pre[..., 2 * attn_width :]
        chunk_q = rotate(q_pre.reshape(head_shape), chunk_pos, 1.0).astype(jnp.bfloat16)
        chunk_k = rotate(k_pre.reshape(head_shape), chunk_pos, 1.0).astype(jnp.bfloat16)
        chunk_v = (
            (0.5 * v_pre + 0.5 * chunk_first.astype(jnp.float32))
            .astype(jnp.bfloat16)
            .reshape(head_shape)
        )
        return chunk_low, chunk_inv, chunk_q, chunk_k, chunk_v

    normed_low, inv_attn, queries, keys, values = project(tokens, initial_layer_values, q_pos)
    if paired:
        _, _, other_q, other_k, other_v = project(other_tokens, other_first, other_pos)
        slot_k = jnp.concatenate([other_k, keys], axis=1)
        slot_v = jnp.concatenate([other_v, values], axis=1)
        k_pos = jnp.concatenate([other_pos, q_pos])
    else:
        slot_k, slot_v = (
            lax.all_gather(keys, "ctx", axis=1, tiled=True),
            lax.all_gather(values, "ctx", axis=1, tiled=True),
        )
        k_pos = jnp.arange(n_ctx * slot_rows)
    if paired:
        attended, lse_rows = block_forward(queries, slot_k, slot_v, q_pos, k_pos, lengths)
    else:
        attn_raw, attn_lse = attend_forward(queries, slot_k, slot_v, q_pos, k_pos, lengths)
        attended = attn_raw.astype(jnp.bfloat16)
    att_flat = attended.reshape(n_slots, slot_rows, model_width)
    branch = jnp.einsum("sre,ed->srd", att_flat, full_out, preferred_element_type=jnp.float32)
    residual = inputs + branch
    normed_mlp, inv_mlp = normalize(residual, mlp_scale)
    mlp_low = normed_mlp.astype(jnp.bfloat16)
    gu_proj = jnp.einsum("srd,df->srf", mlp_low, full_gu, preferred_element_type=jnp.float32)
    gate_proj = gu_proj[..., :ff_width]
    up_proj = gu_proj[..., ff_width:]
    sigmoid_gate = jax.nn.sigmoid(gate_proj)
    hidden = (gate_proj * sigmoid_gate * up_proj).astype(jnp.bfloat16)
    final = residual + jnp.einsum(
        "srf,fd->srd", hidden, full_down, preferred_element_type=jnp.float32
    )
    output = jnp.where(live_rows[..., None], final, 0.0).astype(jnp.bfloat16)
    output_gradient = jnp.where(live_rows[..., None], cotangent.astype(jnp.float32), 0.0)
    g_low = output_gradient.astype(jnp.bfloat16)
    gu_alone = lax.optimization_barrier(gu_proj)
    gate_alone = gu_alone[..., :ff_width]
    hidden_alone = (gate_alone * jax.nn.sigmoid(gate_alone) * gu_alone[..., ff_width:]).astype(
        jnp.bfloat16
    )
    grad_down = jnp.einsum(
        "srf,srd->fd", hidden_alone, g_low, preferred_element_type=jnp.float32
    )
    (part_down,) = scatter_blocks(
        [grad_down.reshape(n_group, -1, model_width).astype(jnp.bfloat16)], True
    )
    g_hidden = jnp.einsum("srd,fd->srf", g_low, full_down, preferred_element_type=jnp.float32)
    gate_gradient = (g_hidden * up_proj * sigmoid_gate * (1.0 + gate_proj * (1.0 - sigmoid_gate))).astype(jnp.bfloat16)
    up_gradient = (g_hidden * gate_proj * sigmoid_gate).astype(jnp.bfloat16)
    gu_gradient = jnp.concatenate([gate_gradient, up_gradient], axis=-1)
    grad_gu = jnp.einsum(
        "srd,srf->df", mlp_low, gu_gradient, preferred_element_type=jnp.float32
    )
    g_normed_mlp = jnp.einsum(
        "srf,df->srd", gu_gradient, full_gu, preferred_element_type=jnp.float32
    )
    g_mlp_in, grad_gain_mlp = normalize_back(residual, inv_mlp, mlp_scale, g_normed_mlp)
    g_residual = output_gradient + g_mlp_in
    g_branch = g_residual.astype(jnp.bfloat16)
    grad_out = jnp.einsum(
        "sre,srd->ed", att_flat, g_branch, preferred_element_type=jnp.float32
    )
    gu_block = grad_gu.reshape(n_group, own_rows, 2 * ff_width).astype(jnp.bfloat16)
    g_attended = (
        jnp.einsum("srd,ed->sre", g_branch, full_out, preferred_element_type=jnp.float32)
        .astype(jnp.bfloat16)
        .reshape(head_shape)
    )
    (part_gu,) = scatter_blocks([gu_block], True, 2)
    row_dots = jnp.sum(g_attended.astype(jnp.float32) * attended.astype(jnp.float32), axis=-1)
    if paired:
        dot_rows = jnp.transpose(row_dots, (0, 2, 1))
        later_g, later_dots, later_lse = lax.ppermute(
            (g_attended, dot_rows, lse_rows), "ctx", [(1, 0)]
        )
        g_queries, g_keys, g_values = block_backward(
            queries, keys, values, g_attended, lse_rows, dot_rows, q_pos, q_pos, lengths
        )
        later = ctx_index == 1
        pick = lambda mine, theirs: jnp.where(later, mine, theirs)
        x_dq, x_dk, x_dv = block_backward(
            pick(queries, other_q),
            pick(other_k, keys),
            pick(other_v, values),
            pick(g_attended, later_g),
            pick(lse_rows, later_lse),
            pick(dot_rows, later_dots),
            pick(q_pos, other_pos),
            pick(other_pos, q_pos),
            lengths,
        )
        g_queries = g_queries + jnp.where(later, x_dq, 0.0)
        g_keys = g_keys + jnp.where(later, 0.0, x_dk)
        g_values = g_values + jnp.where(later, 0.0, x_dv)
    else:
        g_queries, slot_dk, slot_dv = attend_backward(
            queries, slot_k, slot_v, g_attended, row_dots, attn_lse, q_pos, k_pos, lengths
        )
        g_keys, g_values = (
            lax.psum_scatter(
                slot_dk.astype(jnp.bfloat16), "ctx", scatter_dimension=1, tiled=True
            ).astype(jnp.float32),
            lax.psum_scatter(
                slot_dv.astype(jnp.bfloat16), "ctx", scatter_dimension=1, tiled=True
            ).astype(jnp.float32),
        )
    flat_shape = (n_slots, slot_rows, model_width)
    gq_low = rotate(g_queries, q_pos, -1.0).reshape(flat_shape).astype(jnp.bfloat16)
    gk_low = rotate(g_keys, q_pos, -1.0).reshape(flat_shape).astype(jnp.bfloat16)
    gv_rounded = g_values.reshape(flat_shape).astype(jnp.bfloat16).astype(jnp.float32)
    d_first = 0.5 * gv_rounded
    gv_half = d_first.astype(jnp.bfloat16)
    g_qkv = jnp.concatenate([gq_low, gk_low, gv_half], axis=-1)
    grad_qkv = jnp.einsum("srd,sre->de", normed_low, g_qkv, preferred_element_type=jnp.float32)
    g_normed = jnp.einsum("sre,de->srd", g_qkv, full_qkv, preferred_element_type=jnp.float32)
    g_attn_in, grad_gain_attn = normalize_back(inputs, inv_attn, attn_scale, g_normed)
    d_tokens = g_residual + g_attn_in
    part_qkvo, part_gains = scatter_blocks(
        [
            jnp.concatenate([grad_qkv, grad_out], axis=1).reshape(
                n_group, own_rows, qkv_width + model_width
            ),
            gain_block(
                grad_gain_attn.reshape(n_group, own_rows),
                grad_gain_mlp.reshape(n_group, own_rows),
                qkv_width + model_width,
            ),
        ],
        False,
    )
    part_qkv = part_qkvo[:, :qkv_width]
    return (
        output,
        d_tokens,
        d_first,
        part_qkv[:, :attn_width],
        part_qkv[:, attn_width : 2 * attn_width],
        part_qkv[:, 2 * attn_width :],
        part_qkvo[:, qkv_width:],
        part_gu[:, :ff_width],
        part_gu[:, ff_width:],
        part_down,
        part_gains[0, :own_rows],
        part_gains[0, own_rows : 2 * own_rows],
    )


def solution(mesh):
    in_specs = (
        P(("rep", "fsdp"), "ctx", None),
        P(("rep", "fsdp"), "ctx", None),
        P(("rep", "fsdp"), "ctx", None),
        P(("rep", "fsdp")),
        P(("fsdp", "ctx"), None),
        P(("fsdp", "ctx"), None),
        P(("fsdp", "ctx"), None),
        P(("fsdp", "ctx"), None),
        P(("fsdp", "ctx"), None),
        P(("fsdp", "ctx"), None),
        P(("fsdp", "ctx"), None),
        P(("fsdp", "ctx")),
        P(("fsdp", "ctx")),
    )
    out_specs = (
        P(("rep", "fsdp"), "ctx", None),
        P(("rep", "fsdp"), "ctx", None),
        P(("rep", "fsdp"), "ctx", None),
        P(("fsdp", "ctx"), None),
        P(("fsdp", "ctx"), None),
        P(("fsdp", "ctx"), None),
        P(("fsdp", "ctx"), None),
        P(("fsdp", "ctx"), None),
        P(("fsdp", "ctx"), None),
        P(("fsdp", "ctx"), None),
        P(("fsdp", "ctx")),
        P(("fsdp", "ctx")),
    )

    return jax.shard_map(shards, mesh=mesh, in_specs=in_specs, out_specs=out_specs, check_vma=False)
```

```python
import functools

import jax
import jax.numpy as jnp
from jax import lax
from jax.experimental import pallas as pl
from jax.experimental.pallas import tpu as pltpu
from jax.sharding import PartitionSpec as P


HEADS = 16
HEAD_DIM = 64


EPS = 1e-06
NEG = -1e30
THETA = 10000.0
SCORE_CAP = 4194304


def rotate(field, positions, direction):
    head_width = field.shape[-1]
    half_width = head_width // 2
    frequency = THETA ** (-(jnp.arange(half_width, dtype=jnp.float32) * 2.0) / head_width)
    angles = positions.astype(jnp.float32)[:, None] * frequency[None, :]
    cosine = jnp.cos(angles)[:, None, :]
    sine_part = direction * jnp.sin(angles)[:, None, :]
    former = field[..., :half_width]
    latter = field[..., half_width:]
    return jnp.concatenate(
        [former * cosine - latter * sine_part, latter * cosine + former * sine_part], axis=-1
    )


def normalize(values, gain):
    inverse = lax.rsqrt(jnp.mean(values * values, axis=-1, keepdims=True) + EPS)
    return (values * inverse * gain, inverse)


def normalize_back(values, inverse, gain, upstream):
    unit_rows = values * inverse
    scaled = upstream * gain
    grad_gain = jnp.sum(upstream * unit_rows, axis=(0, 1))
    grad_values = inverse * (
        scaled - unit_rows * jnp.mean(scaled * unit_rows, axis=-1, keepdims=True)
    )
    return (grad_values, grad_gain)


def head_groups(n_slots, q_len, n_heads, k_len):
    q_block = min(q_len, 512)
    per_group = max(1, min(n_heads, SCORE_CAP // (n_slots * q_block * k_len)))
    while n_heads % per_group:
        per_group = per_group - 1
    return (q_block, per_group)


def split_heads(packed, n_groups):
    n_slots, length, n_heads, head_width = packed.shape
    return jnp.moveaxis(
        packed.reshape(n_slots, length, n_groups, n_heads // n_groups, head_width), 2, 0
    )


def join_heads(grouped):
    n_groups, n_slots, length, per_group, head_width = grouped.shape
    return jnp.moveaxis(grouped, 0, 2).reshape(n_slots, length, n_groups * per_group, head_width)


def score_block(q_rows, k_rows, q_pos, k_pos, lengths):
    products = jnp.einsum(
        "sqhe,skhe->shqk", q_rows, k_rows, preferred_element_type=jnp.float32
    ) * q_rows.shape[-1] ** (-0.5)
    causal = (k_pos[None, None, None, :] <= q_pos[None, None, :, None]) & (
        k_pos[None, None, None, :] >= 0
    )
    filled = k_pos[None, None, None, :] < lengths[:, None, None, None]
    return jnp.where(causal & filled, products, NEG)


def attend_forward(queries, keys, values, q_pos, k_pos, lengths):
    n_slots, q_len, n_heads, head_width = queries.shape
    q_block, per_group = head_groups(n_slots, q_len, n_heads, keys.shape[1])
    n_groups = n_heads // per_group
    n_blocks = q_len // q_block
    pos_blocks = q_pos.reshape(n_blocks, q_block)

    def one_group(packed):
        q_group, k_group, v_group = packed
        q_blocks = jnp.moveaxis(
            q_group.reshape(n_slots, n_blocks, q_block, per_group, head_width), 1, 0
        )

        def one_block(streams):
            q_rows, pos_rows = streams
            scores = score_block(q_rows, k_group, pos_rows, k_pos, lengths)
            highest = jnp.max(scores, axis=-1, keepdims=True)
            exponent = jnp.exp(scores - highest)
            totals = jnp.sum(exponent, axis=-1, keepdims=True)
            probabilities = (exponent / totals).astype(jnp.bfloat16)
            mixture = jnp.einsum(
                "shqk,skhe->sqhe", probabilities, v_group, preferred_element_type=jnp.float32
            )
            return (mixture, (highest + jnp.log(totals))[..., 0])

        mixture, log_sums = lax.map(one_block, (q_blocks, pos_blocks))
        return (
            jnp.moveaxis(mixture, 0, 1).reshape(n_slots, q_len, per_group, head_width),
            log_sums,
        )

    grouped = (
        split_heads(queries, n_groups),
        split_heads(keys, n_groups),
        split_heads(values, n_groups),
    )
    mixture, log_sums = lax.map(one_group, grouped)
    return (join_heads(mixture), log_sums)


def attend_backward(queries, keys, values, upstream, row_dots, log_sums, q_pos, k_pos, lengths):
    n_slots, q_len, n_heads, head_width = queries.shape
    q_block, per_group = head_groups(n_slots, q_len, n_heads, keys.shape[1])
    n_groups = n_heads // per_group
    n_blocks = q_len // q_block
    score_scale = head_width ** (-0.5)
    pos_blocks = q_pos.reshape(n_blocks, q_block)
    dot_groups = jnp.moveaxis(row_dots.reshape(n_slots, q_len, n_groups, per_group), 2, 0)

    def blocks_of(grouped):
        return jnp.moveaxis(grouped.reshape((n_slots, n_blocks, q_block) + grouped.shape[2:]), 1, 0)

    def one_group(packed):
        q_group, k_group, v_group, g_group, d_group, l_group = packed

        def one_block(running, streams):
            k_grad, v_grad = running
            q_rows, g_rows, d_rows, l_rows, pos_rows = streams
            scores = score_block(q_rows, k_group, pos_rows, k_pos, lengths)
            probabilities = jnp.exp(scores - l_rows[..., None])
            v_grad = v_grad + jnp.einsum(
                "shqk,sqhe->skhe",
                probabilities.astype(jnp.bfloat16),
                g_rows,
                preferred_element_type=jnp.float32,
            )
            p_grad = jnp.einsum(
                "sqhe,skhe->shqk", g_rows, v_group, preferred_element_type=jnp.float32
            )
            s_grad = (probabilities * (p_grad - jnp.moveaxis(d_rows, 2, 1)[..., None])).astype(
                jnp.bfloat16
            )
            q_grad = (
                jnp.einsum("shqk,skhe->sqhe", s_grad, k_group, preferred_element_type=jnp.float32)
                * score_scale
            )
            k_grad = (
                k_grad
                + jnp.einsum("shqk,sqhe->skhe", s_grad, q_rows, preferred_element_type=jnp.float32)
                * score_scale
            )
            return ((k_grad, v_grad), q_grad)

        empty_grads = jnp.zeros(k_group.shape, jnp.float32)
        streams = (blocks_of(q_group), blocks_of(g_group), blocks_of(d_group), l_group, pos_blocks)
        (k_grad, v_grad), q_grads = lax.scan(one_block, (empty_grads, empty_grads), streams)
        return (
            jnp.moveaxis(q_grads, 0, 1).reshape(n_slots, q_len, per_group, head_width),
            k_grad,
            v_grad,
        )

    grouped = (
        split_heads(queries, n_groups),
        split_heads(keys, n_groups),
        split_heads(values, n_groups),
        split_heads(upstream, n_groups),
        dot_groups,
        log_sums,
    )
    q_grads, k_grads, v_grads = lax.map(one_group, grouped)
    return (join_heads(q_grads), join_heads(k_grads), join_heads(v_grads))


FAR = 1 << 30


def _block_backward_kernel(q_ref, k_ref, v_ref, g_ref, lse_ref, dots_ref, qpos_ref, kpos_ref,
                           dq_ref, dk_ref, dv_ref, *, head_width, scale):
    pair = pl.program_id(1)
    allowed = kpos_ref[0] <= qpos_ref[...]
    for j in range(2):
        cols = slice(j * head_width, (j + 1) * head_width)
        q = q_ref[0, :, cols]
        k = k_ref[0, :, cols]
        v = v_ref[0, :, cols]
        g = g_ref[0, :, cols]
        head = 2 * pair + j
        lse = lse_ref[0, pl.ds(head, 1), :]
        dots = dots_ref[0, pl.ds(head, 1), :]
        nt = (((1,), (1,)), ((), ()))
        scores = lax.dot_general(k, q, nt, preferred_element_type=jnp.float32) * scale
        scores = jnp.where(allowed, scores, -1e30)
        probs = jnp.exp(scores - lse)
        dv_ref[0, :, cols] = jnp.dot(probs.astype(jnp.bfloat16), g, preferred_element_type=jnp.float32)
        dprobs = lax.dot_general(v, g, nt, preferred_element_type=jnp.float32)
        dscores = (probs * (dprobs - dots)).astype(jnp.bfloat16)
        dk_ref[0, :, cols] = jnp.dot(dscores, q, preferred_element_type=jnp.float32) * scale
        tn = (((0,), (0,)), ((), ()))
        dq_ref[0, :, cols] = lax.dot_general(dscores, k, tn, preferred_element_type=jnp.float32) * scale


def _block_forward_kernel(q_ref, k_ref, v_ref, qpos_ref, kpos_ref, out_ref, lse_ref, *, head_width, scale):
    pair = pl.program_id(1)
    allowed = kpos_ref[0] <= qpos_ref[...]
    nt = (((1,), (1,)), ((), ()))
    tn = (((0,), (0,)), ((), ()))
    for j in range(2):
        cols = slice(j * head_width, (j + 1) * head_width)
        q = q_ref[0, :, cols]
        k = k_ref[0, :, cols]
        v = v_ref[0, :, cols]
        scores = lax.dot_general(k, q, nt, preferred_element_type=jnp.float32) * scale
        scores = jnp.where(allowed, scores, -1e30)
        highest = jnp.max(scores, axis=0, keepdims=True)
        exponent = jnp.exp(scores - highest)
        totals = jnp.sum(exponent, axis=0, keepdims=True)
        probs = (exponent / totals).astype(jnp.bfloat16)
        mixture = lax.dot_general(probs, v, tn, preferred_element_type=jnp.float32)
        out_ref[0, :, cols] = mixture.astype(out_ref.dtype)
        lse_ref[0, pl.ds(2 * pair + j, 1), :] = highest + jnp.log(totals)


def block_forward(queries, keys, values, q_pos, k_pos, lengths):
    n_slots, q_len, n_heads, head_width = queries.shape
    k_len = keys.shape[1]
    width = n_heads * head_width
    pair_width = 2 * head_width
    flat = lambda a: a.reshape(a.shape[0], a.shape[1], width)
    kpos = jnp.where(
        (k_pos[None, :] < lengths[:, None]) & (k_pos[None, :] >= 0), k_pos[None, :], FAR
    ).astype(jnp.int32)[..., None]
    qpos = q_pos.astype(jnp.int32)[None, :]
    kernel = functools.partial(_block_forward_kernel, head_width=head_width, scale=head_width ** (-0.5))
    q_spec = pl.BlockSpec((1, q_len, pair_width), lambda s, p: (s, 0, p))
    k_spec = pl.BlockSpec((1, k_len, pair_width), lambda s, p: (s, 0, p))
    out, lse = pl.pallas_call(
        kernel,
        grid=(n_slots, n_heads // 2),
        in_specs=[
            q_spec, k_spec, k_spec,
            pl.BlockSpec((1, q_len), lambda s, p: (0, 0)),
            pl.BlockSpec((1, k_len, 1), lambda s, p: (s, 0, 0)),
        ],
        out_specs=[q_spec, pl.BlockSpec((1, n_heads, q_len), lambda s, p: (s, 0, 0))],
        out_shape=[
            jax.ShapeDtypeStruct((n_slots, q_len, width), jnp.bfloat16),
            jax.ShapeDtypeStruct((n_slots, n_heads, q_len), jnp.float32),
        ],
        compiler_params=pltpu.CompilerParams(dimension_semantics=("arbitrary", "arbitrary")),
        cost_estimate=pl.CostEstimate(
            flops=n_slots * n_heads * 4 * q_len * k_len * head_width,
            transcendentals=n_slots * n_heads * q_len * k_len,
            bytes_accessed=2 * (2 * q_len + 2 * k_len) * width * n_slots,
        ),
    )(flat(queries), flat(keys), flat(values), qpos, kpos)
    return out.reshape(n_slots, q_len, n_heads, head_width), lse


def block_backward(queries, keys, values, upstream, lse_rows, dot_rows, q_pos, k_pos, lengths):
    n_slots, q_len, n_heads, head_width = queries.shape
    k_len = keys.shape[1]
    width = n_heads * head_width
    pair_width = 2 * head_width
    flat = lambda a: a.reshape(a.shape[0], a.shape[1], width)
    kpos = jnp.where(
        (k_pos[None, :] < lengths[:, None]) & (k_pos[None, :] >= 0), k_pos[None, :], FAR
    ).astype(jnp.int32)[..., None]
    qpos = q_pos.astype(jnp.int32)[None, :]
    kernel = functools.partial(_block_backward_kernel, head_width=head_width, scale=head_width ** (-0.5))
    q_spec = pl.BlockSpec((1, q_len, pair_width), lambda s, p: (s, 0, p))
    k_spec = pl.BlockSpec((1, k_len, pair_width), lambda s, p: (s, 0, p))
    row_spec = pl.BlockSpec((1, n_heads, q_len), lambda s, p: (s, 0, 0))
    flops = n_slots * n_heads * 10 * q_len * k_len * head_width
    dq, dk, dv = pl.pallas_call(
        kernel,
        grid=(n_slots, n_heads // 2),
        in_specs=[
            q_spec, k_spec, k_spec, q_spec, row_spec, row_spec,
            pl.BlockSpec((1, q_len), lambda s, p: (0, 0)),
            pl.BlockSpec((1, k_len, 1), lambda s, p: (s, 0, 0)),
        ],
        out_specs=[q_spec, k_spec, k_spec],
        out_shape=[
            jax.ShapeDtypeStruct((n_slots, q_len, width), jnp.float32),
            jax.ShapeDtypeStruct((n_slots, k_len, width), jnp.float32),
            jax.ShapeDtypeStruct((n_slots, k_len, width), jnp.float32),
        ],
        cost_estimate=pl.CostEstimate(
            flops=flops,
            transcendentals=n_slots * n_heads * q_len * k_len,
            bytes_accessed=2 * (2 * q_len + 2 * k_len) * width * n_slots + 4 * (q_len + 2 * k_len) * width * n_slots,
        ),
    )(flat(queries), flat(keys), flat(values), flat(upstream), lse_rows, dot_rows, qpos, kpos)
    shape_q = (n_slots, q_len, n_heads, head_width)
    shape_k = (n_slots, k_len, n_heads, head_width)
    return dq.reshape(shape_q), dk.reshape(shape_k), dv.reshape(shape_k)


GROUP = ("fsdp", "ctx")


def gather_blocks(pieces):
    packed = jnp.concatenate(pieces, axis=0)
    gathered = lax.all_gather(packed, GROUP, axis=0, tiled=False)
    fulls, offset = [], 0
    for piece in pieces:
        fulls.append(gathered[:, offset : offset + piece.shape[0], :])
        offset += piece.shape[0]
    return fulls


def rep_chain(x):
    me = lax.axis_index("rep")
    arrived = lax.ppermute(x, "rep", [(0, 1), (3, 2)])
    folded = (x.astype(jnp.float32) + arrived.astype(jnp.float32)).astype(x.dtype)
    arrived = lax.ppermute(folded, "rep", [(1, 2), (2, 1)])
    total = (folded.astype(jnp.float32) + arrived.astype(jnp.float32)).astype(x.dtype)
    sent_out = lax.ppermute(total, "rep", [(1, 0), (2, 3)])
    return jnp.where((me == 0) | (me == 3), sent_out, total)


def rep_sum(x, pieces=1):
    if lax.axis_size("rep") != 4:
        return lax.psum(x, "rep")
    rows = x.shape[1]
    if pieces == 1 or rows % (8 * pieces):
        return rep_chain(x)
    step = rows // pieces
    parts = []
    for i in range(pieces):
        parts.append(rep_chain(x[:, i * step : (i + 1) * step]))
    return jnp.concatenate(parts, axis=1)


def scatter_blocks(blocks, by_permutes, pieces=1):
    packed = jnp.concatenate(blocks, axis=1).astype(jnp.bfloat16)
    summed = lax.psum_scatter(packed, GROUP, scatter_dimension=0, tiled=True)
    summed = (rep_sum(summed, pieces) if by_permutes else lax.psum(summed, "rep"))[0].astype(
        jnp.float32
    )
    parts, offset = [], 0
    for block in blocks:
        parts.append(summed[offset : offset + block.shape[1], :])
        offset += block.shape[1]
    return parts


def gain_block(first, second, width):
    lead = first.shape[:-1]
    row = jnp.concatenate([first, second], axis=-1)
    row = jnp.pad(row, [(0, 0)] * len(lead) + [(0, width - row.shape[-1])])
    return jnp.pad(row[..., None, :], [(0, 0)] * len(lead) + [(0, 7), (0, 0)])


def shards(
    tokens,
    initial_layer_values,
    cotangent,
    lengths,
    w_query,
    w_key,
    w_value,
    w_out,
    w_gate,
    w_up,
    w_down,
    gain_attn,
    gain_mlp,
):
    n_slots, slot_rows, model_width = tokens.shape
    n_ctx = lax.axis_size("ctx")
    n_group = lax.axis_size("fsdp") * n_ctx
    own_rows = gain_attn.shape[0]
    ff_width = w_gate.shape[1]
    attn_width = w_query.shape[1]
    qkv_width = 3 * attn_width
    qkvo_width = qkv_width + model_width
    (qkvo_blocks, gain_rows, down_wide) = gather_blocks(
        [
            jnp.concatenate([w_query, w_key, w_value, w_out], axis=1),
            gain_block(gain_attn, gain_mlp, qkvo_width),
            w_down.reshape(-1, qkvo_width),
        ]
    )
    full_down = down_wide.reshape(-1, model_width)
    full_qkvo = qkvo_blocks.reshape(n_group * own_rows, qkvo_width)
    full_qkv = full_qkvo[:, :qkv_width]
    full_out = full_qkvo[:, qkv_width:]
    full_gain_attn = gain_rows[:, 0, :own_rows].reshape(-1)
    full_gain_mlp = gain_rows[:, 0, own_rows : 2 * own_rows].reshape(-1)
    (gu_blocks,) = gather_blocks([jnp.concatenate([w_gate, w_up], axis=1)])
    full_gu = gu_blocks.reshape(n_group * own_rows, 2 * ff_width)
    ctx_index = lax.axis_index("ctx")
    q_pos = ctx_index * slot_rows + jnp.arange(slot_rows)
    live_rows = q_pos[None, :] < lengths[:, None]
    head_shape = (n_slots, slot_rows, HEADS, HEAD_DIM)
    paired = n_ctx == 2
    if paired:
        other_tokens = lax.ppermute(tokens, "ctx", [(0, 1), (1, 0)])
        other_first = lax.ppermute(initial_layer_values, "ctx", [(0, 1)])
        other_pos = (1 - ctx_index) * slot_rows + jnp.arange(slot_rows)
    inputs = tokens.astype(jnp.float32)
    attn_scale = full_gain_attn.astype(jnp.float32)
    mlp_scale = full_gain_mlp.astype(jnp.float32)

    def project(chunk_tokens, chunk_first, chunk_pos):
        chunk_normed, chunk_inv = normalize(chunk_tokens.astype(jnp.float32), attn_scale)
        chunk_low = chunk_normed.astype(jnp.bfloat16)
        qkv_pre = jnp.einsum(
            "srd,de->sre", chunk_low, full_qkv, preferred_element_type=jnp.float32
        )
        q_pre = qkv_pre[..., :attn_width]
        k_pre = qkv_pre[..., attn_width : 2 * attn_width]
        v_pre = qkv_pre[..., 2 * attn_width :]
        chunk_q = rotate(q_pre.reshape(head_shape), chunk_pos, 1.0).astype(jnp.bfloat16)
        chunk_k = rotate(k_pre.reshape(head_shape), chunk_pos, 1.0).astype(jnp.bfloat16)
        chunk_v = (
            (0.5 * v_pre + 0.5 * chunk_first.astype(jnp.float32))
            .astype(jnp.bfloat16)
            .reshape(head_shape)
        )
        return chunk_low, chunk_inv, chunk_q, chunk_k, chunk_v

    normed_low, inv_attn, queries, keys, values = project(tokens, initial_layer_values, q_pos)
    if paired:
        _, _, other_q, other_k, other_v = project(other_tokens, other_first, other_pos)
        slot_k = jnp.concatenate([other_k, keys], axis=1)
        slot_v = jnp.concatenate([other_v, values], axis=1)
        k_pos = jnp.concatenate([other_pos, q_pos])
    else:
        slot_k, slot_v = (
            lax.all_gather(keys, "ctx", axis=1, tiled=True),
            lax.all_gather(values, "ctx", axis=1, tiled=True),
        )
        k_pos = jnp.arange(n_ctx * slot_rows)
    if paired:
        attended, lse_rows = block_forward(queries, slot_k, slot_v, q_pos, k_pos, lengths)
    else:
        attn_raw, attn_lse = attend_forward(queries, slot_k, slot_v, q_pos, k_pos, lengths)
        attended = attn_raw.astype(jnp.bfloat16)
    att_flat = attended.reshape(n_slots, slot_rows, model_width)
    branch = jnp.einsum("sre,ed->srd", att_flat, full_out, preferred_element_type=jnp.float32)
    residual = inputs + branch
    normed_mlp, inv_mlp = normalize(residual, mlp_scale)
    mlp_low = normed_mlp.astype(jnp.bfloat16)
    gu_proj = jnp.einsum("srd,df->srf", mlp_low, full_gu, preferred_element_type=jnp.float32)
    gate_proj = gu_proj[..., :ff_width]
    up_proj = gu_proj[..., ff_width:]
    sigmoid_gate = jax.nn.sigmoid(gate_proj)
    hidden = (gate_proj * sigmoid_gate * up_proj).astype(jnp.bfloat16)
    final = residual + jnp.einsum(
        "srf,fd->srd", hidden, full_down, preferred_element_type=jnp.float32
    )
    output = jnp.where(live_rows[..., None], final, 0.0).astype(jnp.bfloat16)
    output_gradient = jnp.where(live_rows[..., None], cotangent.astype(jnp.float32), 0.0)
    g_low = output_gradient.astype(jnp.bfloat16)
    gu_alone = lax.optimization_barrier(gu_proj)
    gate_alone = gu_alone[..., :ff_width]
    hidden_alone = (gate_alone * jax.nn.sigmoid(gate_alone) * gu_alone[..., ff_width:]).astype(
        jnp.bfloat16
    )
    grad_down = jnp.einsum(
        "srf,srd->fd", hidden_alone, g_low, preferred_element_type=jnp.float32
    )
    (part_down,) = scatter_blocks(
        [grad_down.reshape(n_group, -1, model_width).astype(jnp.bfloat16)], True
    )
    g_hidden = jnp.einsum("srd,fd->srf", g_low, full_down, preferred_element_type=jnp.float32)
    gate_gradient = (g_hidden * up_proj * sigmoid_gate * (1.0 + gate_proj * (1.0 - sigmoid_gate))).astype(jnp.bfloat16)
    up_gradient = (g_hidden * gate_proj * sigmoid_gate).astype(jnp.bfloat16)
    gu_gradient = jnp.concatenate([gate_gradient, up_gradient], axis=-1)
    grad_gu = jnp.einsum(
        "srd,srf->df", mlp_low, gu_gradient, preferred_element_type=jnp.float32
    )
    g_normed_mlp = jnp.einsum(
        "srf,df->srd", gu_gradient, full_gu, preferred_element_type=jnp.float32
    )
    g_mlp_in, grad_gain_mlp = normalize_back(residual, inv_mlp, mlp_scale, g_normed_mlp)
    g_residual = output_gradient + g_mlp_in
    g_branch = g_residual.astype(jnp.bfloat16)
    grad_out = jnp.einsum(
        "sre,srd->ed", att_flat, g_branch, preferred_element_type=jnp.float32
    )
    gu_block = grad_gu.reshape(n_group, own_rows, 2 * ff_width).astype(jnp.bfloat16)
    g_attended = (
        jnp.einsum("srd,ed->sre", g_branch, full_out, preferred_element_type=jnp.float32)
        .astype(jnp.bfloat16)
        .reshape(head_shape)
    )
    (part_gu,) = scatter_blocks([gu_block], True, 2)
    row_dots = jnp.sum(g_attended.astype(jnp.float32) * attended.astype(jnp.float32), axis=-1)
    if paired:
        dot_rows = jnp.transpose(row_dots, (0, 2, 1))
        later_g, later_dots, later_lse = lax.ppermute(
            (g_attended, dot_rows, lse_rows), "ctx", [(1, 0)]
        )
        g_queries, g_keys, g_values = block_backward(
            queries, keys, values, g_attended, lse_rows, dot_rows, q_pos, q_pos, lengths
        )
        later = ctx_index == 1
        pick = lambda mine, theirs: jnp.where(later, mine, theirs)
        x_dq, x_dk, x_dv = block_backward(
            pick(queries, other_q),
            pick(other_k, keys),
            pick(other_v, values),
            pick(g_attended, later_g),
            pick(lse_rows, later_lse),
            pick(dot_rows, later_dots),
            pick(q_pos, other_pos),
            pick(other_pos, q_pos),
            lengths,
        )
        g_queries = g_queries + jnp.where(later, x_dq, 0.0)
        g_keys = g_keys + jnp.where(later, 0.0, x_dk)
        g_values = g_values + jnp.where(later, 0.0, x_dv)
    else:
        g_queries, slot_dk, slot_dv = attend_backward(
            queries, slot_k, slot_v, g_attended, row_dots, attn_lse, q_pos, k_pos, lengths
        )
        g_keys, g_values = (
            lax.psum_scatter(
                slot_dk.astype(jnp.bfloat16), "ctx", scatter_dimension=1, tiled=True
            ).astype(jnp.float32),
            lax.psum_scatter(
                slot_dv.astype(jnp.bfloat16), "ctx", scatter_dimension=1, tiled=True
            ).astype(jnp.float32),
        )
    flat_shape = (n_slots, slot_rows, model_width)
    gq_low = rotate(g_queries, q_pos, -1.0).reshape(flat_shape).astype(jnp.bfloat16)
    gk_low = rotate(g_keys, q_pos, -1.0).reshape(flat_shape).astype(jnp.bfloat16)
    gv_rounded = g_values.reshape(flat_shape).astype(jnp.bfloat16).astype(jnp.float32)
    d_first = 0.5 * gv_rounded
    gv_half = d_first.astype(jnp.bfloat16)
    g_qkv = jnp.concatenate([gq_low, gk_low, gv_half], axis=-1)
    grad_qkv = jnp.einsum("srd,sre->de", normed_low, g_qkv, preferred_element_type=jnp.float32)
    g_normed = jnp.einsum("sre,de->srd", g_qkv, full_qkv, preferred_element_type=jnp.float32)
    g_attn_in, grad_gain_attn = normalize_back(inputs, inv_attn, attn_scale, g_normed)
    d_tokens = g_residual + g_attn_in
    part_qkvo, part_gains = scatter_blocks(
        [
            jnp.concatenate([grad_qkv, grad_out], axis=1).reshape(
                n_group, own_rows, qkv_width + model_width
            ),
            gain_block(
                grad_gain_attn.reshape(n_group, own_rows),
                grad_gain_mlp.reshape(n_group, own_rows),
                qkv_width + model_width,
            ),
        ],
        False,
    )
    part_qkv = part_qkvo[:, :qkv_width]
    return (
        output,
        d_tokens,
        d_first,
        part_qkv[:, :attn_width],
        part_qkv[:, attn_width : 2 * attn_width],
        part_qkv[:, 2 * attn_width :],
        part_qkvo[:, qkv_width:],
        part_gu[:, :ff_width],
        part_gu[:, ff_width:],
        part_down,
        part_gains[0, :own_rows],
        part_gains[0, own_rows : 2 * own_rows],
    )


def solution(mesh):
    in_specs = (
        P(("rep", "fsdp"), "ctx", None),
        P(("rep", "fsdp"), "ctx", None),
        P(("rep", "fsdp"), "ctx", None),
        P(("rep", "fsdp")),
        P(("fsdp", "ctx"), None),
        P(("fsdp", "ctx"), None),
        P(("fsdp", "ctx"), None),
        P(("fsdp", "ctx"), None),
        P(("fsdp", "ctx"), None),
        P(("fsdp", "ctx"), None),
        P(("fsdp", "ctx"), None),
        P(("fsdp", "ctx")),
        P(("fsdp", "ctx")),
    )
    out_specs = (
        P(("rep", "fsdp"), "ctx", None),
        P(("rep", "fsdp"), "ctx", None),
        P(("rep", "fsdp"), "ctx", None),
        P(("fsdp", "ctx"), None),
        P(("fsdp", "ctx"), None),
        P(("fsdp", "ctx"), None),
        P(("fsdp", "ctx"), None),
        P(("fsdp", "ctx"), None),
        P(("fsdp", "ctx"), None),
        P(("fsdp", "ctx"), None),
        P(("fsdp", "ctx")),
        P(("fsdp", "ctx")),
    )

    return jax.shard_map(shards, mesh=mesh, in_specs=in_specs, out_specs=out_specs, check_vma=False)
```

```python
import functools

import jax
import jax.numpy as jnp
from jax import lax
from jax.experimental import pallas as pl
from jax.experimental.pallas import tpu as pltpu
from jax.sharding import PartitionSpec as P


HEADS = 16
HEAD_DIM = 64


EPS = 1e-06
NEG = -1e30
THETA = 10000.0
SCORE_CAP = 4194304


def rotate(field, positions, direction):
    head_width = field.shape[-1]
    half_width = head_width // 2
    frequency = THETA ** (-(jnp.arange(half_width, dtype=jnp.float32) * 2.0) / head_width)
    angles = positions.astype(jnp.float32)[:, None] * frequency[None, :]
    cosine = jnp.cos(angles)[:, None, :]
    sine_part = direction * jnp.sin(angles)[:, None, :]
    former = field[..., :half_width]
    latter = field[..., half_width:]
    return jnp.concatenate(
        [former * cosine - latter * sine_part, latter * cosine + former * sine_part], axis=-1
    )


def normalize(values, gain):
    inverse = lax.rsqrt(jnp.mean(values * values, axis=-1, keepdims=True) + EPS)
    return (values * inverse * gain, inverse)


def normalize_back(values, inverse, gain, upstream):
    unit_rows = values * inverse
    scaled = upstream * gain
    grad_gain = jnp.sum(upstream * unit_rows, axis=(0, 1))
    grad_values = inverse * (
        scaled - unit_rows * jnp.mean(scaled * unit_rows, axis=-1, keepdims=True)
    )
    return (grad_values, grad_gain)


def head_groups(n_slots, q_len, n_heads, k_len):
    q_block = min(q_len, 512)
    per_group = max(1, min(n_heads, SCORE_CAP // (n_slots * q_block * k_len)))
    while n_heads % per_group:
        per_group = per_group - 1
    return (q_block, per_group)


def split_heads(packed, n_groups):
    n_slots, length, n_heads, head_width = packed.shape
    return jnp.moveaxis(
        packed.reshape(n_slots, length, n_groups, n_heads // n_groups, head_width), 2, 0
    )


def join_heads(grouped):
    n_groups, n_slots, length, per_group, head_width = grouped.shape
    return jnp.moveaxis(grouped, 0, 2).reshape(n_slots, length, n_groups * per_group, head_width)


def score_block(q_rows, k_rows, q_pos, k_pos, lengths):
    products = jnp.einsum(
        "sqhe,skhe->shqk", q_rows, k_rows, preferred_element_type=jnp.float32
    ) * q_rows.shape[-1] ** (-0.5)
    causal = (k_pos[None, None, None, :] <= q_pos[None, None, :, None]) & (
        k_pos[None, None, None, :] >= 0
    )
    filled = k_pos[None, None, None, :] < lengths[:, None, None, None]
    return jnp.where(causal & filled, products, NEG)


def attend_forward(queries, keys, values, q_pos, k_pos, lengths):
    n_slots, q_len, n_heads, head_width = queries.shape
    q_block, per_group = head_groups(n_slots, q_len, n_heads, keys.shape[1])
    n_groups = n_heads // per_group
    n_blocks = q_len // q_block
    pos_blocks = q_pos.reshape(n_blocks, q_block)

    def one_group(packed):
        q_group, k_group, v_group = packed
        q_blocks = jnp.moveaxis(
            q_group.reshape(n_slots, n_blocks, q_block, per_group, head_width), 1, 0
        )

        def one_block(streams):
            q_rows, pos_rows = streams
            scores = score_block(q_rows, k_group, pos_rows, k_pos, lengths)
            highest = jnp.max(scores, axis=-1, keepdims=True)
            exponent = jnp.exp(scores - highest)
            totals = jnp.sum(exponent, axis=-1, keepdims=True)
            probabilities = (exponent / totals).astype(jnp.bfloat16)
            mixture = jnp.einsum(
                "shqk,skhe->sqhe", probabilities, v_group, preferred_element_type=jnp.float32
            )
            return (mixture, (highest + jnp.log(totals))[..., 0])

        mixture, log_sums = lax.map(one_block, (q_blocks, pos_blocks))
        return (
            jnp.moveaxis(mixture, 0, 1).reshape(n_slots, q_len, per_group, head_width),
            log_sums,
        )

    grouped = (
        split_heads(queries, n_groups),
        split_heads(keys, n_groups),
        split_heads(values, n_groups),
    )
    mixture, log_sums = lax.map(one_group, grouped)
    return (join_heads(mixture), log_sums)


def attend_backward(queries, keys, values, upstream, row_dots, log_sums, q_pos, k_pos, lengths):
    n_slots, q_len, n_heads, head_width = queries.shape
    q_block, per_group = head_groups(n_slots, q_len, n_heads, keys.shape[1])
    n_groups = n_heads // per_group
    n_blocks = q_len // q_block
    score_scale = head_width ** (-0.5)
    pos_blocks = q_pos.reshape(n_blocks, q_block)
    dot_groups = jnp.moveaxis(row_dots.reshape(n_slots, q_len, n_groups, per_group), 2, 0)

    def blocks_of(grouped):
        return jnp.moveaxis(grouped.reshape((n_slots, n_blocks, q_block) + grouped.shape[2:]), 1, 0)

    def one_group(packed):
        q_group, k_group, v_group, g_group, d_group, l_group = packed

        def one_block(running, streams):
            k_grad, v_grad = running
            q_rows, g_rows, d_rows, l_rows, pos_rows = streams
            scores = score_block(q_rows, k_group, pos_rows, k_pos, lengths)
            probabilities = jnp.exp(scores - l_rows[..., None])
            v_grad = v_grad + jnp.einsum(
                "shqk,sqhe->skhe",
                probabilities.astype(jnp.bfloat16),
                g_rows,
                preferred_element_type=jnp.float32,
            )
            p_grad = jnp.einsum(
                "sqhe,skhe->shqk", g_rows, v_group, preferred_element_type=jnp.float32
            )
            s_grad = (probabilities * (p_grad - jnp.moveaxis(d_rows, 2, 1)[..., None])).astype(
                jnp.bfloat16
            )
            q_grad = (
                jnp.einsum("shqk,skhe->sqhe", s_grad, k_group, preferred_element_type=jnp.float32)
                * score_scale
            )
            k_grad = (
                k_grad
                + jnp.einsum("shqk,sqhe->skhe", s_grad, q_rows, preferred_element_type=jnp.float32)
                * score_scale
            )
            return ((k_grad, v_grad), q_grad)

        empty_grads = jnp.zeros(k_group.shape, jnp.float32)
        streams = (blocks_of(q_group), blocks_of(g_group), blocks_of(d_group), l_group, pos_blocks)
        (k_grad, v_grad), q_grads = lax.scan(one_block, (empty_grads, empty_grads), streams)
        return (
            jnp.moveaxis(q_grads, 0, 1).reshape(n_slots, q_len, per_group, head_width),
            k_grad,
            v_grad,
        )

    grouped = (
        split_heads(queries, n_groups),
        split_heads(keys, n_groups),
        split_heads(values, n_groups),
        split_heads(upstream, n_groups),
        dot_groups,
        log_sums,
    )
    q_grads, k_grads, v_grads = lax.map(one_group, grouped)
    return (join_heads(q_grads), join_heads(k_grads), join_heads(v_grads))


FAR = 1 << 30


def _block_backward_kernel(q_ref, k_ref, v_ref, g_ref, lse_ref, dots_ref, qpos_ref, kpos_ref,
                           dq_ref, dk_ref, dv_ref, *, head_width, scale):
    pair = pl.program_id(1)
    allowed = kpos_ref[0] <= qpos_ref[...]
    for j in range(2):
        cols = slice(j * head_width, (j + 1) * head_width)
        q = q_ref[0, :, cols]
        k = k_ref[0, :, cols]
        v = v_ref[0, :, cols]
        g = g_ref[0, :, cols]
        head = 2 * pair + j
        lse = lse_ref[0, pl.ds(head, 1), :]
        dots = dots_ref[0, pl.ds(head, 1), :]
        nt = (((1,), (1,)), ((), ()))
        scores = lax.dot_general(k, q, nt, preferred_element_type=jnp.float32) * scale
        scores = jnp.where(allowed, scores, -1e30)
        probs = jnp.exp(scores - lse)
        dv_ref[0, :, cols] = jnp.dot(probs.astype(jnp.bfloat16), g, preferred_element_type=jnp.float32)
        dprobs = lax.dot_general(v, g, nt, preferred_element_type=jnp.float32)
        dscores = (probs * (dprobs - dots)).astype(jnp.bfloat16)
        dk_ref[0, :, cols] = jnp.dot(dscores, q, preferred_element_type=jnp.float32) * scale
        tn = (((0,), (0,)), ((), ()))
        dq_ref[0, :, cols] = lax.dot_general(dscores, k, tn, preferred_element_type=jnp.float32) * scale


def _block_forward_kernel(q_ref, k_ref, v_ref, qpos_ref, kpos_ref, out_ref, lse_ref, *, head_width, scale):
    pair = pl.program_id(1)
    allowed = kpos_ref[0] <= qpos_ref[...]
    nt = (((1,), (1,)), ((), ()))
    tn = (((0,), (0,)), ((), ()))
    for j in range(2):
        cols = slice(j * head_width, (j + 1) * head_width)
        q = q_ref[0, :, cols]
        k = k_ref[0, :, cols]
        v = v_ref[0, :, cols]
        scores = lax.dot_general(k, q, nt, preferred_element_type=jnp.float32) * scale
        scores = jnp.where(allowed, scores, -1e30)
        highest = jnp.max(scores, axis=0, keepdims=True)
        exponent = jnp.exp(scores - highest)
        totals = jnp.sum(exponent, axis=0, keepdims=True)
        probs = (exponent / totals).astype(jnp.bfloat16)
        mixture = lax.dot_general(probs, v, tn, preferred_element_type=jnp.float32)
        out_ref[0, :, cols] = mixture.astype(out_ref.dtype)
        lse_ref[0, pl.ds(2 * pair + j, 1), :] = highest + jnp.log(totals)


def block_forward(queries, keys, values, q_pos, k_pos, lengths):
    n_slots, q_len, n_heads, head_width = queries.shape
    k_len = keys.shape[1]
    width = n_heads * head_width
    pair_width = 2 * head_width
    flat = lambda a: a.reshape(a.shape[0], a.shape[1], width)
    kpos = jnp.where(
        (k_pos[None, :] < lengths[:, None]) & (k_pos[None, :] >= 0), k_pos[None, :], FAR
    ).astype(jnp.int32)[..., None]
    qpos = q_pos.astype(jnp.int32)[None, :]
    kernel = functools.partial(_block_forward_kernel, head_width=head_width, scale=head_width ** (-0.5))
    q_spec = pl.BlockSpec((1, q_len, pair_width), lambda s, p: (s, 0, p))
    k_spec = pl.BlockSpec((1, k_len, pair_width), lambda s, p: (s, 0, p))
    out, lse = pl.pallas_call(
        kernel,
        grid=(n_slots, n_heads // 2),
        in_specs=[
            q_spec, k_spec, k_spec,
            pl.BlockSpec((1, q_len), lambda s, p: (0, 0)),
            pl.BlockSpec((1, k_len, 1), lambda s, p: (s, 0, 0)),
        ],
        out_specs=[q_spec, pl.BlockSpec((1, n_heads, q_len), lambda s, p: (s, 0, 0))],
        out_shape=[
            jax.ShapeDtypeStruct((n_slots, q_len, width), jnp.bfloat16),
            jax.ShapeDtypeStruct((n_slots, n_heads, q_len), jnp.float32),
        ],
        compiler_params=pltpu.CompilerParams(dimension_semantics=("arbitrary", "arbitrary")),
        cost_estimate=pl.CostEstimate(
            flops=n_slots * n_heads * 4 * q_len * k_len * head_width,
            transcendentals=n_slots * n_heads * q_len * k_len,
            bytes_accessed=2 * (2 * q_len + 2 * k_len) * width * n_slots,
        ),
    )(flat(queries), flat(keys), flat(values), qpos, kpos)
    return out.reshape(n_slots, q_len, n_heads, head_width), lse


def block_backward(queries, keys, values, upstream, lse_rows, dot_rows, q_pos, k_pos, lengths):
    n_slots, q_len, n_heads, head_width = queries.shape
    k_len = keys.shape[1]
    width = n_heads * head_width
    pair_width = 2 * head_width
    flat = lambda a: a.reshape(a.shape[0], a.shape[1], width)
    kpos = jnp.where(
        (k_pos[None, :] < lengths[:, None]) & (k_pos[None, :] >= 0), k_pos[None, :], FAR
    ).astype(jnp.int32)[..., None]
    qpos = q_pos.astype(jnp.int32)[None, :]
    kernel = functools.partial(_block_backward_kernel, head_width=head_width, scale=head_width ** (-0.5))
    q_spec = pl.BlockSpec((1, q_len, pair_width), lambda s, p: (s, 0, p))
    k_spec = pl.BlockSpec((1, k_len, pair_width), lambda s, p: (s, 0, p))
    row_spec = pl.BlockSpec((1, n_heads, q_len), lambda s, p: (s, 0, 0))
    flops = n_slots * n_heads * 10 * q_len * k_len * head_width
    dq, dk, dv = pl.pallas_call(
        kernel,
        grid=(n_slots, n_heads // 2),
        in_specs=[
            q_spec, k_spec, k_spec, q_spec, row_spec, row_spec,
            pl.BlockSpec((1, q_len), lambda s, p: (0, 0)),
            pl.BlockSpec((1, k_len, 1), lambda s, p: (s, 0, 0)),
        ],
        out_specs=[q_spec, k_spec, k_spec],
        out_shape=[
            jax.ShapeDtypeStruct((n_slots, q_len, width), jnp.float32),
            jax.ShapeDtypeStruct((n_slots, k_len, width), jnp.float32),
            jax.ShapeDtypeStruct((n_slots, k_len, width), jnp.float32),
        ],
        cost_estimate=pl.CostEstimate(
            flops=flops,
            transcendentals=n_slots * n_heads * q_len * k_len,
            bytes_accessed=2 * (2 * q_len + 2 * k_len) * width * n_slots + 4 * (q_len + 2 * k_len) * width * n_slots,
        ),
    )(flat(queries), flat(keys), flat(values), flat(upstream), lse_rows, dot_rows, qpos, kpos)
    shape_q = (n_slots, q_len, n_heads, head_width)
    shape_k = (n_slots, k_len, n_heads, head_width)
    return dq.reshape(shape_q), dk.reshape(shape_k), dv.reshape(shape_k)


GROUP = ("fsdp", "ctx")


def gather_blocks(pieces):
    packed = jnp.concatenate(pieces, axis=0)
    gathered = lax.all_gather(packed, GROUP, axis=0, tiled=False)
    fulls, offset = [], 0
    for piece in pieces:
        fulls.append(gathered[:, offset : offset + piece.shape[0], :])
        offset += piece.shape[0]
    return fulls


def rep_chain(x):
    me = lax.axis_index("rep")
    arrived = lax.ppermute(x, "rep", [(0, 1), (3, 2)])
    folded = (x.astype(jnp.float32) + arrived.astype(jnp.float32)).astype(x.dtype)
    arrived = lax.ppermute(folded, "rep", [(1, 2), (2, 1)])
    total = (folded.astype(jnp.float32) + arrived.astype(jnp.float32)).astype(x.dtype)
    sent_out = lax.ppermute(total, "rep", [(1, 0), (2, 3)])
    return jnp.where((me == 0) | (me == 3), sent_out, total)


def rep_sum(x, pieces=1):
    if lax.axis_size("rep") != 4:
        return lax.psum(x, "rep")
    rows = x.shape[1]
    if pieces == 1 or rows % (8 * pieces):
        return rep_chain(x)
    step = rows // pieces
    parts = []
    for i in range(pieces):
        parts.append(rep_chain(x[:, i * step : (i + 1) * step]))
    return jnp.concatenate(parts, axis=1)


def scatter_blocks(blocks, by_permutes, pieces=1):
    packed = jnp.concatenate(blocks, axis=1).astype(jnp.bfloat16)
    summed = lax.psum_scatter(packed, GROUP, scatter_dimension=0, tiled=True)
    summed = (rep_sum(summed, pieces) if by_permutes else lax.psum(summed, "rep"))[0].astype(
        jnp.float32
    )
    parts, offset = [], 0
    for block in blocks:
        parts.append(summed[offset : offset + block.shape[1], :])
        offset += block.shape[1]
    return parts


def gain_block(first, second, width):
    lead = first.shape[:-1]
    row = jnp.concatenate([first, second], axis=-1)
    row = jnp.pad(row, [(0, 0)] * len(lead) + [(0, width - row.shape[-1])])
    return jnp.pad(row[..., None, :], [(0, 0)] * len(lead) + [(0, 7), (0, 0)])


def shards(
    tokens,
    initial_layer_values,
    cotangent,
    lengths,
    w_query,
    w_key,
    w_value,
    w_out,
    w_gate,
    w_up,
    w_down,
    gain_attn,
    gain_mlp,
):
    n_slots, slot_rows, model_width = tokens.shape
    n_ctx = lax.axis_size("ctx")
    n_group = lax.axis_size("fsdp") * n_ctx
    own_rows = gain_attn.shape[0]
    ff_width = w_gate.shape[1]
    attn_width = w_query.shape[1]
    qkv_width = 3 * attn_width
    qkvo_width = qkv_width + model_width
    (qkvo_blocks, gain_rows) = gather_blocks(
        [
            jnp.concatenate([w_query, w_key, w_value, w_out], axis=1),
            gain_block(gain_attn, gain_mlp, qkvo_width),
        ]
    )
    full_qkvo = qkvo_blocks.reshape(n_group * own_rows, qkvo_width)
    full_qkv = full_qkvo[:, :qkv_width]
    full_out = full_qkvo[:, qkv_width:]
    full_gain_attn = gain_rows[:, 0, :own_rows].reshape(-1)
    full_gain_mlp = gain_rows[:, 0, own_rows : 2 * own_rows].reshape(-1)
    (gu_blocks,) = gather_blocks([jnp.concatenate([w_gate, w_up], axis=1)])
    full_gu = gu_blocks.reshape(n_group * own_rows, 2 * ff_width)
    (down_blocks,) = gather_blocks([w_down])
    full_down = down_blocks.reshape(-1, model_width)
    ctx_index = lax.axis_index("ctx")
    q_pos = ctx_index * slot_rows + jnp.arange(slot_rows)
    live_rows = q_pos[None, :] < lengths[:, None]
    head_shape = (n_slots, slot_rows, HEADS, HEAD_DIM)
    paired = n_ctx == 2
    if paired:
        earlier_tokens = lax.ppermute(tokens, "ctx", [(0, 1)])
        later_tokens = lax.ppermute(tokens, "ctx", [(1, 0)])
        other_first = lax.ppermute(initial_layer_values, "ctx", [(0, 1)])
        other_pos = (1 - ctx_index) * slot_rows + jnp.arange(slot_rows)
    inputs = tokens.astype(jnp.float32)
    attn_scale = full_gain_attn.astype(jnp.float32)
    mlp_scale = full_gain_mlp.astype(jnp.float32)

    def project(chunk_tokens, chunk_first, chunk_pos):
        chunk_normed, chunk_inv = normalize(chunk_tokens.astype(jnp.float32), attn_scale)
        chunk_low = chunk_normed.astype(jnp.bfloat16)
        qkv_pre = jnp.einsum(
            "srd,de->sre", chunk_low, full_qkv, preferred_element_type=jnp.float32
        )
        q_pre = qkv_pre[..., :attn_width]
        k_pre = qkv_pre[..., attn_width : 2 * attn_width]
        v_pre = qkv_pre[..., 2 * attn_width :]
        chunk_q = rotate(q_pre.reshape(head_shape), chunk_pos, 1.0).astype(jnp.bfloat16)
        chunk_k = rotate(k_pre.reshape(head_shape), chunk_pos, 1.0).astype(jnp.bfloat16)
        chunk_v = (
            (0.5 * v_pre + 0.5 * chunk_first.astype(jnp.float32))
            .astype(jnp.bfloat16)
            .reshape(head_shape)
        )
        return chunk_low, chunk_inv, chunk_q, chunk_k, chunk_v

    normed_low, inv_attn, queries, keys, values = project(tokens, initial_layer_values, q_pos)
    if paired:
        _, _, _, other_k, other_v = project(earlier_tokens, other_first, other_pos)
        _, _, other_q, _, _ = project(later_tokens, other_first, other_pos)
        slot_k = jnp.concatenate([other_k, keys], axis=1)
        slot_v = jnp.concatenate([other_v, values], axis=1)
        k_pos = jnp.concatenate([other_pos, q_pos])
    else:
        slot_k, slot_v = (
            lax.all_gather(keys, "ctx", axis=1, tiled=True),
            lax.all_gather(values, "ctx", axis=1, tiled=True),
        )
        k_pos = jnp.arange(n_ctx * slot_rows)
    if paired:
        attended, lse_rows = block_forward(queries, slot_k, slot_v, q_pos, k_pos, lengths)
    else:
        attn_raw, attn_lse = attend_forward(queries, slot_k, slot_v, q_pos, k_pos, lengths)
        attended = attn_raw.astype(jnp.bfloat16)
    att_flat = attended.reshape(n_slots, slot_rows, model_width)
    branch = jnp.einsum("sre,ed->srd", att_flat, full_out, preferred_element_type=jnp.float32)
    residual = inputs + branch
    normed_mlp, inv_mlp = normalize(residual, mlp_scale)
    mlp_low = normed_mlp.astype(jnp.bfloat16)
    gu_proj = jnp.einsum("srd,df->srf", mlp_low, full_gu, preferred_element_type=jnp.float32)
    gate_proj = gu_proj[..., :ff_width]
    up_proj = gu_proj[..., ff_width:]
    sigmoid_gate = jax.nn.sigmoid(gate_proj)
    hidden = (gate_proj * sigmoid_gate * up_proj).astype(jnp.bfloat16)
    final = residual + jnp.einsum(
        "srf,fd->srd", hidden, full_down, preferred_element_type=jnp.float32
    )
    output = jnp.where(live_rows[..., None], final, 0.0).astype(jnp.bfloat16)
    output_gradient = jnp.where(live_rows[..., None], cotangent.astype(jnp.float32), 0.0)
    g_low = output_gradient.astype(jnp.bfloat16)
    gu_alone = lax.optimization_barrier(gu_proj)
    gate_alone = gu_alone[..., :ff_width]
    hidden_alone = (gate_alone * jax.nn.sigmoid(gate_alone) * gu_alone[..., ff_width:]).astype(
        jnp.bfloat16
    )
    grad_down = jnp.einsum(
        "srf,srd->fd", hidden_alone, g_low, preferred_element_type=jnp.float32
    )
    (part_down,) = scatter_blocks(
        [grad_down.reshape(n_group, -1, model_width).astype(jnp.bfloat16)], True
    )
    g_hidden = jnp.einsum("srd,fd->srf", g_low, full_down, preferred_element_type=jnp.float32)
    gate_gradient = (g_hidden * up_proj * sigmoid_gate * (1.0 + gate_proj * (1.0 - sigmoid_gate))).astype(jnp.bfloat16)
    up_gradient = (g_hidden * gate_proj * sigmoid_gate).astype(jnp.bfloat16)
    gu_gradient = jnp.concatenate([gate_gradient, up_gradient], axis=-1)
    grad_gu = jnp.einsum(
        "srd,srf->df", mlp_low, gu_gradient, preferred_element_type=jnp.float32
    )
    g_normed_mlp = jnp.einsum(
        "srf,df->srd", gu_gradient, full_gu, preferred_element_type=jnp.float32
    )
    g_mlp_in, grad_gain_mlp = normalize_back(residual, inv_mlp, mlp_scale, g_normed_mlp)
    g_residual = output_gradient + g_mlp_in
    g_branch = g_residual.astype(jnp.bfloat16)
    grad_out = jnp.einsum(
        "sre,srd->ed", att_flat, g_branch, preferred_element_type=jnp.float32
    )
    gu_block = grad_gu.reshape(n_group, own_rows, 2 * ff_width).astype(jnp.bfloat16)
    g_attended = (
        jnp.einsum("srd,ed->sre", g_branch, full_out, preferred_element_type=jnp.float32)
        .astype(jnp.bfloat16)
        .reshape(head_shape)
    )
    (part_gu,) = scatter_blocks([gu_block], True, 2)
    row_dots = jnp.sum(g_attended.astype(jnp.float32) * attended.astype(jnp.float32), axis=-1)
    if paired:
        dot_rows = jnp.transpose(row_dots, (0, 2, 1))
        later_g, later_dots, later_lse = lax.ppermute(
            (g_attended, dot_rows, lse_rows), "ctx", [(1, 0)]
        )
        g_queries, g_keys, g_values = block_backward(
            queries, keys, values, g_attended, lse_rows, dot_rows, q_pos, q_pos, lengths
        )
        later = ctx_index == 1
        pick = lambda mine, theirs: jnp.where(later, mine, theirs)
        x_dq, x_dk, x_dv = block_backward(
            pick(queries, other_q),
            pick(other_k, keys),
            pick(other_v, values),
            pick(g_attended, later_g),
            pick(lse_rows, later_lse),
            pick(dot_rows, later_dots),
            pick(q_pos, other_pos),
            pick(other_pos, q_pos),
            lengths,
        )
        g_queries = g_queries + jnp.where(later, x_dq, 0.0)
        g_keys = g_keys + jnp.where(later, 0.0, x_dk)
        g_values = g_values + jnp.where(later, 0.0, x_dv)
    else:
        g_queries, slot_dk, slot_dv = attend_backward(
            queries, slot_k, slot_v, g_attended, row_dots, attn_lse, q_pos, k_pos, lengths
        )
        g_keys, g_values = (
            lax.psum_scatter(
                slot_dk.astype(jnp.bfloat16), "ctx", scatter_dimension=1, tiled=True
            ).astype(jnp.float32),
            lax.psum_scatter(
                slot_dv.astype(jnp.bfloat16), "ctx", scatter_dimension=1, tiled=True
            ).astype(jnp.float32),
        )
    flat_shape = (n_slots, slot_rows, model_width)
    gq_low = rotate(g_queries, q_pos, -1.0).reshape(flat_shape).astype(jnp.bfloat16)
    gk_low = rotate(g_keys, q_pos, -1.0).reshape(flat_shape).astype(jnp.bfloat16)
    gv_rounded = g_values.reshape(flat_shape).astype(jnp.bfloat16).astype(jnp.float32)
    d_first = 0.5 * gv_rounded
    gv_half = d_first.astype(jnp.bfloat16)
    g_qkv = jnp.concatenate([gq_low, gk_low, gv_half], axis=-1)
    grad_qkv = jnp.einsum("srd,sre->de", normed_low, g_qkv, preferred_element_type=jnp.float32)
    g_normed = jnp.einsum("sre,de->srd", g_qkv, full_qkv, preferred_element_type=jnp.float32)
    g_attn_in, grad_gain_attn = normalize_back(inputs, inv_attn, attn_scale, g_normed)
    d_tokens = g_residual + g_attn_in
    part_qkvo, part_gains = scatter_blocks(
        [
            jnp.concatenate([grad_qkv, grad_out], axis=1).reshape(
                n_group, own_rows, qkv_width + model_width
            ),
            gain_block(
                grad_gain_attn.reshape(n_group, own_rows),
                grad_gain_mlp.reshape(n_group, own_rows),
                qkv_width + model_width,
            ),
        ],
        False,
    )
    part_qkv = part_qkvo[:, :qkv_width]
    return (
        output,
        d_tokens,
        d_first,
        part_qkv[:, :attn_width],
        part_qkv[:, attn_width : 2 * attn_width],
        part_qkv[:, 2 * attn_width :],
        part_qkvo[:, qkv_width:],
        part_gu[:, :ff_width],
        part_gu[:, ff_width:],
        part_down,
        part_gains[0, :own_rows],
        part_gains[0, own_rows : 2 * own_rows],
    )


def solution(mesh):
    in_specs = (
        P(("rep", "fsdp"), "ctx", None),
        P(("rep", "fsdp"), "ctx", None),
        P(("rep", "fsdp"), "ctx", None),
        P(("rep", "fsdp")),
        P(("fsdp", "ctx"), None),
        P(("fsdp", "ctx"), None),
        P(("fsdp", "ctx"), None),
        P(("fsdp", "ctx"), None),
        P(("fsdp", "ctx"), None),
        P(("fsdp", "ctx"), None),
        P(("fsdp", "ctx"), None),
        P(("fsdp", "ctx")),
        P(("fsdp", "ctx")),
    )
    out_specs = (
        P(("rep", "fsdp"), "ctx", None),
        P(("rep", "fsdp"), "ctx", None),
        P(("rep", "fsdp"), "ctx", None),
        P(("fsdp", "ctx"), None),
        P(("fsdp", "ctx"), None),
        P(("fsdp", "ctx"), None),
        P(("fsdp", "ctx"), None),
        P(("fsdp", "ctx"), None),
        P(("fsdp", "ctx"), None),
        P(("fsdp", "ctx"), None),
        P(("fsdp", "ctx")),
        P(("fsdp", "ctx")),
    )

    return jax.shard_map(shards, mesh=mesh, in_specs=in_specs, out_specs=out_specs, check_vma=False)
```
